32 devices in a mesh: row: 2 (over core), col: 2 (over x), seq: 8 (over z, y).
Axes of the slice: x: 2, y: 2, z: 4, core: 2. Of those that a mesh axis runs over, the one named last changes fastest.
Arguments:
- states: bfloat16 [128, 4, 5120], P('col', None, 'row'), may hold values from -64 to 64
- norm_gain: float32 [5120], P('row'), may hold values from 0.1 to 1.9
- wq: bfloat16 [5120, 4096], P('row', 'col'), may hold values from -0.078125 to 0.078125
- wk: bfloat16 [5120, 1024], P('row', 'col'), may hold values from -0.21875 to 0.21875
- wv: bfloat16 [5120, 1024], P('row', 'col'), may hold values from -0.078125 to 0.078125
- wo: bfloat16 [4096, 5120], P('col', 'row'), may hold values from -0.09375 to 0.09375
- lengths: int32 [128], P('row'), may hold values from 1 to 8192, as said below
- slot_request: int32 [800], P(('row', 'seq')), may hold values from 0 to 64, as said below
- slot_block_number: int32 [800], P(('row', 'seq')), may hold values from 0 to 63, as said below
- paged_key_cache: bfloat16 [800, 128, 1024], P(('row', 'seq'), None, 'col'), may hold values from -120 to 120
- paged_value_cache: bfloat16 [800, 128, 1024], P(('row', 'seq'), None, 'col'), may hold values from -6 to 6
Outputs:
- attended: bfloat16 [128, 4, 5120], P('col', None, 'row')
- new_keys: bfloat16 [128, 4, 1024], P('row', None, 'col')
- new_values: bfloat16 [128, 4, 1024], P('row', None, 'col')
The draws below stay inside these ranges and needn't reach their ends.
Inputs may be any that keep to these rules, and one draw needn't show every extreme that they name: `lengths`: within every 64 consecutive requests, 8 have exactly 8192 cached tokens and the others fewer than 128. `slot_request`: each request's block 0 and every block that holds a position visible to one of its steps stand in exactly one slot of its index of row; a long request has exactly 33 slots. 64 marks an empty slot; every index of row has empty slots. `slot_block_number`: 0 in empty slots.
All inputs are finite; a program needn't handle non-finite values.
Results may differ from the reference program's by a relative error of at most 0.034.
Values may be sent and summed in bfloat16 or wider, within the bound.
No kernel may reach another device: no remote copies, remote signals or barrier semaphores. Data moves between devices by JAX's collectives and lax.ppermute only.
A program may use at most 192 MiB of HBM per device.

```python
import math
import jax
import jax.numpy as jnp
from jax import lax

D = 5120
QUERY_HEADS = 32
KEY_HEADS = 8
HEAD_SIZE = 128
ROW_REQUESTS = 64
DECODE_COUNT = 4
LONGLEN = 8192
WINDOW = 4096
SINK = 4
BLOCK_POSITIONS = 128
QUERY_PER_KEY = 4
QUERY_FEATURES = 4096
KEY_FEATURES = 1024
REQUEST_COUNT = 128
LONGR = 8
LB = 33
NB = 320
ROW_SLOT_COUNT = 400
POOL = 800
N_ROW = 2
N_COL = 2


def request_tables(key):
    base_key = jax.random.fold_in(key, 11)
    low_block = max(1, (LONGLEN - WINDOW + 1) // BLOCK_POSITIONS)
    steps_in = jnp.arange(LB, dtype=jnp.int32)
    block_ids = jnp.where(steps_in == 0, 0, low_block + steps_in - 1).astype(jnp.int32)

    def single_row_group(group_idx):
        group_key = jax.random.fold_in(base_key, group_idx)
        rank_key, short_key, place_key = jax.random.split(group_key, 3)
        ranking = jax.random.permutation(rank_key, ROW_REQUESTS)
        is_long = ranking < LONGR
        short_len = jax.random.randint(short_key, (ROW_REQUESTS,), 1, BLOCK_POSITIONS, dtype=jnp.int32)
        length = jnp.where(is_long, LONGLEN, short_len).astype(jnp.int32)
        needed = jnp.where(is_long, LB, 1)
        usable = (steps_in[None, :] < needed[:, None]).reshape(-1)
        owners = jnp.repeat(jnp.arange(ROW_REQUESTS, dtype=jnp.int32), LB)
        blocks = jnp.tile(block_ids, ROW_REQUESTS)
        ordering = jnp.argsort(jnp.where(usable, 0, 1).astype(jnp.int32), stable=True)[:NB]
        placing = jax.random.permutation(place_key, ROW_SLOT_COUNT)[:NB]
        owner_of = jnp.full((ROW_SLOT_COUNT,), ROW_REQUESTS, jnp.int32).at[placing].set(owners[ordering])
        block_of = jnp.zeros((ROW_SLOT_COUNT,), jnp.int32).at[placing].set(blocks[ordering])
        return (length, owner_of, block_of)
    length, owner_of, block_of = jax.vmap(single_row_group)(jnp.arange(REQUEST_COUNT // ROW_REQUESTS, dtype=jnp.int32))
    return (length.reshape(-1), owner_of.reshape(-1), block_of.reshape(-1))


def draw_lengths(key, part):
    return request_tables(key)[0]


def draw_slot_request(key, part):
    return request_tables(key)[1]


def draw_slot_block_number(key, part):
    return request_tables(key)[2]


def draw_states(key, part):
    noise_key = jax.random.fold_in(jax.random.fold_in(key, 3), 0)
    columns = jnp.arange(D, dtype=jnp.float32) / D
    values = jnp.clip(jax.random.normal(noise_key, (REQUEST_COUNT, DECODE_COUNT, D), jnp.float32), -6.0, 6.0)
    return (values * jnp.exp(columns * 1.0986123)).astype(jnp.bfloat16)


def draw_paged_key_cache(key, part):
    noise_key = jax.random.fold_in(jax.random.fold_in(key, 5), 0)
    shape_all = (POOL, BLOCK_POSITIONS, KEY_FEATURES)
    return jnp.clip(jax.random.normal(noise_key, shape_all, jnp.float32) * 2.5, -12.0, 12.0).astype(jnp.bfloat16)


def block_scale(key, dims, cuts, low, largest):
    loudness, own = 1.0, jax.random.fold_in(key, 6)
    for dim, parts in cuts:
        draws = jnp.exp(jax.random.uniform(jax.random.fold_in(own, dim), (parts,), jnp.float32, low / len(cuts), largest / len(cuts)))
        loudness = loudness * jnp.repeat(draws, dims[dim] // parts).reshape([-1 if axis == dim else 1 for axis in range(len(dims))])
    return loudness


def bell_draw(rng, extent, scale, reach, cuts=(), held_as=jnp.bfloat16):
    result = jax.random.normal(rng, extent, jnp.float32) * scale
    if len(cuts) > 0:
        result = block_scale(rng, extent, cuts, -0.22, 0.18) * result
    return jnp.clip(result, min=-reach, max=reach).astype(held_as)


def setup_inputs(seed: int = 0) -> dict:
    key_of = jax.random.split(jax.random.key(seed), 12)
    return {
        "states": draw_states(jax.random.fold_in(key_of[11], 71), 0),
        "norm_gain": jnp.clip(1.0 + 0.18 * jax.random.normal(key_of[1], (D,), jnp.float32), 0.1, 1.9),
        "wq": bell_draw(key_of[2], (D, QUERY_FEATURES), D ** -0.5, 0.078125, ((0, 2), (1, 2))),
        "wk": bell_draw(key_of[3], (D, KEY_FEATURES), (D // 6) ** -0.5, 0.21875, ((0, 2), (1, 2))),
        "wv": bell_draw(key_of[4], (D, KEY_FEATURES), D ** -0.5, 0.078125, ((0, 2), (1, 2))),
        "wo": bell_draw(key_of[5], (QUERY_FEATURES, D), QUERY_FEATURES ** -0.5, 0.09375, ((0, 2), (1, 2))),
        "lengths": draw_lengths(jax.random.fold_in(key_of[11], 71), 0),
        "slot_request": draw_slot_request(jax.random.fold_in(key_of[11], 71), 0),
        "slot_block_number": draw_slot_block_number(jax.random.fold_in(key_of[11], 71), 0),
        "paged_key_cache": draw_paged_key_cache(jax.random.fold_in(key_of[11], 71), 0),
        "paged_value_cache": bell_draw(key_of[10], (POOL, BLOCK_POSITIONS, KEY_FEATURES), 1.0, 6.0, ((0, 16), (2, 2))),
    }


EPSILON = 1e-05
NEGATIVE_FILL = -1e+30
ROPE_BASE = 100000000.0

def rotary_apply(values, token_positions):
    half_dim = values.shape[-1] // 2
    frequency = ROPE_BASE ** (-(jnp.arange(half_dim, dtype=jnp.float32) * 2.0 / values.shape[-1]))
    angles = (token_positions.astype(jnp.float32)[..., None] * frequency)[..., None, :]
    cosine = jnp.cos(angles)
    sine_part = jnp.sin(angles)
    lower = values[..., :half_dim]
    upper = values[..., half_dim:]
    return jnp.concatenate([lower * cosine - upper * sine_part, upper * cosine + lower * sine_part], -1)

def slot_parts(query_rows, lengths, slot_request, slot_block_number, key_rows, value_rows, offset):
    req_count = query_rows.shape[0]
    step_count = query_rows.shape[1]
    block_len = key_rows.shape[1]
    picked = jnp.minimum(slot_request, req_count - 1)
    in_use = slot_request < req_count
    slot_queries = query_rows[picked]
    scores = jnp.einsum('nsagh,nbah->nasgb', slot_queries.astype(jnp.float32), key_rows.astype(jnp.float32)) * (1.0 / math.sqrt(HEAD_SIZE))
    key_pos = slot_block_number[:, None] * block_len + jnp.arange(block_len, dtype=jnp.int32)[None, :]
    own_len = lengths[picked]
    query_pos = own_len[:, None] + offset + jnp.arange(step_count, dtype=jnp.int32)[None, :]
    visible = in_use[:, None, None] & (key_pos[:, None, :] < own_len[:, None, None]) & ((key_pos[:, None, :] < SINK) | (key_pos[:, None, :] > query_pos[:, :, None] - WINDOW))
    visible = visible[:, None, :, None, :]
    slot_peak = lax.optimization_barrier(jnp.max(jnp.where(visible, scores, NEGATIVE_FILL), -1))
    weights = jnp.where(visible, jnp.exp(scores - slot_peak[..., None]), 0.0)
    slot_total = lax.optimization_barrier(jnp.sum(weights, -1))
    rounded = lax.optimization_barrier(weights.astype(jnp.bfloat16))
    slot_acc = jnp.einsum('nasgb,nbah->nasgh', rounded.astype(jnp.float32), value_rows.astype(jnp.float32))
    member = slot_request[None, :] == jnp.arange(req_count, dtype=jnp.int32)[:, None]
    local_peak = lax.optimization_barrier(jnp.max(jnp.where(member[:, :, None, None, None], slot_peak[None], NEGATIVE_FILL), 1))
    return (local_peak, (slot_peak, slot_total, slot_acc, member, picked))

def pool_sums(held, running_peak):
    slot_peak, slot_total, slot_acc, member, picked = held
    factor = jnp.exp(slot_peak - running_peak[picked])
    as_member = member.astype(jnp.float32)
    running_totals = jnp.einsum('rn,nasg->rasg', as_member, slot_total * factor, precision=lax.Precision.HIGHEST)
    weighted_values = jnp.einsum('rn,nasgh->rasgh', as_member, slot_acc * factor[..., None], precision=lax.Precision.HIGHEST)
    return (running_totals, weighted_values)

def fresh_part(query_rows, key_all, value_all, offset):
    step_count = query_rows.shape[1]
    used = key_all.shape[1]
    scores = jnp.einsum('rsagh,ruah->rasgu', query_rows.astype(jnp.float32), key_all.astype(jnp.float32)) * (1.0 / math.sqrt(HEAD_SIZE))
    causal = jnp.arange(used, dtype=jnp.int32)[None, :] <= offset + jnp.arange(step_count, dtype=jnp.int32)[:, None]
    causal = causal[None, None, :, None, :]
    running_peak = lax.optimization_barrier(jnp.max(jnp.where(causal, scores, NEGATIVE_FILL), -1))
    weights = jnp.where(causal, jnp.exp(scores - running_peak[..., None]), 0.0)
    running_totals = lax.optimization_barrier(jnp.sum(weights, -1))
    rounded = lax.optimization_barrier(weights.astype(jnp.bfloat16))
    weighted_values = jnp.einsum('rasgu,ruah->rasgh', rounded.astype(jnp.float32), value_all.astype(jnp.float32))
    return (running_peak, running_totals, weighted_values)

def merge_parts(earlier, later):
    running_peak = jnp.maximum(earlier[0], later[0])
    first_factor = jnp.exp(earlier[0] - running_peak)
    second_factor = jnp.exp(later[0] - running_peak)
    running_totals = earlier[1] * first_factor + later[1] * second_factor
    weighted_values = earlier[2] * first_factor[..., None] + later[2] * second_factor[..., None]
    return (running_peak, running_totals, weighted_values)

def reference(states, norm_gain, wq, wk, wv, wo, lengths, slot_request, slot_block_number, paged_key_cache, paged_value_cache):
    as_float = states.astype(jnp.float32)
    squares = lax.optimization_barrier(jnp.sum(as_float * as_float, -1))
    normed = (as_float * lax.rsqrt(squares / D + EPSILON)[..., None] * norm_gain).astype(jnp.bfloat16)
    weights = jnp.concatenate([wq, wk, wv], axis=1)
    row_width = D // N_ROW
    flat_rows = normed.reshape(REQUEST_COUNT * DECODE_COUNT, D)
    output_projected = jnp.zeros((REQUEST_COUNT * DECODE_COUNT, QUERY_FEATURES + 2 * KEY_FEATURES), jnp.float32)
    for shard in range(N_ROW):
        partial_term = jnp.dot(flat_rows[:, shard * row_width:(shard + 1) * row_width], weights[shard * row_width:(shard + 1) * row_width], preferred_element_type=jnp.float32)
        output_projected = output_projected + lax.optimization_barrier(partial_term.astype(jnp.bfloat16)).astype(jnp.float32)
    output_projected = output_projected.reshape(REQUEST_COUNT, DECODE_COUNT, QUERY_FEATURES + 2 * KEY_FEATURES)
    token_positions = lengths[:, None] + jnp.arange(DECODE_COUNT, dtype=jnp.int32)[None, :]
    query_rows = rotary_apply(output_projected[..., :QUERY_FEATURES].reshape(REQUEST_COUNT, DECODE_COUNT, QUERY_HEADS, HEAD_SIZE), token_positions).astype(jnp.bfloat16).reshape(REQUEST_COUNT, DECODE_COUNT, KEY_HEADS, QUERY_PER_KEY, HEAD_SIZE)
    current_key = rotary_apply(output_projected[..., QUERY_FEATURES:QUERY_FEATURES + KEY_FEATURES].reshape(REQUEST_COUNT, DECODE_COUNT, KEY_HEADS, HEAD_SIZE), token_positions).astype(jnp.bfloat16)
    current_value = output_projected[..., QUERY_FEATURES + KEY_FEATURES:].reshape(REQUEST_COUNT, DECODE_COUNT, KEY_HEADS, HEAD_SIZE).astype(jnp.bfloat16)

    def single_row_group(inputs):
        group_q, group_len, group_owner, group_block, group_keys, group_vals = inputs
        running_peak, held = slot_parts(group_q, group_len, group_owner, group_block, group_keys, group_vals, 0)
        running_totals, weighted_values = pool_sums(held, running_peak)
        return (running_peak, running_totals, weighted_values)
    running_peak, running_totals, weighted_values = lax.map(single_row_group, (query_rows.reshape(N_ROW, ROW_REQUESTS, DECODE_COUNT, KEY_HEADS, QUERY_PER_KEY, HEAD_SIZE), lengths.reshape(N_ROW, ROW_REQUESTS), slot_request.reshape(N_ROW, ROW_SLOT_COUNT), slot_block_number.reshape(N_ROW, ROW_SLOT_COUNT), paged_key_cache.reshape(N_ROW, ROW_SLOT_COUNT, BLOCK_POSITIONS, KEY_HEADS, HEAD_SIZE), paged_value_cache.reshape(N_ROW, ROW_SLOT_COUNT, BLOCK_POSITIONS, KEY_HEADS, HEAD_SIZE)))
    running_peak = running_peak.reshape(REQUEST_COUNT, KEY_HEADS, DECODE_COUNT, QUERY_PER_KEY)
    running_totals = running_totals.reshape(REQUEST_COUNT, KEY_HEADS, DECODE_COUNT, QUERY_PER_KEY)
    weighted_values = weighted_values.reshape(REQUEST_COUNT, KEY_HEADS, DECODE_COUNT, QUERY_PER_KEY, HEAD_SIZE)
    fresh = fresh_part(query_rows, current_key, current_value, 0)
    running_peak, running_totals, weighted_values = merge_parts((running_peak, running_totals, weighted_values), fresh)
    heads_out = (weighted_values / running_totals[..., None]).transpose(0, 2, 1, 3, 4).reshape(REQUEST_COUNT * DECODE_COUNT, QUERY_FEATURES).astype(jnp.bfloat16)
    col_width = QUERY_FEATURES // N_COL
    mixed_out = jnp.zeros((REQUEST_COUNT * DECODE_COUNT, D), jnp.float32)
    for shard in range(N_COL):
        partial_term = jnp.dot(heads_out[:, shard * col_width:(shard + 1) * col_width], wo[shard * col_width:(shard + 1) * col_width], preferred_element_type=jnp.float32)
        mixed_out = mixed_out + lax.optimization_barrier(partial_term.astype(jnp.bfloat16)).astype(jnp.float32)
    attended = mixed_out.reshape(REQUEST_COUNT, DECODE_COUNT, D).astype(jnp.bfloat16)
    return (attended, current_key.reshape(REQUEST_COUNT, DECODE_COUNT, KEY_FEATURES), current_value.reshape(REQUEST_COUNT, DECODE_COUNT, KEY_FEATURES))
```

```python
import math

import jax
import jax.numpy as jnp
from jax import lax
from jax.sharding import PartitionSpec as P

D = 5120
HEAD_SIZE = 128
WINDOW = 4096
SINK = 4
QUERY_PER_KEY = 4


EPSILON = 1e-05
NEGATIVE_FILL = -1e30
ROPE_BASE = 100000000.0


def rotary_apply(values, token_positions):
    half_dim = values.shape[-1] // 2
    frequency = ROPE_BASE ** (-(jnp.arange(half_dim, dtype=jnp.float32) * 2.0 / values.shape[-1]))
    angles = (token_positions.astype(jnp.float32)[..., None] * frequency)[..., None, :]
    cosine = jnp.cos(angles)
    sine_part = jnp.sin(angles)
    lower = values[..., :half_dim]
    upper = values[..., half_dim:]
    return jnp.concatenate(
        [lower * cosine - upper * sine_part, upper * cosine + lower * sine_part], -1
    )


def slot_parts(query_rows, lengths, slot_request, slot_block_number, key_rows, value_rows):
    req_count = query_rows.shape[0]
    step_count = query_rows.shape[1]
    block_len = key_rows.shape[1]
    picked = jnp.minimum(slot_request, req_count - 1)
    in_use = slot_request < req_count
    slot_queries = query_rows[picked]
    scores = jnp.einsum(
        "nsagh,nbah->nasgb", slot_queries, key_rows, preferred_element_type=jnp.float32
    ) * (1.0 / math.sqrt(HEAD_SIZE))
    key_pos = (
        slot_block_number[:, None] * block_len + jnp.arange(block_len, dtype=jnp.int32)[None, :]
    )
    own_len = lengths[picked]
    query_pos = own_len[:, None] + jnp.arange(step_count, dtype=jnp.int32)[None, :]
    visible = (
        in_use[:, None, None]
        & (key_pos[:, None, :] < own_len[:, None, None])
        & ((key_pos[:, None, :] < SINK) | (key_pos[:, None, :] > query_pos[:, :, None] - WINDOW))
    )
    visible = visible[:, None, :, None, :]
    slot_peak = jnp.max(jnp.where(visible, scores, NEGATIVE_FILL), -1)
    weights = jnp.where(visible, jnp.exp(scores - slot_peak[..., None]), 0.0)
    slot_total = jnp.sum(weights, -1)
    slot_acc = jnp.einsum(
        "nasgb,nbah->nasgh",
        weights.astype(jnp.bfloat16),
        value_rows,
        preferred_element_type=jnp.float32,
    )
    member = slot_request[None, :] == jnp.arange(req_count, dtype=jnp.int32)[:, None]
    local_peak = jnp.max(
        jnp.where(member[:, :, None, None, None], slot_peak[None], NEGATIVE_FILL), 1
    )
    return (local_peak, (slot_peak, slot_total, slot_acc, member, picked))


def pool_sums(held, running_peak):
    slot_peak, slot_total, slot_acc, member, picked = held
    factor = jnp.exp(slot_peak - running_peak[picked])
    as_member = member.astype(jnp.float32)
    running_totals = jnp.einsum(
        "rn,nasg->rasg", as_member, slot_total * factor, precision=lax.Precision.HIGHEST
    )
    weighted_values = jnp.einsum(
        "rn,nasgh->rasgh", as_member, slot_acc * factor[..., None], precision=lax.Precision.HIGHEST
    )
    return (running_totals, weighted_values)


def fresh_part(query_rows, key_all, value_all):
    step_count = query_rows.shape[1]
    used = key_all.shape[1]
    scores = jnp.einsum(
        "rsagh,ruah->rasgu", query_rows, key_all, preferred_element_type=jnp.float32
    ) * (1.0 / math.sqrt(HEAD_SIZE))
    causal = (
        jnp.arange(used, dtype=jnp.int32)[None, :]
        <= jnp.arange(step_count, dtype=jnp.int32)[:, None]
    )
    causal = causal[None, None, :, None, :]
    running_peak = jnp.max(jnp.where(causal, scores, NEGATIVE_FILL), -1)
    weights = jnp.where(causal, jnp.exp(scores - running_peak[..., None]), 0.0)
    running_totals = jnp.sum(weights, -1)
    weighted_values = jnp.einsum(
        "rasgu,ruah->rasgh",
        weights.astype(jnp.bfloat16),
        value_all,
        preferred_element_type=jnp.float32,
    )
    return (running_peak, running_totals, weighted_values)


def merge_parts(earlier, later):
    running_peak = jnp.maximum(earlier[0], later[0])
    first_factor = jnp.exp(earlier[0] - running_peak)
    second_factor = jnp.exp(later[0] - running_peak)
    running_totals = earlier[1] * first_factor + later[1] * second_factor
    weighted_values = earlier[2] * first_factor[..., None] + later[2] * second_factor[..., None]
    return (running_peak, running_totals, weighted_values)


def seq_merge(peak, total, acc, n_seq, seq_index):
    stages = n_seq.bit_length() - 1
    assert 1 << stages == n_seq
    req_count = peak.shape[0]
    per = req_count // n_seq
    rest = peak.shape[1:]
    split = [2] * stages + [per]
    stats = jnp.stack([peak, total], 0).reshape([2] + split + list(rest))
    values = acc.reshape(split + list(acc.shape[1:]))
    for bit in range(stages):
        axis = stages - 1 - bit
        mine = (seq_index >> bit) & 1
        pairs = [(s, s ^ (1 << bit)) for s in range(n_seq)]
        keep_stats = lax.dynamic_index_in_dim(stats, mine, axis + 1, keepdims=True)
        send_stats = lax.dynamic_index_in_dim(stats, 1 - mine, axis + 1, keepdims=True)
        keep_values = lax.dynamic_index_in_dim(values, mine, axis, keepdims=True)
        send_values = lax.dynamic_index_in_dim(values, 1 - mine, axis, keepdims=True)
        got_stats = lax.ppermute(send_stats, "seq", pairs)
        got_values = lax.ppermute(send_values.astype(jnp.bfloat16), "seq", pairs).astype(
            jnp.float32
        )
        top = jnp.maximum(keep_stats[0], got_stats[0])
        keep_factor = jnp.exp(keep_stats[0] - top)
        got_factor = jnp.exp(got_stats[0] - top)
        stats = jnp.stack(
            [top, keep_stats[1] * keep_factor + got_stats[1] * got_factor], 0
        )
        values = keep_values * keep_factor[..., None] + got_values * got_factor[..., None]
    stats = stats.reshape((2, per) + tuple(rest))
    values = values.reshape((per,) + tuple(acc.shape[1:]))
    return (stats[0], stats[1], values)


def on_device(
    states,
    norm_gain,
    wq,
    wk,
    wv,
    wo,
    lengths,
    slot_request,
    slot_block_number,
    paged_key_cache,
    paged_value_cache,
):
    q_width = wq.shape[1]
    k_width = wk.shape[1]
    heads_kv = k_width // HEAD_SIZE
    req_count = lengths.shape[0]
    block_len = paged_key_cache.shape[1]
    key_rows = paged_key_cache.reshape(paged_key_cache.shape[0], block_len, heads_kv, HEAD_SIZE)
    value_rows = paged_value_cache.reshape(
        paged_value_cache.shape[0], block_len, heads_kv, HEAD_SIZE
    )
    step_count = states.shape[1]
    as_float = states.astype(jnp.float32)
    squares = lax.psum(jnp.sum(as_float * as_float, -1), "row")
    normed = (as_float * lax.rsqrt(squares / D + EPSILON)[..., None] * norm_gain).astype(
        jnp.bfloat16
    )
    gathered = lax.all_gather(normed, "col", axis=0, tiled=True)
    piece_rows = gathered.reshape(req_count * lax.axis_size("row") * step_count, -1)
    parts_out = [
        jnp.dot(piece_rows, matrix, preferred_element_type=jnp.float32) for matrix in (wq, wk, wv)
    ]
    output_projected = lax.psum_scatter(
        jnp.concatenate(parts_out, axis=-1)
        .reshape(req_count * lax.axis_size("row"), step_count, -1)
        .astype(jnp.bfloat16),
        "row",
        scatter_dimension=0,
        tiled=True,
    ).astype(jnp.float32)
    token_positions = lengths[:, None] + jnp.arange(step_count, dtype=jnp.int32)[None, :]
    query_rows = rotary_apply(
        output_projected[..., :q_width].reshape(req_count, step_count, -1, HEAD_SIZE),
        token_positions,
    ).astype(jnp.bfloat16)
    query_rows = query_rows.reshape(req_count, step_count, heads_kv, QUERY_PER_KEY, HEAD_SIZE)
    current_key = rotary_apply(
        output_projected[..., q_width : q_width + k_width].reshape(
            req_count, step_count, heads_kv, HEAD_SIZE
        ),
        token_positions,
    ).astype(jnp.bfloat16)
    current_value = (
        output_projected[..., q_width + k_width :]
        .reshape(req_count, step_count, heads_kv, HEAD_SIZE)
        .astype(jnp.bfloat16)
    )
    local_peak, held = slot_parts(
        query_rows, lengths, slot_request, slot_block_number, key_rows, value_rows
    )
    local_totals, local_values = pool_sums(held, local_peak)
    n_seq = lax.axis_size("seq")
    per = req_count // n_seq
    seq_index = lax.axis_index("seq")
    mine = seq_index * per
    running_peak, running_totals, weighted_values = seq_merge(
        local_peak, local_totals, local_values, n_seq, seq_index
    )
    own_queries = lax.dynamic_slice_in_dim(query_rows, mine, per, 0)
    fresh = fresh_part(
        own_queries,
        lax.dynamic_slice_in_dim(current_key, mine, per, 0),
        lax.dynamic_slice_in_dim(current_value, mine, per, 0),
    )
    running_peak, running_totals, weighted_values = merge_parts(
        (running_peak, running_totals, weighted_values), fresh
    )
    heads_out = (
        (weighted_values / running_totals[..., None])
        .transpose(0, 2, 1, 3, 4)
        .reshape(per, step_count, -1)
        .astype(jnp.bfloat16)
    )
    piece_rows = lax.all_gather(heads_out, "row", axis=0, tiled=False)
    n_row = piece_rows.shape[0]
    product = jnp.dot(
        piece_rows.reshape(n_row * per * step_count, -1), wo, preferred_element_type=jnp.float32
    )
    partials = product.reshape(n_row, per, step_count, -1)
    own_out = lax.psum_scatter(
        partials.astype(jnp.bfloat16), "col", scatter_dimension=0, tiled=True
    ).reshape(per, step_count, -1)
    attended = lax.all_gather(own_out, "seq", axis=0, tiled=True)
    return (
        attended,
        current_key.reshape(req_count, step_count, k_width),
        current_value.reshape(req_count, step_count, k_width),
    )


def solution(mesh):
    in_specs = (
        P("col", None, "row"),
        P("row"),
        P("row", "col"),
        P("row", "col"),
        P("row", "col"),
        P("col", "row"),
        P("row"),
        P(("row", "seq")),
        P(("row", "seq")),
        P(("row", "seq"), None, "col"),
        P(("row", "seq"), None, "col"),
    )
    out_specs = (P("col", None, "row"), P("row", None, "col"), P("row", None, "col"))
    return jax.shard_map(
        on_device, mesh=mesh, in_specs=in_specs, out_specs=out_specs, check_vma=False
    )
```

```python
import math

import jax
import jax.numpy as jnp
from jax import lax
from jax.sharding import PartitionSpec as P

D = 5120
HEAD_SIZE = 128
WINDOW = 4096
SINK = 4
QUERY_PER_KEY = 4


EPSILON = 1e-05
NEGATIVE_FILL = -1e30
ROPE_BASE = 100000000.0


def rotary_apply(values, token_positions):
    half_dim = values.shape[-1] // 2
    frequency = ROPE_BASE ** (-(jnp.arange(half_dim, dtype=jnp.float32) * 2.0 / values.shape[-1]))
    angles = (token_positions.astype(jnp.float32)[..., None] * frequency)[..., None, :]
    cosine = jnp.cos(angles)
    sine_part = jnp.sin(angles)
    lower = values[..., :half_dim]
    upper = values[..., half_dim:]
    return jnp.concatenate(
        [lower * cosine - upper * sine_part, upper * cosine + lower * sine_part], -1
    )


def slot_parts(query_rows, lengths, slot_request, slot_block_number, key_rows, value_rows):
    req_count = query_rows.shape[0]
    step_count = query_rows.shape[1]
    block_len = key_rows.shape[1]
    picked = jnp.minimum(slot_request, req_count - 1)
    in_use = slot_request < req_count
    slot_queries = query_rows[picked]
    scores = jnp.einsum(
        "nsagh,nbah->nasgb", slot_queries, key_rows, preferred_element_type=jnp.float32
    ) * (1.0 / math.sqrt(HEAD_SIZE))
    key_pos = (
        slot_block_number[:, None] * block_len + jnp.arange(block_len, dtype=jnp.int32)[None, :]
    )
    own_len = lengths[picked]
    query_pos = own_len[:, None] + jnp.arange(step_count, dtype=jnp.int32)[None, :]
    visible = (
        in_use[:, None, None]
        & (key_pos[:, None, :] < own_len[:, None, None])
        & ((key_pos[:, None, :] < SINK) | (key_pos[:, None, :] > query_pos[:, :, None] - WINDOW))
    )
    visible = visible[:, None, :, None, :]
    slot_peak = jnp.max(jnp.where(visible, scores, NEGATIVE_FILL), -1)
    weights = jnp.where(visible, jnp.exp(scores - slot_peak[..., None]), 0.0)
    slot_total = jnp.sum(weights, -1)
    slot_acc = jnp.einsum(
        "nasgb,nbah->nasgh",
        weights.astype(jnp.bfloat16),
        value_rows,
        preferred_element_type=jnp.float32,
    )
    member = slot_request[None, :] == jnp.arange(req_count, dtype=jnp.int32)[:, None]
    local_peak = jnp.max(
        jnp.where(member[:, :, None, None, None], slot_peak[None], NEGATIVE_FILL), 1
    )
    return (local_peak, (slot_peak, slot_total, slot_acc, member, picked))


def pool_sums(held, running_peak):
    slot_peak, slot_total, slot_acc, member, picked = held
    factor = jnp.exp(slot_peak - running_peak[picked])
    as_member = member.astype(jnp.float32)
    running_totals = jnp.einsum(
        "rn,nasg->rasg", as_member, slot_total * factor, precision=lax.Precision.HIGHEST
    )
    weighted_values = jnp.einsum(
        "rn,nasgh->rasgh", as_member, slot_acc * factor[..., None], precision=lax.Precision.HIGHEST
    )
    return (running_totals, weighted_values)


def fresh_part(query_rows, key_all, value_all):
    step_count = query_rows.shape[1]
    used = key_all.shape[1]
    scores = jnp.einsum(
        "rsagh,ruah->rasgu", query_rows, key_all, preferred_element_type=jnp.float32
    ) * (1.0 / math.sqrt(HEAD_SIZE))
    causal = (
        jnp.arange(used, dtype=jnp.int32)[None, :]
        <= jnp.arange(step_count, dtype=jnp.int32)[:, None]
    )
    causal = causal[None, None, :, None, :]
    running_peak = jnp.max(jnp.where(causal, scores, NEGATIVE_FILL), -1)
    weights = jnp.where(causal, jnp.exp(scores - running_peak[..., None]), 0.0)
    running_totals = jnp.sum(weights, -1)
    weighted_values = jnp.einsum(
        "rasgu,ruah->rasgh",
        weights.astype(jnp.bfloat16),
        value_all,
        preferred_element_type=jnp.float32,
    )
    return (running_peak, running_totals, weighted_values)


def merge_parts(earlier, later):
    running_peak = jnp.maximum(earlier[0], later[0])
    first_factor = jnp.exp(earlier[0] - running_peak)
    second_factor = jnp.exp(later[0] - running_peak)
    running_totals = earlier[1] * first_factor + later[1] * second_factor
    weighted_values = earlier[2] * first_factor[..., None] + later[2] * second_factor[..., None]
    return (running_peak, running_totals, weighted_values)


def pair_gather(part, axis_name):
    n = lax.axis_size(axis_name)
    assert n == 2
    side = lax.axis_index(axis_name)
    other = lax.ppermute(part, axis_name, [(0, 1), (1, 0)])
    return jnp.where(
        side == 0,
        jnp.concatenate([part, other], 0),
        jnp.concatenate([other, part], 0),
    )


def pair_scatter(parts, axis_name):
    n = lax.axis_size(axis_name)
    assert n == 2 and parts.shape[0] == 2
    side = lax.axis_index(axis_name)
    keep = lax.dynamic_index_in_dim(parts, side, 0, keepdims=True)
    send = lax.dynamic_index_in_dim(parts, 1 - side, 0, keepdims=True)
    got = lax.ppermute(send, axis_name, [(0, 1), (1, 0)])
    return (keep.astype(jnp.float32) + got.astype(jnp.float32)).astype(parts.dtype)


def doubling_gather(part, axis_name):
    n = lax.axis_size(axis_name)
    stages = n.bit_length() - 1
    assert 1 << stages == n
    index = lax.axis_index(axis_name)
    block = part[None]
    for bit in reversed(range(stages)):
        pairs = [(s, s ^ (1 << bit)) for s in range(n)]
        got = lax.ppermute(block, axis_name, pairs)
        low = ((index >> bit) & 1) == 0
        block = jnp.where(
            low, jnp.stack([block, got], 0), jnp.stack([got, block], 0)
        )
    block = block.reshape((2,) * stages + part.shape)
    block = block.transpose(tuple(reversed(range(stages))) + tuple(range(stages, stages + part.ndim)))
    return block.reshape((n * part.shape[0],) + part.shape[1:])


def seq_merge(peak, total, acc, n_seq, seq_index):
    stages = n_seq.bit_length() - 1
    assert 1 << stages == n_seq
    req_count = peak.shape[0]
    per = req_count // n_seq
    rest = peak.shape[1:]
    split = [2] * stages + [per]
    stats = jnp.stack([peak, total], 0).reshape([2] + split + list(rest))
    values = acc.reshape(split + list(acc.shape[1:]))
    for bit in range(stages):
        axis = stages - 1 - bit
        mine = (seq_index >> bit) & 1
        pairs = [(s, s ^ (1 << bit)) for s in range(n_seq)]
        keep_stats = lax.dynamic_index_in_dim(stats, mine, axis + 1, keepdims=True)
        send_stats = lax.dynamic_index_in_dim(stats, 1 - mine, axis + 1, keepdims=True)
        keep_values = lax.dynamic_index_in_dim(values, mine, axis, keepdims=True)
        send_values = lax.dynamic_index_in_dim(values, 1 - mine, axis, keepdims=True)
        got_stats = lax.ppermute(send_stats, "seq", pairs)
        got_values = lax.ppermute(send_values.astype(jnp.bfloat16), "seq", pairs).astype(
            jnp.float32
        )
        top = jnp.maximum(keep_stats[0], got_stats[0])
        keep_factor = jnp.exp(keep_stats[0] - top)
        got_factor = jnp.exp(got_stats[0] - top)
        stats = jnp.stack(
            [top, keep_stats[1] * keep_factor + got_stats[1] * got_factor], 0
        )
        values = keep_values * keep_factor[..., None] + got_values * got_factor[..., None]
    stats = stats.reshape((2, per) + tuple(rest))
    values = values.reshape((per,) + tuple(acc.shape[1:]))
    return (stats[0], stats[1], values)


def on_device(
    states,
    norm_gain,
    wq,
    wk,
    wv,
    wo,
    lengths,
    slot_request,
    slot_block_number,
    paged_key_cache,
    paged_value_cache,
):
    q_width = wq.shape[1]
    k_width = wk.shape[1]
    heads_kv = k_width // HEAD_SIZE
    req_count = lengths.shape[0]
    block_len = paged_key_cache.shape[1]
    key_rows = paged_key_cache.reshape(paged_key_cache.shape[0], block_len, heads_kv, HEAD_SIZE)
    value_rows = paged_value_cache.reshape(
        paged_value_cache.shape[0], block_len, heads_kv, HEAD_SIZE
    )
    step_count = states.shape[1]
    as_float = states.astype(jnp.float32)
    squares = lax.psum(jnp.sum(as_float * as_float, -1), "row")
    normed = (as_float * lax.rsqrt(squares / D + EPSILON)[..., None] * norm_gain).astype(
        jnp.bfloat16
    )
    gathered = pair_gather(normed, "col")
    piece_rows = gathered.reshape(req_count * lax.axis_size("row") * step_count, -1)
    parts_out = [
        jnp.dot(piece_rows, matrix, preferred_element_type=jnp.float32) for matrix in (wq, wk, wv)
    ]
    output_projected = lax.psum_scatter(
        jnp.concatenate(parts_out, axis=-1)
        .reshape(req_count * lax.axis_size("row"), step_count, -1)
        .astype(jnp.bfloat16),
        "row",
        scatter_dimension=0,
        tiled=True,
    ).astype(jnp.float32)
    token_positions = lengths[:, None] + jnp.arange(step_count, dtype=jnp.int32)[None, :]
    query_rows = rotary_apply(
        output_projected[..., :q_width].reshape(req_count, step_count, -1, HEAD_SIZE),
        token_positions,
    ).astype(jnp.bfloat16)
    query_rows = query_rows.reshape(req_count, step_count, heads_kv, QUERY_PER_KEY, HEAD_SIZE)
    current_key = rotary_apply(
        output_projected[..., q_width : q_width + k_width].reshape(
            req_count, step_count, heads_kv, HEAD_SIZE
        ),
        token_positions,
    ).astype(jnp.bfloat16)
    current_value = (
        output_projected[..., q_width + k_width :]
        .reshape(req_count, step_count, heads_kv, HEAD_SIZE)
        .astype(jnp.bfloat16)
    )
    local_peak, held = slot_parts(
        query_rows, lengths, slot_request, slot_block_number, key_rows, value_rows
    )
    local_totals, local_values = pool_sums(held, local_peak)
    n_seq = lax.axis_size("seq")
    per = req_count // n_seq
    seq_index = lax.axis_index("seq")
    mine = seq_index * per
    running_peak, running_totals, weighted_values = seq_merge(
        local_peak, local_totals, local_values, n_seq, seq_index
    )
    own_queries = lax.dynamic_slice_in_dim(query_rows, mine, per, 0)
    fresh = fresh_part(
        own_queries,
        lax.dynamic_slice_in_dim(current_key, mine, per, 0),
        lax.dynamic_slice_in_dim(current_value, mine, per, 0),
    )
    running_peak, running_totals, weighted_values = merge_parts(
        (running_peak, running_totals, weighted_values), fresh
    )
    heads_out = (
        (weighted_values / running_totals[..., None])
        .transpose(0, 2, 1, 3, 4)
        .reshape(per, step_count, -1)
        .astype(jnp.bfloat16)
    )
    piece_rows = lax.all_gather(heads_out, "row", axis=0, tiled=False)
    n_row = piece_rows.shape[0]
    product = jnp.dot(
        piece_rows.reshape(n_row * per * step_count, -1), wo, preferred_element_type=jnp.float32
    )
    partials = product.reshape(n_row, per, step_count, -1)
    own_out = pair_scatter(partials.astype(jnp.bfloat16), "col").reshape(per, step_count, -1)
    attended = doubling_gather(own_out, "seq")
    return (
        attended,
        current_key.reshape(req_count, step_count, k_width),
        current_value.reshape(req_count, step_count, k_width),
    )


def solution(mesh):
    in_specs = (
        P("col", None, "row"),
        P("row"),
        P("row", "col"),
        P("row", "col"),
        P("row", "col"),
        P("col", "row"),
        P("row"),
        P(("row", "seq")),
        P(("row", "seq")),
        P(("row", "seq"), None, "col"),
        P(("row", "seq"), None, "col"),
    )
    out_specs = (P("col", None, "row"), P("row", None, "col"), P("row", None, "col"))
    return jax.shard_map(
        on_device, mesh=mesh, in_specs=in_specs, out_specs=out_specs, check_vma=False
    )
```

```python
import math

import jax
import jax.numpy as jnp
from jax import lax
from jax.sharding import PartitionSpec as P

D = 5120
HEAD_SIZE = 128
WINDOW = 4096
SINK = 4
QUERY_PER_KEY = 4


EPSILON = 1e-05
NEGATIVE_FILL = -1e30
ROPE_BASE = 100000000.0


def rotary_apply(values, token_positions):
    half_dim = values.shape[-1] // 2
    frequency = ROPE_BASE ** (-(jnp.arange(half_dim, dtype=jnp.float32) * 2.0 / values.shape[-1]))
    angles = (token_positions.astype(jnp.float32)[..., None] * frequency)[..., None, :]
    cosine = jnp.cos(angles)
    sine_part = jnp.sin(angles)
    lower = values[..., :half_dim]
    upper = values[..., half_dim:]
    return jnp.concatenate(
        [lower * cosine - upper * sine_part, upper * cosine + lower * sine_part], -1
    )


def slot_parts(query_rows, lengths, slot_request, slot_block_number, key_rows, value_rows):
    req_count = query_rows.shape[0]
    step_count = query_rows.shape[1]
    block_len = key_rows.shape[1]
    picked = jnp.minimum(slot_request, req_count - 1)
    in_use = slot_request < req_count
    slot_queries = query_rows[picked]
    scores = jnp.einsum(
        "nsagh,nbah->nasgb", slot_queries, key_rows, preferred_element_type=jnp.float32
    ) * (1.0 / math.sqrt(HEAD_SIZE))
    key_pos = (
        slot_block_number[:, None] * block_len + jnp.arange(block_len, dtype=jnp.int32)[None, :]
    )
    own_len = lengths[picked]
    query_pos = own_len[:, None] + jnp.arange(step_count, dtype=jnp.int32)[None, :]
    visible = (
        in_use[:, None, None]
        & (key_pos[:, None, :] < own_len[:, None, None])
        & ((key_pos[:, None, :] < SINK) | (key_pos[:, None, :] > query_pos[:, :, None] - WINDOW))
    )
    visible = visible[:, None, :, None, :]
    slot_peak = jnp.max(jnp.where(visible, scores, NEGATIVE_FILL), -1)
    weights = jnp.where(visible, jnp.exp(scores - slot_peak[..., None]), 0.0)
    slot_total = jnp.sum(weights, -1)
    slot_acc = jnp.einsum(
        "nasgb,nbah->nasgh",
        weights.astype(jnp.bfloat16),
        value_rows,
        preferred_element_type=jnp.float32,
    )
    member = slot_request[None, :] == jnp.arange(req_count, dtype=jnp.int32)[:, None]
    local_peak = jnp.max(
        jnp.where(member[:, :, None, None, None], slot_peak[None], NEGATIVE_FILL), 1
    )
    return (local_peak, (slot_peak, slot_total, slot_acc, member, picked))


def pool_sums(held, running_peak):
    slot_peak, slot_total, slot_acc, member, picked = held
    factor = jnp.exp(slot_peak - running_peak[picked])
    as_member = member.astype(jnp.float32)
    running_totals = jnp.einsum(
        "rn,nasg->rasg", as_member, slot_total * factor, precision=lax.Precision.HIGHEST
    )
    weighted_values = jnp.einsum(
        "rn,nasgh->rasgh", as_member, slot_acc * factor[..., None], precision=lax.Precision.HIGHEST
    )
    return (running_totals, weighted_values)


def fresh_part(query_rows, key_all, value_all):
    step_count = query_rows.shape[1]
    used = key_all.shape[1]
    scores = jnp.einsum(
        "rsagh,ruah->rasgu", query_rows, key_all, preferred_element_type=jnp.float32
    ) * (1.0 / math.sqrt(HEAD_SIZE))
    causal = (
        jnp.arange(used, dtype=jnp.int32)[None, :]
        <= jnp.arange(step_count, dtype=jnp.int32)[:, None]
    )
    causal = causal[None, None, :, None, :]
    running_peak = jnp.max(jnp.where(causal, scores, NEGATIVE_FILL), -1)
    weights = jnp.where(causal, jnp.exp(scores - running_peak[..., None]), 0.0)
    running_totals = jnp.sum(weights, -1)
    weighted_values = jnp.einsum(
        "rasgu,ruah->rasgh",
        weights.astype(jnp.bfloat16),
        value_all,
        preferred_element_type=jnp.float32,
    )
    return (running_peak, running_totals, weighted_values)


def merge_parts(earlier, later):
    running_peak = jnp.maximum(earlier[0], later[0])
    first_factor = jnp.exp(earlier[0] - running_peak)
    second_factor = jnp.exp(later[0] - running_peak)
    running_totals = earlier[1] * first_factor + later[1] * second_factor
    weighted_values = earlier[2] * first_factor[..., None] + later[2] * second_factor[..., None]
    return (running_peak, running_totals, weighted_values)


def pair_gather(part, axis_name):
    n = lax.axis_size(axis_name)
    assert n == 2
    side = lax.axis_index(axis_name)
    other = lax.ppermute(part, axis_name, [(0, 1), (1, 0)])
    return jnp.where(
        side == 0,
        jnp.concatenate([part, other], 0),
        jnp.concatenate([other, part], 0),
    )


def pair_scatter(parts, axis_name):
    n = lax.axis_size(axis_name)
    assert n == 2 and parts.shape[0] == 2
    side = lax.axis_index(axis_name)
    keep = lax.dynamic_index_in_dim(parts, side, 0, keepdims=True)
    send = lax.dynamic_index_in_dim(parts, 1 - side, 0, keepdims=True)
    got = lax.ppermute(send, axis_name, [(0, 1), (1, 0)])
    return (keep.astype(jnp.float32) + got.astype(jnp.float32)).astype(parts.dtype)


def doubling_gather(part, axis_name):
    n = lax.axis_size(axis_name)
    stages = n.bit_length() - 1
    assert 1 << stages == n
    index = lax.axis_index(axis_name)
    block = part[None]
    for bit in reversed(range(stages)):
        pairs = [(s, s ^ (1 << bit)) for s in range(n)]
        got = lax.ppermute(block, axis_name, pairs)
        low = ((index >> bit) & 1) == 0
        block = jnp.where(
            low, jnp.stack([block, got], 0), jnp.stack([got, block], 0)
        )
    block = block.reshape((2,) * stages + part.shape)
    block = block.transpose(tuple(reversed(range(stages))) + tuple(range(stages, stages + part.ndim)))
    return block.reshape((n * part.shape[0],) + part.shape[1:])


def seq_merge(peak, total, acc, n_seq, seq_index):
    stages = n_seq.bit_length() - 1
    assert 1 << stages == n_seq
    req_count = peak.shape[0]
    per = req_count // n_seq
    rest = peak.shape[1:]
    split = [2] * stages + [per]
    stats = jnp.stack([peak, total], 0).reshape([2] + split + list(rest))
    values = acc.reshape(split + list(acc.shape[1:]))
    for bit in range(stages):
        axis = stages - 1 - bit
        mine = (seq_index >> bit) & 1
        pairs = [(s, s ^ (1 << bit)) for s in range(n_seq)]
        keep_stats = lax.dynamic_index_in_dim(stats, mine, axis + 1, keepdims=True)
        send_stats = lax.dynamic_index_in_dim(stats, 1 - mine, axis + 1, keepdims=True)
        keep_values = lax.dynamic_index_in_dim(values, mine, axis, keepdims=True)
        send_values = lax.dynamic_index_in_dim(values, 1 - mine, axis, keepdims=True)
        got_stats = lax.ppermute(send_stats, "seq", pairs)
        got_values = lax.ppermute(send_values.astype(jnp.bfloat16), "seq", pairs).astype(
            jnp.float32
        )
        top = jnp.maximum(keep_stats[0], got_stats[0])
        keep_factor = jnp.exp(keep_stats[0] - top)
        got_factor = jnp.exp(got_stats[0] - top)
        stats = jnp.stack(
            [top, keep_stats[1] * keep_factor + got_stats[1] * got_factor], 0
        )
        values = keep_values * keep_factor[..., None] + got_values * got_factor[..., None]
    stats = stats.reshape((2, per) + tuple(rest))
    values = values.reshape((per,) + tuple(acc.shape[1:]))
    return (stats[0], stats[1], values)


def on_device(
    states,
    norm_gain,
    wq,
    wk,
    wv,
    wo,
    lengths,
    slot_request,
    slot_block_number,
    paged_key_cache,
    paged_value_cache,
):
    q_width = wq.shape[1]
    k_width = wk.shape[1]
    heads_kv = k_width // HEAD_SIZE
    req_count = lengths.shape[0]
    block_len = paged_key_cache.shape[1]
    key_rows = paged_key_cache.reshape(paged_key_cache.shape[0], block_len, heads_kv, HEAD_SIZE)
    value_rows = paged_value_cache.reshape(
        paged_value_cache.shape[0], block_len, heads_kv, HEAD_SIZE
    )
    step_count = states.shape[1]
    token_count = states.shape[0] * step_count
    as_float = states.reshape(token_count, -1).astype(jnp.float32)
    squares = lax.psum(jnp.sum(as_float * as_float, -1), "row")
    normed = (as_float * lax.rsqrt(squares / D + EPSILON)[:, None] * norm_gain).astype(
        jnp.bfloat16
    )
    gathered = pair_gather(normed, "col")
    gathered, key_rows, value_rows = lax.optimization_barrier((gathered, key_rows, value_rows))
    parts_out = [
        jnp.dot(gathered, matrix, preferred_element_type=jnp.float32) for matrix in (wq, wk, wv)
    ]
    output_projected = (
        lax.psum_scatter(
            jnp.concatenate(parts_out, axis=-1).astype(jnp.bfloat16),
            "row",
            scatter_dimension=0,
            tiled=True,
        )
        .astype(jnp.float32)
        .reshape(req_count, step_count, -1)
    )
    token_positions = lengths[:, None] + jnp.arange(step_count, dtype=jnp.int32)[None, :]
    query_rows = rotary_apply(
        output_projected[..., :q_width].reshape(req_count, step_count, -1, HEAD_SIZE),
        token_positions,
    ).astype(jnp.bfloat16)
    query_rows = query_rows.reshape(req_count, step_count, heads_kv, QUERY_PER_KEY, HEAD_SIZE)
    current_key = rotary_apply(
        output_projected[..., q_width : q_width + k_width].reshape(
            req_count, step_count, heads_kv, HEAD_SIZE
        ),
        token_positions,
    ).astype(jnp.bfloat16)
    current_value = (
        output_projected[..., q_width + k_width :]
        .reshape(req_count, step_count, heads_kv, HEAD_SIZE)
        .astype(jnp.bfloat16)
    )
    local_peak, held = slot_parts(
        query_rows, lengths, slot_request, slot_block_number, key_rows, value_rows
    )
    local_totals, local_values = pool_sums(held, local_peak)
    n_seq = lax.axis_size("seq")
    per = req_count // n_seq
    seq_index = lax.axis_index("seq")
    mine = seq_index * per
    running_peak, running_totals, weighted_values = seq_merge(
        local_peak, local_totals, local_values, n_seq, seq_index
    )
    own_queries = lax.dynamic_slice_in_dim(query_rows, mine, per, 0)
    fresh = fresh_part(
        own_queries,
        lax.dynamic_slice_in_dim(current_key, mine, per, 0),
        lax.dynamic_slice_in_dim(current_value, mine, per, 0),
    )
    running_peak, running_totals, weighted_values = merge_parts(
        (running_peak, running_totals, weighted_values), fresh
    )
    heads_out = (
        (weighted_values / running_totals[..., None])
        .transpose(0, 2, 1, 3, 4)
        .reshape(per, step_count, -1)
        .astype(jnp.bfloat16)
    )
    piece_rows = lax.all_gather(heads_out, "row", axis=0, tiled=False)
    n_row = piece_rows.shape[0]
    product = jnp.dot(
        piece_rows.reshape(n_row * per * step_count, -1), wo, preferred_element_type=jnp.float32
    )
    partials = product.reshape(n_row, per, step_count, -1)
    own_out = pair_scatter(partials.astype(jnp.bfloat16), "col").reshape(per, step_count, -1)
    attended = doubling_gather(own_out, "seq")
    return (
        attended,
        current_key.reshape(req_count, step_count, k_width),
        current_value.reshape(req_count, step_count, k_width),
    )


def solution(mesh):
    in_specs = (
        P("col", None, "row"),
        P("row"),
        P("row", "col"),
        P("row", "col"),
        P("row", "col"),
        P("col", "row"),
        P("row"),
        P(("row", "seq")),
        P(("row", "seq")),
        P(("row", "seq"), None, "col"),
        P(("row", "seq"), None, "col"),
    )
    out_specs = (P("col", None, "row"), P("row", None, "col"), P("row", None, "col"))
    return jax.shard_map(
        on_device, mesh=mesh, in_specs=in_specs, out_specs=out_specs, check_vma=False
    )
```

```python
import math

import jax
import jax.numpy as jnp
from jax import lax
from jax.sharding import PartitionSpec as P

D = 5120
HEAD_SIZE = 128
WINDOW = 4096
SINK = 4
QUERY_PER_KEY = 4


EPSILON = 1e-05
NEGATIVE_FILL = -1e30
ROPE_BASE = 100000000.0


def rotary_apply(values, token_positions):
    half_dim = values.shape[-1] // 2
    frequency = ROPE_BASE ** (-(jnp.arange(half_dim, dtype=jnp.float32) * 2.0 / values.shape[-1]))
    angles = (token_positions.astype(jnp.float32)[..., None] * frequency)[..., None, :]
    cosine = jnp.cos(angles)
    sine_part = jnp.sin(angles)
    lower = values[..., :half_dim]
    upper = values[..., half_dim:]
    return jnp.concatenate(
        [lower * cosine - upper * sine_part, upper * cosine + lower * sine_part], -1
    )


def slot_parts(query_rows, lengths, slot_request, slot_block_number, key_rows, value_rows):
    req_count = query_rows.shape[0]
    step_count = query_rows.shape[1]
    block_len = key_rows.shape[1]
    picked = jnp.minimum(slot_request, req_count - 1)
    in_use = slot_request < req_count
    slot_queries = query_rows[picked]
    scores = jnp.einsum(
        "nsagh,nbah->nasgb", slot_queries, key_rows, preferred_element_type=jnp.float32
    ) * (1.0 / math.sqrt(HEAD_SIZE))
    key_pos = (
        slot_block_number[:, None] * block_len + jnp.arange(block_len, dtype=jnp.int32)[None, :]
    )
    own_len = lengths[picked]
    query_pos = own_len[:, None] + jnp.arange(step_count, dtype=jnp.int32)[None, :]
    visible = (
        in_use[:, None, None]
        & (key_pos[:, None, :] < own_len[:, None, None])
        & ((key_pos[:, None, :] < SINK) | (key_pos[:, None, :] > query_pos[:, :, None] - WINDOW))
    )
    visible = visible[:, None, :, None, :]
    slot_peak = jnp.max(jnp.where(visible, scores, NEGATIVE_FILL), -1)
    weights = jnp.where(visible, jnp.exp(scores - slot_peak[..., None]), 0.0)
    slot_total = jnp.sum(weights, -1)
    slot_acc = jnp.einsum(
        "nasgb,nbah->nasgh",
        weights.astype(jnp.bfloat16),
        value_rows,
        preferred_element_type=jnp.float32,
    )
    member = slot_request[None, :] == jnp.arange(req_count, dtype=jnp.int32)[:, None]
    local_peak = jnp.max(
        jnp.where(member[:, :, None, None, None], slot_peak[None], NEGATIVE_FILL), 1
    )
    return (local_peak, (slot_peak, slot_total, slot_acc, member, picked))


def pool_sums(held, running_peak):
    slot_peak, slot_total, slot_acc, member, picked = held
    factor = jnp.exp(slot_peak - running_peak[picked])
    as_member = member.astype(jnp.float32)
    running_totals = jnp.einsum(
        "rn,nasg->rasg", as_member, slot_total * factor, precision=lax.Precision.HIGHEST
    )
    weighted_values = jnp.einsum(
        "rn,nasgh->rasgh", as_member, slot_acc * factor[..., None], precision=lax.Precision.HIGHEST
    )
    return (running_totals, weighted_values)


def fresh_part(query_rows, key_all, value_all):
    step_count = query_rows.shape[1]
    used = key_all.shape[1]
    scores = jnp.einsum(
        "rsagh,ruah->rasgu", query_rows, key_all, preferred_element_type=jnp.float32
    ) * (1.0 / math.sqrt(HEAD_SIZE))
    causal = (
        jnp.arange(used, dtype=jnp.int32)[None, :]
        <= jnp.arange(step_count, dtype=jnp.int32)[:, None]
    )
    causal = causal[None, None, :, None, :]
    running_peak = jnp.max(jnp.where(causal, scores, NEGATIVE_FILL), -1)
    weights = jnp.where(causal, jnp.exp(scores - running_peak[..., None]), 0.0)
    running_totals = jnp.sum(weights, -1)
    weighted_values = jnp.einsum(
        "rasgu,ruah->rasgh",
        weights.astype(jnp.bfloat16),
        value_all,
        preferred_element_type=jnp.float32,
    )
    return (running_peak, running_totals, weighted_values)


def merge_parts(earlier, later):
    running_peak = jnp.maximum(earlier[0], later[0])
    first_factor = jnp.exp(earlier[0] - running_peak)
    second_factor = jnp.exp(later[0] - running_peak)
    running_totals = earlier[1] * first_factor + later[1] * second_factor
    weighted_values = earlier[2] * first_factor[..., None] + later[2] * second_factor[..., None]
    return (running_peak, running_totals, weighted_values)


def pair_gather(part, axis_name):
    n = lax.axis_size(axis_name)
    assert n == 2
    side = lax.axis_index(axis_name)
    other = lax.ppermute(part, axis_name, [(0, 1), (1, 0)])
    return jnp.where(
        side == 0,
        jnp.concatenate([part, other], 0),
        jnp.concatenate([other, part], 0),
    )


def pair_scatter(parts, axis_name, rounded=True):
    n = lax.axis_size(axis_name)
    assert n == 2 and parts.shape[0] == 2
    side = lax.axis_index(axis_name)
    keep = lax.dynamic_index_in_dim(parts, side, 0, keepdims=True)
    send = lax.dynamic_index_in_dim(parts, 1 - side, 0, keepdims=True)
    got = lax.ppermute(send, axis_name, [(0, 1), (1, 0)])
    total = (keep.astype(jnp.float32) + got.astype(jnp.float32))[0]
    return total.astype(parts.dtype) if rounded else total


def doubling_gather(part, axis_name):
    n = lax.axis_size(axis_name)
    stages = n.bit_length() - 1
    assert 1 << stages == n
    index = lax.axis_index(axis_name)
    block = part[None]
    for bit in reversed(range(stages)):
        pairs = [(s, s ^ (1 << bit)) for s in range(n)]
        got = lax.ppermute(block, axis_name, pairs)
        low = ((index >> bit) & 1) == 0
        block = jnp.where(
            low, jnp.stack([block, got], 0), jnp.stack([got, block], 0)
        )
    block = block.reshape((2,) * stages + part.shape)
    block = block.transpose(tuple(reversed(range(stages))) + tuple(range(stages, stages + part.ndim)))
    return block.reshape((n * part.shape[0],) + part.shape[1:])


def seq_merge(peak, total, acc, n_seq, seq_index):
    stages = n_seq.bit_length() - 1
    assert 1 << stages == n_seq
    req_count = peak.shape[0]
    per = req_count // n_seq
    rest = peak.shape[1:]
    split = [2] * stages + [per]
    stats = jnp.stack([peak, total], 0).reshape([2] + split + list(rest))
    values = acc.reshape(split + list(acc.shape[1:]))
    for bit in range(stages):
        axis = stages - 1 - bit
        mine = (seq_index >> bit) & 1
        pairs = [(s, s ^ (1 << bit)) for s in range(n_seq)]
        keep_stats = lax.dynamic_index_in_dim(stats, mine, axis + 1, keepdims=True)
        send_stats = lax.dynamic_index_in_dim(stats, 1 - mine, axis + 1, keepdims=True)
        keep_values = lax.dynamic_index_in_dim(values, mine, axis, keepdims=True)
        send_values = lax.dynamic_index_in_dim(values, 1 - mine, axis, keepdims=True)
        got_stats = lax.ppermute(send_stats, "seq", pairs)
        got_values = lax.ppermute(send_values.astype(jnp.bfloat16), "seq", pairs).astype(
            jnp.float32
        )
        top = jnp.maximum(keep_stats[0], got_stats[0])
        keep_factor = jnp.exp(keep_stats[0] - top)
        got_factor = jnp.exp(got_stats[0] - top)
        stats = jnp.stack(
            [top, keep_stats[1] * keep_factor + got_stats[1] * got_factor], 0
        )
        values = keep_values * keep_factor[..., None] + got_values * got_factor[..., None]
    stats = stats.reshape((2, per) + tuple(rest))
    values = values.reshape((per,) + tuple(acc.shape[1:]))
    return (stats[0], stats[1], values)


def on_device(
    states,
    norm_gain,
    wq,
    wk,
    wv,
    wo,
    lengths,
    slot_request,
    slot_block_number,
    paged_key_cache,
    paged_value_cache,
):
    q_width = wq.shape[1]
    k_width = wk.shape[1]
    heads_kv = k_width // HEAD_SIZE
    req_count = lengths.shape[0]
    block_len = paged_key_cache.shape[1]
    key_rows = paged_key_cache.reshape(paged_key_cache.shape[0], block_len, heads_kv, HEAD_SIZE)
    value_rows = paged_value_cache.reshape(
        paged_value_cache.shape[0], block_len, heads_kv, HEAD_SIZE
    )
    step_count = states.shape[1]
    token_count = states.shape[0] * step_count
    own_states = states.reshape(token_count, -1)
    side = lax.axis_index("col")
    swap = [(0, 1), (1, 0)]
    other_states = lax.ppermute(own_states, "col", swap)
    as_float = own_states.astype(jnp.float32)
    squares = lax.psum(jnp.sum(as_float * as_float, -1), "row")
    other_squares = lax.ppermute(squares, "col", swap)

    def rms_norm(rows, sums):
        scale = lax.rsqrt(sums / D + EPSILON)[:, None]
        return (rows.astype(jnp.float32) * scale * norm_gain).astype(jnp.bfloat16)

    first = side == 0
    gathered = jnp.concatenate(
        [
            rms_norm(
                jnp.where(first, own_states, other_states), jnp.where(first, squares, other_squares)
            ),
            rms_norm(
                jnp.where(first, other_states, own_states), jnp.where(first, other_squares, squares)
            ),
        ],
        0,
    )
    gathered, key_rows, value_rows = lax.optimization_barrier((gathered, key_rows, value_rows))
    parts_out = [
        jnp.dot(gathered, matrix, preferred_element_type=jnp.float32) for matrix in (wq, wk, wv)
    ]
    output_projected = (
        pair_scatter(
            jnp.concatenate(parts_out, axis=-1)
            .astype(jnp.bfloat16)
            .reshape(lax.axis_size("row"), token_count, -1),
            "row",
            rounded=False,
        )
        .reshape(req_count, step_count, -1)
    )
    token_positions = lengths[:, None] + jnp.arange(step_count, dtype=jnp.int32)[None, :]
    query_rows = rotary_apply(
        output_projected[..., :q_width].reshape(req_count, step_count, -1, HEAD_SIZE),
        token_positions,
    ).astype(jnp.bfloat16)
    query_rows = query_rows.reshape(req_count, step_count, heads_kv, QUERY_PER_KEY, HEAD_SIZE)
    current_key = rotary_apply(
        output_projected[..., q_width : q_width + k_width].reshape(
            req_count, step_count, heads_kv, HEAD_SIZE
        ),
        token_positions,
    ).astype(jnp.bfloat16)
    current_value = (
        output_projected[..., q_width + k_width :]
        .reshape(req_count, step_count, heads_kv, HEAD_SIZE)
        .astype(jnp.bfloat16)
    )
    local_peak, held = slot_parts(
        query_rows, lengths, slot_request, slot_block_number, key_rows, value_rows
    )
    local_totals, local_values = pool_sums(held, local_peak)
    n_seq = lax.axis_size("seq")
    per = req_count // n_seq
    seq_index = lax.axis_index("seq")
    mine = seq_index * per
    running_peak, running_totals, weighted_values = seq_merge(
        local_peak, local_totals, local_values, n_seq, seq_index
    )
    own_queries = lax.dynamic_slice_in_dim(query_rows, mine, per, 0)
    fresh = fresh_part(
        own_queries,
        lax.dynamic_slice_in_dim(current_key, mine, per, 0),
        lax.dynamic_slice_in_dim(current_value, mine, per, 0),
    )
    running_peak, running_totals, weighted_values = merge_parts(
        (running_peak, running_totals, weighted_values), fresh
    )
    heads_out = (
        (weighted_values / running_totals[..., None])
        .transpose(0, 2, 1, 3, 4)
        .reshape(per, step_count, -1)
        .astype(jnp.bfloat16)
    )
    piece_rows = lax.all_gather(heads_out, "row", axis=0, tiled=False)
    n_row = piece_rows.shape[0]
    product = jnp.dot(
        piece_rows.reshape(n_row * per * step_count, -1), wo, preferred_element_type=jnp.float32
    )
    partials = product.reshape(n_row, per, step_count, -1)
    own_out = pair_scatter(partials.astype(jnp.bfloat16), "col").reshape(per, step_count, -1)
    attended = doubling_gather(own_out, "seq")
    return (
        attended,
        current_key.reshape(req_count, step_count, k_width),
        current_value.reshape(req_count, step_count, k_width),
    )


def solution(mesh):
    in_specs = (
        P("col", None, "row"),
        P("row"),
        P("row", "col"),
        P("row", "col"),
        P("row", "col"),
        P("col", "row"),
        P("row"),
        P(("row", "seq")),
        P(("row", "seq")),
        P(("row", "seq"), None, "col"),
        P(("row", "seq"), None, "col"),
    )
    out_specs = (P("col", None, "row"), P("row", None, "col"), P("row", None, "col"))
    return jax.shard_map(
        on_device, mesh=mesh, in_specs=in_specs, out_specs=out_specs, check_vma=False
    )
```

```python
import math
from functools import partial

import jax
import jax.numpy as jnp
from jax import lax
from jax.experimental import pallas as pl
from jax.experimental.pallas import tpu as pltpu
from jax.sharding import PartitionSpec as P

D = 5120
HEAD_SIZE = 128
WINDOW = 4096
SINK = 4
QUERY_PER_KEY = 4


EPSILON = 1e-05
NEGATIVE_FILL = -1e30
ROPE_BASE = 100000000.0


def rotary_apply(values, token_positions):
    half_dim = values.shape[-1] // 2
    frequency = ROPE_BASE ** (-(jnp.arange(half_dim, dtype=jnp.float32) * 2.0 / values.shape[-1]))
    angles = (token_positions.astype(jnp.float32)[..., None] * frequency)[..., None, :]
    cosine = jnp.cos(angles)
    sine_part = jnp.sin(angles)
    lower = values[..., :half_dim]
    upper = values[..., half_dim:]
    return jnp.concatenate(
        [lower * cosine - upper * sine_part, upper * cosine + lower * sine_part], -1
    )


def slot_parts(query_rows, lengths, slot_request, slot_block_number, key_rows, value_rows):
    req_count = query_rows.shape[0]
    step_count = query_rows.shape[1]
    block_len = key_rows.shape[1]
    picked = jnp.minimum(slot_request, req_count - 1)
    in_use = slot_request < req_count
    slot_queries = query_rows[picked]
    scores = jnp.einsum(
        "nsagh,nbah->nasgb", slot_queries, key_rows, preferred_element_type=jnp.float32
    ) * (1.0 / math.sqrt(HEAD_SIZE))
    key_pos = (
        slot_block_number[:, None] * block_len + jnp.arange(block_len, dtype=jnp.int32)[None, :]
    )
    own_len = lengths[picked]
    query_pos = own_len[:, None] + jnp.arange(step_count, dtype=jnp.int32)[None, :]
    visible = (
        in_use[:, None, None]
        & (key_pos[:, None, :] < own_len[:, None, None])
        & ((key_pos[:, None, :] < SINK) | (key_pos[:, None, :] > query_pos[:, :, None] - WINDOW))
    )
    visible = visible[:, None, :, None, :]
    slot_peak = jnp.max(jnp.where(visible, scores, NEGATIVE_FILL), -1)
    weights = jnp.where(visible, jnp.exp(scores - slot_peak[..., None]), 0.0)
    slot_total = jnp.sum(weights, -1)
    slot_acc = jnp.einsum(
        "nasgb,nbah->nasgh",
        weights.astype(jnp.bfloat16),
        value_rows,
        preferred_element_type=jnp.float32,
    )
    member = slot_request[None, :] == jnp.arange(req_count, dtype=jnp.int32)[:, None]
    local_peak = jnp.max(
        jnp.where(member[:, :, None, None, None], slot_peak[None], NEGATIVE_FILL), 1
    )
    return (local_peak, (slot_peak, slot_total, slot_acc, member, picked))


def pool_sums(held, running_peak):
    slot_peak, slot_total, slot_acc, member, picked = held
    factor = jnp.exp(slot_peak - running_peak[picked])
    as_member = member.astype(jnp.float32)
    running_totals = jnp.einsum(
        "rn,nasg->rasg", as_member, slot_total * factor, precision=lax.Precision.HIGHEST
    )
    weighted_values = jnp.einsum(
        "rn,nasgh->rasgh", as_member, slot_acc * factor[..., None], precision=lax.Precision.HIGHEST
    )
    return (running_totals, weighted_values)


def fresh_part(query_rows, key_all, value_all):
    step_count = query_rows.shape[1]
    used = key_all.shape[1]
    scores = jnp.einsum(
        "rsagh,ruah->rasgu", query_rows, key_all, preferred_element_type=jnp.float32
    ) * (1.0 / math.sqrt(HEAD_SIZE))
    causal = (
        jnp.arange(used, dtype=jnp.int32)[None, :]
        <= jnp.arange(step_count, dtype=jnp.int32)[:, None]
    )
    causal = causal[None, None, :, None, :]
    running_peak = jnp.max(jnp.where(causal, scores, NEGATIVE_FILL), -1)
    weights = jnp.where(causal, jnp.exp(scores - running_peak[..., None]), 0.0)
    running_totals = jnp.sum(weights, -1)
    weighted_values = jnp.einsum(
        "rasgu,ruah->rasgh",
        weights.astype(jnp.bfloat16),
        value_all,
        preferred_element_type=jnp.float32,
    )
    return (running_peak, running_totals, weighted_values)


def merge_parts(earlier, later):
    running_peak = jnp.maximum(earlier[0], later[0])
    first_factor = jnp.exp(earlier[0] - running_peak)
    second_factor = jnp.exp(later[0] - running_peak)
    running_totals = earlier[1] * first_factor + later[1] * second_factor
    weighted_values = earlier[2] * first_factor[..., None] + later[2] * second_factor[..., None]
    return (running_peak, running_totals, weighted_values)


def slot_kernel(len_ref, blk_ref, q_ref, k_ref, v_ref, peak_ref, tot_ref, acc_ref, *, ns, heads, qpk):
    base = pl.program_id(0) * ns
    rows = q_ref.shape[1]
    width = k_ref.shape[1]
    head = k_ref.shape[2] // heads
    row = lax.broadcasted_iota(jnp.int32, (rows, width), 0)
    col = lax.broadcasted_iota(jnp.int32, (rows, width), 1)
    head_of = (row // qpk) % heads
    step_of = row // (heads * qpk)

    def body(i, carry):
        length = len_ref[base + i]
        key_pos = blk_ref[base + i] * width + col
        query_pos = length + step_of
        visible = (key_pos < length) & ((key_pos < SINK) | (key_pos > query_pos - WINDOW))
        q = q_ref[i]
        k = k_ref[i]
        v = v_ref[i]
        scores = jnp.zeros((rows, width), jnp.float32)
        for a in range(heads):
            part = lax.dot_general(
                q,
                k[:, a * head : (a + 1) * head],
                (((1,), (1,)), ((), ())),
                preferred_element_type=jnp.float32,
            )
            scores = jnp.where(head_of == a, part, scores)
        scores = scores * (1.0 / math.sqrt(HEAD_SIZE))
        peak = jnp.max(jnp.where(visible, scores, NEGATIVE_FILL), axis=1, keepdims=True)
        weights = jnp.where(visible, jnp.exp(scores - peak), 0.0)
        total = jnp.sum(weights, axis=1, keepdims=True)
        rounded = weights.astype(jnp.bfloat16)
        acc = jnp.zeros((rows, head), jnp.float32)
        for a in range(heads):
            part = jnp.dot(
                rounded, v[:, a * head : (a + 1) * head], preferred_element_type=jnp.float32
            )
            acc = jnp.where(head_of[:, :head] == a, part, acc)
        peak_ref[i] = peak
        tot_ref[i] = total
        acc_ref[i] = acc
        return carry

    lax.fori_loop(0, ns, body, 0)


def slot_attention(slot_queries, slot_lengths, block_numbers, keys, values, heads, qpk):
    n_slots, rows, head = slot_queries.shape
    width = keys.shape[1]
    ns = max(d for d in range(1, 11) if n_slots % d == 0)
    grid_spec = pltpu.PrefetchScalarGridSpec(
        num_scalar_prefetch=2,
        grid=(n_slots // ns,),
        in_specs=[
            pl.BlockSpec((ns, rows, head), lambda n, lr, br: (n, 0, 0)),
            pl.BlockSpec((ns, width, keys.shape[2]), lambda n, lr, br: (n, 0, 0)),
            pl.BlockSpec((ns, width, values.shape[2]), lambda n, lr, br: (n, 0, 0)),
        ],
        out_specs=[
            pl.BlockSpec((ns, rows, 1), lambda n, lr, br: (n, 0, 0)),
            pl.BlockSpec((ns, rows, 1), lambda n, lr, br: (n, 0, 0)),
            pl.BlockSpec((ns, rows, head), lambda n, lr, br: (n, 0, 0)),
        ],
    )
    return pl.pallas_call(
        partial(slot_kernel, ns=ns, heads=heads, qpk=qpk),
        grid_spec=grid_spec,
        out_shape=[
            jax.ShapeDtypeStruct((n_slots, rows, 1), jnp.float32),
            jax.ShapeDtypeStruct((n_slots, rows, 1), jnp.float32),
            jax.ShapeDtypeStruct((n_slots, rows, head), jnp.float32),
        ],
    )(slot_lengths, block_numbers, slot_queries, keys, values)


def pair_gather(part, axis_name):
    n = lax.axis_size(axis_name)
    assert n == 2
    side = lax.axis_index(axis_name)
    other = lax.ppermute(part, axis_name, [(0, 1), (1, 0)])
    return jnp.where(
        side == 0,
        jnp.concatenate([part, other], 0),
        jnp.concatenate([other, part], 0),
    )


def pair_scatter(parts, axis_name, rounded=True):
    n = lax.axis_size(axis_name)
    assert n == 2 and parts.shape[0] == 2
    side = lax.axis_index(axis_name)
    keep = lax.dynamic_index_in_dim(parts, side, 0, keepdims=True)
    send = lax.dynamic_index_in_dim(parts, 1 - side, 0, keepdims=True)
    got = lax.ppermute(send, axis_name, [(0, 1), (1, 0)])
    total = (keep.astype(jnp.float32) + got.astype(jnp.float32))[0]
    return total.astype(parts.dtype) if rounded else total


def doubling_gather(part, axis_name):
    n = lax.axis_size(axis_name)
    stages = n.bit_length() - 1
    assert 1 << stages == n
    index = lax.axis_index(axis_name)
    block = part[None]
    for bit in reversed(range(stages)):
        pairs = [(s, s ^ (1 << bit)) for s in range(n)]
        got = lax.ppermute(block, axis_name, pairs)
        low = ((index >> bit) & 1) == 0
        block = jnp.where(
            low, jnp.stack([block, got], 0), jnp.stack([got, block], 0)
        )
    block = block.reshape((2,) * stages + part.shape)
    block = block.transpose(tuple(reversed(range(stages))) + tuple(range(stages, stages + part.ndim)))
    return block.reshape((n * part.shape[0],) + part.shape[1:])


def seq_merge(peak, total, acc, n_seq, seq_index):
    stages = n_seq.bit_length() - 1
    assert 1 << stages == n_seq
    req_count = peak.shape[0]
    per = req_count // n_seq
    rest = peak.shape[1:]
    split = [2] * stages + [per]
    stats = jnp.stack([peak, total], 0).reshape([2] + split + list(rest))
    values = acc.reshape(split + list(acc.shape[1:]))
    for bit in range(stages):
        axis = stages - 1 - bit
        mine = (seq_index >> bit) & 1
        pairs = [(s, s ^ (1 << bit)) for s in range(n_seq)]
        keep_stats = lax.dynamic_index_in_dim(stats, mine, axis + 1, keepdims=True)
        send_stats = lax.dynamic_index_in_dim(stats, 1 - mine, axis + 1, keepdims=True)
        keep_values = lax.dynamic_index_in_dim(values, mine, axis, keepdims=True)
        send_values = lax.dynamic_index_in_dim(values, 1 - mine, axis, keepdims=True)
        got_stats = lax.ppermute(send_stats, "seq", pairs)
        got_values = lax.ppermute(send_values.astype(jnp.bfloat16), "seq", pairs).astype(
            jnp.float32
        )
        top = jnp.maximum(keep_stats[0], got_stats[0])
        keep_factor = jnp.exp(keep_stats[0] - top)
        got_factor = jnp.exp(got_stats[0] - top)
        stats = jnp.stack(
            [top, keep_stats[1] * keep_factor + got_stats[1] * got_factor], 0
        )
        values = keep_values * keep_factor[..., None] + got_values * got_factor[..., None]
    stats = stats.reshape((2, per) + tuple(rest))
    values = values.reshape((per,) + tuple(acc.shape[1:]))
    return (stats[0], stats[1], values)


def on_device(
    states,
    norm_gain,
    wq,
    wk,
    wv,
    wo,
    lengths,
    slot_request,
    slot_block_number,
    paged_key_cache,
    paged_value_cache,
):
    q_width = wq.shape[1]
    k_width = wk.shape[1]
    heads_kv = k_width // HEAD_SIZE
    req_count = lengths.shape[0]
    block_len = paged_key_cache.shape[1]
    key_rows = paged_key_cache.reshape(paged_key_cache.shape[0], block_len, heads_kv, HEAD_SIZE)
    value_rows = paged_value_cache.reshape(
        paged_value_cache.shape[0], block_len, heads_kv, HEAD_SIZE
    )
    step_count = states.shape[1]
    token_count = states.shape[0] * step_count
    own_states = states.reshape(token_count, -1)
    side = lax.axis_index("col")
    swap = [(0, 1), (1, 0)]
    other_states = lax.ppermute(own_states, "col", swap)
    as_float = own_states.astype(jnp.float32)
    squares = lax.psum(jnp.sum(as_float * as_float, -1), "row")
    other_squares = lax.ppermute(squares, "col", swap)

    def rms_norm(rows, sums):
        scale = lax.rsqrt(sums / D + EPSILON)[:, None]
        return (rows.astype(jnp.float32) * scale * norm_gain).astype(jnp.bfloat16)

    first = side == 0
    gathered = jnp.concatenate(
        [
            rms_norm(
                jnp.where(first, own_states, other_states), jnp.where(first, squares, other_squares)
            ),
            rms_norm(
                jnp.where(first, other_states, own_states), jnp.where(first, other_squares, squares)
            ),
        ],
        0,
    )
    parts_out = [
        jnp.dot(gathered, matrix, preferred_element_type=jnp.float32) for matrix in (wq, wk, wv)
    ]
    output_projected = (
        pair_scatter(
            jnp.concatenate(parts_out, axis=-1)
            .astype(jnp.bfloat16)
            .reshape(lax.axis_size("row"), token_count, -1),
            "row",
            rounded=False,
        )
        .reshape(req_count, step_count, -1)
    )
    token_positions = lengths[:, None] + jnp.arange(step_count, dtype=jnp.int32)[None, :]
    query_rows = rotary_apply(
        output_projected[..., :q_width].reshape(req_count, step_count, -1, HEAD_SIZE),
        token_positions,
    ).astype(jnp.bfloat16)
    query_rows = query_rows.reshape(req_count, step_count, heads_kv, QUERY_PER_KEY, HEAD_SIZE)
    current_key = rotary_apply(
        output_projected[..., q_width : q_width + k_width].reshape(
            req_count, step_count, heads_kv, HEAD_SIZE
        ),
        token_positions,
    ).astype(jnp.bfloat16)
    current_value = (
        output_projected[..., q_width + k_width :]
        .reshape(req_count, step_count, heads_kv, HEAD_SIZE)
        .astype(jnp.bfloat16)
    )
    picked = jnp.minimum(slot_request, req_count - 1)
    in_use = slot_request < req_count
    slot_lengths = jnp.where(in_use, lengths[picked], 0)
    flat_queries = query_rows.reshape(req_count, -1, HEAD_SIZE)
    slot_peak, slot_total, slot_acc = slot_attention(
        flat_queries[picked],
        slot_lengths,
        slot_block_number,
        paged_key_cache,
        paged_value_cache,
        heads_kv,
        QUERY_PER_KEY,
    )
    slot_peak = slot_peak[..., 0]
    slot_total = slot_total[..., 0]
    member = slot_request[None, :] == jnp.arange(req_count, dtype=jnp.int32)[:, None]
    local_peak = jnp.max(jnp.where(member[:, :, None], slot_peak[None], NEGATIVE_FILL), 1)
    factor = jnp.exp(slot_peak - local_peak[picked])
    as_member = member.astype(jnp.float32)
    local_totals = jnp.einsum(
        "rn,nj->rj", as_member, slot_total * factor, precision=lax.Precision.HIGHEST
    )
    local_values = jnp.einsum(
        "rn,njh->rjh", as_member, slot_acc * factor[..., None], precision=lax.Precision.HIGHEST
    )
    n_seq = lax.axis_size("seq")
    per = req_count // n_seq
    seq_index = lax.axis_index("seq")
    mine = seq_index * per
    running_peak, running_totals, weighted_values = seq_merge(
        local_peak, local_totals, local_values, n_seq, seq_index
    )
    order = (per, step_count, heads_kv, QUERY_PER_KEY)
    running_peak = running_peak.reshape(order).transpose(0, 2, 1, 3)
    running_totals = running_totals.reshape(order).transpose(0, 2, 1, 3)
    weighted_values = weighted_values.reshape(order + (HEAD_SIZE,)).transpose(0, 2, 1, 3, 4)
    own_queries = lax.dynamic_slice_in_dim(query_rows, mine, per, 0)
    fresh = fresh_part(
        own_queries,
        lax.dynamic_slice_in_dim(current_key, mine, per, 0),
        lax.dynamic_slice_in_dim(current_value, mine, per, 0),
    )
    running_peak, running_totals, weighted_values = merge_parts(
        (running_peak, running_totals, weighted_values), fresh
    )
    heads_out = (
        (weighted_values / running_totals[..., None])
        .transpose(0, 2, 1, 3, 4)
        .reshape(per, step_count, -1)
        .astype(jnp.bfloat16)
    )
    piece_rows = lax.all_gather(heads_out, "row", axis=0, tiled=False)
    n_row = piece_rows.shape[0]
    product = jnp.dot(
        piece_rows.reshape(n_row * per * step_count, -1), wo, preferred_element_type=jnp.float32
    )
    partials = product.reshape(n_row, per, step_count, -1)
    own_out = pair_scatter(partials.astype(jnp.bfloat16), "col").reshape(per, step_count, -1)
    attended = doubling_gather(own_out, "seq")
    return (
        attended,
        current_key.reshape(req_count, step_count, k_width),
        current_value.reshape(req_count, step_count, k_width),
    )


def solution(mesh):
    in_specs = (
        P("col", None, "row"),
        P("row"),
        P("row", "col"),
        P("row", "col"),
        P("row", "col"),
        P("col", "row"),
        P("row"),
        P(("row", "seq")),
        P(("row", "seq")),
        P(("row", "seq"), None, "col"),
        P(("row", "seq"), None, "col"),
    )
    out_specs = (P("col", None, "row"), P("row", None, "col"), P("row", None, "col"))
    return jax.shard_map(
        on_device, mesh=mesh, in_specs=in_specs, out_specs=out_specs, check_vma=False
    )
```

```python
import math
from functools import partial

import jax
import jax.numpy as jnp
from jax import lax
from jax.experimental import pallas as pl
from jax.experimental.pallas import tpu as pltpu
from jax.sharding import PartitionSpec as P

D = 5120
HEAD_SIZE = 128
WINDOW = 4096
SINK = 4
QUERY_PER_KEY = 4


EPSILON = 1e-05
NEGATIVE_FILL = -1e30
ROPE_BASE = 100000000.0


def rotary_apply(values, token_positions):
    half_dim = values.shape[-1] // 2
    frequency = ROPE_BASE ** (-(jnp.arange(half_dim, dtype=jnp.float32) * 2.0 / values.shape[-1]))
    angles = (token_positions.astype(jnp.float32)[..., None] * frequency)[..., None, :]
    cosine = jnp.cos(angles)
    sine_part = jnp.sin(angles)
    lower = values[..., :half_dim]
    upper = values[..., half_dim:]
    return jnp.concatenate(
        [lower * cosine - upper * sine_part, upper * cosine + lower * sine_part], -1
    )


def slot_parts(query_rows, lengths, slot_request, slot_block_number, key_rows, value_rows):
    req_count = query_rows.shape[0]
    step_count = query_rows.shape[1]
    block_len = key_rows.shape[1]
    picked = jnp.minimum(slot_request, req_count - 1)
    in_use = slot_request < req_count
    slot_queries = query_rows[picked]
    scores = jnp.einsum(
        "nsagh,nbah->nasgb", slot_queries, key_rows, preferred_element_type=jnp.float32
    ) * (1.0 / math.sqrt(HEAD_SIZE))
    key_pos = (
        slot_block_number[:, None] * block_len + jnp.arange(block_len, dtype=jnp.int32)[None, :]
    )
    own_len = lengths[picked]
    query_pos = own_len[:, None] + jnp.arange(step_count, dtype=jnp.int32)[None, :]
    visible = (
        in_use[:, None, None]
        & (key_pos[:, None, :] < own_len[:, None, None])
        & ((key_pos[:, None, :] < SINK) | (key_pos[:, None, :] > query_pos[:, :, None] - WINDOW))
    )
    visible = visible[:, None, :, None, :]
    slot_peak = jnp.max(jnp.where(visible, scores, NEGATIVE_FILL), -1)
    weights = jnp.where(visible, jnp.exp(scores - slot_peak[..., None]), 0.0)
    slot_total = jnp.sum(weights, -1)
    slot_acc = jnp.einsum(
        "nasgb,nbah->nasgh",
        weights.astype(jnp.bfloat16),
        value_rows,
        preferred_element_type=jnp.float32,
    )
    member = slot_request[None, :] == jnp.arange(req_count, dtype=jnp.int32)[:, None]
    local_peak = jnp.max(
        jnp.where(member[:, :, None, None, None], slot_peak[None], NEGATIVE_FILL), 1
    )
    return (local_peak, (slot_peak, slot_total, slot_acc, member, picked))


def pool_sums(held, running_peak):
    slot_peak, slot_total, slot_acc, member, picked = held
    factor = jnp.exp(slot_peak - running_peak[picked])
    as_member = member.astype(jnp.float32)
    running_totals = jnp.einsum(
        "rn,nasg->rasg", as_member, slot_total * factor, precision=lax.Precision.HIGHEST
    )
    weighted_values = jnp.einsum(
        "rn,nasgh->rasgh", as_member, slot_acc * factor[..., None], precision=lax.Precision.HIGHEST
    )
    return (running_totals, weighted_values)


def fresh_part(query_rows, key_all, value_all):
    step_count = query_rows.shape[1]
    used = key_all.shape[1]
    scores = jnp.einsum(
        "rsagh,ruah->rasgu", query_rows, key_all, preferred_element_type=jnp.float32
    ) * (1.0 / math.sqrt(HEAD_SIZE))
    causal = (
        jnp.arange(used, dtype=jnp.int32)[None, :]
        <= jnp.arange(step_count, dtype=jnp.int32)[:, None]
    )
    causal = causal[None, None, :, None, :]
    running_peak = jnp.max(jnp.where(causal, scores, NEGATIVE_FILL), -1)
    weights = jnp.where(causal, jnp.exp(scores - running_peak[..., None]), 0.0)
    running_totals = jnp.sum(weights, -1)
    weighted_values = jnp.einsum(
        "rasgu,ruah->rasgh",
        weights.astype(jnp.bfloat16),
        value_all,
        preferred_element_type=jnp.float32,
    )
    return (running_peak, running_totals, weighted_values)


def merge_parts(earlier, later):
    running_peak = jnp.maximum(earlier[0], later[0])
    first_factor = jnp.exp(earlier[0] - running_peak)
    second_factor = jnp.exp(later[0] - running_peak)
    running_totals = earlier[1] * first_factor + later[1] * second_factor
    weighted_values = earlier[2] * first_factor[..., None] + later[2] * second_factor[..., None]
    return (running_peak, running_totals, weighted_values)


def slot_kernel(len_ref, blk_ref, q_ref, k_ref, v_ref, peak_ref, tot_ref, acc_ref, *, ns, heads, qpk):
    base = pl.program_id(0) * ns
    rows = q_ref.shape[1]
    group = rows // heads
    width = k_ref.shape[1]
    head = k_ref.shape[2] // heads
    row = lax.broadcasted_iota(jnp.int32, (rows, width), 0)
    col = lax.broadcasted_iota(jnp.int32, (rows, width), 1)
    step_of = (row % group) // qpk

    def body(i, carry):
        length = len_ref[base + i]
        key_pos = blk_ref[base + i] * width + col
        query_pos = length + step_of
        visible = (key_pos < length) & ((key_pos < SINK) | (key_pos > query_pos - WINDOW))
        q = q_ref[i]
        k = k_ref[i]
        v = v_ref[i]
        scores = jnp.concatenate(
            [
                lax.dot_general(
                    q[a * group : (a + 1) * group],
                    k[:, a * head : (a + 1) * head],
                    (((1,), (1,)), ((), ())),
                    preferred_element_type=jnp.float32,
                )
                for a in range(heads)
            ],
            0,
        ) * (1.0 / math.sqrt(HEAD_SIZE))
        peak = jnp.max(jnp.where(visible, scores, NEGATIVE_FILL), axis=1, keepdims=True)
        weights = jnp.where(visible, jnp.exp(scores - peak), 0.0)
        total = jnp.sum(weights, axis=1, keepdims=True)
        rounded = weights.astype(jnp.bfloat16)
        acc = jnp.concatenate(
            [
                jnp.dot(
                    rounded[a * group : (a + 1) * group],
                    v[:, a * head : (a + 1) * head],
                    preferred_element_type=jnp.float32,
                )
                for a in range(heads)
            ],
            0,
        )
        peak_ref[i] = peak
        tot_ref[i] = total
        acc_ref[i] = acc
        return carry

    lax.fori_loop(0, ns, body, 0, unroll=True)


def slot_attention(slot_queries, slot_lengths, block_numbers, keys, values, heads, qpk):
    n_slots, rows, head = slot_queries.shape
    width = keys.shape[1]
    ns = max(d for d in range(1, 11) if n_slots % d == 0)
    grid_spec = pltpu.PrefetchScalarGridSpec(
        num_scalar_prefetch=2,
        grid=(n_slots // ns,),
        in_specs=[
            pl.BlockSpec((ns, rows, head), lambda n, lr, br: (n, 0, 0)),
            pl.BlockSpec((ns, width, keys.shape[2]), lambda n, lr, br: (n, 0, 0)),
            pl.BlockSpec((ns, width, values.shape[2]), lambda n, lr, br: (n, 0, 0)),
        ],
        out_specs=[
            pl.BlockSpec((ns, rows, 1), lambda n, lr, br: (n, 0, 0)),
            pl.BlockSpec((ns, rows, 1), lambda n, lr, br: (n, 0, 0)),
            pl.BlockSpec((ns, rows, head), lambda n, lr, br: (n, 0, 0)),
        ],
    )
    return pl.pallas_call(
        partial(slot_kernel, ns=ns, heads=heads, qpk=qpk),
        grid_spec=grid_spec,
        out_shape=[
            jax.ShapeDtypeStruct((n_slots, rows, 1), jnp.float32),
            jax.ShapeDtypeStruct((n_slots, rows, 1), jnp.float32),
            jax.ShapeDtypeStruct((n_slots, rows, head), jnp.float32),
        ],
    )(slot_lengths, block_numbers, slot_queries, keys, values)


def pair_gather(part, axis_name):
    n = lax.axis_size(axis_name)
    assert n == 2
    side = lax.axis_index(axis_name)
    other = lax.ppermute(part, axis_name, [(0, 1), (1, 0)])
    return jnp.where(
        side == 0,
        jnp.concatenate([part, other], 0),
        jnp.concatenate([other, part], 0),
    )


def pair_scatter(parts, axis_name, rounded=True):
    n = lax.axis_size(axis_name)
    assert n == 2 and parts.shape[0] == 2
    side = lax.axis_index(axis_name)
    keep = lax.dynamic_index_in_dim(parts, side, 0, keepdims=True)
    send = lax.dynamic_index_in_dim(parts, 1 - side, 0, keepdims=True)
    got = lax.ppermute(send, axis_name, [(0, 1), (1, 0)])
    total = (keep.astype(jnp.float32) + got.astype(jnp.float32))[0]
    return total.astype(parts.dtype) if rounded else total


def doubling_gather(part, axis_name):
    n = lax.axis_size(axis_name)
    stages = n.bit_length() - 1
    assert 1 << stages == n
    index = lax.axis_index(axis_name)
    block = part[None]
    for bit in reversed(range(stages)):
        pairs = [(s, s ^ (1 << bit)) for s in range(n)]
        got = lax.ppermute(block, axis_name, pairs)
        low = ((index >> bit) & 1) == 0
        block = jnp.where(
            low, jnp.stack([block, got], 0), jnp.stack([got, block], 0)
        )
    block = block.reshape((2,) * stages + part.shape)
    block = block.transpose(tuple(reversed(range(stages))) + tuple(range(stages, stages + part.ndim)))
    return block.reshape((n * part.shape[0],) + part.shape[1:])


def seq_merge(peak, total, acc, n_seq, seq_index):
    stages = n_seq.bit_length() - 1
    assert 1 << stages == n_seq
    req_count = peak.shape[0]
    per = req_count // n_seq
    rest = peak.shape[1:]
    split = [2] * stages + [per]
    stats = jnp.stack([peak, total], 0).reshape([2] + split + list(rest))
    values = acc.reshape(split + list(acc.shape[1:]))
    for bit in range(stages):
        axis = stages - 1 - bit
        mine = (seq_index >> bit) & 1
        pairs = [(s, s ^ (1 << bit)) for s in range(n_seq)]
        keep_stats = lax.dynamic_index_in_dim(stats, mine, axis + 1, keepdims=True)
        send_stats = lax.dynamic_index_in_dim(stats, 1 - mine, axis + 1, keepdims=True)
        keep_values = lax.dynamic_index_in_dim(values, mine, axis, keepdims=True)
        send_values = lax.dynamic_index_in_dim(values, 1 - mine, axis, keepdims=True)
        got_stats = lax.ppermute(send_stats, "seq", pairs)
        got_values = lax.ppermute(send_values.astype(jnp.bfloat16), "seq", pairs).astype(
            jnp.float32
        )
        top = jnp.maximum(keep_stats[0], got_stats[0])
        keep_factor = jnp.exp(keep_stats[0] - top)
        got_factor = jnp.exp(got_stats[0] - top)
        stats = jnp.stack(
            [top, keep_stats[1] * keep_factor + got_stats[1] * got_factor], 0
        )
        values = keep_values * keep_factor[..., None] + got_values * got_factor[..., None]
    stats = stats.reshape((2, per) + tuple(rest))
    values = values.reshape((per,) + tuple(acc.shape[1:]))
    return (stats[0], stats[1], values)


def on_device(
    states,
    norm_gain,
    wq,
    wk,
    wv,
    wo,
    lengths,
    slot_request,
    slot_block_number,
    paged_key_cache,
    paged_value_cache,
):
    q_width = wq.shape[1]
    k_width = wk.shape[1]
    heads_kv = k_width // HEAD_SIZE
    req_count = lengths.shape[0]
    block_len = paged_key_cache.shape[1]
    key_rows = paged_key_cache.reshape(paged_key_cache.shape[0], block_len, heads_kv, HEAD_SIZE)
    value_rows = paged_value_cache.reshape(
        paged_value_cache.shape[0], block_len, heads_kv, HEAD_SIZE
    )
    step_count = states.shape[1]
    token_count = states.shape[0] * step_count
    own_states = states.reshape(token_count, -1)
    side = lax.axis_index("col")
    swap = [(0, 1), (1, 0)]
    other_states = lax.ppermute(own_states, "col", swap)
    as_float = own_states.astype(jnp.float32)
    squares = lax.psum(jnp.sum(as_float * as_float, -1), "row")
    other_squares = lax.ppermute(squares, "col", swap)

    def rms_norm(rows, sums):
        scale = lax.rsqrt(sums / D + EPSILON)[:, None]
        return (rows.astype(jnp.float32) * scale * norm_gain).astype(jnp.bfloat16)

    first = side == 0
    gathered = jnp.concatenate(
        [
            rms_norm(
                jnp.where(first, own_states, other_states), jnp.where(first, squares, other_squares)
            ),
            rms_norm(
                jnp.where(first, other_states, own_states), jnp.where(first, other_squares, squares)
            ),
        ],
        0,
    )
    parts_out = [
        jnp.dot(gathered, matrix, preferred_element_type=jnp.float32) for matrix in (wq, wk, wv)
    ]
    output_projected = (
        pair_scatter(
            jnp.concatenate(parts_out, axis=-1)
            .astype(jnp.bfloat16)
            .reshape(lax.axis_size("row"), token_count, -1),
            "row",
            rounded=False,
        )
        .reshape(req_count, step_count, -1)
    )
    token_positions = lengths[:, None] + jnp.arange(step_count, dtype=jnp.int32)[None, :]
    query_rows = rotary_apply(
        output_projected[..., :q_width].reshape(req_count, step_count, -1, HEAD_SIZE),
        token_positions,
    ).astype(jnp.bfloat16)
    query_rows = query_rows.reshape(req_count, step_count, heads_kv, QUERY_PER_KEY, HEAD_SIZE)
    current_key = rotary_apply(
        output_projected[..., q_width : q_width + k_width].reshape(
            req_count, step_count, heads_kv, HEAD_SIZE
        ),
        token_positions,
    ).astype(jnp.bfloat16)
    current_value = (
        output_projected[..., q_width + k_width :]
        .reshape(req_count, step_count, heads_kv, HEAD_SIZE)
        .astype(jnp.bfloat16)
    )
    picked = jnp.minimum(slot_request, req_count - 1)
    in_use = slot_request < req_count
    slot_lengths = jnp.where(in_use, lengths[picked], 0)
    flat_queries = query_rows.transpose(0, 2, 1, 3, 4).reshape(req_count, -1, HEAD_SIZE)
    slot_peak, slot_total, slot_acc = slot_attention(
        flat_queries[picked],
        slot_lengths,
        slot_block_number,
        paged_key_cache,
        paged_value_cache,
        heads_kv,
        QUERY_PER_KEY,
    )
    slot_peak = slot_peak[..., 0]
    slot_total = slot_total[..., 0]
    member = slot_request[None, :] == jnp.arange(req_count, dtype=jnp.int32)[:, None]
    local_peak = jnp.max(jnp.where(member[:, :, None], slot_peak[None], NEGATIVE_FILL), 1)
    factor = jnp.exp(slot_peak - local_peak[picked])
    as_member = member.astype(jnp.float32)
    local_totals = jnp.einsum(
        "rn,nj->rj", as_member, slot_total * factor, precision=lax.Precision.HIGHEST
    )
    local_values = jnp.einsum(
        "rn,njh->rjh", as_member, slot_acc * factor[..., None], precision=lax.Precision.HIGHEST
    )
    n_seq = lax.axis_size("seq")
    per = req_count // n_seq
    seq_index = lax.axis_index("seq")
    mine = seq_index * per
    running_peak, running_totals, weighted_values = seq_merge(
        local_peak, local_totals, local_values, n_seq, seq_index
    )
    order = (per, heads_kv, step_count, QUERY_PER_KEY)
    running_peak = running_peak.reshape(order)
    running_totals = running_totals.reshape(order)
    weighted_values = weighted_values.reshape(order + (HEAD_SIZE,))
    own_queries = lax.dynamic_slice_in_dim(query_rows, mine, per, 0)
    fresh = fresh_part(
        own_queries,
        lax.dynamic_slice_in_dim(current_key, mine, per, 0),
        lax.dynamic_slice_in_dim(current_value, mine, per, 0),
    )
    running_peak, running_totals, weighted_values = merge_parts(
        (running_peak, running_totals, weighted_values), fresh
    )
    heads_out = (
        (weighted_values / running_totals[..., None])
        .transpose(0, 2, 1, 3, 4)
        .reshape(per, step_count, -1)
        .astype(jnp.bfloat16)
    )
    piece_rows = lax.all_gather(heads_out, "row", axis=0, tiled=False)
    n_row = piece_rows.shape[0]
    product = jnp.dot(
        piece_rows.reshape(n_row * per * step_count, -1), wo, preferred_element_type=jnp.float32
    )
    partials = product.reshape(n_row, per, step_count, -1)
    own_out = pair_scatter(partials.astype(jnp.bfloat16), "col").reshape(per, step_count, -1)
    attended = doubling_gather(own_out, "seq")
    return (
        attended,
        current_key.reshape(req_count, step_count, k_width),
        current_value.reshape(req_count, step_count, k_width),
    )


def solution(mesh):
    in_specs = (
        P("col", None, "row"),
        P("row"),
        P("row", "col"),
        P("row", "col"),
        P("row", "col"),
        P("col", "row"),
        P("row"),
        P(("row", "seq")),
        P(("row", "seq")),
        P(("row", "seq"), None, "col"),
        P(("row", "seq"), None, "col"),
    )
    out_specs = (P("col", None, "row"), P("row", None, "col"), P("row", None, "col"))
    return jax.shard_map(
        on_device, mesh=mesh, in_specs=in_specs, out_specs=out_specs, check_vma=False
    )
```

```python
import math
from functools import partial

import jax
import jax.numpy as jnp
from jax import lax
from jax.experimental import pallas as pl
from jax.experimental.pallas import tpu as pltpu
from jax.sharding import PartitionSpec as P

D = 5120
HEAD_SIZE = 128
WINDOW = 4096
SINK = 4
QUERY_PER_KEY = 4


EPSILON = 1e-05
NEGATIVE_FILL = -1e30
ROPE_BASE = 100000000.0


def rotary_apply(values, token_positions):
    half_dim = values.shape[-1] // 2
    frequency = ROPE_BASE ** (-(jnp.arange(half_dim, dtype=jnp.float32) * 2.0 / values.shape[-1]))
    angles = (token_positions.astype(jnp.float32)[..., None] * frequency)[..., None, :]
    cosine = jnp.cos(angles)
    sine_part = jnp.sin(angles)
    lower = values[..., :half_dim]
    upper = values[..., half_dim:]
    return jnp.concatenate(
        [lower * cosine - upper * sine_part, upper * cosine + lower * sine_part], -1
    )


def slot_parts(query_rows, lengths, slot_request, slot_block_number, key_rows, value_rows):
    req_count = query_rows.shape[0]
    step_count = query_rows.shape[1]
    block_len = key_rows.shape[1]
    picked = jnp.minimum(slot_request, req_count - 1)
    in_use = slot_request < req_count
    slot_queries = query_rows[picked]
    scores = jnp.einsum(
        "nsagh,nbah->nasgb", slot_queries, key_rows, preferred_element_type=jnp.float32
    ) * (1.0 / math.sqrt(HEAD_SIZE))
    key_pos = (
        slot_block_number[:, None] * block_len + jnp.arange(block_len, dtype=jnp.int32)[None, :]
    )
    own_len = lengths[picked]
    query_pos = own_len[:, None] + jnp.arange(step_count, dtype=jnp.int32)[None, :]
    visible = (
        in_use[:, None, None]
        & (key_pos[:, None, :] < own_len[:, None, None])
        & ((key_pos[:, None, :] < SINK) | (key_pos[:, None, :] > query_pos[:, :, None] - WINDOW))
    )
    visible = visible[:, None, :, None, :]
    slot_peak = jnp.max(jnp.where(visible, scores, NEGATIVE_FILL), -1)
    weights = jnp.where(visible, jnp.exp(scores - slot_peak[..., None]), 0.0)
    slot_total = jnp.sum(weights, -1)
    slot_acc = jnp.einsum(
        "nasgb,nbah->nasgh",
        weights.astype(jnp.bfloat16),
        value_rows,
        preferred_element_type=jnp.float32,
    )
    member = slot_request[None, :] == jnp.arange(req_count, dtype=jnp.int32)[:, None]
    local_peak = jnp.max(
        jnp.where(member[:, :, None, None, None], slot_peak[None], NEGATIVE_FILL), 1
    )
    return (local_peak, (slot_peak, slot_total, slot_acc, member, picked))


def pool_sums(held, running_peak):
    slot_peak, slot_total, slot_acc, member, picked = held
    factor = jnp.exp(slot_peak - running_peak[picked])
    as_member = member.astype(jnp.float32)
    running_totals = jnp.einsum(
        "rn,nasg->rasg", as_member, slot_total * factor, precision=lax.Precision.HIGHEST
    )
    weighted_values = jnp.einsum(
        "rn,nasgh->rasgh", as_member, slot_acc * factor[..., None], precision=lax.Precision.HIGHEST
    )
    return (running_totals, weighted_values)


def fresh_part(query_rows, key_all, value_all):
    step_count = query_rows.shape[1]
    used = key_all.shape[1]
    scores = jnp.einsum(
        "rsagh,ruah->rasgu", query_rows, key_all, preferred_element_type=jnp.float32
    ) * (1.0 / math.sqrt(HEAD_SIZE))
    causal = (
        jnp.arange(used, dtype=jnp.int32)[None, :]
        <= jnp.arange(step_count, dtype=jnp.int32)[:, None]
    )
    causal = causal[None, None, :, None, :]
    running_peak = jnp.max(jnp.where(causal, scores, NEGATIVE_FILL), -1)
    weights = jnp.where(causal, jnp.exp(scores - running_peak[..., None]), 0.0)
    running_totals = jnp.sum(weights, -1)
    weighted_values = jnp.einsum(
        "rasgu,ruah->rasgh",
        weights.astype(jnp.bfloat16),
        value_all,
        preferred_element_type=jnp.float32,
    )
    return (running_peak, running_totals, weighted_values)


def merge_parts(earlier, later):
    running_peak = jnp.maximum(earlier[0], later[0])
    first_factor = jnp.exp(earlier[0] - running_peak)
    second_factor = jnp.exp(later[0] - running_peak)
    running_totals = earlier[1] * first_factor + later[1] * second_factor
    weighted_values = earlier[2] * first_factor[..., None] + later[2] * second_factor[..., None]
    return (running_peak, running_totals, weighted_values)


def slot_kernel(len_ref, blk_ref, q_ref, k_ref, v_ref, peak_ref, tot_ref, acc_ref, *, ns, heads, qpk):
    base = pl.program_id(0) * ns
    rows = q_ref.shape[1]
    group = rows // heads
    width = k_ref.shape[1]
    head = k_ref.shape[2] // heads
    row = lax.broadcasted_iota(jnp.int32, (rows, width), 0)
    col = lax.broadcasted_iota(jnp.int32, (rows, width), 1)
    step_of = (row % group) // qpk

    def body(i, carry):
        length = len_ref[base + i]
        key_pos = blk_ref[base + i] * width + col
        query_pos = length + step_of
        visible = (key_pos < length) & ((key_pos < SINK) | (key_pos > query_pos - WINDOW))
        q = q_ref[i]
        k = k_ref[i]
        v = v_ref[i]
        scores = jnp.concatenate(
            [
                lax.dot_general(
                    q[a * group : (a + 1) * group],
                    k[:, a * head : (a + 1) * head],
                    (((1,), (1,)), ((), ())),
                    preferred_element_type=jnp.float32,
                )
                for a in range(heads)
            ],
            0,
        ) * (1.0 / math.sqrt(HEAD_SIZE))
        peak = jnp.max(jnp.where(visible, scores, NEGATIVE_FILL), axis=1, keepdims=True)
        weights = jnp.where(visible, jnp.exp(scores - peak), 0.0)
        total = jnp.sum(weights, axis=1, keepdims=True)
        rounded = weights.astype(jnp.bfloat16)
        acc = jnp.concatenate(
            [
                jnp.dot(
                    rounded[a * group : (a + 1) * group],
                    v[:, a * head : (a + 1) * head],
                    preferred_element_type=jnp.float32,
                )
                for a in range(heads)
            ],
            0,
        )
        peak_ref[i] = peak
        tot_ref[i] = total
        acc_ref[i] = acc
        return carry

    lax.fori_loop(0, ns, body, 0, unroll=True)


def slot_attention(slot_queries, slot_lengths, block_numbers, keys, values, heads, qpk):
    n_slots, rows, head = slot_queries.shape
    width = keys.shape[1]
    ns = max(d for d in range(1, 11) if n_slots % d == 0)
    grid_spec = pltpu.PrefetchScalarGridSpec(
        num_scalar_prefetch=2,
        grid=(n_slots // ns,),
        in_specs=[
            pl.BlockSpec((ns, rows, head), lambda n, lr, br: (n, 0, 0)),
            pl.BlockSpec((ns, width, keys.shape[2]), lambda n, lr, br: (n, 0, 0)),
            pl.BlockSpec((ns, width, values.shape[2]), lambda n, lr, br: (n, 0, 0)),
        ],
        out_specs=[
            pl.BlockSpec((ns, rows, 1), lambda n, lr, br: (n, 0, 0)),
            pl.BlockSpec((ns, rows, 1), lambda n, lr, br: (n, 0, 0)),
            pl.BlockSpec((ns, rows, head), lambda n, lr, br: (n, 0, 0)),
        ],
    )
    return pl.pallas_call(
        partial(slot_kernel, ns=ns, heads=heads, qpk=qpk),
        grid_spec=grid_spec,
        out_shape=[
            jax.ShapeDtypeStruct((n_slots, rows, 1), jnp.float32),
            jax.ShapeDtypeStruct((n_slots, rows, 1), jnp.float32),
            jax.ShapeDtypeStruct((n_slots, rows, head), jnp.float32),
        ],
    )(slot_lengths, block_numbers, slot_queries, keys, values)


def pair_gather(part, axis_name):
    n = lax.axis_size(axis_name)
    assert n == 2
    side = lax.axis_index(axis_name)
    other = lax.ppermute(part, axis_name, [(0, 1), (1, 0)])
    return jnp.where(
        side == 0,
        jnp.concatenate([part, other], 0),
        jnp.concatenate([other, part], 0),
    )


def pair_scatter(parts, axis_name, rounded=True):
    n = lax.axis_size(axis_name)
    assert n == 2 and parts.shape[0] == 2
    side = lax.axis_index(axis_name)
    keep = lax.dynamic_index_in_dim(parts, side, 0, keepdims=True)
    send = lax.dynamic_index_in_dim(parts, 1 - side, 0, keepdims=True)
    got = lax.ppermute(send, axis_name, [(0, 1), (1, 0)])
    total = (keep.astype(jnp.float32) + got.astype(jnp.float32))[0]
    return total.astype(parts.dtype) if rounded else total


def doubling_gather(part, axis_name):
    n = lax.axis_size(axis_name)
    stages = n.bit_length() - 1
    assert 1 << stages == n
    index = lax.axis_index(axis_name)
    block = part[None]
    for bit in reversed(range(stages)):
        pairs = [(s, s ^ (1 << bit)) for s in range(n)]
        got = lax.ppermute(block, axis_name, pairs)
        low = ((index >> bit) & 1) == 0
        block = jnp.where(
            low, jnp.stack([block, got], 0), jnp.stack([got, block], 0)
        )
    block = block.reshape((2,) * stages + part.shape)
    block = block.transpose(tuple(reversed(range(stages))) + tuple(range(stages, stages + part.ndim)))
    return block.reshape((n * part.shape[0],) + part.shape[1:])


def seq_merge(peak, total, acc, n_seq, seq_index):
    stages = n_seq.bit_length() - 1
    assert 1 << stages == n_seq
    req_count = peak.shape[0]
    per = req_count // n_seq
    rest = peak.shape[1:]
    split = [2] * stages + [per]
    stats = jnp.stack([peak, total], 0).reshape([2] + split + list(rest))
    values = acc.reshape(split + list(acc.shape[1:]))
    for bit in range(stages):
        axis = stages - 1 - bit
        mine = (seq_index >> bit) & 1
        pairs = [(s, s ^ (1 << bit)) for s in range(n_seq)]
        keep_stats = lax.dynamic_index_in_dim(stats, mine, axis + 1, keepdims=True)
        send_stats = lax.dynamic_index_in_dim(stats, 1 - mine, axis + 1, keepdims=True)
        keep_values = lax.dynamic_index_in_dim(values, mine, axis, keepdims=True)
        send_values = lax.dynamic_index_in_dim(values, 1 - mine, axis, keepdims=True)
        got_stats = lax.ppermute(send_stats, "seq", pairs)
        got_values = lax.ppermute(send_values.astype(jnp.bfloat16), "seq", pairs).astype(
            jnp.float32
        )
        top = jnp.maximum(keep_stats[0], got_stats[0])
        keep_factor = jnp.exp(keep_stats[0] - top)
        got_factor = jnp.exp(got_stats[0] - top)
        stats = jnp.stack(
            [top, keep_stats[1] * keep_factor + got_stats[1] * got_factor], 0
        )
        values = keep_values * keep_factor[..., None] + got_values * got_factor[..., None]
    stats = stats.reshape((2, per) + tuple(rest))
    values = values.reshape((per,) + tuple(acc.shape[1:]))
    return (stats[0], stats[1], values)


def on_device(
    states,
    norm_gain,
    wq,
    wk,
    wv,
    wo,
    lengths,
    slot_request,
    slot_block_number,
    paged_key_cache,
    paged_value_cache,
):
    q_width = wq.shape[1]
    k_width = wk.shape[1]
    heads_kv = k_width // HEAD_SIZE
    req_count = lengths.shape[0]
    block_len = paged_key_cache.shape[1]
    key_rows = paged_key_cache.reshape(paged_key_cache.shape[0], block_len, heads_kv, HEAD_SIZE)
    value_rows = paged_value_cache.reshape(
        paged_value_cache.shape[0], block_len, heads_kv, HEAD_SIZE
    )
    step_count = states.shape[1]
    token_count = states.shape[0] * step_count
    own_states = states.reshape(token_count, -1)
    side = lax.axis_index("col")
    swap = [(0, 1), (1, 0)]
    half = token_count // 2
    other_states = jnp.concatenate(
        [
            lax.ppermute(own_states[:half], "col", swap),
            lax.ppermute(own_states[half:], "col", swap),
        ],
        0,
    )
    as_float = own_states.astype(jnp.float32)
    squares = lax.psum(jnp.sum(as_float * as_float, -1), "row")
    other_squares = lax.ppermute(squares, "col", swap)

    def rms_norm(rows, sums):
        scale = lax.rsqrt(sums / D + EPSILON)[:, None]
        return (rows.astype(jnp.float32) * scale * norm_gain).astype(jnp.bfloat16)

    first = side == 0
    gathered = jnp.concatenate(
        [
            rms_norm(
                jnp.where(first, own_states, other_states), jnp.where(first, squares, other_squares)
            ),
            rms_norm(
                jnp.where(first, other_states, own_states), jnp.where(first, other_squares, squares)
            ),
        ],
        0,
    )
    parts_out = [
        jnp.dot(gathered, matrix, preferred_element_type=jnp.float32) for matrix in (wq, wk, wv)
    ]
    output_projected = (
        pair_scatter(
            jnp.concatenate(parts_out, axis=-1)
            .astype(jnp.bfloat16)
            .reshape(lax.axis_size("row"), token_count, -1),
            "row",
            rounded=False,
        )
        .reshape(req_count, step_count, -1)
    )
    token_positions = lengths[:, None] + jnp.arange(step_count, dtype=jnp.int32)[None, :]
    query_rows = rotary_apply(
        output_projected[..., :q_width].reshape(req_count, step_count, -1, HEAD_SIZE),
        token_positions,
    ).astype(jnp.bfloat16)
    query_rows = query_rows.reshape(req_count, step_count, heads_kv, QUERY_PER_KEY, HEAD_SIZE)
    current_key = rotary_apply(
        output_projected[..., q_width : q_width + k_width].reshape(
            req_count, step_count, heads_kv, HEAD_SIZE
        ),
        token_positions,
    ).astype(jnp.bfloat16)
    current_value = (
        output_projected[..., q_width + k_width :]
        .reshape(req_count, step_count, heads_kv, HEAD_SIZE)
        .astype(jnp.bfloat16)
    )
    picked = jnp.minimum(slot_request, req_count - 1)
    in_use = slot_request < req_count
    slot_lengths = jnp.where(in_use, lengths[picked], 0)
    flat_queries = query_rows.transpose(0, 2, 1, 3, 4).reshape(req_count, -1, HEAD_SIZE)
    slot_peak, slot_total, slot_acc = slot_attention(
        flat_queries[picked],
        slot_lengths,
        slot_block_number,
        paged_key_cache,
        paged_value_cache,
        heads_kv,
        QUERY_PER_KEY,
    )
    slot_peak = slot_peak[..., 0]
    slot_total = slot_total[..., 0]
    member = slot_request[None, :] == jnp.arange(req_count, dtype=jnp.int32)[:, None]
    local_peak = jnp.max(jnp.where(member[:, :, None], slot_peak[None], NEGATIVE_FILL), 1)
    factor = jnp.exp(slot_peak - local_peak[picked])
    as_member = member.astype(jnp.float32)
    local_totals = jnp.einsum(
        "rn,nj->rj", as_member, slot_total * factor, precision=lax.Precision.HIGHEST
    )
    local_values = jnp.einsum(
        "rn,njh->rjh", as_member, slot_acc * factor[..., None], precision=lax.Precision.HIGHEST
    )
    n_seq = lax.axis_size("seq")
    per = req_count // n_seq
    seq_index = lax.axis_index("seq")
    mine = seq_index * per
    running_peak, running_totals, weighted_values = seq_merge(
        local_peak, local_totals, local_values, n_seq, seq_index
    )
    order = (per, heads_kv, step_count, QUERY_PER_KEY)
    running_peak = running_peak.reshape(order)
    running_totals = running_totals.reshape(order)
    weighted_values = weighted_values.reshape(order + (HEAD_SIZE,))
    own_queries = lax.dynamic_slice_in_dim(query_rows, mine, per, 0)
    fresh = fresh_part(
        own_queries,
        lax.dynamic_slice_in_dim(current_key, mine, per, 0),
        lax.dynamic_slice_in_dim(current_value, mine, per, 0),
    )
    running_peak, running_totals, weighted_values = merge_parts(
        (running_peak, running_totals, weighted_values), fresh
    )
    heads_out = (
        (weighted_values / running_totals[..., None])
        .transpose(0, 2, 1, 3, 4)
        .reshape(per, step_count, -1)
        .astype(jnp.bfloat16)
    )
    piece_rows = lax.all_gather(heads_out, "row", axis=0, tiled=False)
    n_row = piece_rows.shape[0]
    product = jnp.dot(
        piece_rows.reshape(n_row * per * step_count, -1), wo, preferred_element_type=jnp.float32
    )
    partials = product.reshape(n_row, per, step_count, -1)
    own_out = pair_scatter(partials.astype(jnp.bfloat16), "col").reshape(per, step_count, -1)
    attended = doubling_gather(own_out, "seq")
    return (
        attended,
        current_key.reshape(req_count, step_count, k_width),
        current_value.reshape(req_count, step_count, k_width),
    )


def solution(mesh):
    in_specs = (
        P("col", None, "row"),
        P("row"),
        P("row", "col"),
        P("row", "col"),
        P("row", "col"),
        P("col", "row"),
        P("row"),
        P(("row", "seq")),
        P(("row", "seq")),
        P(("row", "seq"), None, "col"),
        P(("row", "seq"), None, "col"),
    )
    out_specs = (P("col", None, "row"), P("row", None, "col"), P("row", None, "col"))
    return jax.shard_map(
        on_device, mesh=mesh, in_specs=in_specs, out_specs=out_specs, check_vma=False
    )
```

```python
import math
from functools import partial

import jax
import jax.numpy as jnp
from jax import lax
from jax.experimental import pallas as pl
from jax.experimental.pallas import tpu as pltpu
from jax.sharding import PartitionSpec as P

D = 5120
HEAD_SIZE = 128
WINDOW = 4096
SINK = 4
QUERY_PER_KEY = 4


EPSILON = 1e-05
NEGATIVE_FILL = -1e30
ROPE_BASE = 100000000.0


def rotary_apply(values, token_positions):
    half_dim = values.shape[-1] // 2
    frequency = ROPE_BASE ** (-(jnp.arange(half_dim, dtype=jnp.float32) * 2.0 / values.shape[-1]))
    angles = (token_positions.astype(jnp.float32)[..., None] * frequency)[..., None, :]
    cosine = jnp.cos(angles)
    sine_part = jnp.sin(angles)
    lower = values[..., :half_dim]
    upper = values[..., half_dim:]
    return jnp.concatenate(
        [lower * cosine - upper * sine_part, upper * cosine + lower * sine_part], -1
    )


def slot_parts(query_rows, lengths, slot_request, slot_block_number, key_rows, value_rows):
    req_count = query_rows.shape[0]
    step_count = query_rows.shape[1]
    block_len = key_rows.shape[1]
    picked = jnp.minimum(slot_request, req_count - 1)
    in_use = slot_request < req_count
    slot_queries = query_rows[picked]
    scores = jnp.einsum(
        "nsagh,nbah->nasgb", slot_queries, key_rows, preferred_element_type=jnp.float32
    ) * (1.0 / math.sqrt(HEAD_SIZE))
    key_pos = (
        slot_block_number[:, None] * block_len + jnp.arange(block_len, dtype=jnp.int32)[None, :]
    )
    own_len = lengths[picked]
    query_pos = own_len[:, None] + jnp.arange(step_count, dtype=jnp.int32)[None, :]
    visible = (
        in_use[:, None, None]
        & (key_pos[:, None, :] < own_len[:, None, None])
        & ((key_pos[:, None, :] < SINK) | (key_pos[:, None, :] > query_pos[:, :, None] - WINDOW))
    )
    visible = visible[:, None, :, None, :]
    slot_peak = jnp.max(jnp.where(visible, scores, NEGATIVE_FILL), -1)
    weights = jnp.where(visible, jnp.exp(scores - slot_peak[..., None]), 0.0)
    slot_total = jnp.sum(weights, -1)
    slot_acc = jnp.einsum(
        "nasgb,nbah->nasgh",
        weights.astype(jnp.bfloat16),
        value_rows,
        preferred_element_type=jnp.float32,
    )
    member = slot_request[None, :] == jnp.arange(req_count, dtype=jnp.int32)[:, None]
    local_peak = jnp.max(
        jnp.where(member[:, :, None, None, None], slot_peak[None], NEGATIVE_FILL), 1
    )
    return (local_peak, (slot_peak, slot_total, slot_acc, member, picked))


def pool_sums(held, running_peak):
    slot_peak, slot_total, slot_acc, member, picked = held
    factor = jnp.exp(slot_peak - running_peak[picked])
    as_member = member.astype(jnp.float32)
    running_totals = jnp.einsum(
        "rn,nasg->rasg", as_member, slot_total * factor, precision=lax.Precision.HIGHEST
    )
    weighted_values = jnp.einsum(
        "rn,nasgh->rasgh", as_member, slot_acc * factor[..., None], precision=lax.Precision.HIGHEST
    )
    return (running_totals, weighted_values)


def fresh_part(query_rows, key_all, value_all):
    step_count = query_rows.shape[1]
    used = key_all.shape[1]
    scores = jnp.einsum(
        "rsagh,ruah->rasgu", query_rows, key_all, preferred_element_type=jnp.float32
    ) * (1.0 / math.sqrt(HEAD_SIZE))
    causal = (
        jnp.arange(used, dtype=jnp.int32)[None, :]
        <= jnp.arange(step_count, dtype=jnp.int32)[:, None]
    )
    causal = causal[None, None, :, None, :]
    running_peak = jnp.max(jnp.where(causal, scores, NEGATIVE_FILL), -1)
    weights = jnp.where(causal, jnp.exp(scores - running_peak[..., None]), 0.0)
    running_totals = jnp.sum(weights, -1)
    weighted_values = jnp.einsum(
        "rasgu,ruah->rasgh",
        weights.astype(jnp.bfloat16),
        value_all,
        preferred_element_type=jnp.float32,
    )
    return (running_peak, running_totals, weighted_values)


def merge_parts(earlier, later):
    running_peak = jnp.maximum(earlier[0], later[0])
    first_factor = jnp.exp(earlier[0] - running_peak)
    second_factor = jnp.exp(later[0] - running_peak)
    running_totals = earlier[1] * first_factor + later[1] * second_factor
    weighted_values = earlier[2] * first_factor[..., None] + later[2] * second_factor[..., None]
    return (running_peak, running_totals, weighted_values)


def slot_kernel(len_ref, blk_ref, q_ref, k_ref, v_ref, peak_ref, tot_ref, acc_ref, *, ns, heads, qpk):
    base = pl.program_id(0) * ns
    rows = q_ref.shape[1]
    group = rows // heads
    width = k_ref.shape[1]
    head = k_ref.shape[2] // heads
    row = lax.broadcasted_iota(jnp.int32, (rows, width), 0)
    col = lax.broadcasted_iota(jnp.int32, (rows, width), 1)
    step_of = (row % group) // qpk

    def body(i, carry):
        length = len_ref[base + i]
        key_pos = blk_ref[base + i] * width + col
        query_pos = length + step_of
        visible = (key_pos < length) & ((key_pos < SINK) | (key_pos > query_pos - WINDOW))
        q = q_ref[i]
        k = k_ref[i]
        v = v_ref[i]
        scores = jnp.concatenate(
            [
                lax.dot_general(
                    q[a * group : (a + 1) * group],
                    k[:, a * head : (a + 1) * head],
                    (((1,), (1,)), ((), ())),
                    preferred_element_type=jnp.float32,
                )
                for a in range(heads)
            ],
            0,
        ) * (1.0 / math.sqrt(HEAD_SIZE))
        peak = jnp.max(jnp.where(visible, scores, NEGATIVE_FILL), axis=1, keepdims=True)
        weights = jnp.where(visible, jnp.exp(scores - peak), 0.0)
        total = jnp.sum(weights, axis=1, keepdims=True)
        rounded = weights.astype(jnp.bfloat16)
        acc = jnp.concatenate(
            [
                jnp.dot(
                    rounded[a * group : (a + 1) * group],
                    v[:, a * head : (a + 1) * head],
                    preferred_element_type=jnp.float32,
                )
                for a in range(heads)
            ],
            0,
        )
        peak_ref[i] = peak
        tot_ref[i] = total
        acc_ref[i] = acc
        return carry

    lax.fori_loop(0, ns, body, 0, unroll=True)


def slot_attention(slot_queries, slot_lengths, block_numbers, keys, values, heads, qpk):
    n_slots, rows, head = slot_queries.shape
    width = keys.shape[1]
    ns = max(d for d in range(1, 11) if n_slots % d == 0)
    grid_spec = pltpu.PrefetchScalarGridSpec(
        num_scalar_prefetch=2,
        grid=(n_slots // ns,),
        in_specs=[
            pl.BlockSpec((ns, rows, head), lambda n, lr, br: (n, 0, 0)),
            pl.BlockSpec((ns, width, keys.shape[2]), lambda n, lr, br: (n, 0, 0)),
            pl.BlockSpec((ns, width, values.shape[2]), lambda n, lr, br: (n, 0, 0)),
        ],
        out_specs=[
            pl.BlockSpec((ns, rows, 1), lambda n, lr, br: (n, 0, 0)),
            pl.BlockSpec((ns, rows, 1), lambda n, lr, br: (n, 0, 0)),
            pl.BlockSpec((ns, rows, head), lambda n, lr, br: (n, 0, 0)),
        ],
    )
    return pl.pallas_call(
        partial(slot_kernel, ns=ns, heads=heads, qpk=qpk),
        grid_spec=grid_spec,
        out_shape=[
            jax.ShapeDtypeStruct((n_slots, rows, 1), jnp.float32),
            jax.ShapeDtypeStruct((n_slots, rows, 1), jnp.float32),
            jax.ShapeDtypeStruct((n_slots, rows, head), jnp.float32),
        ],
    )(slot_lengths, block_numbers, slot_queries, keys, values)


def pair_gather(part, axis_name):
    n = lax.axis_size(axis_name)
    assert n == 2
    side = lax.axis_index(axis_name)
    other = lax.ppermute(part, axis_name, [(0, 1), (1, 0)])
    return jnp.where(
        side == 0,
        jnp.concatenate([part, other], 0),
        jnp.concatenate([other, part], 0),
    )


def pair_scatter(parts, axis_name, rounded=True):
    n = lax.axis_size(axis_name)
    assert n == 2 and parts.shape[0] == 2
    side = lax.axis_index(axis_name)
    keep = lax.dynamic_index_in_dim(parts, side, 0, keepdims=True)
    send = lax.dynamic_index_in_dim(parts, 1 - side, 0, keepdims=True)
    got = lax.ppermute(send, axis_name, [(0, 1), (1, 0)])
    total = (keep.astype(jnp.float32) + got.astype(jnp.float32))[0]
    return total.astype(parts.dtype) if rounded else total


def doubling_gather(part, axis_name):
    n = lax.axis_size(axis_name)
    stages = n.bit_length() - 1
    assert 1 << stages == n
    index = lax.axis_index(axis_name)
    block = part[None]
    for bit in reversed(range(stages)):
        pairs = [(s, s ^ (1 << bit)) for s in range(n)]
        got = lax.ppermute(block, axis_name, pairs)
        low = ((index >> bit) & 1) == 0
        block = jnp.where(
            low, jnp.stack([block, got], 0), jnp.stack([got, block], 0)
        )
    block = block.reshape((2,) * stages + part.shape)
    block = block.transpose(tuple(reversed(range(stages))) + tuple(range(stages, stages + part.ndim)))
    return block.reshape((n * part.shape[0],) + part.shape[1:])


def seq_merge(peak, total, acc, n_seq, seq_index):
    stages = n_seq.bit_length() - 1
    assert 1 << stages == n_seq
    req_count = peak.shape[0]
    per = req_count // n_seq
    rest = peak.shape[1:]
    split = [2] * stages + [per]
    stats = jnp.stack([peak, total], 0).reshape([2] + split + list(rest))
    values = acc.reshape(split + list(acc.shape[1:]))
    for bit in range(stages):
        axis = stages - 1 - bit
        mine = (seq_index >> bit) & 1
        pairs = [(s, s ^ (1 << bit)) for s in range(n_seq)]
        keep_stats = lax.dynamic_index_in_dim(stats, mine, axis + 1, keepdims=True)
        send_stats = lax.dynamic_index_in_dim(stats, 1 - mine, axis + 1, keepdims=True)
        keep_values = lax.dynamic_index_in_dim(values, mine, axis, keepdims=True)
        send_values = lax.dynamic_index_in_dim(values, 1 - mine, axis, keepdims=True)
        got_stats = lax.ppermute(send_stats, "seq", pairs)
        got_values = lax.ppermute(send_values.astype(jnp.bfloat16), "seq", pairs).astype(
            jnp.float32
        )
        top = jnp.maximum(keep_stats[0], got_stats[0])
        keep_factor = jnp.exp(keep_stats[0] - top)
        got_factor = jnp.exp(got_stats[0] - top)
        stats = jnp.stack(
            [top, keep_stats[1] * keep_factor + got_stats[1] * got_factor], 0
        )
        values = keep_values * keep_factor[..., None] + got_values * got_factor[..., None]
    stats = stats.reshape((2, per) + tuple(rest))
    values = values.reshape((per,) + tuple(acc.shape[1:]))
    return (stats[0], stats[1], values)


def on_device(
    states,
    norm_gain,
    wq,
    wk,
    wv,
    wo,
    lengths,
    slot_request,
    slot_block_number,
    paged_key_cache,
    paged_value_cache,
):
    q_width = wq.shape[1]
    k_width = wk.shape[1]
    heads_kv = k_width // HEAD_SIZE
    req_count = lengths.shape[0]
    block_len = paged_key_cache.shape[1]
    key_rows = paged_key_cache.reshape(paged_key_cache.shape[0], block_len, heads_kv, HEAD_SIZE)
    value_rows = paged_value_cache.reshape(
        paged_value_cache.shape[0], block_len, heads_kv, HEAD_SIZE
    )
    step_count = states.shape[1]
    token_count = states.shape[0] * step_count
    own_states = states.reshape(token_count, -1)
    side = lax.axis_index("col")
    swap = [(0, 1), (1, 0)]
    other_states = lax.ppermute(own_states, "col", swap)
    as_float = own_states.astype(jnp.float32)
    squares = lax.psum(jnp.sum(as_float * as_float, -1), "row")
    other_squares = lax.ppermute(squares, "col", swap)

    def rms_norm(rows, sums):
        scale = lax.rsqrt(sums / D + EPSILON)[:, None]
        return (rows.astype(jnp.float32) * scale * norm_gain).astype(jnp.bfloat16)

    first = side == 0
    gathered = jnp.concatenate(
        [
            rms_norm(
                jnp.where(first, own_states, other_states), jnp.where(first, squares, other_squares)
            ),
            rms_norm(
                jnp.where(first, other_states, own_states), jnp.where(first, other_squares, squares)
            ),
        ],
        0,
    )
    parts_out = [
        jnp.dot(gathered, matrix, preferred_element_type=jnp.float32) for matrix in (wq, wk, wv)
    ]
    head_count = (q_width + 2 * k_width) // HEAD_SIZE
    output_projected = pair_scatter(
        jnp.concatenate(parts_out, axis=-1)
        .astype(jnp.bfloat16)
        .reshape(lax.axis_size("row"), token_count, -1),
        "row",
        rounded=False,
    ).reshape(token_count, head_count, HEAD_SIZE)
    q_heads = q_width // HEAD_SIZE
    token_positions = (
        lengths[:, None] + jnp.arange(step_count, dtype=jnp.int32)[None, :]
    ).reshape(token_count)
    query_rows = rotary_apply(output_projected[:, :q_heads], token_positions).astype(jnp.bfloat16)
    query_rows = query_rows.reshape(req_count, step_count, heads_kv, QUERY_PER_KEY, HEAD_SIZE)
    current_key = (
        rotary_apply(output_projected[:, q_heads : q_heads + heads_kv], token_positions)
        .astype(jnp.bfloat16)
        .reshape(req_count, step_count, heads_kv, HEAD_SIZE)
    )
    current_value = (
        output_projected[:, q_heads + heads_kv :]
        .astype(jnp.bfloat16)
        .reshape(req_count, step_count, heads_kv, HEAD_SIZE)
    )
    picked = jnp.minimum(slot_request, req_count - 1)
    in_use = slot_request < req_count
    slot_queries = query_rows[picked]
    scores = jnp.einsum(
        "nsagh,nbah->nasgb", slot_queries, key_rows, preferred_element_type=jnp.float32
    ) * (1.0 / math.sqrt(HEAD_SIZE))
    key_pos = (
        slot_block_number[:, None] * block_len + jnp.arange(block_len, dtype=jnp.int32)[None, :]
    )
    own_len = lengths[picked]
    query_pos = own_len[:, None] + jnp.arange(step_count, dtype=jnp.int32)[None, :]
    visible = (
        in_use[:, None, None]
        & (key_pos[:, None, :] < own_len[:, None, None])
        & ((key_pos[:, None, :] < SINK) | (key_pos[:, None, :] > query_pos[:, :, None] - WINDOW))
    )
    visible = visible[:, None, :, None, :]
    slot_peak = jnp.max(jnp.where(visible, scores, NEGATIVE_FILL), -1)
    weights = jnp.where(visible, jnp.exp(scores - slot_peak[..., None]), 0.0)
    slot_total = jnp.sum(weights, -1)
    slot_acc = jnp.einsum(
        "nasgb,nbah->nasgh",
        weights.astype(jnp.bfloat16),
        value_rows,
        preferred_element_type=jnp.float32,
    )
    member = slot_request[None, :] == jnp.arange(req_count, dtype=jnp.int32)[:, None]
    local_peak = jnp.max(
        jnp.where(member[:, :, None, None, None], slot_peak[None], NEGATIVE_FILL), 1
    )
    return (local_peak, (slot_peak, slot_total, slot_acc, member, picked))


def pool_sums(held, running_peak):
    slot_peak, slot_total, slot_acc, member, picked = held
    factor = jnp.exp(slot_peak - running_peak[picked])
    as_member = member.astype(jnp.float32)
    running_totals = jnp.einsum(
        "rn,nasg->rasg", as_member, slot_total * factor, precision=lax.Precision.HIGHEST
    )
    weighted_values = jnp.einsum(
        "rn,nasgh->rasgh", as_member, slot_acc * factor[..., None], precision=lax.Precision.HIGHEST
    )
    return (running_totals, weighted_values)


def fresh_part(query_rows, key_all, value_all):
    step_count = query_rows.shape[1]
    used = key_all.shape[1]
    scores = jnp.einsum(
        "rsagh,ruah->rasgu", query_rows, key_all, preferred_element_type=jnp.float32
    ) * (1.0 / math.sqrt(HEAD_SIZE))
    causal = (
        jnp.arange(used, dtype=jnp.int32)[None, :]
        <= jnp.arange(step_count, dtype=jnp.int32)[:, None]
    )
    causal = causal[None, None, :, None, :]
    running_peak = jnp.max(jnp.where(causal, scores, NEGATIVE_FILL), -1)
    weights = jnp.where(causal, jnp.exp(scores - running_peak[..., None]), 0.0)
    running_totals = jnp.sum(weights, -1)
    weighted_values = jnp.einsum(
        "rasgu,ruah->rasgh",
        weights.astype(jnp.bfloat16),
        value_all,
        preferred_element_type=jnp.float32,
    )
    return (running_peak, running_totals, weighted_values)


def merge_parts(earlier, later):
    running_peak = jnp.maximum(earlier[0], later[0])
    first_factor = jnp.exp(earlier[0] - running_peak)
    second_factor = jnp.exp(later[0] - running_peak)
    running_totals = earlier[1] * first_factor + later[1] * second_factor
    weighted_values = earlier[2] * first_factor[..., None] + later[2] * second_factor[..., None]
    return (running_peak, running_totals, weighted_values)


def slot_kernel(len_ref, blk_ref, q_ref, k_ref, v_ref, peak_ref, tot_ref, acc_ref, *, ns, heads, qpk):
    base = pl.program_id(0) * ns
    rows = q_ref.shape[1]
    group = rows // heads
    width = k_ref.shape[1]
    head = k_ref.shape[2] // heads
    row = lax.broadcasted_iota(jnp.int32, (rows, width), 0)
    col = lax.broadcasted_iota(jnp.int32, (rows, width), 1)
    step_of = (row % group) // qpk

    def body(i, carry):
        length = len_ref[base + i]
        key_pos = blk_ref[base + i] * width + col
        query_pos = length + step_of
        visible = (key_pos < length) & ((key_pos < SINK) | (key_pos > query_pos - WINDOW))
        q = q_ref[i]
        k = k_ref[i]
        v = v_ref[i]
        scores = jnp.concatenate(
            [
                lax.dot_general(
                    q[a * group : (a + 1) * group],
                    k[:, a * head : (a + 1) * head],
                    (((1,), (1,)), ((), ())),
                    preferred_element_type=jnp.float32,
                )
                for a in range(heads)
            ],
            0,
        ) * (1.0 / math.sqrt(HEAD_SIZE))
        peak = jnp.max(jnp.where(visible, scores, NEGATIVE_FILL), axis=1, keepdims=True)
        weights = jnp.where(visible, jnp.exp(scores - peak), 0.0)
        total = jnp.sum(weights, axis=1, keepdims=True)
        rounded = weights.astype(jnp.bfloat16)
        acc = jnp.concatenate(
            [
                jnp.dot(
                    rounded[a * group : (a + 1) * group],
                    v[:, a * head : (a + 1) * head],
                    preferred_element_type=jnp.float32,
                )
                for a in range(heads)
            ],
            0,
        )
        peak_ref[i] = peak
        tot_ref[i] = total
        acc_ref[i] = acc
        return carry

    lax.fori_loop(0, ns, body, 0, unroll=True)


def slot_attention(slot_queries, slot_lengths, block_numbers, keys, values, heads, qpk):
    n_slots, rows, head = slot_queries.shape
    width = keys.shape[1]
    ns = max(d for d in range(1, 11) if n_slots % d == 0)
    grid_spec = pltpu.PrefetchScalarGridSpec(
        num_scalar_prefetch=2,
        grid=(n_slots // ns,),
        in_specs=[
            pl.BlockSpec((ns, rows, head), lambda n, lr, br: (n, 0, 0)),
            pl.BlockSpec((ns, width, keys.shape[2]), lambda n, lr, br: (n, 0, 0)),
            pl.BlockSpec((ns, width, values.shape[2]), lambda n, lr, br: (n, 0, 0)),
        ],
        out_specs=[
            pl.BlockSpec((ns, rows, 1), lambda n, lr, br: (n, 0, 0)),
            pl.BlockSpec((ns, rows, 1), lambda n, lr, br: (n, 0, 0)),
            pl.BlockSpec((ns, rows, head), lambda n, lr, br: (n, 0, 0)),
        ],
    )
    return pl.pallas_call(
        partial(slot_kernel, ns=ns, heads=heads, qpk=qpk),
        grid_spec=grid_spec,
        out_shape=[
            jax.ShapeDtypeStruct((n_slots, rows, 1), jnp.float32),
            jax.ShapeDtypeStruct((n_slots, rows, 1), jnp.float32),
            jax.ShapeDtypeStruct((n_slots, rows, head), jnp.float32),
        ],
    )(slot_lengths, block_numbers, slot_queries, keys, values)


def pair_gather(part, axis_name):
    n = lax.axis_size(axis_name)
    assert n == 2
    side = lax.axis_index(axis_name)
    other = lax.ppermute(part, axis_name, [(0, 1), (1, 0)])
    return jnp.where(
        side == 0,
        jnp.concatenate([part, other], 0),
        jnp.concatenate([other, part], 0),
    )


def pair_scatter(parts, axis_name, rounded=True):
    n = lax.axis_size(axis_name)
    assert n == 2 and parts.shape[0] == 2
    side = lax.axis_index(axis_name)
    keep = lax.dynamic_index_in_dim(parts, side, 0, keepdims=True)
    send = lax.dynamic_index_in_dim(parts, 1 - side, 0, keepdims=True)
    got = lax.ppermute(send, axis_name, [(0, 1), (1, 0)])
    total = (keep.astype(jnp.float32) + got.astype(jnp.float32))[0]
    return total.astype(parts.dtype) if rounded else total


def doubling_gather(part, axis_name):
    n = lax.axis_size(axis_name)
    stages = n.bit_length() - 1
    assert 1 << stages == n
    index = lax.axis_index(axis_name)
    block = part[None]
    for bit in reversed(range(stages)):
        pairs = [(s, s ^ (1 << bit)) for s in range(n)]
        got = lax.ppermute(block, axis_name, pairs)
        low = ((index >> bit) & 1) == 0
        block = jnp.where(
            low, jnp.stack([block, got], 0), jnp.stack([got, block], 0)
        )
    block = block.reshape((2,) * stages + part.shape)
    block = block.transpose(tuple(reversed(range(stages))) + tuple(range(stages, stages + part.ndim)))
    return block.reshape((n * part.shape[0],) + part.shape[1:])


def seq_merge(peak, total, acc, n_seq, seq_index):
    stages = n_seq.bit_length() - 1
    assert 1 << stages == n_seq
    req_count = peak.shape[0]
    per = req_count // n_seq
    rest = peak.shape[1:]
    split = [2] * stages + [per]
    stats = jnp.stack([peak, total], 0).reshape([2] + split + list(rest))
    values = acc.reshape(split + list(acc.shape[1:]))
    for bit in range(stages):
        axis = stages - 1 - bit
        mine = (seq_index >> bit) & 1
        pairs = [(s, s ^ (1 << bit)) for s in range(n_seq)]
        keep_stats = lax.dynamic_index_in_dim(stats, mine, axis + 1, keepdims=True)
        send_stats = lax.dynamic_index_in_dim(stats, 1 - mine, axis + 1, keepdims=True)
        keep_values = lax.dynamic_index_in_dim(values, mine, axis, keepdims=True)
        send_values = lax.dynamic_index_in_dim(values, 1 - mine, axis, keepdims=True)
        got_stats = lax.ppermute(send_stats, "seq", pairs)
        got_values = lax.ppermute(send_values.astype(jnp.bfloat16), "seq", pairs).astype(
            jnp.float32
        )
        top = jnp.maximum(keep_stats[0], got_stats[0])
        keep_factor = jnp.exp(keep_stats[0] - top)
        got_factor = jnp.exp(got_stats[0] - top)
        stats = jnp.stack(
            [top, keep_stats[1] * keep_factor + got_stats[1] * got_factor], 0
        )
        values = keep_values * keep_factor[..., None] + got_values * got_factor[..., None]
    stats = stats.reshape((2, per) + tuple(rest))
    values = values.reshape((per,) + tuple(acc.shape[1:]))
    return (stats[0], stats[1], values)


def on_device(
    states,
    norm_gain,
    wq,
    wk,
    wv,
    wo,
    lengths,
    slot_request,
    slot_block_number,
    paged_key_cache,
    paged_value_cache,
):
    q_width = wq.shape[1]
    k_width = wk.shape[1]
    heads_kv = k_width // HEAD_SIZE
    req_count = lengths.shape[0]
    block_len = paged_key_cache.shape[1]
    key_rows = paged_key_cache.reshape(paged_key_cache.shape[0], block_len, heads_kv, HEAD_SIZE)
    value_rows = paged_value_cache.reshape(
        paged_value_cache.shape[0], block_len, heads_kv, HEAD_SIZE
    )
    step_count = states.shape[1]
    token_count = states.shape[0] * step_count
    own_states = states.reshape(token_count, -1)
    side = lax.axis_index("col")
    swap = [(0, 1), (1, 0)]
    other_states = lax.ppermute(own_states, "col", swap)
    as_float = own_states.astype(jnp.float32)
    squares = lax.psum(jnp.sum(as_float * as_float, -1), "row")
    other_squares = lax.ppermute(squares, "col", swap)

    def rms_norm(rows, sums):
        scale = lax.rsqrt(sums / D + EPSILON)[:, None]
        return (rows.astype(jnp.float32) * scale * norm_gain).astype(jnp.bfloat16)

    first = side == 0
    gathered = jnp.concatenate(
        [
            rms_norm(
                jnp.where(first, own_states, other_states), jnp.where(first, squares, other_squares)
            ),
            rms_norm(
                jnp.where(first, other_states, own_states), jnp.where(first, other_squares, squares)
            ),
        ],
        0,
    )
    parts_out = [
        jnp.dot(gathered, matrix, preferred_element_type=jnp.float32) for matrix in (wq, wk, wv)
    ]
    output_projected = (
        pair_scatter(
            jnp.concatenate(parts_out, axis=-1)
            .astype(jnp.bfloat16)
            .reshape(lax.axis_size("row"), token_count, -1),
            "row",
            rounded=False,
        )
        .reshape(req_count, step_count, -1)
    )
    token_positions = lengths[:, None] + jnp.arange(step_count, dtype=jnp.int32)[None, :]
    query_rows = rotary_apply(
        output_projected[..., :q_width].reshape(req_count, step_count, -1, HEAD_SIZE),
        token_positions,
    ).astype(jnp.bfloat16)
    query_rows = query_rows.reshape(req_count, step_count, heads_kv, QUERY_PER_KEY, HEAD_SIZE)
    current_key = rotary_apply(
        output_projected[..., q_width : q_width + k_width].reshape(
            req_count, step_count, heads_kv, HEAD_SIZE
        ),
        token_positions,
    ).astype(jnp.bfloat16)
    current_value = (
        output_projected[..., q_width + k_width :]
        .reshape(req_count, step_count, heads_kv, HEAD_SIZE)
        .astype(jnp.bfloat16)
    )
    picked = jnp.minimum(slot_request, req_count - 1)
    in_use = slot_request < req_count
    slot_lengths = jnp.where(in_use, lengths[picked], 0)
    flat_queries = query_rows.transpose(0, 2, 1, 3, 4).reshape(req_count, -1, HEAD_SIZE)
    slot_peak, slot_total, slot_acc = slot_attention(
        flat_queries[picked],
        slot_lengths,
        slot_block_number,
        paged_key_cache,
        paged_value_cache,
        heads_kv,
        QUERY_PER_KEY,
    )
    slot_peak = slot_peak[..., 0]
    slot_total = slot_total[..., 0]
    member = slot_request[None, :] == jnp.arange(req_count, dtype=jnp.int32)[:, None]
    local_peak = jnp.max(jnp.where(member[:, :, None], slot_peak[None], NEGATIVE_FILL), 1)
    factor = jnp.exp(slot_peak - local_peak[picked])
    as_member = member.astype(jnp.float32)
    local_totals = jnp.einsum(
        "rn,nj->rj", as_member, slot_total * factor, precision=lax.Precision.HIGHEST
    )
    local_values = jnp.einsum(
        "rn,njh->rjh", as_member, slot_acc * factor[..., None], precision=lax.Precision.HIGHEST
    )
    n_seq = lax.axis_size("seq")
    per = req_count // n_seq
    seq_index = lax.axis_index("seq")
    mine = seq_index * per
    running_peak, running_totals, weighted_values = seq_merge(
        local_peak, local_totals, local_values, n_seq, seq_index
    )
    order = (per, heads_kv, step_count, QUERY_PER_KEY)
    running_peak = running_peak.reshape(order)
    running_totals = running_totals.reshape(order)
    weighted_values = weighted_values.reshape(order + (HEAD_SIZE,))
    own_queries = lax.dynamic_slice_in_dim(query_rows, mine, per, 0)
    fresh = fresh_part(
        own_queries,
        lax.dynamic_slice_in_dim(current_key, mine, per, 0),
        lax.dynamic_slice_in_dim(current_value, mine, per, 0),
    )
    running_peak, running_totals, weighted_values = merge_parts(
        (running_peak, running_totals, weighted_values), fresh
    )
    heads_out = (
        (weighted_values / running_totals[..., None])
        .transpose(0, 2, 1, 3, 4)
        .reshape(per, step_count, -1)
        .astype(jnp.bfloat16)
    )
    piece_rows = lax.all_gather(heads_out, "row", axis=0, tiled=False)
    n_row = piece_rows.shape[0]
    product = jnp.dot(
        piece_rows.reshape(n_row * per * step_count, -1), wo, preferred_element_type=jnp.float32
    )
    partials = product.reshape(n_row, per, step_count, -1)
    own_out = pair_scatter(partials.astype(jnp.bfloat16), "col").reshape(per, step_count, -1)
    attended = doubling_gather(own_out, "seq")
    return (
        attended,
        current_key.reshape(req_count, step_count, k_width),
        current_value.reshape(req_count, step_count, k_width),
    )


def solution(mesh):
    in_specs = (
        P("col", None, "row"),
        P("row"),
        P("row", "col"),
        P("row", "col"),
        P("row", "col"),
        P("col", "row"),
        P("row"),
        P(("row", "seq")),
        P(("row", "seq")),
        P(("row", "seq"), None, "col"),
        P(("row", "seq"), None, "col"),
    )
    out_specs = (P("col", None, "row"), P("row", None, "col"), P("row", None, "col"))
    return jax.shard_map(
        on_device, mesh=mesh, in_specs=in_specs, out_specs=out_specs, check_vma=False
    )
```

```python
import math
from functools import partial

import jax
import jax.numpy as jnp
from jax import lax
from jax.experimental import pallas as pl
from jax.experimental.pallas import tpu as pltpu
from jax.sharding import PartitionSpec as P

D = 5120
HEAD_SIZE = 128
WINDOW = 4096
SINK = 4
QUERY_PER_KEY = 4


EPSILON = 1e-05
NEGATIVE_FILL = -1e30
ROPE_BASE = 100000000.0


def rotary_apply(values, token_positions):
    half_dim = values.shape[-1] // 2
    frequency = ROPE_BASE ** (-(jnp.arange(half_dim, dtype=jnp.float32) * 2.0 / values.shape[-1]))
    angles = (token_positions.astype(jnp.float32)[..., None] * frequency)[..., None, :]
    cosine = jnp.cos(angles)
    sine_part = jnp.sin(angles)
    lower = values[..., :half_dim]
    upper = values[..., half_dim:]
    return jnp.concatenate(
        [lower * cosine - upper * sine_part, upper * cosine + lower * sine_part], -1
    )


def slot_parts(query_rows, lengths, slot_request, slot_block_number, key_rows, value_rows):
    req_count = query_rows.shape[0]
    step_count = query_rows.shape[1]
    block_len = key_rows.shape[1]
    picked = jnp.minimum(slot_request, req_count - 1)
    in_use = slot_request < req_count
    slot_queries = query_rows[picked]
    scores = jnp.einsum(
        "nsagh,nbah->nasgb", slot_queries, key_rows, preferred_element_type=jnp.float32
    ) * (1.0 / math.sqrt(HEAD_SIZE))
    key_pos = (
        slot_block_number[:, None] * block_len + jnp.arange(block_len, dtype=jnp.int32)[None, :]
    )
    own_len = lengths[picked]
    query_pos = own_len[:, None] + jnp.arange(step_count, dtype=jnp.int32)[None, :]
    visible = (
        in_use[:, None, None]
        & (key_pos[:, None, :] < own_len[:, None, None])
        & ((key_pos[:, None, :] < SINK) | (key_pos[:, None, :] > query_pos[:, :, None] - WINDOW))
    )
    visible = visible[:, None, :, None, :]
    slot_peak = jnp.max(jnp.where(visible, scores, NEGATIVE_FILL), -1)
    weights = jnp.where(visible, jnp.exp(scores - slot_peak[..., None]), 0.0)
    slot_total = jnp.sum(weights, -1)
    slot_acc = jnp.einsum(
        "nasgb,nbah->nasgh",
        weights.astype(jnp.bfloat16),
        value_rows,
        preferred_element_type=jnp.float32,
    )
    member = slot_request[None, :] == jnp.arange(req_count, dtype=jnp.int32)[:, None]
    local_peak = jnp.max(
        jnp.where(member[:, :, None, None, None], slot_peak[None], NEGATIVE_FILL), 1
    )
    return (local_peak, (slot_peak, slot_total, slot_acc, member, picked))


def pool_sums(held, running_peak):
    slot_peak, slot_total, slot_acc, member, picked = held
    factor = jnp.exp(slot_peak - running_peak[picked])
    as_member = member.astype(jnp.float32)
    running_totals = jnp.einsum(
        "rn,nasg->rasg", as_member, slot_total * factor, precision=lax.Precision.HIGHEST
    )
    weighted_values = jnp.einsum(
        "rn,nasgh->rasgh", as_member, slot_acc * factor[..., None], precision=lax.Precision.HIGHEST
    )
    return (running_totals, weighted_values)


def fresh_part(query_rows, key_all, value_all):
    step_count = query_rows.shape[1]
    used = key_all.shape[1]
    scores = jnp.einsum(
        "rsagh,ruah->rasgu", query_rows, key_all, preferred_element_type=jnp.float32
    ) * (1.0 / math.sqrt(HEAD_SIZE))
    causal = (
        jnp.arange(used, dtype=jnp.int32)[None, :]
        <= jnp.arange(step_count, dtype=jnp.int32)[:, None]
    )
    causal = causal[None, None, :, None, :]
    running_peak = jnp.max(jnp.where(causal, scores, NEGATIVE_FILL), -1)
    weights = jnp.where(causal, jnp.exp(scores - running_peak[..., None]), 0.0)
    running_totals = jnp.sum(weights, -1)
    weighted_values = jnp.einsum(
        "rasgu,ruah->rasgh",
        weights.astype(jnp.bfloat16),
        value_all,
        preferred_element_type=jnp.float32,
    )
    return (running_peak, running_totals, weighted_values)


def merge_parts(earlier, later):
    running_peak = jnp.maximum(earlier[0], later[0])
    first_factor = jnp.exp(earlier[0] - running_peak)
    second_factor = jnp.exp(later[0] - running_peak)
    running_totals = earlier[1] * first_factor + later[1] * second_factor
    weighted_values = earlier[2] * first_factor[..., None] + later[2] * second_factor[..., None]
    return (running_peak, running_totals, weighted_values)


def slot_kernel(len_ref, blk_ref, q_ref, k_ref, v_ref, peak_ref, tot_ref, acc_ref, *, ns, heads, qpk):
    base = pl.program_id(0) * ns
    rows = q_ref.shape[1]
    group = rows // heads
    width = k_ref.shape[1]
    head = k_ref.shape[2] // heads
    row = lax.broadcasted_iota(jnp.int32, (rows, width), 0)
    col = lax.broadcasted_iota(jnp.int32, (rows, width), 1)
    step_of = (row % group) // qpk

    def body(i, carry):
        length = len_ref[base + i]
        key_pos = blk_ref[base + i] * width + col
        query_pos = length + step_of
        visible = (key_pos < length) & ((key_pos < SINK) | (key_pos > query_pos - WINDOW))
        q = q_ref[i]
        k = k_ref[i]
        v = v_ref[i]
        scores = jnp.concatenate(
            [
                lax.dot_general(
                    q[a * group : (a + 1) * group],
                    k[:, a * head : (a + 1) * head],
                    (((1,), (1,)), ((), ())),
                    preferred_element_type=jnp.float32,
                )
                for a in range(heads)
            ],
            0,
        ) * (1.0 / math.sqrt(HEAD_SIZE))
        peak = jnp.max(jnp.where(visible, scores, NEGATIVE_FILL), axis=1, keepdims=True)
        weights = jnp.where(visible, jnp.exp(scores - peak), 0.0)
        total = jnp.sum(weights, axis=1, keepdims=True)
        rounded = weights.astype(jnp.bfloat16)
        acc = jnp.concatenate(
            [
                jnp.dot(
                    rounded[a * group : (a + 1) * group],
                    v[:, a * head : (a + 1) * head],
                    preferred_element_type=jnp.float32,
                )
                for a in range(heads)
            ],
            0,
        )
        peak_ref[i] = peak
        tot_ref[i] = total
        acc_ref[i] = acc
        return carry

    lax.fori_loop(0, ns, body, 0, unroll=True)


def slot_attention(slot_queries, slot_lengths, block_numbers, keys, values, heads, qpk):
    n_slots, rows, head = slot_queries.shape
    width = keys.shape[1]
    ns = max(d for d in range(1, 11) if n_slots % d == 0)
    grid_spec = pltpu.PrefetchScalarGridSpec(
        num_scalar_prefetch=2,
        grid=(n_slots // ns,),
        in_specs=[
            pl.BlockSpec((ns, rows, head), lambda n, lr, br: (n, 0, 0)),
            pl.BlockSpec((ns, width, keys.shape[2]), lambda n, lr, br: (n, 0, 0)),
            pl.BlockSpec((ns, width, values.shape[2]), lambda n, lr, br: (n, 0, 0)),
        ],
        out_specs=[
            pl.BlockSpec((ns, rows, 1), lambda n, lr, br: (n, 0, 0)),
            pl.BlockSpec((ns, rows, 1), lambda n, lr, br: (n, 0, 0)),
            pl.BlockSpec((ns, rows, head), lambda n, lr, br: (n, 0, 0)),
        ],
    )
    return pl.pallas_call(
        partial(slot_kernel, ns=ns, heads=heads, qpk=qpk),
        grid_spec=grid_spec,
        out_shape=[
            jax.ShapeDtypeStruct((n_slots, rows, 1), jnp.float32),
            jax.ShapeDtypeStruct((n_slots, rows, 1), jnp.float32),
            jax.ShapeDtypeStruct((n_slots, rows, head), jnp.float32),
        ],
    )(slot_lengths, block_numbers, slot_queries, keys, values)


def pair_gather(part, axis_name):
    n = lax.axis_size(axis_name)
    assert n == 2
    side = lax.axis_index(axis_name)
    other = lax.ppermute(part, axis_name, [(0, 1), (1, 0)])
    return jnp.where(
        side == 0,
        jnp.concatenate([part, other], 0),
        jnp.concatenate([other, part], 0),
    )


def pair_scatter(parts, axis_name, rounded=True):
    n = lax.axis_size(axis_name)
    assert n == 2 and parts.shape[0] == 2
    side = lax.axis_index(axis_name)
    keep = lax.dynamic_index_in_dim(parts, side, 0, keepdims=True)
    send = lax.dynamic_index_in_dim(parts, 1 - side, 0, keepdims=True)
    got = lax.ppermute(send, axis_name, [(0, 1), (1, 0)])
    total = (keep.astype(jnp.float32) + got.astype(jnp.float32))[0]
    return total.astype(parts.dtype) if rounded else total


def doubling_gather(part, axis_name):
    n = lax.axis_size(axis_name)
    stages = n.bit_length() - 1
    assert 1 << stages == n
    index = lax.axis_index(axis_name)
    block = part[None]
    for bit in reversed(range(stages)):
        pairs = [(s, s ^ (1 << bit)) for s in range(n)]
        got = lax.ppermute(block, axis_name, pairs)
        low = ((index >> bit) & 1) == 0
        block = jnp.where(
            low, jnp.stack([block, got], 0), jnp.stack([got, block], 0)
        )
    block = block.reshape((2,) * stages + part.shape)
    block = block.transpose(tuple(reversed(range(stages))) + tuple(range(stages, stages + part.ndim)))
    return block.reshape((n * part.shape[0],) + part.shape[1:])


def seq_merge(peak, total, acc, n_seq, seq_index):
    stages = n_seq.bit_length() - 1
    assert 1 << stages == n_seq
    req_count = peak.shape[0]
    per = req_count // n_seq
    rest = peak.shape[1:]
    split = [2] * stages + [per]
    stats = jnp.stack([peak, total], 0).reshape([2] + split + list(rest))
    values = acc.reshape(split + list(acc.shape[1:]))
    for bit in range(stages):
        axis = stages - 1 - bit
        mine = (seq_index >> bit) & 1
        pairs = [(s, s ^ (1 << bit)) for s in range(n_seq)]
        keep_stats = lax.dynamic_index_in_dim(stats, mine, axis + 1, keepdims=True)
        send_stats = lax.dynamic_index_in_dim(stats, 1 - mine, axis + 1, keepdims=True)
        keep_values = lax.dynamic_index_in_dim(values, mine, axis, keepdims=True)
        send_values = lax.dynamic_index_in_dim(values, 1 - mine, axis, keepdims=True)
        got_stats = lax.ppermute(send_stats, "seq", pairs)
        got_values = lax.ppermute(send_values.astype(jnp.bfloat16), "seq", pairs).astype(
            jnp.float32
        )
        top = jnp.maximum(keep_stats[0], got_stats[0])
        keep_factor = jnp.exp(keep_stats[0] - top)
        got_factor = jnp.exp(got_stats[0] - top)
        stats = jnp.stack(
            [top, keep_stats[1] * keep_factor + got_stats[1] * got_factor], 0
        )
        values = keep_values * keep_factor[..., None] + got_values * got_factor[..., None]
    stats = stats.reshape((2, per) + tuple(rest))
    values = values.reshape((per,) + tuple(acc.shape[1:]))
    return (stats[0], stats[1], values)


def on_device(
    states,
    norm_gain,
    wq,
    wk,
    wv,
    wo,
    lengths,
    slot_request,
    slot_block_number,
    paged_key_cache,
    paged_value_cache,
):
    q_width = wq.shape[1]
    k_width = wk.shape[1]
    heads_kv = k_width // HEAD_SIZE
    req_count = lengths.shape[0]
    block_len = paged_key_cache.shape[1]
    key_rows = paged_key_cache.reshape(paged_key_cache.shape[0], block_len, heads_kv, HEAD_SIZE)
    value_rows = paged_value_cache.reshape(
        paged_value_cache.shape[0], block_len, heads_kv, HEAD_SIZE
    )
    step_count = states.shape[1]
    token_count = states.shape[0] * step_count
    side = lax.axis_index("col")
    swap = [(0, 1), (1, 0)]
    other_states = lax.ppermute(states, "col", swap)
    as_float = states.astype(jnp.float32)
    squares = lax.psum(jnp.sum(as_float * as_float, -1), "row").reshape(token_count)
    other_squares = lax.ppermute(squares, "col", swap)
    own_states = states

    def rms_norm(rows, sums):
        scale = lax.rsqrt(sums / D + EPSILON)[:, None]
        rows = rows.reshape(token_count, -1)
        return (rows.astype(jnp.float32) * scale * norm_gain).astype(jnp.bfloat16)

    first = side == 0
    gathered = jnp.concatenate(
        [
            rms_norm(
                jnp.where(first, own_states, other_states), jnp.where(first, squares, other_squares)
            ),
            rms_norm(
                jnp.where(first, other_states, own_states), jnp.where(first, other_squares, squares)
            ),
        ],
        0,
    )
    parts_out = [
        jnp.dot(gathered, matrix, preferred_element_type=jnp.float32) for matrix in (wq, wk, wv)
    ]
    head_count = (q_width + 2 * k_width) // HEAD_SIZE
    output_projected = pair_scatter(
        jnp.concatenate(parts_out, axis=-1)
        .astype(jnp.bfloat16)
        .reshape(lax.axis_size("row"), token_count, -1),
        "row",
        rounded=False,
    ).reshape(token_count, head_count, HEAD_SIZE)
    q_heads = q_width // HEAD_SIZE
    token_positions = (
        lengths[:, None] + jnp.arange(step_count, dtype=jnp.int32)[None, :]
    ).reshape(token_count)
    query_rows = rotary_apply(output_projected[:, :q_heads], token_positions).astype(jnp.bfloat16)
    query_rows = query_rows.reshape(req_count, step_count, heads_kv, QUERY_PER_KEY, HEAD_SIZE)
    current_key = (
        rotary_apply(output_projected[:, q_heads : q_heads + heads_kv], token_positions)
        .astype(jnp.bfloat16)
        .reshape(req_count, step_count, heads_kv, HEAD_SIZE)
    )
    current_value = (
        output_projected[:, q_heads + heads_kv :]
        .astype(jnp.bfloat16)
        .reshape(req_count, step_count, heads_kv, HEAD_SIZE)
    )
    picked = jnp.minimum(slot_request, req_count - 1)
    in_use = slot_request < req_count
    slot_queries = query_rows[picked]
    scores = jnp.einsum(
        "nsagh,nbah->nasgb", slot_queries, key_rows, preferred_element_type=jnp.float32
    ) * (1.0 / math.sqrt(HEAD_SIZE))
    key_pos = (
        slot_block_number[:, None] * block_len + jnp.arange(block_len, dtype=jnp.int32)[None, :]
    )
    own_len = lengths[picked]
    query_pos = own_len[:, None] + jnp.arange(step_count, dtype=jnp.int32)[None, :]
    visible = (
        in_use[:, None, None]
        & (key_pos[:, None, :] < own_len[:, None, None])
        & ((key_pos[:, None, :] < SINK) | (key_pos[:, None, :] > query_pos[:, :, None] - WINDOW))
    )
    visible = visible[:, None, :, None, :]
    slot_peak = jnp.max(jnp.where(visible, scores, NEGATIVE_FILL), -1)
    weights = jnp.where(visible, jnp.exp(scores - slot_peak[..., None]), 0.0)
    slot_total = jnp.sum(weights, -1)
    slot_acc = jnp.einsum(
        "nasgb,nbah->nasgh",
        weights.astype(jnp.bfloat16),
        value_rows,
        preferred_element_type=jnp.float32,
    )
    member = slot_request[None, :] == jnp.arange(req_count, dtype=jnp.int32)[:, None]
    local_peak = jnp.max(
        jnp.where(member[:, :, None, None, None], slot_peak[None], NEGATIVE_FILL), 1
    )
    return (local_peak, (slot_peak, slot_total, slot_acc, member, picked))


def pool_sums(held, running_peak):
    slot_peak, slot_total, slot_acc, member, picked = held
    factor = jnp.exp(slot_peak - running_peak[picked])
    as_member = member.astype(jnp.float32)
    running_totals = jnp.einsum(
        "rn,nasg->rasg", as_member, slot_total * factor, precision=lax.Precision.HIGHEST
    )
    weighted_values = jnp.einsum(
        "rn,nasgh->rasgh", as_member, slot_acc * factor[..., None], precision=lax.Precision.HIGHEST
    )
    return (running_totals, weighted_values)


def fresh_part(query_rows, key_all, value_all):
    step_count = query_rows.shape[1]
    used = key_all.shape[1]
    scores = jnp.einsum(
        "rsagh,ruah->rasgu", query_rows, key_all, preferred_element_type=jnp.float32
    ) * (1.0 / math.sqrt(HEAD_SIZE))
    causal = (
        jnp.arange(used, dtype=jnp.int32)[None, :]
        <= jnp.arange(step_count, dtype=jnp.int32)[:, None]
    )
    causal = causal[None, None, :, None, :]
    running_peak = jnp.max(jnp.where(causal, scores, NEGATIVE_FILL), -1)
    weights = jnp.where(causal, jnp.exp(scores - running_peak[..., None]), 0.0)
    running_totals = jnp.sum(weights, -1)
    weighted_values = jnp.einsum(
        "rasgu,ruah->rasgh",
        weights.astype(jnp.bfloat16),
        value_all,
        preferred_element_type=jnp.float32,
    )
    return (running_peak, running_totals, weighted_values)


def merge_parts(earlier, later):
    running_peak = jnp.maximum(earlier[0], later[0])
    first_factor = jnp.exp(earlier[0] - running_peak)
    second_factor = jnp.exp(later[0] - running_peak)
    running_totals = earlier[1] * first_factor + later[1] * second_factor
    weighted_values = earlier[2] * first_factor[..., None] + later[2] * second_factor[..., None]
    return (running_peak, running_totals, weighted_values)


def slot_kernel(len_ref, blk_ref, q_ref, k_ref, v_ref, peak_ref, tot_ref, acc_ref, *, ns, heads, qpk):
    base = pl.program_id(0) * ns
    rows = q_ref.shape[1]
    group = rows // heads
    width = k_ref.shape[1]
    head = k_ref.shape[2] // heads
    row = lax.broadcasted_iota(jnp.int32, (rows, width), 0)
    col = lax.broadcasted_iota(jnp.int32, (rows, width), 1)
    step_of = (row % group) // qpk

    def body(i, carry):
        length = len_ref[base + i]
        key_pos = blk_ref[base + i] * width + col
        query_pos = length + step_of
        visible = (key_pos < length) & ((key_pos < SINK) | (key_pos > query_pos - WINDOW))
        q = q_ref[i]
        k = k_ref[i]
        v = v_ref[i]
        scores = jnp.concatenate(
            [
                lax.dot_general(
                    q[a * group : (a + 1) * group],
                    k[:, a * head : (a + 1) * head],
                    (((1,), (1,)), ((), ())),
                    preferred_element_type=jnp.float32,
                )
                for a in range(heads)
            ],
            0,
        ) * (1.0 / math.sqrt(HEAD_SIZE))
        peak = jnp.max(jnp.where(visible, scores, NEGATIVE_FILL), axis=1, keepdims=True)
        weights = jnp.where(visible, jnp.exp(scores - peak), 0.0)
        total = jnp.sum(weights, axis=1, keepdims=True)
        rounded = weights.astype(jnp.bfloat16)
        acc = jnp.concatenate(
            [
                jnp.dot(
                    rounded[a * group : (a + 1) * group],
                    v[:, a * head : (a + 1) * head],
                    preferred_element_type=jnp.float32,
                )
                for a in range(heads)
            ],
            0,
        )
        peak_ref[i] = peak
        tot_ref[i] = total
        acc_ref[i] = acc
        return carry

    lax.fori_loop(0, ns, body, 0, unroll=True)


def slot_attention(slot_queries, slot_lengths, block_numbers, keys, values, heads, qpk):
    n_slots, rows, head = slot_queries.shape
    width = keys.shape[1]
    ns = max(d for d in range(1, 11) if n_slots % d == 0)
    grid_spec = pltpu.PrefetchScalarGridSpec(
        num_scalar_prefetch=2,
        grid=(n_slots // ns,),
        in_specs=[
            pl.BlockSpec((ns, rows, head), lambda n, lr, br: (n, 0, 0)),
            pl.BlockSpec((ns, width, keys.shape[2]), lambda n, lr, br: (n, 0, 0)),
            pl.BlockSpec((ns, width, values.shape[2]), lambda n, lr, br: (n, 0, 0)),
        ],
        out_specs=[
            pl.BlockSpec((ns, rows, 1), lambda n, lr, br: (n, 0, 0)),
            pl.BlockSpec((ns, rows, 1), lambda n, lr, br: (n, 0, 0)),
            pl.BlockSpec((ns, rows, head), lambda n, lr, br: (n, 0, 0)),
        ],
    )
    return pl.pallas_call(
        partial(slot_kernel, ns=ns, heads=heads, qpk=qpk),
        grid_spec=grid_spec,
        out_shape=[
            jax.ShapeDtypeStruct((n_slots, rows, 1), jnp.float32),
            jax.ShapeDtypeStruct((n_slots, rows, 1), jnp.float32),
            jax.ShapeDtypeStruct((n_slots, rows, head), jnp.float32),
        ],
    )(slot_lengths, block_numbers, slot_queries, keys, values)


def pair_gather(part, axis_name):
    n = lax.axis_size(axis_name)
    assert n == 2
    side = lax.axis_index(axis_name)
    other = lax.ppermute(part, axis_name, [(0, 1), (1, 0)])
    return jnp.where(
        side == 0,
        jnp.concatenate([part, other], 0),
        jnp.concatenate([other, part], 0),
    )


def pair_scatter(parts, axis_name, rounded=True):
    n = lax.axis_size(axis_name)
    assert n == 2 and parts.shape[0] == 2
    side = lax.axis_index(axis_name)
    keep = lax.dynamic_index_in_dim(parts, side, 0, keepdims=True)
    send = lax.dynamic_index_in_dim(parts, 1 - side, 0, keepdims=True)
    got = lax.ppermute(send, axis_name, [(0, 1), (1, 0)])
    total = (keep.astype(jnp.float32) + got.astype(jnp.float32))[0]
    return total.astype(parts.dtype) if rounded else total


def doubling_gather(part, axis_name):
    n = lax.axis_size(axis_name)
    stages = n.bit_length() - 1
    assert 1 << stages == n
    index = lax.axis_index(axis_name)
    block = part[None]
    for bit in reversed(range(stages)):
        pairs = [(s, s ^ (1 << bit)) for s in range(n)]
        got = lax.ppermute(block, axis_name, pairs)
        low = ((index >> bit) & 1) == 0
        block = jnp.where(
            low, jnp.stack([block, got], 0), jnp.stack([got, block], 0)
        )
    block = block.reshape((2,) * stages + part.shape)
    block = block.transpose(tuple(reversed(range(stages))) + tuple(range(stages, stages + part.ndim)))
    return block.reshape((n * part.shape[0],) + part.shape[1:])


def seq_merge(peak, total, acc, n_seq, seq_index):
    stages = n_seq.bit_length() - 1
    assert 1 << stages == n_seq
    req_count = peak.shape[0]
    per = req_count // n_seq
    rest = peak.shape[1:]
    split = [2] * stages + [per]
    stats = jnp.stack([peak, total], 0).reshape([2] + split + list(rest))
    values = acc.reshape(split + list(acc.shape[1:]))
    for bit in range(stages):
        axis = stages - 1 - bit
        mine = (seq_index >> bit) & 1
        pairs = [(s, s ^ (1 << bit)) for s in range(n_seq)]
        keep_stats = lax.dynamic_index_in_dim(stats, mine, axis + 1, keepdims=True)
        send_stats = lax.dynamic_index_in_dim(stats, 1 - mine, axis + 1, keepdims=True)
        keep_values = lax.dynamic_index_in_dim(values, mine, axis, keepdims=True)
        send_values = lax.dynamic_index_in_dim(values, 1 - mine, axis, keepdims=True)
        got_stats = lax.ppermute(send_stats, "seq", pairs)
        got_values = lax.ppermute(send_values.astype(jnp.bfloat16), "seq", pairs).astype(
            jnp.float32
        )
        top = jnp.maximum(keep_stats[0], got_stats[0])
        keep_factor = jnp.exp(keep_stats[0] - top)
        got_factor = jnp.exp(got_stats[0] - top)
        stats = jnp.stack(
            [top, keep_stats[1] * keep_factor + got_stats[1] * got_factor], 0
        )
        values = keep_values * keep_factor[..., None] + got_values * got_factor[..., None]
    stats = stats.reshape((2, per) + tuple(rest))
    values = values.reshape((per,) + tuple(acc.shape[1:]))
    return (stats[0], stats[1], values)


def on_device(
    states,
    norm_gain,
    wq,
    wk,
    wv,
    wo,
    lengths,
    slot_request,
    slot_block_number,
    paged_key_cache,
    paged_value_cache,
):
    q_width = wq.shape[1]
    k_width = wk.shape[1]
    heads_kv = k_width // HEAD_SIZE
    req_count = lengths.shape[0]
    block_len = paged_key_cache.shape[1]
    key_rows = paged_key_cache.reshape(paged_key_cache.shape[0], block_len, heads_kv, HEAD_SIZE)
    value_rows = paged_value_cache.reshape(
        paged_value_cache.shape[0], block_len, heads_kv, HEAD_SIZE
    )
    step_count = states.shape[1]
    token_count = states.shape[0] * step_count
    side = lax.axis_index("col")
    swap = [(0, 1), (1, 0)]
    other_states = lax.ppermute(states, "col", swap)
    as_float = states.astype(jnp.float32)
    squares = lax.psum(jnp.sum(as_float * as_float, -1), "row").reshape(token_count)
    other_squares = lax.ppermute(squares, "col", swap)
    own_states = states

    def rms_norm(rows, sums):
        scale = lax.rsqrt(sums / D + EPSILON)[:, None]
        rows = rows.reshape(token_count, -1)
        return (rows.astype(jnp.float32) * scale * norm_gain).astype(jnp.bfloat16)

    first = side == 0
    gathered = jnp.concatenate(
        [
            rms_norm(
                jnp.where(first, own_states, other_states), jnp.where(first, squares, other_squares)
            ),
            rms_norm(
                jnp.where(first, other_states, own_states), jnp.where(first, other_squares, squares)
            ),
        ],
        0,
    )
    parts_out = [
        jnp.dot(gathered, matrix, preferred_element_type=jnp.float32) for matrix in (wq, wk, wv)
    ]
    output_projected = (
        pair_scatter(
            jnp.concatenate(parts_out, axis=-1)
            .astype(jnp.bfloat16)
            .reshape(lax.axis_size("row"), token_count, -1),
            "row",
            rounded=False,
        )
        .reshape(req_count, step_count, -1)
    )
    token_positions = lengths[:, None] + jnp.arange(step_count, dtype=jnp.int32)[None, :]
    query_rows = rotary_apply(
        output_projected[..., :q_width].reshape(req_count, step_count, -1, HEAD_SIZE),
        token_positions,
    ).astype(jnp.bfloat16)
    query_rows = query_rows.reshape(req_count, step_count, heads_kv, QUERY_PER_KEY, HEAD_SIZE)
    current_key = rotary_apply(
        output_projected[..., q_width : q_width + k_width].reshape(
            req_count, step_count, heads_kv, HEAD_SIZE
        ),
        token_positions,
    ).astype(jnp.bfloat16)
    current_value = (
        output_projected[..., q_width + k_width :]
        .reshape(req_count, step_count, heads_kv, HEAD_SIZE)
        .astype(jnp.bfloat16)
    )
    picked = jnp.minimum(slot_request, req_count - 1)
    in_use = slot_request < req_count
    slot_lengths = jnp.where(in_use, lengths[picked], 0)
    flat_queries = query_rows.transpose(0, 2, 1, 3, 4).reshape(req_count, -1, HEAD_SIZE)
    slot_peak, slot_total, slot_acc = slot_attention(
        flat_queries[picked],
        slot_lengths,
        slot_block_number,
        paged_key_cache,
        paged_value_cache,
        heads_kv,
        QUERY_PER_KEY,
    )
    slot_peak = slot_peak[..., 0]
    slot_total = slot_total[..., 0]
    member = slot_request[None, :] == jnp.arange(req_count, dtype=jnp.int32)[:, None]
    local_peak = jnp.max(jnp.where(member[:, :, None], slot_peak[None], NEGATIVE_FILL), 1)
    factor = jnp.exp(slot_peak - local_peak[picked])
    as_member = member.astype(jnp.float32)
    local_totals = jnp.einsum(
        "rn,nj->rj", as_member, slot_total * factor, precision=lax.Precision.HIGHEST
    )
    local_values = jnp.einsum(
        "rn,njh->rjh", as_member, slot_acc * factor[..., None], precision=lax.Precision.HIGHEST
    )
    n_seq = lax.axis_size("seq")
    per = req_count // n_seq
    seq_index = lax.axis_index("seq")
    mine = seq_index * per
    running_peak, running_totals, weighted_values = seq_merge(
        local_peak, local_totals, local_values, n_seq, seq_index
    )
    order = (per, heads_kv, step_count, QUERY_PER_KEY)
    running_peak = running_peak.reshape(order)
    running_totals = running_totals.reshape(order)
    weighted_values = weighted_values.reshape(order + (HEAD_SIZE,))
    own_queries = lax.dynamic_slice_in_dim(query_rows, mine, per, 0)
    fresh = fresh_part(
        own_queries,
        lax.dynamic_slice_in_dim(current_key, mine, per, 0),
        lax.dynamic_slice_in_dim(current_value, mine, per, 0),
    )
    running_peak, running_totals, weighted_values = merge_parts(
        (running_peak, running_totals, weighted_values), fresh
    )
    heads_out = (
        (weighted_values / running_totals[..., None])
        .transpose(0, 2, 1, 3, 4)
        .reshape(per, step_count, -1)
        .astype(jnp.bfloat16)
    )
    piece_rows = lax.all_gather(heads_out, "row", axis=0, tiled=False)
    n_row = piece_rows.shape[0]
    product = jnp.dot(
        piece_rows.reshape(n_row * per * step_count, -1), wo, preferred_element_type=jnp.float32
    )
    partials = product.reshape(n_row, per, step_count, -1)
    own_out = pair_scatter(partials.astype(jnp.bfloat16), "col").reshape(per, step_count, -1)
    attended = doubling_gather(own_out, "seq")
    return (
        attended,
        current_key.reshape(req_count, step_count, k_width),
        current_value.reshape(req_count, step_count, k_width),
    )


def solution(mesh):
    in_specs = (
        P("col", None, "row"),
        P("row"),
        P("row", "col"),
        P("row", "col"),
        P("row", "col"),
        P("col", "row"),
        P("row"),
        P(("row", "seq")),
        P(("row", "seq")),
        P(("row", "seq"), None, "col"),
        P(("row", "seq"), None, "col"),
    )
    out_specs = (P("col", None, "row"), P("row", None, "col"), P("row", None, "col"))
    return jax.shard_map(
        on_device, mesh=mesh, in_specs=in_specs, out_specs=out_specs, check_vma=False
    )
```

```python
import math
from functools import partial

import jax
import jax.numpy as jnp
from jax import lax
from jax.experimental import pallas as pl
from jax.experimental.pallas import tpu as pltpu
from jax.sharding import PartitionSpec as P

D = 5120
HEAD_SIZE = 128
WINDOW = 4096
SINK = 4
QUERY_PER_KEY = 4


EPSILON = 1e-05
NEGATIVE_FILL = -1e30
ROPE_BASE = 100000000.0


def rotary_apply(values, token_positions):
    half_dim = values.shape[-1] // 2
    frequency = ROPE_BASE ** (-(jnp.arange(half_dim, dtype=jnp.float32) * 2.0 / values.shape[-1]))
    angles = (token_positions.astype(jnp.float32)[..., None] * frequency)[..., None, :]
    cosine = jnp.cos(angles)
    sine_part = jnp.sin(angles)
    lower = values[..., :half_dim]
    upper = values[..., half_dim:]
    return jnp.concatenate(
        [lower * cosine - upper * sine_part, upper * cosine + lower * sine_part], -1
    )


def slot_parts(query_rows, lengths, slot_request, slot_block_number, key_rows, value_rows):
    req_count = query_rows.shape[0]
    step_count = query_rows.shape[1]
    block_len = key_rows.shape[1]
    picked = jnp.minimum(slot_request, req_count - 1)
    in_use = slot_request < req_count
    slot_queries = query_rows[picked]
    scores = jnp.einsum(
        "nsagh,nbah->nasgb", slot_queries, key_rows, preferred_element_type=jnp.float32
    ) * (1.0 / math.sqrt(HEAD_SIZE))
    key_pos = (
        slot_block_number[:, None] * block_len + jnp.arange(block_len, dtype=jnp.int32)[None, :]
    )
    own_len = lengths[picked]
    query_pos = own_len[:, None] + jnp.arange(step_count, dtype=jnp.int32)[None, :]
    visible = (
        in_use[:, None, None]
        & (key_pos[:, None, :] < own_len[:, None, None])
        & ((key_pos[:, None, :] < SINK) | (key_pos[:, None, :] > query_pos[:, :, None] - WINDOW))
    )
    visible = visible[:, None, :, None, :]
    slot_peak = jnp.max(jnp.where(visible, scores, NEGATIVE_FILL), -1)
    weights = jnp.where(visible, jnp.exp(scores - slot_peak[..., None]), 0.0)
    slot_total = jnp.sum(weights, -1)
    slot_acc = jnp.einsum(
        "nasgb,nbah->nasgh",
        weights.astype(jnp.bfloat16),
        value_rows,
        preferred_element_type=jnp.float32,
    )
    member = slot_request[None, :] == jnp.arange(req_count, dtype=jnp.int32)[:, None]
    local_peak = jnp.max(
        jnp.where(member[:, :, None, None, None], slot_peak[None], NEGATIVE_FILL), 1
    )
    return (local_peak, (slot_peak, slot_total, slot_acc, member, picked))


def pool_sums(held, running_peak):
    slot_peak, slot_total, slot_acc, member, picked = held
    factor = jnp.exp(slot_peak - running_peak[picked])
    as_member = member.astype(jnp.float32)
    running_totals = jnp.einsum(
        "rn,nasg->rasg", as_member, slot_total * factor, precision=lax.Precision.HIGHEST
    )
    weighted_values = jnp.einsum(
        "rn,nasgh->rasgh", as_member, slot_acc * factor[..., None], precision=lax.Precision.HIGHEST
    )
    return (running_totals, weighted_values)


def fresh_part(query_rows, key_all, value_all):
    step_count = query_rows.shape[1]
    used = key_all.shape[1]
    scores = jnp.einsum(
        "rsagh,ruah->rasgu", query_rows, key_all, preferred_element_type=jnp.float32
    ) * (1.0 / math.sqrt(HEAD_SIZE))
    causal = (
        jnp.arange(used, dtype=jnp.int32)[None, :]
        <= jnp.arange(step_count, dtype=jnp.int32)[:, None]
    )
    causal = causal[None, None, :, None, :]
    running_peak = jnp.max(jnp.where(causal, scores, NEGATIVE_FILL), -1)
    weights = jnp.where(causal, jnp.exp(scores - running_peak[..., None]), 0.0)
    running_totals = jnp.sum(weights, -1)
    weighted_values = jnp.einsum(
        "rasgu,ruah->rasgh",
        weights.astype(jnp.bfloat16),
        value_all,
        preferred_element_type=jnp.float32,
    )
    return (running_peak, running_totals, weighted_values)


def merge_parts(earlier, later):
    running_peak = jnp.maximum(earlier[0], later[0])
    first_factor = jnp.exp(earlier[0] - running_peak)
    second_factor = jnp.exp(later[0] - running_peak)
    running_totals = earlier[1] * first_factor + later[1] * second_factor
    weighted_values = earlier[2] * first_factor[..., None] + later[2] * second_factor[..., None]
    return (running_peak, running_totals, weighted_values)


def slot_kernel(len_ref, blk_ref, q_ref, k_ref, v_ref, peak_ref, tot_ref, acc_ref, *, ns, heads, qpk):
    base = pl.program_id(0) * ns
    rows = q_ref.shape[1]
    group = rows // heads
    width = k_ref.shape[1]
    head = k_ref.shape[2] // heads
    row = lax.broadcasted_iota(jnp.int32, (rows, width), 0)
    col = lax.broadcasted_iota(jnp.int32, (rows, width), 1)
    step_of = (row % group) // qpk

    def body(i, carry):
        length = len_ref[base + i]
        key_pos = blk_ref[base + i] * width + col
        query_pos = length + step_of
        visible = (key_pos < length) & ((key_pos < SINK) | (key_pos > query_pos - WINDOW))
        q = q_ref[i]
        k = k_ref[i]
        v = v_ref[i]
        scores = jnp.concatenate(
            [
                lax.dot_general(
                    q[a * group : (a + 1) * group],
                    k[:, a * head : (a + 1) * head],
                    (((1,), (1,)), ((), ())),
                    preferred_element_type=jnp.float32,
                )
                for a in range(heads)
            ],
            0,
        ) * (1.0 / math.sqrt(HEAD_SIZE))
        peak = jnp.max(jnp.where(visible, scores, NEGATIVE_FILL), axis=1, keepdims=True)
        weights = jnp.where(visible, jnp.exp(scores - peak), 0.0)
        total = jnp.sum(weights, axis=1, keepdims=True)
        rounded = weights.astype(jnp.bfloat16)
        acc = jnp.concatenate(
            [
                jnp.dot(
                    rounded[a * group : (a + 1) * group],
                    v[:, a * head : (a + 1) * head],
                    preferred_element_type=jnp.float32,
                )
                for a in range(heads)
            ],
            0,
        )
        peak_ref[i] = peak
        tot_ref[i] = total
        acc_ref[i] = acc
        return carry

    lax.fori_loop(0, ns, body, 0, unroll=True)


def slot_attention(slot_queries, slot_lengths, block_numbers, keys, values, heads, qpk):
    n_slots, rows, head = slot_queries.shape
    width = keys.shape[1]
    ns = max(d for d in range(1, 11) if n_slots % d == 0)
    grid_spec = pltpu.PrefetchScalarGridSpec(
        num_scalar_prefetch=2,
        grid=(n_slots // ns,),
        in_specs=[
            pl.BlockSpec((ns, rows, head), lambda n, lr, br: (n, 0, 0)),
            pl.BlockSpec((ns, width, keys.shape[2]), lambda n, lr, br: (n, 0, 0)),
            pl.BlockSpec((ns, width, values.shape[2]), lambda n, lr, br: (n, 0, 0)),
        ],
        out_specs=[
            pl.BlockSpec((ns, rows, 1), lambda n, lr, br: (n, 0, 0)),
            pl.BlockSpec((ns, rows, 1), lambda n, lr, br: (n, 0, 0)),
            pl.BlockSpec((ns, rows, head), lambda n, lr, br: (n, 0, 0)),
        ],
    )
    return pl.pallas_call(
        partial(slot_kernel, ns=ns, heads=heads, qpk=qpk),
        grid_spec=grid_spec,
        out_shape=[
            jax.ShapeDtypeStruct((n_slots, rows, 1), jnp.float32),
            jax.ShapeDtypeStruct((n_slots, rows, 1), jnp.float32),
            jax.ShapeDtypeStruct((n_slots, rows, head), jnp.float32),
        ],
    )(slot_lengths, block_numbers, slot_queries, keys, values)


def pair_gather(part, axis_name):
    n = lax.axis_size(axis_name)
    assert n == 2
    side = lax.axis_index(axis_name)
    other = lax.ppermute(part, axis_name, [(0, 1), (1, 0)])
    return jnp.where(
        side == 0,
        jnp.concatenate([part, other], 0),
        jnp.concatenate([other, part], 0),
    )


def pair_scatter(parts, axis_name, rounded=True):
    n = lax.axis_size(axis_name)
    assert n == 2 and parts.shape[0] == 2
    side = lax.axis_index(axis_name)
    keep = lax.dynamic_index_in_dim(parts, side, 0, keepdims=True)
    send = lax.dynamic_index_in_dim(parts, 1 - side, 0, keepdims=True)
    got = lax.ppermute(send, axis_name, [(0, 1), (1, 0)])
    total = (keep.astype(jnp.float32) + got.astype(jnp.float32))[0]
    return total.astype(parts.dtype) if rounded else total


def doubling_gather(part, axis_name):
    n = lax.axis_size(axis_name)
    stages = n.bit_length() - 1
    assert 1 << stages == n
    index = lax.axis_index(axis_name)
    block = part[None]
    for bit in reversed(range(stages)):
        pairs = [(s, s ^ (1 << bit)) for s in range(n)]
        got = lax.ppermute(block, axis_name, pairs)
        low = ((index >> bit) & 1) == 0
        block = jnp.where(
            low, jnp.stack([block, got], 0), jnp.stack([got, block], 0)
        )
    block = block.reshape((2,) * stages + part.shape)
    block = block.transpose(tuple(reversed(range(stages))) + tuple(range(stages, stages + part.ndim)))
    return block.reshape((n * part.shape[0],) + part.shape[1:])


def seq_merge(peak, total, acc, n_seq, seq_index):
    stages = n_seq.bit_length() - 1
    assert 1 << stages == n_seq
    req_count = peak.shape[0]
    per = req_count // n_seq
    rest = peak.shape[1:]
    split = [2] * stages + [per]
    stats = jnp.stack([peak, total], 0).reshape([2] + split + list(rest))
    values = acc.reshape(split + list(acc.shape[1:]))
    for bit in range(stages):
        axis = stages - 1 - bit
        mine = (seq_index >> bit) & 1
        pairs = [(s, s ^ (1 << bit)) for s in range(n_seq)]
        keep_stats = lax.dynamic_index_in_dim(stats, mine, axis + 1, keepdims=True)
        send_stats = lax.dynamic_index_in_dim(stats, 1 - mine, axis + 1, keepdims=True)
        keep_values = lax.dynamic_index_in_dim(values, mine, axis, keepdims=True)
        send_values = lax.dynamic_index_in_dim(values, 1 - mine, axis, keepdims=True)
        got_stats = lax.ppermute(send_stats, "seq", pairs)
        got_values = lax.ppermute(send_values.astype(jnp.bfloat16), "seq", pairs).astype(
            jnp.float32
        )
        top = jnp.maximum(keep_stats[0], got_stats[0])
        keep_factor = jnp.exp(keep_stats[0] - top)
        got_factor = jnp.exp(got_stats[0] - top)
        stats = jnp.stack(
            [top, keep_stats[1] * keep_factor + got_stats[1] * got_factor], 0
        )
        values = keep_values * keep_factor[..., None] + got_values * got_factor[..., None]
    stats = stats.reshape((2, per) + tuple(rest))
    values = values.reshape((per,) + tuple(acc.shape[1:]))
    return (stats[0], stats[1], values)


def on_device(
    states,
    norm_gain,
    wq,
    wk,
    wv,
    wo,
    lengths,
    slot_request,
    slot_block_number,
    paged_key_cache,
    paged_value_cache,
):
    q_width = wq.shape[1]
    k_width = wk.shape[1]
    heads_kv = k_width // HEAD_SIZE
    req_count = lengths.shape[0]
    block_len = paged_key_cache.shape[1]
    key_rows = paged_key_cache.reshape(paged_key_cache.shape[0], block_len, heads_kv, HEAD_SIZE)
    value_rows = paged_value_cache.reshape(
        paged_value_cache.shape[0], block_len, heads_kv, HEAD_SIZE
    )
    step_count = states.shape[1]
    token_count = states.shape[0] * step_count
    own_states = states.reshape(token_count, -1)
    side = lax.axis_index("col")
    swap = [(0, 1), (1, 0)]
    other_states = lax.ppermute(own_states, "col", swap)
    as_float = own_states.astype(jnp.float32)
    squares = lax.psum(jnp.sum(as_float * as_float, -1), "row")
    other_squares = lax.ppermute(squares, "col", swap)

    def rms_norm(rows, sums):
        scale = lax.rsqrt(sums / D + EPSILON)[:, None]
        return (rows.astype(jnp.float32) * scale * norm_gain).astype(jnp.bfloat16)

    first = side == 0
    gathered = jnp.concatenate(
        [
            rms_norm(
                jnp.where(first, own_states, other_states), jnp.where(first, squares, other_squares)
            ),
            rms_norm(
                jnp.where(first, other_states, own_states), jnp.where(first, other_squares, squares)
            ),
        ],
        0,
    )
    parts_out = [
        jnp.dot(gathered, matrix, preferred_element_type=jnp.float32) for matrix in (wq, wk, wv)
    ]
    head_count = (q_width + 2 * k_width) // HEAD_SIZE
    output_projected = pair_scatter(
        jnp.concatenate(parts_out, axis=-1)
        .astype(jnp.bfloat16)
        .reshape(lax.axis_size("row"), token_count, -1),
        "row",
        rounded=False,
    ).reshape(token_count, head_count, HEAD_SIZE)
    q_heads = q_width // HEAD_SIZE
    token_positions = (
        lengths[:, None] + jnp.arange(step_count, dtype=jnp.int32)[None, :]
    ).reshape(token_count)
    query_rows = rotary_apply(output_projected[:, :q_heads], token_positions).astype(jnp.bfloat16)
    query_rows = query_rows.reshape(req_count, step_count, heads_kv, QUERY_PER_KEY, HEAD_SIZE)
    current_key = (
        rotary_apply(output_projected[:, q_heads : q_heads + heads_kv], token_positions)
        .astype(jnp.bfloat16)
        .reshape(req_count, step_count, heads_kv, HEAD_SIZE)
    )
    current_value = (
        output_projected[:, q_heads + heads_kv :]
        .astype(jnp.bfloat16)
        .reshape(req_count, step_count, heads_kv, HEAD_SIZE)
    )
    picked = jnp.minimum(slot_request, req_count - 1)
    in_use = slot_request < req_count
    slot_lengths = jnp.where(in_use, lengths[picked], 0)
    flat_queries = query_rows.transpose(0, 2, 1, 3, 4).reshape(req_count, -1, HEAD_SIZE)
    slot_peak, slot_total, slot_acc = slot_attention(
        flat_queries[picked],
        slot_lengths,
        slot_block_number,
        paged_key_cache,
        paged_value_cache,
        heads_kv,
        QUERY_PER_KEY,
    )
    slot_peak = slot_peak[..., 0]
    slot_total = slot_total[..., 0]
    member = slot_request[None, :] == jnp.arange(req_count, dtype=jnp.int32)[:, None]
    local_peak = jnp.max(jnp.where(member[:, :, None], slot_peak[None], NEGATIVE_FILL), 1)
    factor = jnp.exp(slot_peak - local_peak[picked])
    as_member = member.astype(jnp.float32)
    local_totals = jnp.einsum(
        "rn,nj->rj", as_member, slot_total * factor, precision=lax.Precision.HIGHEST
    )
    local_values = jnp.einsum(
        "rn,njh->rjh", as_member, slot_acc * factor[..., None], precision=lax.Precision.HIGHEST
    )
    n_seq = lax.axis_size("seq")
    per = req_count // n_seq
    seq_index = lax.axis_index("seq")
    mine = seq_index * per
    running_peak, running_totals, weighted_values = seq_merge(
        local_peak, local_totals, local_values, n_seq, seq_index
    )
    order = (per, heads_kv, step_count, QUERY_PER_KEY)
    running_peak = running_peak.reshape(order)
    running_totals = running_totals.reshape(order)
    weighted_values = weighted_values.reshape(order + (HEAD_SIZE,))
    own_queries = lax.dynamic_slice_in_dim(query_rows, mine, per, 0)
    fresh = fresh_part(
        own_queries,
        lax.dynamic_slice_in_dim(current_key, mine, per, 0),
        lax.dynamic_slice_in_dim(current_value, mine, per, 0),
    )
    running_peak, running_totals, weighted_values = merge_parts(
        (running_peak, running_totals, weighted_values), fresh
    )
    heads_out = (
        (weighted_values / running_totals[..., None])
        .transpose(0, 2, 1, 3, 4)
        .reshape(per, step_count, -1)
        .astype(jnp.bfloat16)
    )
    piece_rows = lax.all_gather(heads_out, "row", axis=0, tiled=False)
    n_row = piece_rows.shape[0]
    product = jnp.dot(
        piece_rows.reshape(n_row * per * step_count, -1), wo, preferred_element_type=jnp.float32
    )
    partials = product.reshape(n_row, per, step_count, -1)
    own_out = pair_scatter(partials.astype(jnp.bfloat16), "col").reshape(per, step_count, -1)
    attended = doubling_gather(own_out, "seq")
    return (
        attended,
        current_key.reshape(req_count, step_count, k_width),
        current_value.reshape(req_count, step_count, k_width),
    )


def solution(mesh):
    in_specs = (
        P("col", None, "row"),
        P("row"),
        P("row", "col"),
        P("row", "col"),
        P("row", "col"),
        P("col", "row"),
        P("row"),
        P(("row", "seq")),
        P(("row", "seq")),
        P(("row", "seq"), None, "col"),
        P(("row", "seq"), None, "col"),
    )
    out_specs = (P("col", None, "row"), P("row", None, "col"), P("row", None, "col"))
    return jax.shard_map(
        on_device, mesh=mesh, in_specs=in_specs, out_specs=out_specs, check_vma=False
    )
```

```python
import math
from functools import partial

import jax
import jax.numpy as jnp
from jax import lax
from jax.experimental import pallas as pl
from jax.experimental.pallas import tpu as pltpu
from jax.sharding import PartitionSpec as P

D = 5120
HEAD_SIZE = 128
WINDOW = 4096
SINK = 4
QUERY_PER_KEY = 4


EPSILON = 1e-05
NEGATIVE_FILL = -1e30
ROPE_BASE = 100000000.0


def rotary_apply(values, token_positions):
    half_dim = values.shape[-1] // 2
    frequency = ROPE_BASE ** (-(jnp.arange(half_dim, dtype=jnp.float32) * 2.0 / values.shape[-1]))
    angles = (token_positions.astype(jnp.float32)[..., None] * frequency)[..., None, :]
    cosine = jnp.cos(angles)
    sine_part = jnp.sin(angles)
    lower = values[..., :half_dim]
    upper = values[..., half_dim:]
    return jnp.concatenate(
        [lower * cosine - upper * sine_part, upper * cosine + lower * sine_part], -1
    )


def slot_parts(query_rows, lengths, slot_request, slot_block_number, key_rows, value_rows):
    req_count = query_rows.shape[0]
    step_count = query_rows.shape[1]
    block_len = key_rows.shape[1]
    picked = jnp.minimum(slot_request, req_count - 1)
    in_use = slot_request < req_count
    slot_queries = query_rows[picked]
    scores = jnp.einsum(
        "nsagh,nbah->nasgb", slot_queries, key_rows, preferred_element_type=jnp.float32
    ) * (1.0 / math.sqrt(HEAD_SIZE))
    key_pos = (
        slot_block_number[:, None] * block_len + jnp.arange(block_len, dtype=jnp.int32)[None, :]
    )
    own_len = lengths[picked]
    query_pos = own_len[:, None] + jnp.arange(step_count, dtype=jnp.int32)[None, :]
    visible = (
        in_use[:, None, None]
        & (key_pos[:, None, :] < own_len[:, None, None])
        & ((key_pos[:, None, :] < SINK) | (key_pos[:, None, :] > query_pos[:, :, None] - WINDOW))
    )
    visible = visible[:, None, :, None, :]
    slot_peak = jnp.max(jnp.where(visible, scores, NEGATIVE_FILL), -1)
    weights = jnp.where(visible, jnp.exp(scores - slot_peak[..., None]), 0.0)
    slot_total = jnp.sum(weights, -1)
    slot_acc = jnp.einsum(
        "nasgb,nbah->nasgh",
        weights.astype(jnp.bfloat16),
        value_rows,
        preferred_element_type=jnp.float32,
    )
    member = slot_request[None, :] == jnp.arange(req_count, dtype=jnp.int32)[:, None]
    local_peak = jnp.max(
        jnp.where(member[:, :, None, None, None], slot_peak[None], NEGATIVE_FILL), 1
    )
    return (local_peak, (slot_peak, slot_total, slot_acc, member, picked))


def pool_sums(held, running_peak):
    slot_peak, slot_total, slot_acc, member, picked = held
    factor = jnp.exp(slot_peak - running_peak[picked])
    as_member = member.astype(jnp.float32)
    running_totals = jnp.einsum(
        "rn,nasg->rasg", as_member, slot_total * factor, precision=lax.Precision.HIGHEST
    )
    weighted_values = jnp.einsum(
        "rn,nasgh->rasgh", as_member, slot_acc * factor[..., None], precision=lax.Precision.HIGHEST
    )
    return (running_totals, weighted_values)


def fresh_part(query_rows, key_all, value_all):
    step_count = query_rows.shape[1]
    used = key_all.shape[1]
    scores = jnp.einsum(
        "rsagh,ruah->rasgu", query_rows, key_all, preferred_element_type=jnp.float32
    ) * (1.0 / math.sqrt(HEAD_SIZE))
    causal = (
        jnp.arange(used, dtype=jnp.int32)[None, :]
        <= jnp.arange(step_count, dtype=jnp.int32)[:, None]
    )
    causal = causal[None, None, :, None, :]
    running_peak = jnp.max(jnp.where(causal, scores, NEGATIVE_FILL), -1)
    weights = jnp.where(causal, jnp.exp(scores - running_peak[..., None]), 0.0)
    running_totals = jnp.sum(weights, -1)
    weighted_values = jnp.einsum(
        "rasgu,ruah->rasgh",
        weights.astype(jnp.bfloat16),
        value_all,
        preferred_element_type=jnp.float32,
    )
    return (running_peak, running_totals, weighted_values)


def merge_parts(earlier, later):
    running_peak = jnp.maximum(earlier[0], later[0])
    first_factor = jnp.exp(earlier[0] - running_peak)
    second_factor = jnp.exp(later[0] - running_peak)
    running_totals = earlier[1] * first_factor + later[1] * second_factor
    weighted_values = earlier[2] * first_factor[..., None] + later[2] * second_factor[..., None]
    return (running_peak, running_totals, weighted_values)


def slot_kernel(len_ref, blk_ref, q_ref, k_ref, v_ref, peak_ref, tot_ref, acc_ref, *, ns, heads, qpk):
    base = pl.program_id(0) * ns
    rows = q_ref.shape[1]
    group = rows // heads
    width = k_ref.shape[1]
    head = k_ref.shape[2] // heads
    row = lax.broadcasted_iota(jnp.int32, (rows, width), 0)
    col = lax.broadcasted_iota(jnp.int32, (rows, width), 1)
    step_of = (row % group) // qpk

    def body(i, carry):
        length = len_ref[base + i]
        key_pos = blk_ref[base + i] * width + col
        query_pos = length + step_of
        visible = (key_pos < length) & ((key_pos < SINK) | (key_pos > query_pos - WINDOW))
        q = q_ref[i]
        k = k_ref[i]
        v = v_ref[i]
        scores = jnp.concatenate(
            [
                lax.dot_general(
                    q[a * group : (a + 1) * group],
                    k[:, a * head : (a + 1) * head],
                    (((1,), (1,)), ((), ())),
                    preferred_element_type=jnp.float32,
                )
                for a in range(heads)
            ],
            0,
        ) * (1.0 / math.sqrt(HEAD_SIZE))
        peak = jnp.max(jnp.where(visible, scores, NEGATIVE_FILL), axis=1, keepdims=True)
        weights = jnp.where(visible, jnp.exp(scores - peak), 0.0)
        total = jnp.sum(weights, axis=1, keepdims=True)
        rounded = weights.astype(jnp.bfloat16)
        acc = jnp.concatenate(
            [
                jnp.dot(
                    rounded[a * group : (a + 1) * group],
                    v[:, a * head : (a + 1) * head],
                    preferred_element_type=jnp.float32,
                )
                for a in range(heads)
            ],
            0,
        )
        peak_ref[i] = peak
        tot_ref[i] = total
        acc_ref[i] = acc
        return carry

    lax.fori_loop(0, ns, body, 0, unroll=True)


def slot_attention(slot_queries, slot_lengths, block_numbers, keys, values, heads, qpk):
    n_slots, rows, head = slot_queries.shape
    width = keys.shape[1]
    ns = max(d for d in range(1, 11) if n_slots % d == 0)
    grid_spec = pltpu.PrefetchScalarGridSpec(
        num_scalar_prefetch=2,
        grid=(n_slots // ns,),
        in_specs=[
            pl.BlockSpec((ns, rows, head), lambda n, lr, br: (n, 0, 0)),
            pl.BlockSpec((ns, width, keys.shape[2]), lambda n, lr, br: (n, 0, 0)),
            pl.BlockSpec((ns, width, values.shape[2]), lambda n, lr, br: (n, 0, 0)),
        ],
        out_specs=[
            pl.BlockSpec((ns, rows, 1), lambda n, lr, br: (n, 0, 0)),
            pl.BlockSpec((ns, rows, 1), lambda n, lr, br: (n, 0, 0)),
            pl.BlockSpec((ns, rows, head), lambda n, lr, br: (n, 0, 0)),
        ],
    )
    return pl.pallas_call(
        partial(slot_kernel, ns=ns, heads=heads, qpk=qpk),
        grid_spec=grid_spec,
        out_shape=[
            jax.ShapeDtypeStruct((n_slots, rows, 1), jnp.float32),
            jax.ShapeDtypeStruct((n_slots, rows, 1), jnp.float32),
            jax.ShapeDtypeStruct((n_slots, rows, head), jnp.float32),
        ],
    )(slot_lengths, block_numbers, slot_queries, keys, values)


def pair_gather(part, axis_name):
    n = lax.axis_size(axis_name)
    assert n == 2
    side = lax.axis_index(axis_name)
    other = lax.ppermute(part, axis_name, [(0, 1), (1, 0)])
    return jnp.where(
        side == 0,
        jnp.concatenate([part, other], 0),
        jnp.concatenate([other, part], 0),
    )


def pair_scatter(parts, axis_name, rounded=True):
    n = lax.axis_size(axis_name)
    assert n == 2 and parts.shape[0] == 2
    side = lax.axis_index(axis_name)
    keep = lax.dynamic_index_in_dim(parts, side, 0, keepdims=True)
    send = lax.dynamic_index_in_dim(parts, 1 - side, 0, keepdims=True)
    got = lax.ppermute(send, axis_name, [(0, 1), (1, 0)])
    total = (keep.astype(jnp.float32) + got.astype(jnp.float32))[0]
    return total.astype(parts.dtype) if rounded else total


def doubling_gather(part, axis_name):
    n = lax.axis_size(axis_name)
    stages = n.bit_length() - 1
    assert 1 << stages == n
    index = lax.axis_index(axis_name)
    block = part[None]
    for bit in reversed(range(stages)):
        pairs = [(s, s ^ (1 << bit)) for s in range(n)]
        got = lax.ppermute(block, axis_name, pairs)
        low = ((index >> bit) & 1) == 0
        block = jnp.where(
            low, jnp.stack([block, got], 0), jnp.stack([got, block], 0)
        )
    block = block.reshape((2,) * stages + part.shape)
    block = block.transpose(tuple(reversed(range(stages))) + tuple(range(stages, stages + part.ndim)))
    return block.reshape((n * part.shape[0],) + part.shape[1:])


def seq_merge(peak, total, acc, n_seq, seq_index):
    stages = n_seq.bit_length() - 1
    assert 1 << stages == n_seq
    req_count = peak.shape[0]
    per = req_count // n_seq
    rest = peak.shape[1:]
    split = [2] * stages + [per]
    stats = jnp.stack([peak, total], 0).reshape([2] + split + list(rest))
    values = acc.reshape(split + list(acc.shape[1:]))
    for bit in range(stages):
        axis = stages - 1 - bit
        mine = (seq_index >> bit) & 1
        pairs = [(s, s ^ (1 << bit)) for s in range(n_seq)]
        keep_stats = lax.dynamic_index_in_dim(stats, mine, axis + 1, keepdims=True)
        send_stats = lax.dynamic_index_in_dim(stats, 1 - mine, axis + 1, keepdims=True)
        keep_values = lax.dynamic_index_in_dim(values, mine, axis, keepdims=True)
        send_values = lax.dynamic_index_in_dim(values, 1 - mine, axis, keepdims=True)
        got_stats = lax.ppermute(send_stats, "seq", pairs)
        got_values = lax.ppermute(send_values.astype(jnp.bfloat16), "seq", pairs).astype(
            jnp.float32
        )
        top = jnp.maximum(keep_stats[0], got_stats[0])
        keep_factor = jnp.exp(keep_stats[0] - top)
        got_factor = jnp.exp(got_stats[0] - top)
        stats = jnp.stack(
            [top, keep_stats[1] * keep_factor + got_stats[1] * got_factor], 0
        )
        values = keep_values * keep_factor[..., None] + got_values * got_factor[..., None]
    stats = stats.reshape((2, per) + tuple(rest))
    values = values.reshape((per,) + tuple(acc.shape[1:]))
    return (stats[0], stats[1], values)


def on_device(
    states,
    norm_gain,
    wq,
    wk,
    wv,
    wo,
    lengths,
    slot_request,
    slot_block_number,
    paged_key_cache,
    paged_value_cache,
):
    q_width = wq.shape[1]
    k_width = wk.shape[1]
    heads_kv = k_width // HEAD_SIZE
    req_count = lengths.shape[0]
    block_len = paged_key_cache.shape[1]
    key_rows = paged_key_cache.reshape(paged_key_cache.shape[0], block_len, heads_kv, HEAD_SIZE)
    value_rows = paged_value_cache.reshape(
        paged_value_cache.shape[0], block_len, heads_kv, HEAD_SIZE
    )
    step_count = states.shape[1]
    token_count = states.shape[0] * step_count
    own_states = states.reshape(token_count, -1)
    side = lax.axis_index("col")
    swap = [(0, 1), (1, 0)]
    other_states = lax.ppermute(own_states, "col", swap)
    as_float = own_states.astype(jnp.float32)
    squares = lax.psum(jnp.sum(as_float * as_float, -1), "row")
    other_squares = lax.ppermute(squares, "col", swap)

    def rms_norm(rows, sums):
        scale = lax.rsqrt(sums / D + EPSILON)[:, None]
        return (rows.astype(jnp.float32) * scale * norm_gain).astype(jnp.bfloat16)

    first = side == 0

    def project(rows):
        return jnp.concatenate(
            [jnp.dot(rows, matrix, preferred_element_type=jnp.float32) for matrix in (wq, wk, wv)],
            axis=-1,
        ).astype(jnp.bfloat16)

    own_part = project(rms_norm(own_states, squares))
    other_part = project(rms_norm(other_states, other_squares))
    parts_out = jnp.where(
        first, jnp.stack([own_part, other_part], 0), jnp.stack([other_part, own_part], 0)
    )
    head_count = (q_width + 2 * k_width) // HEAD_SIZE
    output_projected = pair_scatter(
        parts_out,
        "row",
        rounded=False,
    ).reshape(token_count, head_count, HEAD_SIZE)
    q_heads = q_width // HEAD_SIZE
    token_positions = (
        lengths[:, None] + jnp.arange(step_count, dtype=jnp.int32)[None, :]
    ).reshape(token_count)
    query_rows = rotary_apply(output_projected[:, :q_heads], token_positions).astype(jnp.bfloat16)
    query_rows = query_rows.reshape(req_count, step_count, heads_kv, QUERY_PER_KEY, HEAD_SIZE)
    current_key = (
        rotary_apply(output_projected[:, q_heads : q_heads + heads_kv], token_positions)
        .astype(jnp.bfloat16)
        .reshape(req_count, step_count, heads_kv, HEAD_SIZE)
    )
    current_value = (
        output_projected[:, q_heads + heads_kv :]
        .astype(jnp.bfloat16)
        .reshape(req_count, step_count, heads_kv, HEAD_SIZE)
    )
    picked = jnp.minimum(slot_request, req_count - 1)
    in_use = slot_request < req_count
    slot_lengths = jnp.where(in_use, lengths[picked], 0)
    flat_queries = query_rows.transpose(0, 2, 1, 3, 4).reshape(req_count, -1, HEAD_SIZE)
    slot_peak, slot_total, slot_acc = slot_attention(
        flat_queries[picked],
        slot_lengths,
        slot_block_number,
        paged_key_cache,
        paged_value_cache,
        heads_kv,
        QUERY_PER_KEY,
    )
    slot_peak = slot_peak[..., 0]
    slot_total = slot_total[..., 0]
    member = slot_request[None, :] == jnp.arange(req_count, dtype=jnp.int32)[:, None]
    local_peak = jnp.max(jnp.where(member[:, :, None], slot_peak[None], NEGATIVE_FILL), 1)
    factor = jnp.exp(slot_peak - local_peak[picked])
    as_member = member.astype(jnp.float32)
    local_totals = jnp.einsum(
        "rn,nj->rj", as_member, slot_total * factor, precision=lax.Precision.HIGHEST
    )
    local_values = jnp.einsum(
        "rn,njh->rjh", as_member, slot_acc * factor[..., None], precision=lax.Precision.HIGHEST
    )
    n_seq = lax.axis_size("seq")
    per = req_count // n_seq
    seq_index = lax.axis_index("seq")
    mine = seq_index * per
    running_peak, running_totals, weighted_values = seq_merge(
        local_peak, local_totals, local_values, n_seq, seq_index
    )
    order = (per, heads_kv, step_count, QUERY_PER_KEY)
    running_peak = running_peak.reshape(order)
    running_totals = running_totals.reshape(order)
    weighted_values = weighted_values.reshape(order + (HEAD_SIZE,))
    own_queries = lax.dynamic_slice_in_dim(query_rows, mine, per, 0)
    fresh = fresh_part(
        own_queries,
        lax.dynamic_slice_in_dim(current_key, mine, per, 0),
        lax.dynamic_slice_in_dim(current_value, mine, per, 0),
    )
    running_peak, running_totals, weighted_values = merge_parts(
        (running_peak, running_totals, weighted_values), fresh
    )
    heads_out = (
        (weighted_values / running_totals[..., None])
        .transpose(0, 2, 1, 3, 4)
        .reshape(per, step_count, -1)
        .astype(jnp.bfloat16)
    )
    piece_rows = lax.all_gather(heads_out, "row", axis=0, tiled=False)
    n_row = piece_rows.shape[0]
    product = jnp.dot(
        piece_rows.reshape(n_row * per * step_count, -1), wo, preferred_element_type=jnp.float32
    )
    partials = product.reshape(n_row, per, step_count, -1)
    own_out = pair_scatter(partials.astype(jnp.bfloat16), "col").reshape(per, step_count, -1)
    attended = doubling_gather(own_out, "seq")
    return (
        attended,
        current_key.reshape(req_count, step_count, k_width),
        current_value.reshape(req_count, step_count, k_width),
    )


def solution(mesh):
    in_specs = (
        P("col", None, "row"),
        P("row"),
        P("row", "col"),
        P("row", "col"),
        P("row", "col"),
        P("col", "row"),
        P("row"),
        P(("row", "seq")),
        P(("row", "seq")),
        P(("row", "seq"), None, "col"),
        P(("row", "seq"), None, "col"),
    )
    out_specs = (P("col", None, "row"), P("row", None, "col"), P("row", None, "col"))
    return jax.shard_map(
        on_device, mesh=mesh, in_specs=in_specs, out_specs=out_specs, check_vma=False
    )
```

```python
import math
from functools import partial

import jax
import jax.numpy as jnp
from jax import lax
from jax.experimental import pallas as pl
from jax.experimental.pallas import tpu as pltpu
from jax.sharding import PartitionSpec as P

D = 5120
HEAD_SIZE = 128
WINDOW = 4096
SINK = 4
QUERY_PER_KEY = 4


EPSILON = 1e-05
NEGATIVE_FILL = -1e30
ROPE_BASE = 100000000.0


def rotary_apply(values, token_positions):
    half_dim = values.shape[-1] // 2
    frequency = ROPE_BASE ** (-(jnp.arange(half_dim, dtype=jnp.float32) * 2.0 / values.shape[-1]))
    angles = (token_positions.astype(jnp.float32)[..., None] * frequency)[..., None, :]
    cosine = jnp.cos(angles)
    sine_part = jnp.sin(angles)
    lower = values[..., :half_dim]
    upper = values[..., half_dim:]
    return jnp.concatenate(
        [lower * cosine - upper * sine_part, upper * cosine + lower * sine_part], -1
    )


def slot_parts(query_rows, lengths, slot_request, slot_block_number, key_rows, value_rows):
    req_count = query_rows.shape[0]
    step_count = query_rows.shape[1]
    block_len = key_rows.shape[1]
    picked = jnp.minimum(slot_request, req_count - 1)
    in_use = slot_request < req_count
    slot_queries = query_rows[picked]
    scores = jnp.einsum(
        "nsagh,nbah->nasgb", slot_queries, key_rows, preferred_element_type=jnp.float32
    ) * (1.0 / math.sqrt(HEAD_SIZE))
    key_pos = (
        slot_block_number[:, None] * block_len + jnp.arange(block_len, dtype=jnp.int32)[None, :]
    )
    own_len = lengths[picked]
    query_pos = own_len[:, None] + jnp.arange(step_count, dtype=jnp.int32)[None, :]
    visible = (
        in_use[:, None, None]
        & (key_pos[:, None, :] < own_len[:, None, None])
        & ((key_pos[:, None, :] < SINK) | (key_pos[:, None, :] > query_pos[:, :, None] - WINDOW))
    )
    visible = visible[:, None, :, None, :]
    slot_peak = jnp.max(jnp.where(visible, scores, NEGATIVE_FILL), -1)
    weights = jnp.where(visible, jnp.exp(scores - slot_peak[..., None]), 0.0)
    slot_total = jnp.sum(weights, -1)
    slot_acc = jnp.einsum(
        "nasgb,nbah->nasgh",
        weights.astype(jnp.bfloat16),
        value_rows,
        preferred_element_type=jnp.float32,
    )
    member = slot_request[None, :] == jnp.arange(req_count, dtype=jnp.int32)[:, None]
    local_peak = jnp.max(
        jnp.where(member[:, :, None, None, None], slot_peak[None], NEGATIVE_FILL), 1
    )
    return (local_peak, (slot_peak, slot_total, slot_acc, member, picked))


def pool_sums(held, running_peak):
    slot_peak, slot_total, slot_acc, member, picked = held
    factor = jnp.exp(slot_peak - running_peak[picked])
    as_member = member.astype(jnp.float32)
    running_totals = jnp.einsum(
        "rn,nasg->rasg", as_member, slot_total * factor, precision=lax.Precision.HIGHEST
    )
    weighted_values = jnp.einsum(
        "rn,nasgh->rasgh", as_member, slot_acc * factor[..., None], precision=lax.Precision.HIGHEST
    )
    return (running_totals, weighted_values)


def fresh_part(query_rows, key_all, value_all):
    step_count = query_rows.shape[1]
    used = key_all.shape[1]
    scores = jnp.einsum(
        "rsagh,ruah->rasgu", query_rows, key_all, preferred_element_type=jnp.float32
    ) * (1.0 / math.sqrt(HEAD_SIZE))
    causal = (
        jnp.arange(used, dtype=jnp.int32)[None, :]
        <= jnp.arange(step_count, dtype=jnp.int32)[:, None]
    )
    causal = causal[None, None, :, None, :]
    running_peak = jnp.max(jnp.where(causal, scores, NEGATIVE_FILL), -1)
    weights = jnp.where(causal, jnp.exp(scores - running_peak[..., None]), 0.0)
    running_totals = jnp.sum(weights, -1)
    weighted_values = jnp.einsum(
        "rasgu,ruah->rasgh",
        weights.astype(jnp.bfloat16),
        value_all,
        preferred_element_type=jnp.float32,
    )
    return (running_peak, running_totals, weighted_values)


def merge_parts(earlier, later):
    running_peak = jnp.maximum(earlier[0], later[0])
    first_factor = jnp.exp(earlier[0] - running_peak)
    second_factor = jnp.exp(later[0] - running_peak)
    running_totals = earlier[1] * first_factor + later[1] * second_factor
    weighted_values = earlier[2] * first_factor[..., None] + later[2] * second_factor[..., None]
    return (running_peak, running_totals, weighted_values)


def slot_kernel(
    req_ref, len_ref, blk_ref, q_ref, k_ref, v_ref, peak_ref, tot_ref, acc_ref, *, ns, heads, qpk
):
    @pl.when(pl.program_id(0) == 0)
    def _():
        peak_ref[...] = jnp.full(peak_ref.shape, NEGATIVE_FILL, jnp.float32)
        tot_ref[...] = jnp.zeros(tot_ref.shape, jnp.float32)
        acc_ref[...] = jnp.zeros(acc_ref.shape, jnp.float32)

    base = pl.program_id(0) * ns
    req_count = q_ref.shape[0]
    rows = q_ref.shape[1]
    group = rows // heads
    width = k_ref.shape[1]
    head = k_ref.shape[2] // heads
    row = lax.broadcasted_iota(jnp.int32, (rows, width), 0)
    col = lax.broadcasted_iota(jnp.int32, (rows, width), 1)
    step_of = (row % group) // qpk

    def body(i, carry):
        req = req_ref[base + i]

        @pl.when(req < req_count)
        def _():
            owner = jnp.minimum(req, req_count - 1)
            length = len_ref[owner]
            key_pos = blk_ref[base + i] * width + col
            query_pos = length + step_of
            visible = (key_pos < length) & ((key_pos < SINK) | (key_pos > query_pos - WINDOW))
            q = q_ref[owner]
            k = k_ref[i]
            v = v_ref[i]
            scores = jnp.concatenate(
                [
                    lax.dot_general(
                        q[a * group : (a + 1) * group],
                        k[:, a * head : (a + 1) * head],
                        (((1,), (1,)), ((), ())),
                        preferred_element_type=jnp.float32,
                    )
                    for a in range(heads)
                ],
                0,
            ) * (1.0 / math.sqrt(HEAD_SIZE))
            peak = jnp.max(jnp.where(visible, scores, NEGATIVE_FILL), axis=1, keepdims=True)
            weights = jnp.where(visible, jnp.exp(scores - peak), 0.0)
            total = jnp.sum(weights, axis=1, keepdims=True)
            rounded = weights.astype(jnp.bfloat16)
            acc = jnp.concatenate(
                [
                    jnp.dot(
                        rounded[a * group : (a + 1) * group],
                        v[:, a * head : (a + 1) * head],
                        preferred_element_type=jnp.float32,
                    )
                    for a in range(heads)
                ],
                0,
            )
            old = peak_ref[owner]
            top = jnp.maximum(old, peak)
            old_factor = jnp.exp(old - top)
            new_factor = jnp.exp(peak - top)
            tot_ref[owner] = tot_ref[owner] * old_factor + total * new_factor
            acc_ref[owner] = acc_ref[owner] * old_factor + acc * new_factor
            peak_ref[owner] = top

        return carry

    lax.fori_loop(0, ns, body, 0, unroll=True)


def slot_attention(queries, lengths, slot_request, block_numbers, keys, values, heads, qpk):
    req_count, rows, head = queries.shape
    n_slots = keys.shape[0]
    width = keys.shape[1]
    ns = max(d for d in range(1, 11) if n_slots % d == 0)
    fixed = lambda n, sr, lr, br: (0, 0, 0)
    grid_spec = pltpu.PrefetchScalarGridSpec(
        num_scalar_prefetch=3,
        grid=(n_slots // ns,),
        in_specs=[
            pl.BlockSpec((req_count, rows, head), fixed),
            pl.BlockSpec((ns, width, keys.shape[2]), lambda n, sr, lr, br: (n, 0, 0)),
            pl.BlockSpec((ns, width, values.shape[2]), lambda n, sr, lr, br: (n, 0, 0)),
        ],
        out_specs=[
            pl.BlockSpec((req_count, rows, 1), fixed),
            pl.BlockSpec((req_count, rows, 1), fixed),
            pl.BlockSpec((req_count, rows, head), fixed),
        ],
    )
    return pl.pallas_call(
        partial(slot_kernel, ns=ns, heads=heads, qpk=qpk),
        grid_spec=grid_spec,
        out_shape=[
            jax.ShapeDtypeStruct((req_count, rows, 1), jnp.float32),
            jax.ShapeDtypeStruct((req_count, rows, 1), jnp.float32),
            jax.ShapeDtypeStruct((req_count, rows, head), jnp.float32),
        ],
    )(slot_request, lengths, block_numbers, queries, keys, values)

def pair_gather(part, axis_name):
    n = lax.axis_size(axis_name)
    assert n == 2
    side = lax.axis_index(axis_name)
    other = lax.ppermute(part, axis_name, [(0, 1), (1, 0)])
    return jnp.where(
        side == 0,
        jnp.concatenate([part, other], 0),
        jnp.concatenate([other, part], 0),
    )


def pair_scatter(parts, axis_name, rounded=True):
    n = lax.axis_size(axis_name)
    assert n == 2 and parts.shape[0] == 2
    side = lax.axis_index(axis_name)
    keep = lax.dynamic_index_in_dim(parts, side, 0, keepdims=True)
    send = lax.dynamic_index_in_dim(parts, 1 - side, 0, keepdims=True)
    got = lax.ppermute(send, axis_name, [(0, 1), (1, 0)])
    total = (keep.astype(jnp.float32) + got.astype(jnp.float32))[0]
    return total.astype(parts.dtype) if rounded else total


def doubling_gather(part, axis_name):
    n = lax.axis_size(axis_name)
    stages = n.bit_length() - 1
    assert 1 << stages == n
    index = lax.axis_index(axis_name)
    block = part[None]
    for bit in reversed(range(stages)):
        pairs = [(s, s ^ (1 << bit)) for s in range(n)]
        got = lax.ppermute(block, axis_name, pairs)
        low = ((index >> bit) & 1) == 0
        block = jnp.where(
            low, jnp.stack([block, got], 0), jnp.stack([got, block], 0)
        )
    block = block.reshape((2,) * stages + part.shape)
    block = block.transpose(tuple(reversed(range(stages))) + tuple(range(stages, stages + part.ndim)))
    return block.reshape((n * part.shape[0],) + part.shape[1:])


def seq_merge(peak, total, acc, n_seq, seq_index):
    stages = n_seq.bit_length() - 1
    assert 1 << stages == n_seq
    req_count = peak.shape[0]
    per = req_count // n_seq
    rest = peak.shape[1:]
    split = [2] * stages + [per]
    stats = jnp.stack([peak, total], 0).reshape([2] + split + list(rest))
    values = acc.reshape(split + list(acc.shape[1:]))
    for bit in range(stages):
        axis = stages - 1 - bit
        mine = (seq_index >> bit) & 1
        pairs = [(s, s ^ (1 << bit)) for s in range(n_seq)]
        keep_stats = lax.dynamic_index_in_dim(stats, mine, axis + 1, keepdims=True)
        send_stats = lax.dynamic_index_in_dim(stats, 1 - mine, axis + 1, keepdims=True)
        keep_values = lax.dynamic_index_in_dim(values, mine, axis, keepdims=True)
        send_values = lax.dynamic_index_in_dim(values, 1 - mine, axis, keepdims=True)
        got_stats = lax.ppermute(send_stats, "seq", pairs)
        got_values = lax.ppermute(send_values.astype(jnp.bfloat16), "seq", pairs).astype(
            jnp.float32
        )
        top = jnp.maximum(keep_stats[0], got_stats[0])
        keep_factor = jnp.exp(keep_stats[0] - top)
        got_factor = jnp.exp(got_stats[0] - top)
        stats = jnp.stack(
            [top, keep_stats[1] * keep_factor + got_stats[1] * got_factor], 0
        )
        values = keep_values * keep_factor[..., None] + got_values * got_factor[..., None]
    stats = stats.reshape((2, per) + tuple(rest))
    values = values.reshape((per,) + tuple(acc.shape[1:]))
    return (stats[0], stats[1], values)


def on_device(
    states,
    norm_gain,
    wq,
    wk,
    wv,
    wo,
    lengths,
    slot_request,
    slot_block_number,
    paged_key_cache,
    paged_value_cache,
):
    q_width = wq.shape[1]
    k_width = wk.shape[1]
    heads_kv = k_width // HEAD_SIZE
    req_count = lengths.shape[0]
    block_len = paged_key_cache.shape[1]
    key_rows = paged_key_cache.reshape(paged_key_cache.shape[0], block_len, heads_kv, HEAD_SIZE)
    value_rows = paged_value_cache.reshape(
        paged_value_cache.shape[0], block_len, heads_kv, HEAD_SIZE
    )
    step_count = states.shape[1]
    token_count = states.shape[0] * step_count
    own_states = states.reshape(token_count, -1)
    side = lax.axis_index("col")
    swap = [(0, 1), (1, 0)]
    other_states = lax.ppermute(own_states, "col", swap)
    as_float = own_states.astype(jnp.float32)
    squares = lax.psum(jnp.sum(as_float * as_float, -1), "row")
    other_squares = lax.ppermute(squares, "col", swap)

    def rms_norm(rows, sums):
        scale = lax.rsqrt(sums / D + EPSILON)[:, None]
        return (rows.astype(jnp.float32) * scale * norm_gain).astype(jnp.bfloat16)

    first = side == 0
    gathered = jnp.concatenate(
        [
            rms_norm(
                jnp.where(first, own_states, other_states), jnp.where(first, squares, other_squares)
            ),
            rms_norm(
                jnp.where(first, other_states, own_states), jnp.where(first, other_squares, squares)
            ),
        ],
        0,
    )
    parts_out = [
        jnp.dot(gathered, matrix, preferred_element_type=jnp.float32) for matrix in (wq, wk, wv)
    ]
    head_count = (q_width + 2 * k_width) // HEAD_SIZE
    output_projected = pair_scatter(
        jnp.concatenate(parts_out, axis=-1)
        .astype(jnp.bfloat16)
        .reshape(lax.axis_size("row"), token_count, -1),
        "row",
        rounded=False,
    ).reshape(token_count, head_count, HEAD_SIZE)
    q_heads = q_width // HEAD_SIZE
    token_positions = (
        lengths[:, None] + jnp.arange(step_count, dtype=jnp.int32)[None, :]
    ).reshape(token_count)
    query_rows = rotary_apply(output_projected[:, :q_heads], token_positions).astype(jnp.bfloat16)
    query_rows = query_rows.reshape(req_count, step_count, heads_kv, QUERY_PER_KEY, HEAD_SIZE)
    current_key = (
        rotary_apply(output_projected[:, q_heads : q_heads + heads_kv], token_positions)
        .astype(jnp.bfloat16)
        .reshape(req_count, step_count, heads_kv, HEAD_SIZE)
    )
    current_value = (
        output_projected[:, q_heads + heads_kv :]
        .astype(jnp.bfloat16)
        .reshape(req_count, step_count, heads_kv, HEAD_SIZE)
    )
    local_peak, local_totals, local_values = slot_attention(
        query_rows.transpose(0, 2, 1, 3, 4).reshape(req_count, -1, HEAD_SIZE),
        lengths,
        slot_request,
        slot_block_number,
        paged_key_cache,
        paged_value_cache,
        heads_kv,
        QUERY_PER_KEY,
    )
    local_peak = local_peak[..., 0]
    local_totals = local_totals[..., 0]
    n_seq = lax.axis_size("seq")
    per = req_count // n_seq
    seq_index = lax.axis_index("seq")
    mine = seq_index * per
    running_peak, running_totals, weighted_values = seq_merge(
        local_peak, local_totals, local_values, n_seq, seq_index
    )
    order = (per, heads_kv, step_count, QUERY_PER_KEY)
    running_peak = running_peak.reshape(order)
    running_totals = running_totals.reshape(order)
    weighted_values = weighted_values.reshape(order + (HEAD_SIZE,))
    own_queries = lax.dynamic_slice_in_dim(query_rows, mine, per, 0)
    fresh = fresh_part(
        own_queries,
        lax.dynamic_slice_in_dim(current_key, mine, per, 0),
        lax.dynamic_slice_in_dim(current_value, mine, per, 0),
    )
    running_peak, running_totals, weighted_values = merge_parts(
        (running_peak, running_totals, weighted_values), fresh
    )
    heads_out = (
        (weighted_values / running_totals[..., None])
        .transpose(0, 2, 1, 3, 4)
        .reshape(per, step_count, -1)
        .astype(jnp.bfloat16)
    )
    piece_rows = lax.all_gather(heads_out, "row", axis=0, tiled=False)
    n_row = piece_rows.shape[0]
    product = jnp.dot(
        piece_rows.reshape(n_row * per * step_count, -1), wo, preferred_element_type=jnp.float32
    )
    partials = product.reshape(n_row, per, step_count, -1)
    own_out = pair_scatter(partials.astype(jnp.bfloat16), "col").reshape(per, step_count, -1)
    attended = doubling_gather(own_out, "seq")
    return (
        attended,
        current_key.reshape(req_count, step_count, k_width),
        current_value.reshape(req_count, step_count, k_width),
    )


def solution(mesh):
    in_specs = (
        P("col", None, "row"),
        P("row"),
        P("row", "col"),
        P("row", "col"),
        P("row", "col"),
        P("col", "row"),
        P("row"),
        P(("row", "seq")),
        P(("row", "seq")),
        P(("row", "seq"), None, "col"),
        P(("row", "seq"), None, "col"),
    )
    out_specs = (P("col", None, "row"), P("row", None, "col"), P("row", None, "col"))
    return jax.shard_map(
        on_device, mesh=mesh, in_specs=in_specs, out_specs=out_specs, check_vma=False
    )
```

```python
import math
from functools import partial

import jax
import jax.numpy as jnp
from jax import lax
from jax.experimental import pallas as pl
from jax.experimental.pallas import tpu as pltpu
from jax.sharding import PartitionSpec as P

D = 5120
HEAD_SIZE = 128
WINDOW = 4096
SINK = 4
QUERY_PER_KEY = 4


EPSILON = 1e-05
NEGATIVE_FILL = -1e30
ROPE_BASE = 100000000.0


def rotary_apply(values, token_positions):
    half_dim = values.shape[-1] // 2
    frequency = ROPE_BASE ** (-(jnp.arange(half_dim, dtype=jnp.float32) * 2.0 / values.shape[-1]))
    angles = (token_positions.astype(jnp.float32)[..., None] * frequency)[..., None, :]
    cosine = jnp.cos(angles)
    sine_part = jnp.sin(angles)
    lower = values[..., :half_dim]
    upper = values[..., half_dim:]
    return jnp.concatenate(
        [lower * cosine - upper * sine_part, upper * cosine + lower * sine_part], -1
    )


def slot_parts(query_rows, lengths, slot_request, slot_block_number, key_rows, value_rows):
    req_count = query_rows.shape[0]
    step_count = query_rows.shape[1]
    block_len = key_rows.shape[1]
    picked = jnp.minimum(slot_request, req_count - 1)
    in_use = slot_request < req_count
    slot_queries = query_rows[picked]
    scores = jnp.einsum(
        "nsagh,nbah->nasgb", slot_queries, key_rows, preferred_element_type=jnp.float32
    ) * (1.0 / math.sqrt(HEAD_SIZE))
    key_pos = (
        slot_block_number[:, None] * block_len + jnp.arange(block_len, dtype=jnp.int32)[None, :]
    )
    own_len = lengths[picked]
    query_pos = own_len[:, None] + jnp.arange(step_count, dtype=jnp.int32)[None, :]
    visible = (
        in_use[:, None, None]
        & (key_pos[:, None, :] < own_len[:, None, None])
        & ((key_pos[:, None, :] < SINK) | (key_pos[:, None, :] > query_pos[:, :, None] - WINDOW))
    )
    visible = visible[:, None, :, None, :]
    slot_peak = jnp.max(jnp.where(visible, scores, NEGATIVE_FILL), -1)
    weights = jnp.where(visible, jnp.exp(scores - slot_peak[..., None]), 0.0)
    slot_total = jnp.sum(weights, -1)
    slot_acc = jnp.einsum(
        "nasgb,nbah->nasgh",
        weights.astype(jnp.bfloat16),
        value_rows,
        preferred_element_type=jnp.float32,
    )
    member = slot_request[None, :] == jnp.arange(req_count, dtype=jnp.int32)[:, None]
    local_peak = jnp.max(
        jnp.where(member[:, :, None, None, None], slot_peak[None], NEGATIVE_FILL), 1
    )
    return (local_peak, (slot_peak, slot_total, slot_acc, member, picked))


def pool_sums(held, running_peak):
    slot_peak, slot_total, slot_acc, member, picked = held
    factor = jnp.exp(slot_peak - running_peak[picked])
    as_member = member.astype(jnp.float32)
    running_totals = jnp.einsum(
        "rn,nasg->rasg", as_member, slot_total * factor, precision=lax.Precision.HIGHEST
    )
    weighted_values = jnp.einsum(
        "rn,nasgh->rasgh", as_member, slot_acc * factor[..., None], precision=lax.Precision.HIGHEST
    )
    return (running_totals, weighted_values)


def fresh_part(query_rows, key_all, value_all):
    step_count = query_rows.shape[1]
    used = key_all.shape[1]
    scores = jnp.einsum(
        "rsagh,ruah->rasgu", query_rows, key_all, preferred_element_type=jnp.float32
    ) * (1.0 / math.sqrt(HEAD_SIZE))
    causal = (
        jnp.arange(used, dtype=jnp.int32)[None, :]
        <= jnp.arange(step_count, dtype=jnp.int32)[:, None]
    )
    causal = causal[None, None, :, None, :]
    running_peak = jnp.max(jnp.where(causal, scores, NEGATIVE_FILL), -1)
    weights = jnp.where(causal, jnp.exp(scores - running_peak[..., None]), 0.0)
    running_totals = jnp.sum(weights, -1)
    weighted_values = jnp.einsum(
        "rasgu,ruah->rasgh",
        weights.astype(jnp.bfloat16),
        value_all,
        preferred_element_type=jnp.float32,
    )
    return (running_peak, running_totals, weighted_values)


def merge_parts(earlier, later):
    running_peak = jnp.maximum(earlier[0], later[0])
    first_factor = jnp.exp(earlier[0] - running_peak)
    second_factor = jnp.exp(later[0] - running_peak)
    running_totals = earlier[1] * first_factor + later[1] * second_factor
    weighted_values = earlier[2] * first_factor[..., None] + later[2] * second_factor[..., None]
    return (running_peak, running_totals, weighted_values)


def slot_kernel(
    req_ref, len_ref, blk_ref, q_ref, k_ref, v_ref, peak_ref, tot_ref, acc_ref, *, ns, heads, qpk
):
    @pl.when(pl.program_id(0) == 0)
    def _():
        peak_ref[...] = jnp.full(peak_ref.shape, NEGATIVE_FILL, jnp.float32)
        tot_ref[...] = jnp.zeros(tot_ref.shape, jnp.float32)
        acc_ref[...] = jnp.zeros(acc_ref.shape, jnp.float32)

    base = pl.program_id(0) * ns
    req_count = q_ref.shape[0]
    rows = q_ref.shape[1]
    group = rows // heads
    width = k_ref.shape[1]
    head = k_ref.shape[2] // heads
    row = lax.broadcasted_iota(jnp.int32, (rows, width), 0)
    col = lax.broadcasted_iota(jnp.int32, (rows, width), 1)
    step_of = (row % group) // qpk

    results = []
    for i in range(ns):
        req = req_ref[base + i]
        owner = jnp.minimum(req, req_count - 1)
        length = len_ref[owner]
        key_pos = blk_ref[base + i] * width + col
        query_pos = length + step_of
        visible = (
            (req < req_count)
            & (key_pos < length)
            & ((key_pos < SINK) | (key_pos > query_pos - WINDOW))
        )
        q = q_ref[owner]
        k = k_ref[i]
        v = v_ref[i]
        scores = jnp.concatenate(
            [
                lax.dot_general(
                    q[a * group : (a + 1) * group],
                    k[:, a * head : (a + 1) * head],
                    (((1,), (1,)), ((), ())),
                    preferred_element_type=jnp.float32,
                )
                for a in range(heads)
            ],
            0,
        ) * (1.0 / math.sqrt(HEAD_SIZE))
        peak = jnp.max(jnp.where(visible, scores, NEGATIVE_FILL), axis=1, keepdims=True)
        weights = jnp.where(visible, jnp.exp(scores - peak), 0.0)
        total = jnp.sum(weights, axis=1, keepdims=True)
        rounded = weights.astype(jnp.bfloat16)
        acc = jnp.concatenate(
            [
                jnp.dot(
                    rounded[a * group : (a + 1) * group],
                    v[:, a * head : (a + 1) * head],
                    preferred_element_type=jnp.float32,
                )
                for a in range(heads)
            ],
            0,
        )
        results.append((owner, peak, total, acc))
    for owner, peak, total, acc in results:
        old = peak_ref[owner]
        top = jnp.maximum(old, peak)
        old_factor = jnp.exp(old - top)
        new_factor = jnp.exp(peak - top)
        tot_ref[owner] = tot_ref[owner] * old_factor + total * new_factor
        acc_ref[owner] = acc_ref[owner] * old_factor + acc * new_factor
        peak_ref[owner] = top

def slot_attention(queries, lengths, slot_request, block_numbers, keys, values, heads, qpk):
    req_count, rows, head = queries.shape
    n_slots = keys.shape[0]
    width = keys.shape[1]
    ns = max(d for d in range(1, 11) if n_slots % d == 0)
    fixed = lambda n, sr, lr, br: (0, 0, 0)
    grid_spec = pltpu.PrefetchScalarGridSpec(
        num_scalar_prefetch=3,
        grid=(n_slots // ns,),
        in_specs=[
            pl.BlockSpec((req_count, rows, head), fixed),
            pl.BlockSpec((ns, width, keys.shape[2]), lambda n, sr, lr, br: (n, 0, 0)),
            pl.BlockSpec((ns, width, values.shape[2]), lambda n, sr, lr, br: (n, 0, 0)),
        ],
        out_specs=[
            pl.BlockSpec((req_count, rows, 1), fixed),
            pl.BlockSpec((req_count, rows, 1), fixed),
            pl.BlockSpec((req_count, rows, head), fixed),
        ],
    )
    return pl.pallas_call(
        partial(slot_kernel, ns=ns, heads=heads, qpk=qpk),
        grid_spec=grid_spec,
        out_shape=[
            jax.ShapeDtypeStruct((req_count, rows, 1), jnp.float32),
            jax.ShapeDtypeStruct((req_count, rows, 1), jnp.float32),
            jax.ShapeDtypeStruct((req_count, rows, head), jnp.float32),
        ],
    )(slot_request, lengths, block_numbers, queries, keys, values)

def pair_gather(part, axis_name):
    n = lax.axis_size(axis_name)
    assert n == 2
    side = lax.axis_index(axis_name)
    other = lax.ppermute(part, axis_name, [(0, 1), (1, 0)])
    return jnp.where(
        side == 0,
        jnp.concatenate([part, other], 0),
        jnp.concatenate([other, part], 0),
    )


def pair_scatter(parts, axis_name, rounded=True):
    n = lax.axis_size(axis_name)
    assert n == 2 and parts.shape[0] == 2
    side = lax.axis_index(axis_name)
    keep = lax.dynamic_index_in_dim(parts, side, 0, keepdims=True)
    send = lax.dynamic_index_in_dim(parts, 1 - side, 0, keepdims=True)
    got = lax.ppermute(send, axis_name, [(0, 1), (1, 0)])
    total = (keep.astype(jnp.float32) + got.astype(jnp.float32))[0]
    return total.astype(parts.dtype) if rounded else total


def doubling_gather(part, axis_name):
    n = lax.axis_size(axis_name)
    stages = n.bit_length() - 1
    assert 1 << stages == n
    index = lax.axis_index(axis_name)
    block = part[None]
    for bit in reversed(range(stages)):
        pairs = [(s, s ^ (1 << bit)) for s in range(n)]
        got = lax.ppermute(block, axis_name, pairs)
        low = ((index >> bit) & 1) == 0
        block = jnp.where(
            low, jnp.stack([block, got], 0), jnp.stack([got, block], 0)
        )
    block = block.reshape((2,) * stages + part.shape)
    block = block.transpose(tuple(reversed(range(stages))) + tuple(range(stages, stages + part.ndim)))
    return block.reshape((n * part.shape[0],) + part.shape[1:])


def seq_merge(peak, total, acc, n_seq, seq_index):
    stages = n_seq.bit_length() - 1
    assert 1 << stages == n_seq
    req_count = peak.shape[0]
    per = req_count // n_seq
    rest = peak.shape[1:]
    split = [2] * stages + [per]
    stats = jnp.stack([peak, total], 0).reshape([2] + split + list(rest))
    values = acc.reshape(split + list(acc.shape[1:]))
    for bit in range(stages):
        axis = stages - 1 - bit
        mine = (seq_index >> bit) & 1
        pairs = [(s, s ^ (1 << bit)) for s in range(n_seq)]
        keep_stats = lax.dynamic_index_in_dim(stats, mine, axis + 1, keepdims=True)
        send_stats = lax.dynamic_index_in_dim(stats, 1 - mine, axis + 1, keepdims=True)
        keep_values = lax.dynamic_index_in_dim(values, mine, axis, keepdims=True)
        send_values = lax.dynamic_index_in_dim(values, 1 - mine, axis, keepdims=True)
        got_stats = lax.ppermute(send_stats, "seq", pairs)
        got_values = lax.ppermute(send_values.astype(jnp.bfloat16), "seq", pairs).astype(
            jnp.float32
        )
        top = jnp.maximum(keep_stats[0], got_stats[0])
        keep_factor = jnp.exp(keep_stats[0] - top)
        got_factor = jnp.exp(got_stats[0] - top)
        stats = jnp.stack(
            [top, keep_stats[1] * keep_factor + got_stats[1] * got_factor], 0
        )
        values = keep_values * keep_factor[..., None] + got_values * got_factor[..., None]
    stats = stats.reshape((2, per) + tuple(rest))
    values = values.reshape((per,) + tuple(acc.shape[1:]))
    return (stats[0], stats[1], values)


def on_device(
    states,
    norm_gain,
    wq,
    wk,
    wv,
    wo,
    lengths,
    slot_request,
    slot_block_number,
    paged_key_cache,
    paged_value_cache,
):
    q_width = wq.shape[1]
    k_width = wk.shape[1]
    heads_kv = k_width // HEAD_SIZE
    req_count = lengths.shape[0]
    block_len = paged_key_cache.shape[1]
    key_rows = paged_key_cache.reshape(paged_key_cache.shape[0], block_len, heads_kv, HEAD_SIZE)
    value_rows = paged_value_cache.reshape(
        paged_value_cache.shape[0], block_len, heads_kv, HEAD_SIZE
    )
    step_count = states.shape[1]
    token_count = states.shape[0] * step_count
    own_states = states.reshape(token_count, -1)
    side = lax.axis_index("col")
    swap = [(0, 1), (1, 0)]
    other_states = lax.ppermute(own_states, "col", swap)
    as_float = own_states.astype(jnp.float32)
    squares = lax.psum(jnp.sum(as_float * as_float, -1), "row")
    other_squares = lax.ppermute(squares, "col", swap)

    def rms_norm(rows, sums):
        scale = lax.rsqrt(sums / D + EPSILON)[:, None]
        return (rows.astype(jnp.float32) * scale * norm_gain).astype(jnp.bfloat16)

    first = side == 0
    gathered = jnp.concatenate(
        [
            rms_norm(
                jnp.where(first, own_states, other_states), jnp.where(first, squares, other_squares)
            ),
            rms_norm(
                jnp.where(first, other_states, own_states), jnp.where(first, other_squares, squares)
            ),
        ],
        0,
    )
    parts_out = [
        jnp.dot(gathered, matrix, preferred_element_type=jnp.float32) for matrix in (wq, wk, wv)
    ]
    head_count = (q_width + 2 * k_width) // HEAD_SIZE
    output_projected = pair_scatter(
        jnp.concatenate(parts_out, axis=-1)
        .astype(jnp.bfloat16)
        .reshape(lax.axis_size("row"), token_count, -1),
        "row",
        rounded=False,
    ).reshape(token_count, head_count, HEAD_SIZE)
    q_heads = q_width // HEAD_SIZE
    token_positions = (
        lengths[:, None] + jnp.arange(step_count, dtype=jnp.int32)[None, :]
    ).reshape(token_count)
    query_rows = rotary_apply(output_projected[:, :q_heads], token_positions).astype(jnp.bfloat16)
    query_rows = query_rows.reshape(req_count, step_count, heads_kv, QUERY_PER_KEY, HEAD_SIZE)
    current_key = (
        rotary_apply(output_projected[:, q_heads : q_heads + heads_kv], token_positions)
        .astype(jnp.bfloat16)
        .reshape(req_count, step_count, heads_kv, HEAD_SIZE)
    )
    current_value = (
        output_projected[:, q_heads + heads_kv :]
        .astype(jnp.bfloat16)
        .reshape(req_count, step_count, heads_kv, HEAD_SIZE)
    )
    local_peak, local_totals, local_values = slot_attention(
        query_rows.transpose(0, 2, 1, 3, 4).reshape(req_count, -1, HEAD_SIZE),
        lengths,
        slot_request,
        slot_block_number,
        paged_key_cache,
        paged_value_cache,
        heads_kv,
        QUERY_PER_KEY,
    )
    local_peak = local_peak[..., 0]
    local_totals = local_totals[..., 0]
    n_seq = lax.axis_size("seq")
    per = req_count // n_seq
    seq_index = lax.axis_index("seq")
    mine = seq_index * per
    running_peak, running_totals, weighted_values = seq_merge(
        local_peak, local_totals, local_values, n_seq, seq_index
    )
    order = (per, heads_kv, step_count, QUERY_PER_KEY)
    running_peak = running_peak.reshape(order)
    running_totals = running_totals.reshape(order)
    weighted_values = weighted_values.reshape(order + (HEAD_SIZE,))
    own_queries = lax.dynamic_slice_in_dim(query_rows, mine, per, 0)
    fresh = fresh_part(
        own_queries,
        lax.dynamic_slice_in_dim(current_key, mine, per, 0),
        lax.dynamic_slice_in_dim(current_value, mine, per, 0),
    )
    running_peak, running_totals, weighted_values = merge_parts(
        (running_peak, running_totals, weighted_values), fresh
    )
    heads_out = (
        (weighted_values / running_totals[..., None])
        .transpose(0, 2, 1, 3, 4)
        .reshape(per, step_count, -1)
        .astype(jnp.bfloat16)
    )
    piece_rows = lax.all_gather(heads_out, "row", axis=0, tiled=False)
    n_row = piece_rows.shape[0]
    product = jnp.dot(
        piece_rows.reshape(n_row * per * step_count, -1), wo, preferred_element_type=jnp.float32
    )
    partials = product.reshape(n_row, per, step_count, -1)
    own_out = pair_scatter(partials.astype(jnp.bfloat16), "col").reshape(per, step_count, -1)
    attended = doubling_gather(own_out, "seq")
    return (
        attended,
        current_key.reshape(req_count, step_count, k_width),
        current_value.reshape(req_count, step_count, k_width),
    )


def solution(mesh):
    in_specs = (
        P("col", None, "row"),
        P("row"),
        P("row", "col"),
        P("row", "col"),
        P("row", "col"),
        P("col", "row"),
        P("row"),
        P(("row", "seq")),
        P(("row", "seq")),
        P(("row", "seq"), None, "col"),
        P(("row", "seq"), None, "col"),
    )
    out_specs = (P("col", None, "row"), P("row", None, "col"), P("row", None, "col"))
    return jax.shard_map(
        on_device, mesh=mesh, in_specs=in_specs, out_specs=out_specs, check_vma=False
    )
```

```python
import math
from functools import partial

import jax
import jax.numpy as jnp
from jax import lax
from jax.experimental import pallas as pl
from jax.experimental.pallas import tpu as pltpu
from jax.sharding import PartitionSpec as P

D = 5120
HEAD_SIZE = 128
WINDOW = 4096
SINK = 4
QUERY_PER_KEY = 4


EPSILON = 1e-05
NEGATIVE_FILL = -1e30
ROPE_BASE = 100000000.0


def rotary_apply(values, token_positions):
    half_dim = values.shape[-1] // 2
    frequency = ROPE_BASE ** (-(jnp.arange(half_dim, dtype=jnp.float32) * 2.0 / values.shape[-1]))
    angles = (token_positions.astype(jnp.float32)[..., None] * frequency)[..., None, :]
    cosine = jnp.cos(angles)
    sine_part = jnp.sin(angles)
    lower = values[..., :half_dim]
    upper = values[..., half_dim:]
    return jnp.concatenate(
        [lower * cosine - upper * sine_part, upper * cosine + lower * sine_part], -1
    )


def slot_parts(query_rows, lengths, slot_request, slot_block_number, key_rows, value_rows):
    req_count = query_rows.shape[0]
    step_count = query_rows.shape[1]
    block_len = key_rows.shape[1]
    picked = jnp.minimum(slot_request, req_count - 1)
    in_use = slot_request < req_count
    slot_queries = query_rows[picked]
    scores = jnp.einsum(
        "nsagh,nbah->nasgb", slot_queries, key_rows, preferred_element_type=jnp.float32
    ) * (1.0 / math.sqrt(HEAD_SIZE))
    key_pos = (
        slot_block_number[:, None] * block_len + jnp.arange(block_len, dtype=jnp.int32)[None, :]
    )
    own_len = lengths[picked]
    query_pos = own_len[:, None] + jnp.arange(step_count, dtype=jnp.int32)[None, :]
    visible = (
        in_use[:, None, None]
        & (key_pos[:, None, :] < own_len[:, None, None])
        & ((key_pos[:, None, :] < SINK) | (key_pos[:, None, :] > query_pos[:, :, None] - WINDOW))
    )
    visible = visible[:, None, :, None, :]
    slot_peak = jnp.max(jnp.where(visible, scores, NEGATIVE_FILL), -1)
    weights = jnp.where(visible, jnp.exp(scores - slot_peak[..., None]), 0.0)
    slot_total = jnp.sum(weights, -1)
    slot_acc = jnp.einsum(
        "nasgb,nbah->nasgh",
        weights.astype(jnp.bfloat16),
        value_rows,
        preferred_element_type=jnp.float32,
    )
    member = slot_request[None, :] == jnp.arange(req_count, dtype=jnp.int32)[:, None]
    local_peak = jnp.max(
        jnp.where(member[:, :, None, None, None], slot_peak[None], NEGATIVE_FILL), 1
    )
    return (local_peak, (slot_peak, slot_total, slot_acc, member, picked))


def pool_sums(held, running_peak):
    slot_peak, slot_total, slot_acc, member, picked = held
    factor = jnp.exp(slot_peak - running_peak[picked])
    as_member = member.astype(jnp.float32)
    running_totals = jnp.einsum(
        "rn,nasg->rasg", as_member, slot_total * factor, precision=lax.Precision.HIGHEST
    )
    weighted_values = jnp.einsum(
        "rn,nasgh->rasgh", as_member, slot_acc * factor[..., None], precision=lax.Precision.HIGHEST
    )
    return (running_totals, weighted_values)


def fresh_part(query_rows, key_all, value_all):
    step_count = query_rows.shape[1]
    used = key_all.shape[1]
    scores = jnp.einsum(
        "rsagh,ruah->rasgu", query_rows, key_all, preferred_element_type=jnp.float32
    ) * (1.0 / math.sqrt(HEAD_SIZE))
    causal = (
        jnp.arange(used, dtype=jnp.int32)[None, :]
        <= jnp.arange(step_count, dtype=jnp.int32)[:, None]
    )
    causal = causal[None, None, :, None, :]
    running_peak = jnp.max(jnp.where(causal, scores, NEGATIVE_FILL), -1)
    weights = jnp.where(causal, jnp.exp(scores - running_peak[..., None]), 0.0)
    running_totals = jnp.sum(weights, -1)
    weighted_values = jnp.einsum(
        "rasgu,ruah->rasgh",
        weights.astype(jnp.bfloat16),
        value_all,
        preferred_element_type=jnp.float32,
    )
    return (running_peak, running_totals, weighted_values)


def merge_parts(earlier, later):
    running_peak = jnp.maximum(earlier[0], later[0])
    first_factor = jnp.exp(earlier[0] - running_peak)
    second_factor = jnp.exp(later[0] - running_peak)
    running_totals = earlier[1] * first_factor + later[1] * second_factor
    weighted_values = earlier[2] * first_factor[..., None] + later[2] * second_factor[..., None]
    return (running_peak, running_totals, weighted_values)


def slot_kernel(
    req_ref, len_ref, blk_ref, q_ref, k_ref, v_ref, peak_ref, tot_ref, acc_ref, *, ns, heads, qpk
):
    @pl.when(pl.program_id(0) == 0)
    def _():
        peak_ref[...] = jnp.full(peak_ref.shape, NEGATIVE_FILL, jnp.float32)
        tot_ref[...] = jnp.zeros(tot_ref.shape, jnp.float32)
        acc_ref[...] = jnp.zeros(acc_ref.shape, jnp.float32)

    base = pl.program_id(0) * ns
    req_count = q_ref.shape[0]
    rows = q_ref.shape[1]
    group = rows // heads
    width = k_ref.shape[1]
    head = k_ref.shape[2] // heads
    row = lax.broadcasted_iota(jnp.int32, (rows, width), 0)
    col = lax.broadcasted_iota(jnp.int32, (rows, width), 1)
    step_of = (row % group) // qpk

    results = []
    for i in range(ns):
        req = req_ref[base + i]
        owner = jnp.minimum(req, req_count - 1)
        length = len_ref[owner]
        key_pos = blk_ref[base + i] * width + col
        query_pos = length + step_of
        visible = (
            (req < req_count)
            & (key_pos < length)
            & ((key_pos < SINK) | (key_pos > query_pos - WINDOW))
        )
        q = q_ref[owner]
        k = k_ref[i]
        v = v_ref[i]
        scores = jnp.concatenate(
            [
                lax.dot_general(
                    q[a * group : (a + 1) * group],
                    k[:, a * head : (a + 1) * head],
                    (((1,), (1,)), ((), ())),
                    preferred_element_type=jnp.float32,
                )
                for a in range(heads)
            ],
            0,
        ) * (1.0 / math.sqrt(HEAD_SIZE))
        peak = jnp.max(jnp.where(visible, scores, NEGATIVE_FILL), axis=1, keepdims=True)
        weights = jnp.where(visible, jnp.exp(scores - peak), 0.0)
        total = jnp.sum(weights, axis=1, keepdims=True)
        rounded = weights.astype(jnp.bfloat16)
        acc = jnp.concatenate(
            [
                jnp.dot(
                    rounded[a * group : (a + 1) * group],
                    v[:, a * head : (a + 1) * head],
                    preferred_element_type=jnp.float32,
                )
                for a in range(heads)
            ],
            0,
        )
        results.append((owner, peak, total, acc))
    for owner, peak, total, acc in results:
        old = peak_ref[owner]
        top = jnp.maximum(old, peak)
        old_factor = jnp.exp(old - top)
        new_factor = jnp.exp(peak - top)
        tot_ref[owner] = tot_ref[owner] * old_factor + total * new_factor
        acc_ref[owner] = acc_ref[owner] * old_factor + acc * new_factor
        peak_ref[owner] = top

def slot_attention(queries, lengths, slot_request, block_numbers, keys, values, heads, qpk):
    req_count, rows, head = queries.shape
    n_slots = keys.shape[0]
    width = keys.shape[1]
    ns = max(d for d in range(1, 11) if n_slots % d == 0)
    fixed = lambda n, sr, lr, br: (0, 0, 0)
    grid_spec = pltpu.PrefetchScalarGridSpec(
        num_scalar_prefetch=3,
        grid=(n_slots // ns,),
        in_specs=[
            pl.BlockSpec((req_count, rows, head), fixed),
            pl.BlockSpec((ns, width, keys.shape[2]), lambda n, sr, lr, br: (n, 0, 0)),
            pl.BlockSpec((ns, width, values.shape[2]), lambda n, sr, lr, br: (n, 0, 0)),
        ],
        out_specs=[
            pl.BlockSpec((req_count, rows, 1), fixed),
            pl.BlockSpec((req_count, rows, 1), fixed),
            pl.BlockSpec((req_count, rows, head), fixed),
        ],
    )
    return pl.pallas_call(
        partial(slot_kernel, ns=ns, heads=heads, qpk=qpk),
        grid_spec=grid_spec,
        out_shape=[
            jax.ShapeDtypeStruct((req_count, rows, 1), jnp.float32),
            jax.ShapeDtypeStruct((req_count, rows, 1), jnp.float32),
            jax.ShapeDtypeStruct((req_count, rows, head), jnp.float32),
        ],
    )(slot_request, lengths, block_numbers, queries, keys, values)

def pair_gather(part, axis_name):
    n = lax.axis_size(axis_name)
    assert n == 2
    side = lax.axis_index(axis_name)
    other = lax.ppermute(part, axis_name, [(0, 1), (1, 0)])
    return jnp.where(
        side == 0,
        jnp.concatenate([part, other], 0),
        jnp.concatenate([other, part], 0),
    )


def pair_scatter(parts, axis_name, rounded=True):
    n = lax.axis_size(axis_name)
    assert n == 2 and parts.shape[0] == 2
    side = lax.axis_index(axis_name)
    keep = lax.dynamic_index_in_dim(parts, side, 0, keepdims=True)
    send = lax.dynamic_index_in_dim(parts, 1 - side, 0, keepdims=True)
    got = lax.ppermute(send, axis_name, [(0, 1), (1, 0)])
    total = (keep.astype(jnp.float32) + got.astype(jnp.float32))[0]
    return total.astype(parts.dtype) if rounded else total


def doubling_gather(part, axis_name):
    n = lax.axis_size(axis_name)
    stages = n.bit_length() - 1
    assert 1 << stages == n
    index = lax.axis_index(axis_name)
    block = part[None]
    for bit in reversed(range(stages)):
        pairs = [(s, s ^ (1 << bit)) for s in range(n)]
        got = lax.ppermute(block, axis_name, pairs)
        low = ((index >> bit) & 1) == 0
        block = jnp.where(
            low, jnp.stack([block, got], 0), jnp.stack([got, block], 0)
        )
    block = block.reshape((2,) * stages + part.shape)
    block = block.transpose(tuple(reversed(range(stages))) + tuple(range(stages, stages + part.ndim)))
    return block.reshape((n * part.shape[0],) + part.shape[1:])


def pack_message(stats, values):
    lanes = jnp.concatenate([stats[0], stats[1]], -1)
    high = lax.reduce_precision(lanes, exponent_bits=8, mantissa_bits=7)
    rest = lanes - high
    middle = lax.reduce_precision(rest, exponent_bits=8, mantissa_bits=7)
    low = rest - middle
    extra = jnp.stack([high, middle, low], -2).astype(jnp.bfloat16)
    return jnp.concatenate([values.astype(jnp.bfloat16), extra], -2)


def unpack_message(message, rows):
    values = message[..., :rows, :].astype(jnp.float32)
    extra = message[..., rows:, :].astype(jnp.float32)
    lanes = extra[..., 0, :] + (extra[..., 1, :] + extra[..., 2, :])
    return jnp.stack([lanes[..., :rows], lanes[..., rows:]], 0), values


def seq_merge(peak, total, acc, n_seq, seq_index):
    stages = n_seq.bit_length() - 1
    assert 1 << stages == n_seq
    req_count = peak.shape[0]
    per = req_count // n_seq
    rest = peak.shape[1:]
    split = [2] * stages + [per]
    stats = jnp.stack([peak, total], 0).reshape([2] + split + list(rest))
    values = acc.reshape(split + list(acc.shape[1:]))
    for bit in range(stages):
        axis = stages - 1 - bit
        mine = (seq_index >> bit) & 1
        pairs = [(s, s ^ (1 << bit)) for s in range(n_seq)]
        keep_stats = lax.dynamic_index_in_dim(stats, mine, axis + 1, keepdims=True)
        send_stats = lax.dynamic_index_in_dim(stats, 1 - mine, axis + 1, keepdims=True)
        keep_values = lax.dynamic_index_in_dim(values, mine, axis, keepdims=True)
        send_values = lax.dynamic_index_in_dim(values, 1 - mine, axis, keepdims=True)
        if 2 * rest[-1] == values.shape[-1]:
            got_stats, got_values = unpack_message(
                lax.ppermute(pack_message(send_stats, send_values), "seq", pairs), rest[-1]
            )
        else:
            got_stats = lax.ppermute(send_stats, "seq", pairs)
            got_values = lax.ppermute(send_values.astype(jnp.bfloat16), "seq", pairs).astype(
                jnp.float32
            )
        top = jnp.maximum(keep_stats[0], got_stats[0])
        keep_factor = jnp.exp(keep_stats[0] - top)
        got_factor = jnp.exp(got_stats[0] - top)
        stats = jnp.stack(
            [top, keep_stats[1] * keep_factor + got_stats[1] * got_factor], 0
        )
        values = keep_values * keep_factor[..., None] + got_values * got_factor[..., None]
    stats = stats.reshape((2, per) + tuple(rest))
    values = values.reshape((per,) + tuple(acc.shape[1:]))
    return (stats[0], stats[1], values)


def on_device(
    states,
    norm_gain,
    wq,
    wk,
    wv,
    wo,
    lengths,
    slot_request,
    slot_block_number,
    paged_key_cache,
    paged_value_cache,
):
    q_width = wq.shape[1]
    k_width = wk.shape[1]
    heads_kv = k_width // HEAD_SIZE
    req_count = lengths.shape[0]
    block_len = paged_key_cache.shape[1]
    key_rows = paged_key_cache.reshape(paged_key_cache.shape[0], block_len, heads_kv, HEAD_SIZE)
    value_rows = paged_value_cache.reshape(
        paged_value_cache.shape[0], block_len, heads_kv, HEAD_SIZE
    )
    step_count = states.shape[1]
    token_count = states.shape[0] * step_count
    own_states = states.reshape(token_count, -1)
    side = lax.axis_index("col")
    swap = [(0, 1), (1, 0)]
    other_states = lax.ppermute(own_states, "col", swap)
    as_float = own_states.astype(jnp.float32)
    squares = lax.psum(jnp.sum(as_float * as_float, -1), "row")
    other_squares = lax.ppermute(squares, "col", swap)

    def rms_norm(rows, sums):
        scale = lax.rsqrt(sums / D + EPSILON)[:, None]
        return (rows.astype(jnp.float32) * scale * norm_gain).astype(jnp.bfloat16)

    first = side == 0
    gathered = jnp.concatenate(
        [
            rms_norm(
                jnp.where(first, own_states, other_states), jnp.where(first, squares, other_squares)
            ),
            rms_norm(
                jnp.where(first, other_states, own_states), jnp.where(first, other_squares, squares)
            ),
        ],
        0,
    )
    parts_out = [
        jnp.dot(gathered, matrix, preferred_element_type=jnp.float32) for matrix in (wq, wk, wv)
    ]
    head_count = (q_width + 2 * k_width) // HEAD_SIZE
    output_projected = pair_scatter(
        jnp.concatenate(parts_out, axis=-1)
        .astype(jnp.bfloat16)
        .reshape(lax.axis_size("row"), token_count, -1),
        "row",
        rounded=False,
    ).reshape(token_count, head_count, HEAD_SIZE)
    q_heads = q_width // HEAD_SIZE
    token_positions = (
        lengths[:, None] + jnp.arange(step_count, dtype=jnp.int32)[None, :]
    ).reshape(token_count)
    query_rows = rotary_apply(output_projected[:, :q_heads], token_positions).astype(jnp.bfloat16)
    query_rows = query_rows.reshape(req_count, step_count, heads_kv, QUERY_PER_KEY, HEAD_SIZE)
    current_key = (
        rotary_apply(output_projected[:, q_heads : q_heads + heads_kv], token_positions)
        .astype(jnp.bfloat16)
        .reshape(req_count, step_count, heads_kv, HEAD_SIZE)
    )
    current_value = (
        output_projected[:, q_heads + heads_kv :]
        .astype(jnp.bfloat16)
        .reshape(req_count, step_count, heads_kv, HEAD_SIZE)
    )
    local_peak, local_totals, local_values = slot_attention(
        query_rows.transpose(0, 2, 1, 3, 4).reshape(req_count, -1, HEAD_SIZE),
        lengths,
        slot_request,
        slot_block_number,
        paged_key_cache,
        paged_value_cache,
        heads_kv,
        QUERY_PER_KEY,
    )
    local_peak = local_peak[..., 0]
    local_totals = local_totals[..., 0]
    n_seq = lax.axis_size("seq")
    per = req_count // n_seq
    seq_index = lax.axis_index("seq")
    mine = seq_index * per
    running_peak, running_totals, weighted_values = seq_merge(
        local_peak, local_totals, local_values, n_seq, seq_index
    )
    order = (per, heads_kv, step_count, QUERY_PER_KEY)
    running_peak = running_peak.reshape(order)
    running_totals = running_totals.reshape(order)
    weighted_values = weighted_values.reshape(order + (HEAD_SIZE,))
    own_queries = lax.dynamic_slice_in_dim(query_rows, mine, per, 0)
    fresh = fresh_part(
        own_queries,
        lax.dynamic_slice_in_dim(current_key, mine, per, 0),
        lax.dynamic_slice_in_dim(current_value, mine, per, 0),
    )
    running_peak, running_totals, weighted_values = merge_parts(
        (running_peak, running_totals, weighted_values), fresh
    )
    heads_out = (
        (weighted_values / running_totals[..., None])
        .transpose(0, 2, 1, 3, 4)
        .reshape(per, step_count, -1)
        .astype(jnp.bfloat16)
    )
    piece_rows = lax.all_gather(heads_out, "row", axis=0, tiled=False)
    n_row = piece_rows.shape[0]
    product = jnp.dot(
        piece_rows.reshape(n_row * per * step_count, -1), wo, preferred_element_type=jnp.float32
    )
    partials = product.reshape(n_row, per, step_count, -1)
    own_out = pair_scatter(partials.astype(jnp.bfloat16), "col").reshape(per, step_count, -1)
    attended = doubling_gather(own_out, "seq")
    return (
        attended,
        current_key.reshape(req_count, step_count, k_width),
        current_value.reshape(req_count, step_count, k_width),
    )


def solution(mesh):
    in_specs = (
        P("col", None, "row"),
        P("row"),
        P("row", "col"),
        P("row", "col"),
        P("row", "col"),
        P("col", "row"),
        P("row"),
        P(("row", "seq")),
        P(("row", "seq")),
        P(("row", "seq"), None, "col"),
        P(("row", "seq"), None, "col"),
    )
    out_specs = (P("col", None, "row"), P("row", None, "col"), P("row", None, "col"))
    return jax.shard_map(
        on_device, mesh=mesh, in_specs=in_specs, out_specs=out_specs, check_vma=False
    )
```

```python
import math
from functools import partial

import jax
import jax.numpy as jnp
from jax import lax
from jax.experimental import pallas as pl
from jax.experimental.pallas import tpu as pltpu
from jax.sharding import PartitionSpec as P

D = 5120
HEAD_SIZE = 128
WINDOW = 4096
SINK = 4
QUERY_PER_KEY = 4


EPSILON = 1e-05
NEGATIVE_FILL = -1e30
ROPE_BASE = 100000000.0


def rotary_apply(values, token_positions):
    half_dim = values.shape[-1] // 2
    frequency = ROPE_BASE ** (-(jnp.arange(half_dim, dtype=jnp.float32) * 2.0 / values.shape[-1]))
    angles = (token_positions.astype(jnp.float32)[..., None] * frequency)[..., None, :]
    cosine = jnp.cos(angles)
    sine_part = jnp.sin(angles)
    lower = values[..., :half_dim]
    upper = values[..., half_dim:]
    return jnp.concatenate(
        [lower * cosine - upper * sine_part, upper * cosine + lower * sine_part], -1
    )


def slot_parts(query_rows, lengths, slot_request, slot_block_number, key_rows, value_rows):
    req_count = query_rows.shape[0]
    step_count = query_rows.shape[1]
    block_len = key_rows.shape[1]
    picked = jnp.minimum(slot_request, req_count - 1)
    in_use = slot_request < req_count
    slot_queries = query_rows[picked]
    scores = jnp.einsum(
        "nsagh,nbah->nasgb", slot_queries, key_rows, preferred_element_type=jnp.float32
    ) * (1.0 / math.sqrt(HEAD_SIZE))
    key_pos = (
        slot_block_number[:, None] * block_len + jnp.arange(block_len, dtype=jnp.int32)[None, :]
    )
    own_len = lengths[picked]
    query_pos = own_len[:, None] + jnp.arange(step_count, dtype=jnp.int32)[None, :]
    visible = (
        in_use[:, None, None]
        & (key_pos[:, None, :] < own_len[:, None, None])
        & ((key_pos[:, None, :] < SINK) | (key_pos[:, None, :] > query_pos[:, :, None] - WINDOW))
    )
    visible = visible[:, None, :, None, :]
    slot_peak = jnp.max(jnp.where(visible, scores, NEGATIVE_FILL), -1)
    weights = jnp.where(visible, jnp.exp(scores - slot_peak[..., None]), 0.0)
    slot_total = jnp.sum(weights, -1)
    slot_acc = jnp.einsum(
        "nasgb,nbah->nasgh",
        weights.astype(jnp.bfloat16),
        value_rows,
        preferred_element_type=jnp.float32,
    )
    member = slot_request[None, :] == jnp.arange(req_count, dtype=jnp.int32)[:, None]
    local_peak = jnp.max(
        jnp.where(member[:, :, None, None, None], slot_peak[None], NEGATIVE_FILL), 1
    )
    return (local_peak, (slot_peak, slot_total, slot_acc, member, picked))


def pool_sums(held, running_peak):
    slot_peak, slot_total, slot_acc, member, picked = held
    factor = jnp.exp(slot_peak - running_peak[picked])
    as_member = member.astype(jnp.float32)
    running_totals = jnp.einsum(
        "rn,nasg->rasg", as_member, slot_total * factor, precision=lax.Precision.HIGHEST
    )
    weighted_values = jnp.einsum(
        "rn,nasgh->rasgh", as_member, slot_acc * factor[..., None], precision=lax.Precision.HIGHEST
    )
    return (running_totals, weighted_values)


def fresh_part(query_rows, key_all, value_all):
    step_count = query_rows.shape[1]
    used = key_all.shape[1]
    scores = jnp.einsum(
        "rsagh,ruah->rasgu", query_rows, key_all, preferred_element_type=jnp.float32
    ) * (1.0 / math.sqrt(HEAD_SIZE))
    causal = (
        jnp.arange(used, dtype=jnp.int32)[None, :]
        <= jnp.arange(step_count, dtype=jnp.int32)[:, None]
    )
    causal = causal[None, None, :, None, :]
    running_peak = jnp.max(jnp.where(causal, scores, NEGATIVE_FILL), -1)
    weights = jnp.where(causal, jnp.exp(scores - running_peak[..., None]), 0.0)
    running_totals = jnp.sum(weights, -1)
    weighted_values = jnp.einsum(
        "rasgu,ruah->rasgh",
        weights.astype(jnp.bfloat16),
        value_all,
        preferred_element_type=jnp.float32,
    )
    return (running_peak, running_totals, weighted_values)


def merge_parts(earlier, later):
    running_peak = jnp.maximum(earlier[0], later[0])
    first_factor = jnp.exp(earlier[0] - running_peak)
    second_factor = jnp.exp(later[0] - running_peak)
    running_totals = earlier[1] * first_factor + later[1] * second_factor
    weighted_values = earlier[2] * first_factor[..., None] + later[2] * second_factor[..., None]
    return (running_peak, running_totals, weighted_values)


def slot_kernel(
    req_ref, len_ref, blk_ref, q_ref, k_ref, v_ref, peak_ref, tot_ref, acc_ref, *, ns, heads, qpk
):
    @pl.when(pl.program_id(0) == 0)
    def _():
        peak_ref[...] = jnp.full(peak_ref.shape, NEGATIVE_FILL, jnp.float32)
        tot_ref[...] = jnp.zeros(tot_ref.shape, jnp.float32)
        acc_ref[...] = jnp.zeros(acc_ref.shape, jnp.float32)

    base = pl.program_id(0) * ns
    req_count = q_ref.shape[0]
    rows = q_ref.shape[1]
    group = rows // heads
    width = k_ref.shape[1]
    head = k_ref.shape[2] // heads
    row = lax.broadcasted_iota(jnp.int32, (rows, width), 0)
    col = lax.broadcasted_iota(jnp.int32, (rows, width), 1)
    step_of = (row % group) // qpk

    results = []
    for i in range(ns):
        req = req_ref[base + i]
        owner = jnp.minimum(req, req_count - 1)
        length = len_ref[owner]
        key_pos = blk_ref[base + i] * width + col
        query_pos = length + step_of
        visible = (
            (req < req_count)
            & (key_pos < length)
            & ((key_pos < SINK) | (key_pos > query_pos - WINDOW))
        )
        q = q_ref[owner]
        k = k_ref[i]
        v = v_ref[i]
        scores = jnp.concatenate(
            [
                lax.dot_general(
                    q[a * group : (a + 1) * group],
                    k[:, a * head : (a + 1) * head],
                    (((1,), (1,)), ((), ())),
                    preferred_element_type=jnp.float32,
                )
                for a in range(heads)
            ],
            0,
        ) * (1.0 / math.sqrt(HEAD_SIZE))
        peak = jnp.max(jnp.where(visible, scores, NEGATIVE_FILL), axis=1, keepdims=True)
        weights = jnp.where(visible, jnp.exp(scores - peak), 0.0)
        total = jnp.sum(weights, axis=1, keepdims=True)
        rounded = weights.astype(jnp.bfloat16)
        acc = jnp.concatenate(
            [
                jnp.dot(
                    rounded[a * group : (a + 1) * group],
                    v[:, a * head : (a + 1) * head],
                    preferred_element_type=jnp.float32,
                )
                for a in range(heads)
            ],
            0,
        )
        results.append((owner, peak, total, acc))
    for owner, peak, total, acc in results:
        old = peak_ref[owner]
        top = jnp.maximum(old, peak)
        old_factor = jnp.exp(old - top)
        new_factor = jnp.exp(peak - top)
        tot_ref[owner] = tot_ref[owner] * old_factor + total * new_factor
        acc_ref[owner] = acc_ref[owner] * old_factor + acc * new_factor
        peak_ref[owner] = top

def slot_attention(queries, lengths, slot_request, block_numbers, keys, values, heads, qpk):
    req_count, rows, head = queries.shape
    n_slots = keys.shape[0]
    width = keys.shape[1]
    ns = max(d for d in range(1, 11) if n_slots % d == 0)
    fixed = lambda n, sr, lr, br: (0, 0, 0)
    grid_spec = pltpu.PrefetchScalarGridSpec(
        num_scalar_prefetch=3,
        grid=(n_slots // ns,),
        in_specs=[
            pl.BlockSpec((req_count, rows, head), fixed),
            pl.BlockSpec((ns, width, keys.shape[2]), lambda n, sr, lr, br: (n, 0, 0)),
            pl.BlockSpec((ns, width, values.shape[2]), lambda n, sr, lr, br: (n, 0, 0)),
        ],
        out_specs=[
            pl.BlockSpec((req_count, rows, 1), fixed),
            pl.BlockSpec((req_count, rows, 1), fixed),
            pl.BlockSpec((req_count, rows, head), fixed),
        ],
    )
    return pl.pallas_call(
        partial(slot_kernel, ns=ns, heads=heads, qpk=qpk),
        grid_spec=grid_spec,
        out_shape=[
            jax.ShapeDtypeStruct((req_count, rows, 1), jnp.float32),
            jax.ShapeDtypeStruct((req_count, rows, 1), jnp.float32),
            jax.ShapeDtypeStruct((req_count, rows, head), jnp.float32),
        ],
    )(slot_request, lengths, block_numbers, queries, keys, values)

def pair_gather(part, axis_name):
    n = lax.axis_size(axis_name)
    assert n == 2
    side = lax.axis_index(axis_name)
    other = lax.ppermute(part, axis_name, [(0, 1), (1, 0)])
    return jnp.where(
        side == 0,
        jnp.concatenate([part, other], 0),
        jnp.concatenate([other, part], 0),
    )


def pair_scatter(parts, axis_name, rounded=True):
    n = lax.axis_size(axis_name)
    assert n == 2 and parts.shape[0] == 2
    side = lax.axis_index(axis_name)
    keep = lax.dynamic_index_in_dim(parts, side, 0, keepdims=True)
    send = lax.dynamic_index_in_dim(parts, 1 - side, 0, keepdims=True)
    got = lax.ppermute(send, axis_name, [(0, 1), (1, 0)])
    total = (keep.astype(jnp.float32) + got.astype(jnp.float32))[0]
    return total.astype(parts.dtype) if rounded else total


def doubling_gather(part, axis_name):
    n = lax.axis_size(axis_name)
    stages = n.bit_length() - 1
    assert 1 << stages == n
    index = lax.axis_index(axis_name)
    block = part[None]
    order = [stages - 1] + list(range(stages - 1))
    for bit in order:
        pairs = [(s, s ^ (1 << bit)) for s in range(n)]
        got = lax.ppermute(block, axis_name, pairs)
        low = ((index >> bit) & 1) == 0
        block = jnp.where(
            low, jnp.stack([block, got], 0), jnp.stack([got, block], 0)
        )
    block = block.reshape((2,) * stages + part.shape)
    axes = list(reversed(order))
    block = block.transpose(
        tuple(axes.index(stages - 1 - p) for p in range(stages))
        + tuple(range(stages, stages + part.ndim))
    )
    return block.reshape((n * part.shape[0],) + part.shape[1:])


def seq_merge(peak, total, acc, n_seq, seq_index):
    stages = n_seq.bit_length() - 1
    assert 1 << stages == n_seq
    req_count = peak.shape[0]
    per = req_count // n_seq
    rest = peak.shape[1:]
    split = [2] * stages + [per]
    stats = jnp.stack([peak, total], 0).reshape([2] + split + list(rest))
    values = acc.reshape(split + list(acc.shape[1:]))
    for bit in range(stages):
        axis = stages - 1 - bit
        mine = (seq_index >> bit) & 1
        pairs = [(s, s ^ (1 << bit)) for s in range(n_seq)]
        keep_stats = lax.dynamic_index_in_dim(stats, mine, axis + 1, keepdims=True)
        send_stats = lax.dynamic_index_in_dim(stats, 1 - mine, axis + 1, keepdims=True)
        keep_values = lax.dynamic_index_in_dim(values, mine, axis, keepdims=True)
        send_values = lax.dynamic_index_in_dim(values, 1 - mine, axis, keepdims=True)
        got_stats = lax.ppermute(send_stats, "seq", pairs)
        got_values = lax.ppermute(send_values.astype(jnp.bfloat16), "seq", pairs).astype(
            jnp.float32
        )
        top = jnp.maximum(keep_stats[0], got_stats[0])
        keep_factor = jnp.exp(keep_stats[0] - top)
        got_factor = jnp.exp(got_stats[0] - top)
        stats = jnp.stack(
            [top, keep_stats[1] * keep_factor + got_stats[1] * got_factor], 0
        )
        values = keep_values * keep_factor[..., None] + got_values * got_factor[..., None]
    stats = stats.reshape((2, per) + tuple(rest))
    values = values.reshape((per,) + tuple(acc.shape[1:]))
    return (stats[0], stats[1], values)


def on_device(
    states,
    norm_gain,
    wq,
    wk,
    wv,
    wo,
    lengths,
    slot_request,
    slot_block_number,
    paged_key_cache,
    paged_value_cache,
):
    q_width = wq.shape[1]
    k_width = wk.shape[1]
    heads_kv = k_width // HEAD_SIZE
    req_count = lengths.shape[0]
    block_len = paged_key_cache.shape[1]
    key_rows = paged_key_cache.reshape(paged_key_cache.shape[0], block_len, heads_kv, HEAD_SIZE)
    value_rows = paged_value_cache.reshape(
        paged_value_cache.shape[0], block_len, heads_kv, HEAD_SIZE
    )
    step_count = states.shape[1]
    token_count = states.shape[0] * step_count
    own_states = states.reshape(token_count, -1)
    side = lax.axis_index("col")
    swap = [(0, 1), (1, 0)]
    other_states = lax.ppermute(own_states, "col", swap)
    as_float = own_states.astype(jnp.float32)
    squares = lax.psum(jnp.sum(as_float * as_float, -1), "row")
    other_squares = lax.ppermute(squares, "col", swap)

    def rms_norm(rows, sums):
        scale = lax.rsqrt(sums / D + EPSILON)[:, None]
        return (rows.astype(jnp.float32) * scale * norm_gain).astype(jnp.bfloat16)

    first = side == 0
    gathered = jnp.concatenate(
        [
            rms_norm(
                jnp.where(first, own_states, other_states), jnp.where(first, squares, other_squares)
            ),
            rms_norm(
                jnp.where(first, other_states, own_states), jnp.where(first, other_squares, squares)
            ),
        ],
        0,
    )
    parts_out = [
        jnp.dot(gathered, matrix, preferred_element_type=jnp.float32) for matrix in (wq, wk, wv)
    ]
    head_count = (q_width + 2 * k_width) // HEAD_SIZE
    output_projected = pair_scatter(
        jnp.concatenate(parts_out, axis=-1)
        .astype(jnp.bfloat16)
        .reshape(lax.axis_size("row"), token_count, -1),
        "row",
        rounded=False,
    ).reshape(token_count, head_count, HEAD_SIZE)
    q_heads = q_width // HEAD_SIZE
    token_positions = (
        lengths[:, None] + jnp.arange(step_count, dtype=jnp.int32)[None, :]
    ).reshape(token_count)
    query_rows = rotary_apply(output_projected[:, :q_heads], token_positions).astype(jnp.bfloat16)
    query_rows = query_rows.reshape(req_count, step_count, heads_kv, QUERY_PER_KEY, HEAD_SIZE)
    current_key = (
        rotary_apply(output_projected[:, q_heads : q_heads + heads_kv], token_positions)
        .astype(jnp.bfloat16)
        .reshape(req_count, step_count, heads_kv, HEAD_SIZE)
    )
    current_value = (
        output_projected[:, q_heads + heads_kv :]
        .astype(jnp.bfloat16)
        .reshape(req_count, step_count, heads_kv, HEAD_SIZE)
    )
    local_peak, local_totals, local_values = slot_attention(
        query_rows.transpose(0, 2, 1, 3, 4).reshape(req_count, -1, HEAD_SIZE),
        lengths,
        slot_request,
        slot_block_number,
        paged_key_cache,
        paged_value_cache,
        heads_kv,
        QUERY_PER_KEY,
    )
    local_peak = local_peak[..., 0]
    local_totals = local_totals[..., 0]
    n_seq = lax.axis_size("seq")
    per = req_count // n_seq
    seq_index = lax.axis_index("seq")
    mine = seq_index * per
    running_peak, running_totals, weighted_values = seq_merge(
        local_peak, local_totals, local_values, n_seq, seq_index
    )
    order = (per, heads_kv, step_count, QUERY_PER_KEY)
    running_peak = running_peak.reshape(order)
    running_totals = running_totals.reshape(order)
    weighted_values = weighted_values.reshape(order + (HEAD_SIZE,))
    own_queries = lax.dynamic_slice_in_dim(query_rows, mine, per, 0)
    fresh = fresh_part(
        own_queries,
        lax.dynamic_slice_in_dim(current_key, mine, per, 0),
        lax.dynamic_slice_in_dim(current_value, mine, per, 0),
    )
    running_peak, running_totals, weighted_values = merge_parts(
        (running_peak, running_totals, weighted_values), fresh
    )
    heads_out = (
        (weighted_values / running_totals[..., None])
        .transpose(0, 2, 1, 3, 4)
        .reshape(per, step_count, -1)
        .astype(jnp.bfloat16)
    )
    piece_rows = lax.all_gather(heads_out, "row", axis=0, tiled=False)
    n_row = piece_rows.shape[0]
    product = jnp.dot(
        piece_rows.reshape(n_row * per * step_count, -1), wo, preferred_element_type=jnp.float32
    )
    partials = product.reshape(n_row, per, step_count, -1)
    own_out = pair_scatter(partials.astype(jnp.bfloat16), "col").reshape(per, step_count, -1)
    attended = doubling_gather(own_out, "seq")
    return (
        attended,
        current_key.reshape(req_count, step_count, k_width),
        current_value.reshape(req_count, step_count, k_width),
    )


def solution(mesh):
    in_specs = (
        P("col", None, "row"),
        P("row"),
        P("row", "col"),
        P("row", "col"),
        P("row", "col"),
        P("col", "row"),
        P("row"),
        P(("row", "seq")),
        P(("row", "seq")),
        P(("row", "seq"), None, "col"),
        P(("row", "seq"), None, "col"),
    )
    out_specs = (P("col", None, "row"), P("row", None, "col"), P("row", None, "col"))
    return jax.shard_map(
        on_device, mesh=mesh, in_specs=in_specs, out_specs=out_specs, check_vma=False
    )
```

```python
import math
from functools import partial

import jax
import jax.numpy as jnp
from jax import lax
from jax.experimental import pallas as pl
from jax.experimental.pallas import tpu as pltpu
from jax.sharding import PartitionSpec as P

D = 5120
HEAD_SIZE = 128
WINDOW = 4096
SINK = 4
QUERY_PER_KEY = 4


EPSILON = 1e-05
NEGATIVE_FILL = -1e30
ROPE_BASE = 100000000.0


def rotary_apply(values, token_positions):
    half_dim = values.shape[-1] // 2
    frequency = ROPE_BASE ** (-(jnp.arange(half_dim, dtype=jnp.float32) * 2.0 / values.shape[-1]))
    angles = (token_positions.astype(jnp.float32)[..., None] * frequency)[..., None, :]
    cosine = jnp.cos(angles)
    sine_part = jnp.sin(angles)
    lower = values[..., :half_dim]
    upper = values[..., half_dim:]
    return jnp.concatenate(
        [lower * cosine - upper * sine_part, upper * cosine + lower * sine_part], -1
    )


def slot_parts(query_rows, lengths, slot_request, slot_block_number, key_rows, value_rows):
    req_count = query_rows.shape[0]
    step_count = query_rows.shape[1]
    block_len = key_rows.shape[1]
    picked = jnp.minimum(slot_request, req_count - 1)
    in_use = slot_request < req_count
    slot_queries = query_rows[picked]
    scores = jnp.einsum(
        "nsagh,nbah->nasgb", slot_queries, key_rows, preferred_element_type=jnp.float32
    ) * (1.0 / math.sqrt(HEAD_SIZE))
    key_pos = (
        slot_block_number[:, None] * block_len + jnp.arange(block_len, dtype=jnp.int32)[None, :]
    )
    own_len = lengths[picked]
    query_pos = own_len[:, None] + jnp.arange(step_count, dtype=jnp.int32)[None, :]
    visible = (
        in_use[:, None, None]
        & (key_pos[:, None, :] < own_len[:, None, None])
        & ((key_pos[:, None, :] < SINK) | (key_pos[:, None, :] > query_pos[:, :, None] - WINDOW))
    )
    visible = visible[:, None, :, None, :]
    slot_peak = jnp.max(jnp.where(visible, scores, NEGATIVE_FILL), -1)
    weights = jnp.where(visible, jnp.exp(scores - slot_peak[..., None]), 0.0)
    slot_total = jnp.sum(weights, -1)
    slot_acc = jnp.einsum(
        "nasgb,nbah->nasgh",
        weights.astype(jnp.bfloat16),
        value_rows,
        preferred_element_type=jnp.float32,
    )
    member = slot_request[None, :] == jnp.arange(req_count, dtype=jnp.int32)[:, None]
    local_peak = jnp.max(
        jnp.where(member[:, :, None, None, None], slot_peak[None], NEGATIVE_FILL), 1
    )
    return (local_peak, (slot_peak, slot_total, slot_acc, member, picked))


def pool_sums(held, running_peak):
    slot_peak, slot_total, slot_acc, member, picked = held
    factor = jnp.exp(slot_peak - running_peak[picked])
    as_member = member.astype(jnp.float32)
    running_totals = jnp.einsum(
        "rn,nasg->rasg", as_member, slot_total * factor, precision=lax.Precision.HIGHEST
    )
    weighted_values = jnp.einsum(
        "rn,nasgh->rasgh", as_member, slot_acc * factor[..., None], precision=lax.Precision.HIGHEST
    )
    return (running_totals, weighted_values)


def fresh_part(query_rows, key_all, value_all):
    step_count = query_rows.shape[1]
    used = key_all.shape[1]
    scores = jnp.einsum(
        "rsagh,ruah->rasgu", query_rows, key_all, preferred_element_type=jnp.float32
    ) * (1.0 / math.sqrt(HEAD_SIZE))
    causal = (
        jnp.arange(used, dtype=jnp.int32)[None, :]
        <= jnp.arange(step_count, dtype=jnp.int32)[:, None]
    )
    causal = causal[None, None, :, None, :]
    running_peak = jnp.max(jnp.where(causal, scores, NEGATIVE_FILL), -1)
    weights = jnp.where(causal, jnp.exp(scores - running_peak[..., None]), 0.0)
    running_totals = jnp.sum(weights, -1)
    weighted_values = jnp.einsum(
        "rasgu,ruah->rasgh",
        weights.astype(jnp.bfloat16),
        value_all,
        preferred_element_type=jnp.float32,
    )
    return (running_peak, running_totals, weighted_values)


def merge_parts(earlier, later):
    running_peak = jnp.maximum(earlier[0], later[0])
    first_factor = jnp.exp(earlier[0] - running_peak)
    second_factor = jnp.exp(later[0] - running_peak)
    running_totals = earlier[1] * first_factor + later[1] * second_factor
    weighted_values = earlier[2] * first_factor[..., None] + later[2] * second_factor[..., None]
    return (running_peak, running_totals, weighted_values)


def slot_kernel(
    req_ref, len_ref, blk_ref, q_ref, k_ref, v_ref, peak_ref, tot_ref, acc_ref, *, ns, heads, qpk
):
    @pl.when(pl.program_id(0) == 0)
    def _():
        peak_ref[...] = jnp.full(peak_ref.shape, NEGATIVE_FILL, jnp.float32)
        tot_ref[...] = jnp.zeros(tot_ref.shape, jnp.float32)
        acc_ref[...] = jnp.zeros(acc_ref.shape, jnp.float32)

    base = pl.program_id(0) * ns
    req_count = q_ref.shape[0]
    rows = q_ref.shape[1]
    group = rows // heads
    width = k_ref.shape[1]
    head = k_ref.shape[2] // heads
    row = lax.broadcasted_iota(jnp.int32, (rows, width), 0)
    col = lax.broadcasted_iota(jnp.int32, (rows, width), 1)
    step_of = (row % group) // qpk

    results = []
    for i in range(ns):
        req = req_ref[base + i]
        owner = jnp.minimum(req, req_count - 1)
        length = len_ref[owner]
        key_pos = blk_ref[base + i] * width + col
        query_pos = length + step_of
        visible = (
            (req < req_count)
            & (key_pos < length)
            & ((key_pos < SINK) | (key_pos > query_pos - WINDOW))
        )
        q = q_ref[owner]
        k = k_ref[i]
        v = v_ref[i]
        scores = jnp.concatenate(
            [
                lax.dot_general(
                    q[a * group : (a + 1) * group],
                    k[:, a * head : (a + 1) * head],
                    (((1,), (1,)), ((), ())),
                    preferred_element_type=jnp.float32,
                )
                for a in range(heads)
            ],
            0,
        ) * (1.0 / math.sqrt(HEAD_SIZE))
        peak = jnp.max(jnp.where(visible, scores, NEGATIVE_FILL), axis=1, keepdims=True)
        weights = jnp.where(visible, jnp.exp(scores - peak), 0.0)
        total = jnp.sum(weights, axis=1, keepdims=True)
        rounded = weights.astype(jnp.bfloat16)
        acc = jnp.concatenate(
            [
                jnp.dot(
                    rounded[a * group : (a + 1) * group],
                    v[:, a * head : (a + 1) * head],
                    preferred_element_type=jnp.float32,
                )
                for a in range(heads)
            ],
            0,
        )
        results.append((owner, peak, total, acc))
    for owner, peak, total, acc in results:
        old = peak_ref[owner]
        top = jnp.maximum(old, peak)
        old_factor = jnp.exp(old - top)
        new_factor = jnp.exp(peak - top)
        tot_ref[owner] = tot_ref[owner] * old_factor + total * new_factor
        acc_ref[owner] = acc_ref[owner] * old_factor + acc * new_factor
        peak_ref[owner] = top

def slot_attention(queries, lengths, slot_request, block_numbers, keys, values, heads, qpk):
    req_count, rows, head = queries.shape
    n_slots = keys.shape[0]
    width = keys.shape[1]
    ns = max(d for d in range(1, 11) if n_slots % d == 0)
    fixed = lambda n, sr, lr, br: (0, 0, 0)
    grid_spec = pltpu.PrefetchScalarGridSpec(
        num_scalar_prefetch=3,
        grid=(n_slots // ns,),
        in_specs=[
            pl.BlockSpec((req_count, rows, head), fixed),
            pl.BlockSpec((ns, width, keys.shape[2]), lambda n, sr, lr, br: (n, 0, 0)),
            pl.BlockSpec((ns, width, values.shape[2]), lambda n, sr, lr, br: (n, 0, 0)),
        ],
        out_specs=[
            pl.BlockSpec((req_count, rows, 1), fixed),
            pl.BlockSpec((req_count, rows, 1), fixed),
            pl.BlockSpec((req_count, rows, head), fixed),
        ],
    )
    return pl.pallas_call(
        partial(slot_kernel, ns=ns, heads=heads, qpk=qpk),
        grid_spec=grid_spec,
        out_shape=[
            jax.ShapeDtypeStruct((req_count, rows, 1), jnp.float32),
            jax.ShapeDtypeStruct((req_count, rows, 1), jnp.float32),
            jax.ShapeDtypeStruct((req_count, rows, head), jnp.float32),
        ],
    )(slot_request, lengths, block_numbers, queries, keys, values)

def pair_gather(part, axis_name):
    n = lax.axis_size(axis_name)
    assert n == 2
    side = lax.axis_index(axis_name)
    other = lax.ppermute(part, axis_name, [(0, 1), (1, 0)])
    return jnp.where(
        side == 0,
        jnp.concatenate([part, other], 0),
        jnp.concatenate([other, part], 0),
    )


def pair_scatter(parts, axis_name, rounded=True):
    n = lax.axis_size(axis_name)
    assert n == 2 and parts.shape[0] == 2
    side = lax.axis_index(axis_name)
    keep = lax.dynamic_index_in_dim(parts, side, 0, keepdims=True)
    send = lax.dynamic_index_in_dim(parts, 1 - side, 0, keepdims=True)
    got = lax.ppermute(send, axis_name, [(0, 1), (1, 0)])
    total = (keep.astype(jnp.float32) + got.astype(jnp.float32))[0]
    return total.astype(parts.dtype) if rounded else total


def doubling_gather(part, axis_name, swap_last=False):
    n = lax.axis_size(axis_name)
    stages = n.bit_length() - 1
    assert 1 << stages == n
    index = lax.axis_index(axis_name)
    block = part[None]
    order = list(reversed(range(stages)))
    if swap_last and stages >= 2:
        order[-2], order[-1] = order[-1], order[-2]
    for bit in order:
        pairs = [(s, s ^ (1 << bit)) for s in range(n)]
        got = lax.ppermute(block, axis_name, pairs)
        low = ((index >> bit) & 1) == 0
        block = jnp.where(
            low, jnp.stack([block, got], 0), jnp.stack([got, block], 0)
        )
    block = block.reshape((2,) * stages + part.shape)
    axes = list(reversed(order))
    block = block.transpose(
        tuple(axes.index(stages - 1 - p) for p in range(stages))
        + tuple(range(stages, stages + part.ndim))
    )
    return block.reshape((n * part.shape[0],) + part.shape[1:])


def seq_merge(peak, total, acc, n_seq, seq_index):
    stages = n_seq.bit_length() - 1
    assert 1 << stages == n_seq
    req_count = peak.shape[0]
    per = req_count // n_seq
    rest = peak.shape[1:]
    split = [2] * stages + [per]
    stats = jnp.stack([peak, total], 0).reshape([2] + split + list(rest))
    values = acc.reshape(split + list(acc.shape[1:]))
    for bit in range(stages):
        axis = stages - 1 - bit
        mine = (seq_index >> bit) & 1
        pairs = [(s, s ^ (1 << bit)) for s in range(n_seq)]
        keep_stats = lax.dynamic_index_in_dim(stats, mine, axis + 1, keepdims=True)
        send_stats = lax.dynamic_index_in_dim(stats, 1 - mine, axis + 1, keepdims=True)
        keep_values = lax.dynamic_index_in_dim(values, mine, axis, keepdims=True)
        send_values = lax.dynamic_index_in_dim(values, 1 - mine, axis, keepdims=True)
        got_stats = lax.ppermute(send_stats, "seq", pairs)
        got_values = lax.ppermute(send_values.astype(jnp.bfloat16), "seq", pairs).astype(
            jnp.float32
        )
        top = jnp.maximum(keep_stats[0], got_stats[0])
        keep_factor = jnp.exp(keep_stats[0] - top)
        got_factor = jnp.exp(got_stats[0] - top)
        stats = jnp.stack(
            [top, keep_stats[1] * keep_factor + got_stats[1] * got_factor], 0
        )
        values = keep_values * keep_factor[..., None] + got_values * got_factor[..., None]
    stats = stats.reshape((2, per) + tuple(rest))
    values = values.reshape((per,) + tuple(acc.shape[1:]))
    return (stats[0], stats[1], values)


def on_device(
    states,
    norm_gain,
    wq,
    wk,
    wv,
    wo,
    lengths,
    slot_request,
    slot_block_number,
    paged_key_cache,
    paged_value_cache,
):
    q_width = wq.shape[1]
    k_width = wk.shape[1]
    heads_kv = k_width // HEAD_SIZE
    req_count = lengths.shape[0]
    block_len = paged_key_cache.shape[1]
    key_rows = paged_key_cache.reshape(paged_key_cache.shape[0], block_len, heads_kv, HEAD_SIZE)
    value_rows = paged_value_cache.reshape(
        paged_value_cache.shape[0], block_len, heads_kv, HEAD_SIZE
    )
    step_count = states.shape[1]
    token_count = states.shape[0] * step_count
    own_states = states.reshape(token_count, -1)
    side = lax.axis_index("col")
    swap = [(0, 1), (1, 0)]
    other_states = lax.ppermute(own_states, "col", swap)
    as_float = own_states.astype(jnp.float32)
    squares = lax.psum(jnp.sum(as_float * as_float, -1), "row")
    other_squares = lax.ppermute(squares, "col", swap)

    def rms_norm(rows, sums):
        scale = lax.rsqrt(sums / D + EPSILON)[:, None]
        return (rows.astype(jnp.float32) * scale * norm_gain).astype(jnp.bfloat16)

    first = side == 0
    gathered = jnp.concatenate(
        [
            rms_norm(
                jnp.where(first, own_states, other_states), jnp.where(first, squares, other_squares)
            ),
            rms_norm(
                jnp.where(first, other_states, own_states), jnp.where(first, other_squares, squares)
            ),
        ],
        0,
    )
    parts_out = [
        jnp.dot(gathered, matrix, preferred_element_type=jnp.float32) for matrix in (wq, wk, wv)
    ]
    head_count = (q_width + 2 * k_width) // HEAD_SIZE
    output_projected = pair_scatter(
        jnp.concatenate(parts_out, axis=-1)
        .astype(jnp.bfloat16)
        .reshape(lax.axis_size("row"), token_count, -1),
        "row",
        rounded=False,
    ).reshape(token_count, head_count, HEAD_SIZE)
    q_heads = q_width // HEAD_SIZE
    token_positions = (
        lengths[:, None] + jnp.arange(step_count, dtype=jnp.int32)[None, :]
    ).reshape(token_count)
    query_rows = rotary_apply(output_projected[:, :q_heads], token_positions).astype(jnp.bfloat16)
    query_rows = query_rows.reshape(req_count, step_count, heads_kv, QUERY_PER_KEY, HEAD_SIZE)
    current_key = (
        rotary_apply(output_projected[:, q_heads : q_heads + heads_kv], token_positions)
        .astype(jnp.bfloat16)
        .reshape(req_count, step_count, heads_kv, HEAD_SIZE)
    )
    current_value = (
        output_projected[:, q_heads + heads_kv :]
        .astype(jnp.bfloat16)
        .reshape(req_count, step_count, heads_kv, HEAD_SIZE)
    )
    local_peak, local_totals, local_values = slot_attention(
        query_rows.transpose(0, 2, 1, 3, 4).reshape(req_count, -1, HEAD_SIZE),
        lengths,
        slot_request,
        slot_block_number,
        paged_key_cache,
        paged_value_cache,
        heads_kv,
        QUERY_PER_KEY,
    )
    local_peak = local_peak[..., 0]
    local_totals = local_totals[..., 0]
    n_seq = lax.axis_size("seq")
    per = req_count // n_seq
    seq_index = lax.axis_index("seq")
    mine = seq_index * per
    running_peak, running_totals, weighted_values = seq_merge(
        local_peak, local_totals, local_values, n_seq, seq_index
    )
    order = (per, heads_kv, step_count, QUERY_PER_KEY)
    running_peak = running_peak.reshape(order)
    running_totals = running_totals.reshape(order)
    weighted_values = weighted_values.reshape(order + (HEAD_SIZE,))
    own_queries = lax.dynamic_slice_in_dim(query_rows, mine, per, 0)
    fresh = fresh_part(
        own_queries,
        lax.dynamic_slice_in_dim(current_key, mine, per, 0),
        lax.dynamic_slice_in_dim(current_value, mine, per, 0),
    )
    running_peak, running_totals, weighted_values = merge_parts(
        (running_peak, running_totals, weighted_values), fresh
    )
    heads_out = (
        (weighted_values / running_totals[..., None])
        .transpose(0, 2, 1, 3, 4)
        .reshape(per, step_count, -1)
        .astype(jnp.bfloat16)
    )
    piece_rows = lax.all_gather(heads_out, "row", axis=0, tiled=False)
    n_row = piece_rows.shape[0]
    product = jnp.dot(
        piece_rows.reshape(n_row * per * step_count, -1), wo, preferred_element_type=jnp.float32
    )
    partials = product.reshape(n_row, per, step_count, -1)
    own_out = pair_scatter(partials.astype(jnp.bfloat16), "col").reshape(per, step_count, -1)
    split = own_out.shape[-1] // 2
    attended = jnp.concatenate(
        [
            doubling_gather(own_out[..., :split], "seq"),
            doubling_gather(own_out[..., split:], "seq", swap_last=True),
        ],
        -1,
    )
    return (
        attended,
        current_key.reshape(req_count, step_count, k_width),
        current_value.reshape(req_count, step_count, k_width),
    )


def solution(mesh):
    in_specs = (
        P("col", None, "row"),
        P("row"),
        P("row", "col"),
        P("row", "col"),
        P("row", "col"),
        P("col", "row"),
        P("row"),
        P(("row", "seq")),
        P(("row", "seq")),
        P(("row", "seq"), None, "col"),
        P(("row", "seq"), None, "col"),
    )
    out_specs = (P("col", None, "row"), P("row", None, "col"), P("row", None, "col"))
    return jax.shard_map(
        on_device, mesh=mesh, in_specs=in_specs, out_specs=out_specs, check_vma=False
    )
```

```python
import math
from functools import partial

import jax
import jax.numpy as jnp
from jax import lax
from jax.experimental import pallas as pl
from jax.experimental.pallas import tpu as pltpu
from jax.sharding import PartitionSpec as P

D = 5120
HEAD_SIZE = 128
WINDOW = 4096
SINK = 4
QUERY_PER_KEY = 4


EPSILON = 1e-05
NEGATIVE_FILL = -1e30
ROPE_BASE = 100000000.0


def rotary_apply(values, token_positions):
    half_dim = values.shape[-1] // 2
    frequency = ROPE_BASE ** (-(jnp.arange(half_dim, dtype=jnp.float32) * 2.0 / values.shape[-1]))
    angles = (token_positions.astype(jnp.float32)[..., None] * frequency)[..., None, :]
    cosine = jnp.cos(angles)
    sine_part = jnp.sin(angles)
    lower = values[..., :half_dim]
    upper = values[..., half_dim:]
    return jnp.concatenate(
        [lower * cosine - upper * sine_part, upper * cosine + lower * sine_part], -1
    )


def slot_parts(query_rows, lengths, slot_request, slot_block_number, key_rows, value_rows):
    req_count = query_rows.shape[0]
    step_count = query_rows.shape[1]
    block_len = key_rows.shape[1]
    picked = jnp.minimum(slot_request, req_count - 1)
    in_use = slot_request < req_count
    slot_queries = query_rows[picked]
    scores = jnp.einsum(
        "nsagh,nbah->nasgb", slot_queries, key_rows, preferred_element_type=jnp.float32
    ) * (1.0 / math.sqrt(HEAD_SIZE))
    key_pos = (
        slot_block_number[:, None] * block_len + jnp.arange(block_len, dtype=jnp.int32)[None, :]
    )
    own_len = lengths[picked]
    query_pos = own_len[:, None] + jnp.arange(step_count, dtype=jnp.int32)[None, :]
    visible = (
        in_use[:, None, None]
        & (key_pos[:, None, :] < own_len[:, None, None])
        & ((key_pos[:, None, :] < SINK) | (key_pos[:, None, :] > query_pos[:, :, None] - WINDOW))
    )
    visible = visible[:, None, :, None, :]
    slot_peak = jnp.max(jnp.where(visible, scores, NEGATIVE_FILL), -1)
    weights = jnp.where(visible, jnp.exp(scores - slot_peak[..., None]), 0.0)
    slot_total = jnp.sum(weights, -1)
    slot_acc = jnp.einsum(
        "nasgb,nbah->nasgh",
        weights.astype(jnp.bfloat16),
        value_rows,
        preferred_element_type=jnp.float32,
    )
    member = slot_request[None, :] == jnp.arange(req_count, dtype=jnp.int32)[:, None]
    local_peak = jnp.max(
        jnp.where(member[:, :, None, None, None], slot_peak[None], NEGATIVE_FILL), 1
    )
    return (local_peak, (slot_peak, slot_total, slot_acc, member, picked))


def pool_sums(held, running_peak):
    slot_peak, slot_total, slot_acc, member, picked = held
    factor = jnp.exp(slot_peak - running_peak[picked])
    as_member = member.astype(jnp.float32)
    running_totals = jnp.einsum(
        "rn,nasg->rasg", as_member, slot_total * factor, precision=lax.Precision.HIGHEST
    )
    weighted_values = jnp.einsum(
        "rn,nasgh->rasgh", as_member, slot_acc * factor[..., None], precision=lax.Precision.HIGHEST
    )
    return (running_totals, weighted_values)


def fresh_part(query_rows, key_all, value_all):
    step_count = query_rows.shape[1]
    used = key_all.shape[1]
    scores = jnp.einsum(
        "rsagh,ruah->rasgu", query_rows, key_all, preferred_element_type=jnp.float32
    ) * (1.0 / math.sqrt(HEAD_SIZE))
    causal = (
        jnp.arange(used, dtype=jnp.int32)[None, :]
        <= jnp.arange(step_count, dtype=jnp.int32)[:, None]
    )
    causal = causal[None, None, :, None, :]
    running_peak = jnp.max(jnp.where(causal, scores, NEGATIVE_FILL), -1)
    weights = jnp.where(causal, jnp.exp(scores - running_peak[..., None]), 0.0)
    running_totals = jnp.sum(weights, -1)
    weighted_values = jnp.einsum(
        "rasgu,ruah->rasgh",
        weights.astype(jnp.bfloat16),
        value_all,
        preferred_element_type=jnp.float32,
    )
    return (running_peak, running_totals, weighted_values)


def merge_parts(earlier, later):
    running_peak = jnp.maximum(earlier[0], later[0])
    first_factor = jnp.exp(earlier[0] - running_peak)
    second_factor = jnp.exp(later[0] - running_peak)
    running_totals = earlier[1] * first_factor + later[1] * second_factor
    weighted_values = earlier[2] * first_factor[..., None] + later[2] * second_factor[..., None]
    return (running_peak, running_totals, weighted_values)


def slot_kernel(
    req_ref, len_ref, blk_ref, q_ref, k_ref, v_ref, peak_ref, tot_ref, acc_ref, *, ns, heads, qpk
):
    @pl.when(pl.program_id(0) == 0)
    def _():
        peak_ref[...] = jnp.full(peak_ref.shape, NEGATIVE_FILL, jnp.float32)
        tot_ref[...] = jnp.zeros(tot_ref.shape, jnp.float32)
        acc_ref[...] = jnp.zeros(acc_ref.shape, jnp.float32)

    base = pl.program_id(0) * ns
    req_count = q_ref.shape[0]
    rows = q_ref.shape[1]
    group = rows // heads
    width = k_ref.shape[1]
    head = k_ref.shape[2] // heads
    row = lax.broadcasted_iota(jnp.int32, (rows, width), 0)
    col = lax.broadcasted_iota(jnp.int32, (rows, width), 1)
    step_of = (row % group) // qpk

    results = []
    for i in range(ns):
        req = req_ref[base + i]
        owner = jnp.minimum(req, req_count - 1)
        length = len_ref[owner]
        key_pos = blk_ref[base + i] * width + col
        query_pos = length + step_of
        visible = (
            (req < req_count)
            & (key_pos < length)
            & ((key_pos < SINK) | (key_pos > query_pos - WINDOW))
        )
        q = q_ref[owner]
        k = k_ref[i]
        v = v_ref[i]
        scores = jnp.concatenate(
            [
                lax.dot_general(
                    q[a * group : (a + 1) * group],
                    k[:, a * head : (a + 1) * head],
                    (((1,), (1,)), ((), ())),
                    preferred_element_type=jnp.float32,
                )
                for a in range(heads)
            ],
            0,
        ) * (1.0 / math.sqrt(HEAD_SIZE))
        peak = jnp.max(jnp.where(visible, scores, NEGATIVE_FILL), axis=1, keepdims=True)
        weights = jnp.where(visible, jnp.exp(scores - peak), 0.0)
        total = jnp.sum(weights, axis=1, keepdims=True)
        rounded = weights.astype(jnp.bfloat16)
        acc = jnp.concatenate(
            [
                jnp.dot(
                    rounded[a * group : (a + 1) * group],
                    v[:, a * head : (a + 1) * head],
                    preferred_element_type=jnp.float32,
                )
                for a in range(heads)
            ],
            0,
        )
        results.append((owner, peak, total, acc))
    for owner, peak, total, acc in results:
        old = jnp.transpose(peak_ref[owner])
        top = jnp.maximum(old, peak)
        old_factor = jnp.exp(old - top)
        new_factor = jnp.exp(peak - top)
        tot_ref[owner] = jnp.transpose(
            jnp.transpose(tot_ref[owner]) * old_factor + total * new_factor
        )
        acc_ref[owner] = acc_ref[owner] * old_factor + acc * new_factor
        peak_ref[owner] = jnp.transpose(top)

def slot_attention(queries, lengths, slot_request, block_numbers, keys, values, heads, qpk):
    req_count, rows, head = queries.shape
    n_slots = keys.shape[0]
    width = keys.shape[1]
    ns = max(d for d in range(1, 11) if n_slots % d == 0)
    fixed = lambda n, sr, lr, br: (0, 0, 0)
    grid_spec = pltpu.PrefetchScalarGridSpec(
        num_scalar_prefetch=3,
        grid=(n_slots // ns,),
        in_specs=[
            pl.BlockSpec((req_count, rows, head), fixed),
            pl.BlockSpec((ns, width, keys.shape[2]), lambda n, sr, lr, br: (n, 0, 0)),
            pl.BlockSpec((ns, width, values.shape[2]), lambda n, sr, lr, br: (n, 0, 0)),
        ],
        out_specs=[
            pl.BlockSpec((req_count, 1, rows), fixed),
            pl.BlockSpec((req_count, 1, rows), fixed),
            pl.BlockSpec((req_count, rows, head), fixed),
        ],
    )
    return pl.pallas_call(
        partial(slot_kernel, ns=ns, heads=heads, qpk=qpk),
        grid_spec=grid_spec,
        out_shape=[
            jax.ShapeDtypeStruct((req_count, 1, rows), jnp.float32),
            jax.ShapeDtypeStruct((req_count, 1, rows), jnp.float32),
            jax.ShapeDtypeStruct((req_count, rows, head), jnp.float32),
        ],
    )(slot_request, lengths, block_numbers, queries, keys, values)

def pair_gather(part, axis_name):
    n = lax.axis_size(axis_name)
    assert n == 2
    side = lax.axis_index(axis_name)
    other = lax.ppermute(part, axis_name, [(0, 1), (1, 0)])
    return jnp.where(
        side == 0,
        jnp.concatenate([part, other], 0),
        jnp.concatenate([other, part], 0),
    )


def pair_scatter(parts, axis_name, rounded=True):
    n = lax.axis_size(axis_name)
    assert n == 2 and parts.shape[0] == 2
    side = lax.axis_index(axis_name)
    keep = lax.dynamic_index_in_dim(parts, side, 0, keepdims=True)
    send = lax.dynamic_index_in_dim(parts, 1 - side, 0, keepdims=True)
    got = lax.ppermute(send, axis_name, [(0, 1), (1, 0)])
    total = (keep.astype(jnp.float32) + got.astype(jnp.float32))[0]
    return total.astype(parts.dtype) if rounded else total


def doubling_gather(part, axis_name, swap_last=False):
    n = lax.axis_size(axis_name)
    stages = n.bit_length() - 1
    assert 1 << stages == n
    index = lax.axis_index(axis_name)
    block = part[None]
    order = list(reversed(range(stages)))
    if swap_last and stages >= 2:
        order[-2], order[-1] = order[-1], order[-2]
    for bit in order:
        pairs = [(s, s ^ (1 << bit)) for s in range(n)]
        got = lax.ppermute(block, axis_name, pairs)
        low = ((index >> bit) & 1) == 0
        block = jnp.where(
            low, jnp.stack([block, got], 0), jnp.stack([got, block], 0)
        )
    block = block.reshape((2,) * stages + part.shape)
    axes = list(reversed(order))
    block = block.transpose(
        tuple(axes.index(stages - 1 - p) for p in range(stages))
        + tuple(range(stages, stages + part.ndim))
    )
    return block.reshape((n * part.shape[0],) + part.shape[1:])


def seq_merge(peak, total, acc, n_seq, seq_index):
    stages = n_seq.bit_length() - 1
    assert 1 << stages == n_seq
    req_count = peak.shape[0]
    per = req_count // n_seq
    rest = peak.shape[1:]
    split = [2] * stages + [per]
    stats = jnp.stack([peak, total], 0).reshape([2] + split + list(rest))
    values = acc.reshape(split + list(acc.shape[1:]))
    for bit in range(stages):
        axis = stages - 1 - bit
        mine = (seq_index >> bit) & 1
        pairs = [(s, s ^ (1 << bit)) for s in range(n_seq)]
        keep_stats = lax.dynamic_index_in_dim(stats, mine, axis + 1, keepdims=True)
        send_stats = lax.dynamic_index_in_dim(stats, 1 - mine, axis + 1, keepdims=True)
        keep_values = lax.dynamic_index_in_dim(values, mine, axis, keepdims=True)
        send_values = lax.dynamic_index_in_dim(values, 1 - mine, axis, keepdims=True)
        got_stats = lax.ppermute(send_stats, "seq", pairs)
        got_values = lax.ppermute(send_values.astype(jnp.bfloat16), "seq", pairs).astype(
            jnp.float32
        )
        top = jnp.maximum(keep_stats[0], got_stats[0])
        keep_factor = jnp.exp(keep_stats[0] - top)
        got_factor = jnp.exp(got_stats[0] - top)
        stats = jnp.stack(
            [top, keep_stats[1] * keep_factor + got_stats[1] * got_factor], 0
        )
        values = keep_values * keep_factor[..., None] + got_values * got_factor[..., None]
    stats = stats.reshape((2, per) + tuple(rest))
    values = values.reshape((per,) + tuple(acc.shape[1:]))
    return (stats[0], stats[1], values)


def on_device(
    states,
    norm_gain,
    wq,
    wk,
    wv,
    wo,
    lengths,
    slot_request,
    slot_block_number,
    paged_key_cache,
    paged_value_cache,
):
    q_width = wq.shape[1]
    k_width = wk.shape[1]
    heads_kv = k_width // HEAD_SIZE
    req_count = lengths.shape[0]
    block_len = paged_key_cache.shape[1]
    key_rows = paged_key_cache.reshape(paged_key_cache.shape[0], block_len, heads_kv, HEAD_SIZE)
    value_rows = paged_value_cache.reshape(
        paged_value_cache.shape[0], block_len, heads_kv, HEAD_SIZE
    )
    step_count = states.shape[1]
    token_count = states.shape[0] * step_count
    own_states = states.reshape(token_count, -1)
    side = lax.axis_index("col")
    swap = [(0, 1), (1, 0)]
    other_states = lax.ppermute(own_states, "col", swap)
    as_float = own_states.astype(jnp.float32)
    squares = lax.psum(jnp.sum(as_float * as_float, -1), "row")
    other_squares = lax.ppermute(squares, "col", swap)

    def rms_norm(rows, sums):
        scale = lax.rsqrt(sums / D + EPSILON)[:, None]
        return (rows.astype(jnp.float32) * scale * norm_gain).astype(jnp.bfloat16)

    first = side == 0
    gathered = jnp.concatenate(
        [
            rms_norm(
                jnp.where(first, own_states, other_states), jnp.where(first, squares, other_squares)
            ),
            rms_norm(
                jnp.where(first, other_states, own_states), jnp.where(first, other_squares, squares)
            ),
        ],
        0,
    )
    parts_out = [
        jnp.dot(gathered, matrix, preferred_element_type=jnp.float32) for matrix in (wq, wk, wv)
    ]
    head_count = (q_width + 2 * k_width) // HEAD_SIZE
    output_projected = pair_scatter(
        jnp.concatenate(parts_out, axis=-1)
        .astype(jnp.bfloat16)
        .reshape(lax.axis_size("row"), token_count, -1),
        "row",
        rounded=False,
    ).reshape(token_count, head_count, HEAD_SIZE)
    q_heads = q_width // HEAD_SIZE
    token_positions = (
        lengths[:, None] + jnp.arange(step_count, dtype=jnp.int32)[None, :]
    ).reshape(token_count)
    query_rows = rotary_apply(output_projected[:, :q_heads], token_positions).astype(jnp.bfloat16)
    query_rows = query_rows.reshape(req_count, step_count, heads_kv, QUERY_PER_KEY, HEAD_SIZE)
    current_key = (
        rotary_apply(output_projected[:, q_heads : q_heads + heads_kv], token_positions)
        .astype(jnp.bfloat16)
        .reshape(req_count, step_count, heads_kv, HEAD_SIZE)
    )
    current_value = (
        output_projected[:, q_heads + heads_kv :]
        .astype(jnp.bfloat16)
        .reshape(req_count, step_count, heads_kv, HEAD_SIZE)
    )
    local_peak, local_totals, local_values = slot_attention(
        query_rows.transpose(0, 2, 1, 3, 4).reshape(req_count, -1, HEAD_SIZE),
        lengths,
        slot_request,
        slot_block_number,
        paged_key_cache,
        paged_value_cache,
        heads_kv,
        QUERY_PER_KEY,
    )
    local_peak = local_peak[:, 0]
    local_totals = local_totals[:, 0]
    n_seq = lax.axis_size("seq")
    per = req_count // n_seq
    seq_index = lax.axis_index("seq")
    mine = seq_index * per
    running_peak, running_totals, weighted_values = seq_merge(
        local_peak, local_totals, local_values, n_seq, seq_index
    )
    order = (per, heads_kv, step_count, QUERY_PER_KEY)
    running_peak = running_peak.reshape(order)
    running_totals = running_totals.reshape(order)
    weighted_values = weighted_values.reshape(order + (HEAD_SIZE,))
    own_queries = lax.dynamic_slice_in_dim(query_rows, mine, per, 0)
    fresh = fresh_part(
        own_queries,
        lax.dynamic_slice_in_dim(current_key, mine, per, 0),
        lax.dynamic_slice_in_dim(current_value, mine, per, 0),
    )
    running_peak, running_totals, weighted_values = merge_parts(
        (running_peak, running_totals, weighted_values), fresh
    )
    heads_out = (
        (weighted_values / running_totals[..., None])
        .transpose(0, 2, 1, 3, 4)
        .reshape(per, step_count, -1)
        .astype(jnp.bfloat16)
    )
    piece_rows = lax.all_gather(heads_out, "row", axis=0, tiled=False)
    n_row = piece_rows.shape[0]
    product = jnp.dot(
        piece_rows.reshape(n_row * per * step_count, -1), wo, preferred_element_type=jnp.float32
    )
    partials = product.reshape(n_row, per, step_count, -1)
    own_out = pair_scatter(partials.astype(jnp.bfloat16), "col").reshape(per, step_count, -1)
    split = own_out.shape[-1] // 2
    attended = jnp.concatenate(
        [
            doubling_gather(own_out[..., :split], "seq"),
            doubling_gather(own_out[..., split:], "seq", swap_last=True),
        ],
        -1,
    )
    return (
        attended,
        current_key.reshape(req_count, step_count, k_width),
        current_value.reshape(req_count, step_count, k_width),
    )


def solution(mesh):
    in_specs = (
        P("col", None, "row"),
        P("row"),
        P("row", "col"),
        P("row", "col"),
        P("row", "col"),
        P("col", "row"),
        P("row"),
        P(("row", "seq")),
        P(("row", "seq")),
        P(("row", "seq"), None, "col"),
        P(("row", "seq"), None, "col"),
    )
    out_specs = (P("col", None, "row"), P("row", None, "col"), P("row", None, "col"))
    return jax.shard_map(
        on_device, mesh=mesh, in_specs=in_specs, out_specs=out_specs, check_vma=False
    )
```

```python
import math
from functools import partial

import jax
import jax.numpy as jnp
from jax import lax
from jax.experimental import pallas as pl
from jax.experimental.pallas import tpu as pltpu
from jax.sharding import PartitionSpec as P

D = 5120
HEAD_SIZE = 128
WINDOW = 4096
SINK = 4
QUERY_PER_KEY = 4


EPSILON = 1e-05
NEGATIVE_FILL = -1e30
ROPE_BASE = 100000000.0


def rotary_apply(values, token_positions):
    half_dim = values.shape[-1] // 2
    frequency = ROPE_BASE ** (-(jnp.arange(half_dim, dtype=jnp.float32) * 2.0 / values.shape[-1]))
    angles = (token_positions.astype(jnp.float32)[..., None] * frequency)[..., None, :]
    cosine = jnp.cos(angles)
    sine_part = jnp.sin(angles)
    lower = values[..., :half_dim]
    upper = values[..., half_dim:]
    return jnp.concatenate(
        [lower * cosine - upper * sine_part, upper * cosine + lower * sine_part], -1
    )


def slot_parts(query_rows, lengths, slot_request, slot_block_number, key_rows, value_rows):
    req_count = query_rows.shape[0]
    step_count = query_rows.shape[1]
    block_len = key_rows.shape[1]
    picked = jnp.minimum(slot_request, req_count - 1)
    in_use = slot_request < req_count
    slot_queries = query_rows[picked]
    scores = jnp.einsum(
        "nsagh,nbah->nasgb", slot_queries, key_rows, preferred_element_type=jnp.float32
    ) * (1.0 / math.sqrt(HEAD_SIZE))
    key_pos = (
        slot_block_number[:, None] * block_len + jnp.arange(block_len, dtype=jnp.int32)[None, :]
    )
    own_len = lengths[picked]
    query_pos = own_len[:, None] + jnp.arange(step_count, dtype=jnp.int32)[None, :]
    visible = (
        in_use[:, None, None]
        & (key_pos[:, None, :] < own_len[:, None, None])
        & ((key_pos[:, None, :] < SINK) | (key_pos[:, None, :] > query_pos[:, :, None] - WINDOW))
    )
    visible = visible[:, None, :, None, :]
    slot_peak = jnp.max(jnp.where(visible, scores, NEGATIVE_FILL), -1)
    weights = jnp.where(visible, jnp.exp(scores - slot_peak[..., None]), 0.0)
    slot_total = jnp.sum(weights, -1)
    slot_acc = jnp.einsum(
        "nasgb,nbah->nasgh",
        weights.astype(jnp.bfloat16),
        value_rows,
        preferred_element_type=jnp.float32,
    )
    member = slot_request[None, :] == jnp.arange(req_count, dtype=jnp.int32)[:, None]
    local_peak = jnp.max(
        jnp.where(member[:, :, None, None, None], slot_peak[None], NEGATIVE_FILL), 1
    )
    return (local_peak, (slot_peak, slot_total, slot_acc, member, picked))


def pool_sums(held, running_peak):
    slot_peak, slot_total, slot_acc, member, picked = held
    factor = jnp.exp(slot_peak - running_peak[picked])
    as_member = member.astype(jnp.float32)
    running_totals = jnp.einsum(
        "rn,nasg->rasg", as_member, slot_total * factor, precision=lax.Precision.HIGHEST
    )
    weighted_values = jnp.einsum(
        "rn,nasgh->rasgh", as_member, slot_acc * factor[..., None], precision=lax.Precision.HIGHEST
    )
    return (running_totals, weighted_values)


def fresh_part(query_rows, key_all, value_all):
    step_count = query_rows.shape[1]
    used = key_all.shape[1]
    scores = jnp.einsum(
        "rsagh,ruah->rasgu", query_rows, key_all, preferred_element_type=jnp.float32
    ) * (1.0 / math.sqrt(HEAD_SIZE))
    causal = (
        jnp.arange(used, dtype=jnp.int32)[None, :]
        <= jnp.arange(step_count, dtype=jnp.int32)[:, None]
    )
    causal = causal[None, None, :, None, :]
    running_peak = jnp.max(jnp.where(causal, scores, NEGATIVE_FILL), -1)
    weights = jnp.where(causal, jnp.exp(scores - running_peak[..., None]), 0.0)
    running_totals = jnp.sum(weights, -1)
    weighted_values = jnp.einsum(
        "rasgu,ruah->rasgh",
        weights.astype(jnp.bfloat16),
        value_all,
        preferred_element_type=jnp.float32,
    )
    return (running_peak, running_totals, weighted_values)


def merge_parts(earlier, later):
    running_peak = jnp.maximum(earlier[0], later[0])
    first_factor = jnp.exp(earlier[0] - running_peak)
    second_factor = jnp.exp(later[0] - running_peak)
    running_totals = earlier[1] * first_factor + later[1] * second_factor
    weighted_values = earlier[2] * first_factor[..., None] + later[2] * second_factor[..., None]
    return (running_peak, running_totals, weighted_values)


def slot_kernel(
    req_ref, len_ref, blk_ref, q_ref, k_ref, v_ref, peak_ref, tot_ref, acc_ref, *, ns, heads, qpk
):
    @pl.when(pl.program_id(0) == 0)
    def _():
        peak_ref[...] = jnp.full(peak_ref.shape, NEGATIVE_FILL, jnp.float32)
        tot_ref[...] = jnp.zeros(tot_ref.shape, jnp.float32)
        acc_ref[...] = jnp.zeros(acc_ref.shape, jnp.float32)

    base = pl.program_id(0) * ns
    req_count = q_ref.shape[0]
    rows = q_ref.shape[1]
    group = rows // heads
    width = k_ref.shape[1]
    head = k_ref.shape[2] // heads
    row = lax.broadcasted_iota(jnp.int32, (rows, width), 0)
    col = lax.broadcasted_iota(jnp.int32, (rows, width), 1)
    step_of = (row % group) // qpk

    results = []
    for i in range(ns):
        req = req_ref[base + i]
        owner = jnp.minimum(req, req_count - 1)
        length = len_ref[owner]
        key_pos = blk_ref[base + i] * width + col
        query_pos = length + step_of
        visible = (
            (req < req_count)
            & (key_pos < length)
            & ((key_pos < SINK) | (key_pos > query_pos - WINDOW))
        )
        q = q_ref[owner]
        k = k_ref[i]
        v = v_ref[i]
        scores = jnp.concatenate(
            [
                lax.dot_general(
                    q[a * group : (a + 1) * group],
                    k[:, a * head : (a + 1) * head],
                    (((1,), (1,)), ((), ())),
                    preferred_element_type=jnp.float32,
                )
                for a in range(heads)
            ],
            0,
        ) * (1.0 / math.sqrt(HEAD_SIZE))
        peak = jnp.max(jnp.where(visible, scores, NEGATIVE_FILL), axis=1, keepdims=True)
        weights = jnp.where(visible, jnp.exp(scores - peak), 0.0)
        total = jnp.sum(weights, axis=1, keepdims=True)
        rounded = weights.astype(jnp.bfloat16)
        acc = jnp.concatenate(
            [
                jnp.dot(
                    rounded[a * group : (a + 1) * group],
                    v[:, a * head : (a + 1) * head],
                    preferred_element_type=jnp.float32,
                )
                for a in range(heads)
            ],
            0,
        )
        results.append((owner, peak, total, acc))
    for owner, peak, total, acc in results:
        old = peak_ref[owner]
        top = jnp.maximum(old, peak)
        old_factor = jnp.exp(old - top)
        new_factor = jnp.exp(peak - top)
        tot_ref[owner] = tot_ref[owner] * old_factor + total * new_factor
        acc_ref[owner] = acc_ref[owner] * old_factor + acc * new_factor
        peak_ref[owner] = top

def slot_attention(queries, lengths, slot_request, block_numbers, keys, values, heads, qpk):
    req_count, rows, head = queries.shape
    n_slots = keys.shape[0]
    width = keys.shape[1]
    ns = max(d for d in range(1, 11) if n_slots % d == 0)
    fixed = lambda n, sr, lr, br: (0, 0, 0)
    grid_spec = pltpu.PrefetchScalarGridSpec(
        num_scalar_prefetch=3,
        grid=(n_slots // ns,),
        in_specs=[
            pl.BlockSpec((req_count, rows, head), fixed),
            pl.BlockSpec((ns, width, keys.shape[2]), lambda n, sr, lr, br: (n, 0, 0)),
            pl.BlockSpec((ns, width, values.shape[2]), lambda n, sr, lr, br: (n, 0, 0)),
        ],
        out_specs=[
            pl.BlockSpec((req_count, rows, 1), fixed),
            pl.BlockSpec((req_count, rows, 1), fixed),
            pl.BlockSpec((req_count, rows, head), fixed),
        ],
    )
    return pl.pallas_call(
        partial(slot_kernel, ns=ns, heads=heads, qpk=qpk),
        grid_spec=grid_spec,
        out_shape=[
            jax.ShapeDtypeStruct((req_count, rows, 1), jnp.float32),
            jax.ShapeDtypeStruct((req_count, rows, 1), jnp.float32),
            jax.ShapeDtypeStruct((req_count, rows, head), jnp.float32),
        ],
    )(slot_request, lengths, block_numbers, queries, keys, values)

def pair_gather(part, axis_name):
    n = lax.axis_size(axis_name)
    assert n == 2
    side = lax.axis_index(axis_name)
    other = lax.ppermute(part, axis_name, [(0, 1), (1, 0)])
    return jnp.where(
        side == 0,
        jnp.concatenate([part, other], 0),
        jnp.concatenate([other, part], 0),
    )


def pair_scatter(parts, axis_name, rounded=True):
    n = lax.axis_size(axis_name)
    assert n == 2 and parts.shape[0] == 2
    side = lax.axis_index(axis_name)
    keep = lax.dynamic_index_in_dim(parts, side, 0, keepdims=True)
    send = lax.dynamic_index_in_dim(parts, 1 - side, 0, keepdims=True)
    got = lax.ppermute(send, axis_name, [(0, 1), (1, 0)])
    total = (keep.astype(jnp.float32) + got.astype(jnp.float32))[0]
    return total.astype(parts.dtype) if rounded else total


def doubling_gather(part, axis_name, swap_last=False):
    n = lax.axis_size(axis_name)
    stages = n.bit_length() - 1
    assert 1 << stages == n
    index = lax.axis_index(axis_name)
    block = part[None]
    order = list(reversed(range(stages)))
    if swap_last and stages >= 2:
        order[-2], order[-1] = order[-1], order[-2]
    for bit in order:
        pairs = [(s, s ^ (1 << bit)) for s in range(n)]
        got = lax.ppermute(block, axis_name, pairs)
        low = ((index >> bit) & 1) == 0
        block = jnp.where(
            low, jnp.stack([block, got], 0), jnp.stack([got, block], 0)
        )
    block = block.reshape((2,) * stages + part.shape)
    axes = list(reversed(order))
    block = block.transpose(
        tuple(axes.index(stages - 1 - p) for p in range(stages))
        + tuple(range(stages, stages + part.ndim))
    )
    return block.reshape((n * part.shape[0],) + part.shape[1:])


def pack_rows(stats, values):
    lanes = jnp.concatenate([stats[0], stats[1]], -1)
    high = lax.reduce_precision(lanes, exponent_bits=8, mantissa_bits=7)
    rest = lanes - high
    middle = lax.reduce_precision(rest, exponent_bits=8, mantissa_bits=7)
    low = rest - middle
    pieces = jnp.stack([high, middle, low, jnp.zeros_like(low)], -2)
    width = values.shape[-1]
    return jnp.concatenate(
        [
            values.astype(jnp.bfloat16).reshape(-1, width),
            pieces.astype(jnp.bfloat16).reshape(-1, width),
        ],
        0,
    )


def unpack_rows(message, stats_shape, values_shape):
    width = values_shape[-1]
    count = math.prod(values_shape) // width
    values = message[:count].astype(jnp.float32).reshape(values_shape)
    pieces = message[count:].astype(jnp.float32).reshape(stats_shape[1:-1] + (4, width))
    lanes = pieces[..., 0, :] + (pieces[..., 1, :] + pieces[..., 2, :])
    rows = stats_shape[-1]
    return jnp.stack([lanes[..., :rows], lanes[..., rows:]], 0), values


def seq_merge(peak, total, acc, n_seq, seq_index):
    stages = n_seq.bit_length() - 1
    assert 1 << stages == n_seq
    req_count = peak.shape[0]
    per = req_count // n_seq
    rest = peak.shape[1:]
    split = [2] * stages + [per]
    stats = jnp.stack([peak, total], 0).reshape([2] + split + list(rest))
    values = acc.reshape(split + list(acc.shape[1:]))
    for bit in range(stages):
        axis = stages - 1 - bit
        mine = (seq_index >> bit) & 1
        pairs = [(s, s ^ (1 << bit)) for s in range(n_seq)]
        keep_stats = lax.dynamic_index_in_dim(stats, mine, axis + 1, keepdims=True)
        send_stats = lax.dynamic_index_in_dim(stats, 1 - mine, axis + 1, keepdims=True)
        keep_values = lax.dynamic_index_in_dim(values, mine, axis, keepdims=True)
        send_values = lax.dynamic_index_in_dim(values, 1 - mine, axis, keepdims=True)
        if 2 * rest[-1] == values.shape[-1]:
            got_stats, got_values = unpack_rows(
                lax.ppermute(pack_rows(send_stats, send_values), "seq", pairs),
                send_stats.shape,
                send_values.shape,
            )
        else:
            got_stats = lax.ppermute(send_stats, "seq", pairs)
            got_values = lax.ppermute(send_values.astype(jnp.bfloat16), "seq", pairs).astype(
                jnp.float32
            )
        top = jnp.maximum(keep_stats[0], got_stats[0])
        keep_factor = jnp.exp(keep_stats[0] - top)
        got_factor = jnp.exp(got_stats[0] - top)
        stats = jnp.stack(
            [top, keep_stats[1] * keep_factor + got_stats[1] * got_factor], 0
        )
        values = keep_values * keep_factor[..., None] + got_values * got_factor[..., None]
    stats = stats.reshape((2, per) + tuple(rest))
    values = values.reshape((per,) + tuple(acc.shape[1:]))
    return (stats[0], stats[1], values)


def on_device(
    states,
    norm_gain,
    wq,
    wk,
    wv,
    wo,
    lengths,
    slot_request,
    slot_block_number,
    paged_key_cache,
    paged_value_cache,
):
    q_width = wq.shape[1]
    k_width = wk.shape[1]
    heads_kv = k_width // HEAD_SIZE
    req_count = lengths.shape[0]
    block_len = paged_key_cache.shape[1]
    key_rows = paged_key_cache.reshape(paged_key_cache.shape[0], block_len, heads_kv, HEAD_SIZE)
    value_rows = paged_value_cache.reshape(
        paged_value_cache.shape[0], block_len, heads_kv, HEAD_SIZE
    )
    step_count = states.shape[1]
    token_count = states.shape[0] * step_count
    own_states = states.reshape(token_count, -1)
    side = lax.axis_index("col")
    swap = [(0, 1), (1, 0)]
    other_states = lax.ppermute(own_states, "col", swap)
    as_float = own_states.astype(jnp.float32)
    squares = lax.psum(jnp.sum(as_float * as_float, -1), "row")
    other_squares = lax.ppermute(squares, "col", swap)

    def rms_norm(rows, sums):
        scale = lax.rsqrt(sums / D + EPSILON)[:, None]
        return (rows.astype(jnp.float32) * scale * norm_gain).astype(jnp.bfloat16)

    first = side == 0
    gathered = jnp.concatenate(
        [
            rms_norm(
                jnp.where(first, own_states, other_states), jnp.where(first, squares, other_squares)
            ),
            rms_norm(
                jnp.where(first, other_states, own_states), jnp.where(first, other_squares, squares)
            ),
        ],
        0,
    )
    parts_out = [
        jnp.dot(gathered, matrix, preferred_element_type=jnp.float32) for matrix in (wq, wk, wv)
    ]
    head_count = (q_width + 2 * k_width) // HEAD_SIZE
    output_projected = pair_scatter(
        jnp.concatenate(parts_out, axis=-1)
        .astype(jnp.bfloat16)
        .reshape(lax.axis_size("row"), token_count, -1),
        "row",
        rounded=False,
    ).reshape(token_count, head_count, HEAD_SIZE)
    q_heads = q_width // HEAD_SIZE
    token_positions = (
        lengths[:, None] + jnp.arange(step_count, dtype=jnp.int32)[None, :]
    ).reshape(token_count)
    query_rows = rotary_apply(output_projected[:, :q_heads], token_positions).astype(jnp.bfloat16)
    query_rows = query_rows.reshape(req_count, step_count, heads_kv, QUERY_PER_KEY, HEAD_SIZE)
    current_key = (
        rotary_apply(output_projected[:, q_heads : q_heads + heads_kv], token_positions)
        .astype(jnp.bfloat16)
        .reshape(req_count, step_count, heads_kv, HEAD_SIZE)
    )
    current_value = (
        output_projected[:, q_heads + heads_kv :]
        .astype(jnp.bfloat16)
        .reshape(req_count, step_count, heads_kv, HEAD_SIZE)
    )
    local_peak, local_totals, local_values = slot_attention(
        query_rows.transpose(0, 2, 1, 3, 4).reshape(req_count, -1, HEAD_SIZE),
        lengths,
        slot_request,
        slot_block_number,
        paged_key_cache,
        paged_value_cache,
        heads_kv,
        QUERY_PER_KEY,
    )
    local_peak = local_peak[..., 0]
    local_totals = local_totals[..., 0]
    n_seq = lax.axis_size("seq")
    per = req_count // n_seq
    seq_index = lax.axis_index("seq")
    mine = seq_index * per
    running_peak, running_totals, weighted_values = seq_merge(
        local_peak, local_totals, local_values, n_seq, seq_index
    )
    order = (per, heads_kv, step_count, QUERY_PER_KEY)
    running_peak = running_peak.reshape(order)
    running_totals = running_totals.reshape(order)
    weighted_values = weighted_values.reshape(order + (HEAD_SIZE,))
    own_queries = lax.dynamic_slice_in_dim(query_rows, mine, per, 0)
    fresh = fresh_part(
        own_queries,
        lax.dynamic_slice_in_dim(current_key, mine, per, 0),
        lax.dynamic_slice_in_dim(current_value, mine, per, 0),
    )
    running_peak, running_totals, weighted_values = merge_parts(
        (running_peak, running_totals, weighted_values), fresh
    )
    heads_out = (
        (weighted_values / running_totals[..., None])
        .transpose(0, 2, 1, 3, 4)
        .reshape(per, step_count, -1)
        .astype(jnp.bfloat16)
    )
    piece_rows = lax.all_gather(heads_out, "row", axis=0, tiled=False)
    n_row = piece_rows.shape[0]
    product = jnp.dot(
        piece_rows.reshape(n_row * per * step_count, -1), wo, preferred_element_type=jnp.float32
    )
    partials = product.reshape(n_row, per, step_count, -1)
    own_out = pair_scatter(partials.astype(jnp.bfloat16), "col").reshape(per, step_count, -1)
    split = own_out.shape[-1] // 2
    attended = jnp.concatenate(
        [
            doubling_gather(own_out[..., :split], "seq"),
            doubling_gather(own_out[..., split:], "seq", swap_last=True),
        ],
        -1,
    )
    return (
        attended,
        current_key.reshape(req_count, step_count, k_width),
        current_value.reshape(req_count, step_count, k_width),
    )


def solution(mesh):
    in_specs = (
        P("col", None, "row"),
        P("row"),
        P("row", "col"),
        P("row", "col"),
        P("row", "col"),
        P("col", "row"),
        P("row"),
        P(("row", "seq")),
        P(("row", "seq")),
        P(("row", "seq"), None, "col"),
        P(("row", "seq"), None, "col"),
    )
    out_specs = (P("col", None, "row"), P("row", None, "col"), P("row", None, "col"))
    return jax.shard_map(
        on_device, mesh=mesh, in_specs=in_specs, out_specs=out_specs, check_vma=False
    )
```

```python
import math
from functools import partial

import jax
import jax.numpy as jnp
from jax import lax
from jax.experimental import pallas as pl
from jax.experimental.pallas import tpu as pltpu
from jax.sharding import PartitionSpec as P

D = 5120
HEAD_SIZE = 128
WINDOW = 4096
SINK = 4
QUERY_PER_KEY = 4


EPSILON = 1e-05
NEGATIVE_FILL = -1e30
ROPE_BASE = 100000000.0


def rotary_apply(values, token_positions):
    half_dim = values.shape[-1] // 2
    frequency = ROPE_BASE ** (-(jnp.arange(half_dim, dtype=jnp.float32) * 2.0 / values.shape[-1]))
    angles = (token_positions.astype(jnp.float32)[..., None] * frequency)[..., None, :]
    cosine = jnp.cos(angles)
    sine_part = jnp.sin(angles)
    lower = values[..., :half_dim]
    upper = values[..., half_dim:]
    return jnp.concatenate(
        [lower * cosine - upper * sine_part, upper * cosine + lower * sine_part], -1
    )


def slot_parts(query_rows, lengths, slot_request, slot_block_number, key_rows, value_rows):
    req_count = query_rows.shape[0]
    step_count = query_rows.shape[1]
    block_len = key_rows.shape[1]
    picked = jnp.minimum(slot_request, req_count - 1)
    in_use = slot_request < req_count
    slot_queries = query_rows[picked]
    scores = jnp.einsum(
        "nsagh,nbah->nasgb", slot_queries, key_rows, preferred_element_type=jnp.float32
    ) * (1.0 / math.sqrt(HEAD_SIZE))
    key_pos = (
        slot_block_number[:, None] * block_len + jnp.arange(block_len, dtype=jnp.int32)[None, :]
    )
    own_len = lengths[picked]
    query_pos = own_len[:, None] + jnp.arange(step_count, dtype=jnp.int32)[None, :]
    visible = (
        in_use[:, None, None]
        & (key_pos[:, None, :] < own_len[:, None, None])
        & ((key_pos[:, None, :] < SINK) | (key_pos[:, None, :] > query_pos[:, :, None] - WINDOW))
    )
    visible = visible[:, None, :, None, :]
    slot_peak = jnp.max(jnp.where(visible, scores, NEGATIVE_FILL), -1)
    weights = jnp.where(visible, jnp.exp(scores - slot_peak[..., None]), 0.0)
    slot_total = jnp.sum(weights, -1)
    slot_acc = jnp.einsum(
        "nasgb,nbah->nasgh",
        weights.astype(jnp.bfloat16),
        value_rows,
        preferred_element_type=jnp.float32,
    )
    member = slot_request[None, :] == jnp.arange(req_count, dtype=jnp.int32)[:, None]
    local_peak = jnp.max(
        jnp.where(member[:, :, None, None, None], slot_peak[None], NEGATIVE_FILL), 1
    )
    return (local_peak, (slot_peak, slot_total, slot_acc, member, picked))


def pool_sums(held, running_peak):
    slot_peak, slot_total, slot_acc, member, picked = held
    factor = jnp.exp(slot_peak - running_peak[picked])
    as_member = member.astype(jnp.float32)
    running_totals = jnp.einsum(
        "rn,nasg->rasg", as_member, slot_total * factor, precision=lax.Precision.HIGHEST
    )
    weighted_values = jnp.einsum(
        "rn,nasgh->rasgh", as_member, slot_acc * factor[..., None], precision=lax.Precision.HIGHEST
    )
    return (running_totals, weighted_values)


def fresh_part(query_rows, key_all, value_all):
    step_count = query_rows.shape[1]
    used = key_all.shape[1]
    scores = jnp.einsum(
        "rsagh,ruah->rasgu", query_rows, key_all, preferred_element_type=jnp.float32
    ) * (1.0 / math.sqrt(HEAD_SIZE))
    causal = (
        jnp.arange(used, dtype=jnp.int32)[None, :]
        <= jnp.arange(step_count, dtype=jnp.int32)[:, None]
    )
    causal = causal[None, None, :, None, :]
    running_peak = jnp.max(jnp.where(causal, scores, NEGATIVE_FILL), -1)
    weights = jnp.where(causal, jnp.exp(scores - running_peak[..., None]), 0.0)
    running_totals = jnp.sum(weights, -1)
    weighted_values = jnp.einsum(
        "rasgu,ruah->rasgh",
        weights.astype(jnp.bfloat16),
        value_all,
        preferred_element_type=jnp.float32,
    )
    return (running_peak, running_totals, weighted_values)


def merge_parts(earlier, later):
    running_peak = jnp.maximum(earlier[0], later[0])
    first_factor = jnp.exp(earlier[0] - running_peak)
    second_factor = jnp.exp(later[0] - running_peak)
    running_totals = earlier[1] * first_factor + later[1] * second_factor
    weighted_values = earlier[2] * first_factor[..., None] + later[2] * second_factor[..., None]
    return (running_peak, running_totals, weighted_values)


def slot_kernel(
    req_ref, len_ref, blk_ref, q_ref, k_ref, v_ref, peak_ref, tot_ref, acc_ref, *, ns, heads, qpk
):
    @pl.when(pl.program_id(0) == 0)
    def _():
        peak_ref[...] = jnp.full(peak_ref.shape, NEGATIVE_FILL, jnp.float32)
        tot_ref[...] = jnp.zeros(tot_ref.shape, jnp.float32)
        acc_ref[...] = jnp.zeros(acc_ref.shape, jnp.float32)

    base = pl.program_id(0) * ns
    req_count = q_ref.shape[0]
    rows = q_ref.shape[1]
    group = rows // heads
    width = k_ref.shape[1]
    head = k_ref.shape[2] // heads
    row = lax.broadcasted_iota(jnp.int32, (rows, width), 0)
    col = lax.broadcasted_iota(jnp.int32, (rows, width), 1)
    step_of = (row % group) // qpk

    results = []
    for i in range(ns):
        req = req_ref[base + i]
        owner = jnp.minimum(req, req_count - 1)
        length = len_ref[owner]
        key_pos = blk_ref[base + i] * width + col
        query_pos = length + step_of
        visible = (
            (req < req_count)
            & (key_pos < length)
            & ((key_pos < SINK) | (key_pos > query_pos - WINDOW))
        )
        q = q_ref[owner]
        k = k_ref[i]
        v = v_ref[i]
        scores = jnp.concatenate(
            [
                lax.dot_general(
                    q[a * group : (a + 1) * group],
                    k[:, a * head : (a + 1) * head],
                    (((1,), (1,)), ((), ())),
                    preferred_element_type=jnp.float32,
                )
                for a in range(heads)
            ],
            0,
        ) * (1.0 / math.sqrt(HEAD_SIZE))
        peak = jnp.max(jnp.where(visible, scores, NEGATIVE_FILL), axis=1, keepdims=True)
        weights = jnp.where(visible, jnp.exp(scores - peak), 0.0)
        total = jnp.sum(weights, axis=1, keepdims=True)
        rounded = weights.astype(jnp.bfloat16)
        acc = jnp.concatenate(
            [
                jnp.dot(
                    rounded[a * group : (a + 1) * group],
                    v[:, a * head : (a + 1) * head],
                    preferred_element_type=jnp.float32,
                )
                for a in range(heads)
            ],
            0,
        )
        results.append((owner, peak, total, acc))
    for owner, peak, total, acc in results:
        old = peak_ref[owner]
        top = jnp.maximum(old, peak)
        old_factor = jnp.exp(old - top)
        new_factor = jnp.exp(peak - top)
        tot_ref[owner] = tot_ref[owner] * old_factor + total * new_factor
        acc_ref[owner] = acc_ref[owner] * old_factor + acc * new_factor
        peak_ref[owner] = top

def slot_attention(queries, lengths, slot_request, block_numbers, keys, values, heads, qpk):
    req_count, rows, head = queries.shape
    n_slots = keys.shape[0]
    width = keys.shape[1]
    ns = max(d for d in range(1, 26) if n_slots % d == 0)
    fixed = lambda n, sr, lr, br: (0, 0, 0)
    grid_spec = pltpu.PrefetchScalarGridSpec(
        num_scalar_prefetch=3,
        grid=(n_slots // ns,),
        in_specs=[
            pl.BlockSpec((req_count, rows, head), fixed),
            pl.BlockSpec((ns, width, keys.shape[2]), lambda n, sr, lr, br: (n, 0, 0)),
            pl.BlockSpec((ns, width, values.shape[2]), lambda n, sr, lr, br: (n, 0, 0)),
        ],
        out_specs=[
            pl.BlockSpec((req_count, rows, 1), fixed),
            pl.BlockSpec((req_count, rows, 1), fixed),
            pl.BlockSpec((req_count, rows, head), fixed),
        ],
    )
    return pl.pallas_call(
        partial(slot_kernel, ns=ns, heads=heads, qpk=qpk),
        grid_spec=grid_spec,
        compiler_params=pltpu.CompilerParams(vmem_limit_bytes=48 * 1024 * 1024),
        out_shape=[
            jax.ShapeDtypeStruct((req_count, rows, 1), jnp.float32),
            jax.ShapeDtypeStruct((req_count, rows, 1), jnp.float32),
            jax.ShapeDtypeStruct((req_count, rows, head), jnp.float32),
        ],
    )(slot_request, lengths, block_numbers, queries, keys, values)

def pair_gather(part, axis_name):
    n = lax.axis_size(axis_name)
    assert n == 2
    side = lax.axis_index(axis_name)
    other = lax.ppermute(part, axis_name, [(0, 1), (1, 0)])
    return jnp.where(
        side == 0,
        jnp.concatenate([part, other], 0),
        jnp.concatenate([other, part], 0),
    )


def pair_scatter(parts, axis_name, rounded=True):
    n = lax.axis_size(axis_name)
    assert n == 2 and parts.shape[0] == 2
    side = lax.axis_index(axis_name)
    keep = lax.dynamic_index_in_dim(parts, side, 0, keepdims=True)
    send = lax.dynamic_index_in_dim(parts, 1 - side, 0, keepdims=True)
    got = lax.ppermute(send, axis_name, [(0, 1), (1, 0)])
    total = (keep.astype(jnp.float32) + got.astype(jnp.float32))[0]
    return total.astype(parts.dtype) if rounded else total


def doubling_gather(part, axis_name, swap_last=False):
    n = lax.axis_size(axis_name)
    stages = n.bit_length() - 1
    assert 1 << stages == n
    index = lax.axis_index(axis_name)
    block = part[None]
    order = list(reversed(range(stages)))
    if swap_last and stages >= 2:
        order[-2], order[-1] = order[-1], order[-2]
    for bit in order:
        pairs = [(s, s ^ (1 << bit)) for s in range(n)]
        got = lax.ppermute(block, axis_name, pairs)
        low = ((index >> bit) & 1) == 0
        block = jnp.where(
            low, jnp.stack([block, got], 0), jnp.stack([got, block], 0)
        )
    block = block.reshape((2,) * stages + part.shape)
    axes = list(reversed(order))
    block = block.transpose(
        tuple(axes.index(stages - 1 - p) for p in range(stages))
        + tuple(range(stages, stages + part.ndim))
    )
    return block.reshape((n * part.shape[0],) + part.shape[1:])


def seq_merge(peak, total, acc, n_seq, seq_index):
    stages = n_seq.bit_length() - 1
    assert 1 << stages == n_seq
    req_count = peak.shape[0]
    per = req_count // n_seq
    rest = peak.shape[1:]
    split = [2] * stages + [per]
    stats = jnp.stack([peak, total], 0).reshape([2] + split + list(rest))
    values = acc.reshape(split + list(acc.shape[1:]))
    for bit in range(stages):
        axis = stages - 1 - bit
        mine = (seq_index >> bit) & 1
        pairs = [(s, s ^ (1 << bit)) for s in range(n_seq)]
        keep_stats = lax.dynamic_index_in_dim(stats, mine, axis + 1, keepdims=True)
        send_stats = lax.dynamic_index_in_dim(stats, 1 - mine, axis + 1, keepdims=True)
        keep_values = lax.dynamic_index_in_dim(values, mine, axis, keepdims=True)
        send_values = lax.dynamic_index_in_dim(values, 1 - mine, axis, keepdims=True)
        got_stats = lax.ppermute(send_stats, "seq", pairs)
        got_values = lax.ppermute(send_values.astype(jnp.bfloat16), "seq", pairs).astype(
            jnp.float32
        )
        top = jnp.maximum(keep_stats[0], got_stats[0])
        keep_factor = jnp.exp(keep_stats[0] - top)
        got_factor = jnp.exp(got_stats[0] - top)
        stats = jnp.stack(
            [top, keep_stats[1] * keep_factor + got_stats[1] * got_factor], 0
        )
        values = keep_values * keep_factor[..., None] + got_values * got_factor[..., None]
    stats = stats.reshape((2, per) + tuple(rest))
    values = values.reshape((per,) + tuple(acc.shape[1:]))
    return (stats[0], stats[1], values)


def on_device(
    states,
    norm_gain,
    wq,
    wk,
    wv,
    wo,
    lengths,
    slot_request,
    slot_block_number,
    paged_key_cache,
    paged_value_cache,
):
    q_width = wq.shape[1]
    k_width = wk.shape[1]
    heads_kv = k_width // HEAD_SIZE
    req_count = lengths.shape[0]
    block_len = paged_key_cache.shape[1]
    key_rows = paged_key_cache.reshape(paged_key_cache.shape[0], block_len, heads_kv, HEAD_SIZE)
    value_rows = paged_value_cache.reshape(
        paged_value_cache.shape[0], block_len, heads_kv, HEAD_SIZE
    )
    step_count = states.shape[1]
    token_count = states.shape[0] * step_count
    own_states = states.reshape(token_count, -1)
    side = lax.axis_index("col")
    swap = [(0, 1), (1, 0)]
    other_states = lax.ppermute(own_states, "col", swap)
    as_float = own_states.astype(jnp.float32)
    squares = lax.psum(jnp.sum(as_float * as_float, -1), "row")
    other_squares = lax.ppermute(squares, "col", swap)

    def rms_norm(rows, sums):
        scale = lax.rsqrt(sums / D + EPSILON)[:, None]
        return (rows.astype(jnp.float32) * scale * norm_gain).astype(jnp.bfloat16)

    first = side == 0
    gathered = jnp.concatenate(
        [
            rms_norm(
                jnp.where(first, own_states, other_states), jnp.where(first, squares, other_squares)
            ),
            rms_norm(
                jnp.where(first, other_states, own_states), jnp.where(first, other_squares, squares)
            ),
        ],
        0,
    )
    parts_out = [
        jnp.dot(gathered, matrix, preferred_element_type=jnp.float32) for matrix in (wq, wk, wv)
    ]
    head_count = (q_width + 2 * k_width) // HEAD_SIZE
    output_projected = pair_scatter(
        jnp.concatenate(parts_out, axis=-1)
        .astype(jnp.bfloat16)
        .reshape(lax.axis_size("row"), token_count, -1),
        "row",
        rounded=False,
    ).reshape(token_count, head_count, HEAD_SIZE)
    q_heads = q_width // HEAD_SIZE
    token_positions = (
        lengths[:, None] + jnp.arange(step_count, dtype=jnp.int32)[None, :]
    ).reshape(token_count)
    query_rows = rotary_apply(output_projected[:, :q_heads], token_positions).astype(jnp.bfloat16)
    query_rows = query_rows.reshape(req_count, step_count, heads_kv, QUERY_PER_KEY, HEAD_SIZE)
    current_key = (
        rotary_apply(output_projected[:, q_heads : q_heads + heads_kv], token_positions)
        .astype(jnp.bfloat16)
        .reshape(req_count, step_count, heads_kv, HEAD_SIZE)
    )
    current_value = (
        output_projected[:, q_heads + heads_kv :]
        .astype(jnp.bfloat16)
        .reshape(req_count, step_count, heads_kv, HEAD_SIZE)
    )
    local_peak, local_totals, local_values = slot_attention(
        query_rows.transpose(0, 2, 1, 3, 4).reshape(req_count, -1, HEAD_SIZE),
        lengths,
        slot_request,
        slot_block_number,
        paged_key_cache,
        paged_value_cache,
        heads_kv,
        QUERY_PER_KEY,
    )
    local_peak = local_peak[..., 0]
    local_totals = local_totals[..., 0]
    n_seq = lax.axis_size("seq")
    per = req_count // n_seq
    seq_index = lax.axis_index("seq")
    mine = seq_index * per
    running_peak, running_totals, weighted_values = seq_merge(
        local_peak, local_totals, local_values, n_seq, seq_index
    )
    order = (per, heads_kv, step_count, QUERY_PER_KEY)
    running_peak = running_peak.reshape(order)
    running_totals = running_totals.reshape(order)
    weighted_values = weighted_values.reshape(order + (HEAD_SIZE,))
    own_queries = lax.dynamic_slice_in_dim(query_rows, mine, per, 0)
    fresh = fresh_part(
        own_queries,
        lax.dynamic_slice_in_dim(current_key, mine, per, 0),
        lax.dynamic_slice_in_dim(current_value, mine, per, 0),
    )
    running_peak, running_totals, weighted_values = merge_parts(
        (running_peak, running_totals, weighted_values), fresh
    )
    heads_out = (
        (weighted_values / running_totals[..., None])
        .transpose(0, 2, 1, 3, 4)
        .reshape(per, step_count, -1)
        .astype(jnp.bfloat16)
    )
    piece_rows = lax.all_gather(heads_out, "row", axis=0, tiled=False)
    n_row = piece_rows.shape[0]
    product = jnp.dot(
        piece_rows.reshape(n_row * per * step_count, -1), wo, preferred_element_type=jnp.float32
    )
    partials = product.reshape(n_row, per, step_count, -1)
    own_out = pair_scatter(partials.astype(jnp.bfloat16), "col").reshape(per, step_count, -1)
    split = own_out.shape[-1] // 2
    attended = jnp.concatenate(
        [
            doubling_gather(own_out[..., :split], "seq"),
            doubling_gather(own_out[..., split:], "seq", swap_last=True),
        ],
        -1,
    )
    return (
        attended,
        current_key.reshape(req_count, step_count, k_width),
        current_value.reshape(req_count, step_count, k_width),
    )


def solution(mesh):
    in_specs = (
        P("col", None, "row"),
        P("row"),
        P("row", "col"),
        P("row", "col"),
        P("row", "col"),
        P("col", "row"),
        P("row"),
        P(("row", "seq")),
        P(("row", "seq")),
        P(("row", "seq"), None, "col"),
        P(("row", "seq"), None, "col"),
    )
    out_specs = (P("col", None, "row"), P("row", None, "col"), P("row", None, "col"))
    return jax.shard_map(
        on_device, mesh=mesh, in_specs=in_specs, out_specs=out_specs, check_vma=False
    )
```

```python
import math
from functools import partial

import jax
import jax.numpy as jnp
from jax import lax
from jax.experimental import pallas as pl
from jax.experimental.pallas import tpu as pltpu
from jax.sharding import PartitionSpec as P

D = 5120
HEAD_SIZE = 128
WINDOW = 4096
SINK = 4
QUERY_PER_KEY = 4


EPSILON = 1e-05
NEGATIVE_FILL = -1e30
ROPE_BASE = 100000000.0


def rotary_apply(values, token_positions):
    half_dim = values.shape[-1] // 2
    frequency = ROPE_BASE ** (-(jnp.arange(half_dim, dtype=jnp.float32) * 2.0 / values.shape[-1]))
    angles = (token_positions.astype(jnp.float32)[..., None] * frequency)[..., None, :]
    cosine = jnp.cos(angles)
    sine_part = jnp.sin(angles)
    lower = values[..., :half_dim]
    upper = values[..., half_dim:]
    return jnp.concatenate(
        [lower * cosine - upper * sine_part, upper * cosine + lower * sine_part], -1
    )


def slot_parts(query_rows, lengths, slot_request, slot_block_number, key_rows, value_rows):
    req_count = query_rows.shape[0]
    step_count = query_rows.shape[1]
    block_len = key_rows.shape[1]
    picked = jnp.minimum(slot_request, req_count - 1)
    in_use = slot_request < req_count
    slot_queries = query_rows[picked]
    scores = jnp.einsum(
        "nsagh,nbah->nasgb", slot_queries, key_rows, preferred_element_type=jnp.float32
    ) * (1.0 / math.sqrt(HEAD_SIZE))
    key_pos = (
        slot_block_number[:, None] * block_len + jnp.arange(block_len, dtype=jnp.int32)[None, :]
    )
    own_len = lengths[picked]
    query_pos = own_len[:, None] + jnp.arange(step_count, dtype=jnp.int32)[None, :]
    visible = (
        in_use[:, None, None]
        & (key_pos[:, None, :] < own_len[:, None, None])
        & ((key_pos[:, None, :] < SINK) | (key_pos[:, None, :] > query_pos[:, :, None] - WINDOW))
    )
    visible = visible[:, None, :, None, :]
    slot_peak = jnp.max(jnp.where(visible, scores, NEGATIVE_FILL), -1)
    weights = jnp.where(visible, jnp.exp(scores - slot_peak[..., None]), 0.0)
    slot_total = jnp.sum(weights, -1)
    slot_acc = jnp.einsum(
        "nasgb,nbah->nasgh",
        weights.astype(jnp.bfloat16),
        value_rows,
        preferred_element_type=jnp.float32,
    )
    member = slot_request[None, :] == jnp.arange(req_count, dtype=jnp.int32)[:, None]
    local_peak = jnp.max(
        jnp.where(member[:, :, None, None, None], slot_peak[None], NEGATIVE_FILL), 1
    )
    return (local_peak, (slot_peak, slot_total, slot_acc, member, picked))


def pool_sums(held, running_peak):
    slot_peak, slot_total, slot_acc, member, picked = held
    factor = jnp.exp(slot_peak - running_peak[picked])
    as_member = member.astype(jnp.float32)
    running_totals = jnp.einsum(
        "rn,nasg->rasg", as_member, slot_total * factor, precision=lax.Precision.HIGHEST
    )
    weighted_values = jnp.einsum(
        "rn,nasgh->rasgh", as_member, slot_acc * factor[..., None], precision=lax.Precision.HIGHEST
    )
    return (running_totals, weighted_values)


def fresh_part(query_rows, key_all, value_all):
    step_count = query_rows.shape[1]
    used = key_all.shape[1]
    scores = jnp.einsum(
        "rsagh,ruah->rasgu", query_rows, key_all, preferred_element_type=jnp.float32
    ) * (1.0 / math.sqrt(HEAD_SIZE))
    causal = (
        jnp.arange(used, dtype=jnp.int32)[None, :]
        <= jnp.arange(step_count, dtype=jnp.int32)[:, None]
    )
    causal = causal[None, None, :, None, :]
    running_peak = jnp.max(jnp.where(causal, scores, NEGATIVE_FILL), -1)
    weights = jnp.where(causal, jnp.exp(scores - running_peak[..., None]), 0.0)
    running_totals = jnp.sum(weights, -1)
    weighted_values = jnp.einsum(
        "rasgu,ruah->rasgh",
        weights.astype(jnp.bfloat16),
        value_all,
        preferred_element_type=jnp.float32,
    )
    return (running_peak, running_totals, weighted_values)


def merge_parts(earlier, later):
    running_peak = jnp.maximum(earlier[0], later[0])
    first_factor = jnp.exp(earlier[0] - running_peak)
    second_factor = jnp.exp(later[0] - running_peak)
    running_totals = earlier[1] * first_factor + later[1] * second_factor
    weighted_values = earlier[2] * first_factor[..., None] + later[2] * second_factor[..., None]
    return (running_peak, running_totals, weighted_values)


def slot_kernel(
    req_ref, len_ref, blk_ref, q_ref, k_ref, v_ref, peak_ref, tot_ref, acc_ref, *, ns, heads, qpk
):
    @pl.when(pl.program_id(0) == 0)
    def _():
        peak_ref[...] = jnp.full(peak_ref.shape, NEGATIVE_FILL, jnp.float32)
        tot_ref[...] = jnp.zeros(tot_ref.shape, jnp.float32)
        acc_ref[...] = jnp.zeros(acc_ref.shape, jnp.float32)

    base = pl.program_id(0) * ns
    req_count = q_ref.shape[0]
    rows = q_ref.shape[1]
    group = rows // heads
    width = k_ref.shape[1]
    head = k_ref.shape[2] // heads
    row = lax.broadcasted_iota(jnp.int32, (rows, width), 0)
    col = lax.broadcasted_iota(jnp.int32, (rows, width), 1)
    step_of = (row % group) // qpk

    results = []
    for i in range(ns):
        req = req_ref[base + i]
        owner = jnp.minimum(req, req_count - 1)
        length = len_ref[owner]
        key_pos = blk_ref[base + i] * width + col
        query_pos = length + step_of
        visible = (
            (req < req_count)
            & (key_pos < length)
            & ((key_pos < SINK) | (key_pos > query_pos - WINDOW))
        )
        q = q_ref[owner]
        k = k_ref[i]
        v = v_ref[i]
        scores = jnp.concatenate(
            [
                lax.dot_general(
                    q[a * group : (a + 1) * group],
                    k[:, a * head : (a + 1) * head],
                    (((1,), (1,)), ((), ())),
                    preferred_element_type=jnp.float32,
                )
                for a in range(heads)
            ],
            0,
        ) * (1.0 / math.sqrt(HEAD_SIZE))
        peak = jnp.max(jnp.where(visible, scores, NEGATIVE_FILL), axis=1, keepdims=True)
        weights = jnp.where(visible, jnp.exp(scores - peak), 0.0)
        total = jnp.sum(weights, axis=1, keepdims=True)
        rounded = weights.astype(jnp.bfloat16)
        acc = jnp.concatenate(
            [
                jnp.dot(
                    rounded[a * group : (a + 1) * group],
                    v[:, a * head : (a + 1) * head],
                    preferred_element_type=jnp.float32,
                )
                for a in range(heads)
            ],
            0,
        )
        results.append((owner, peak, total, acc))
    for owner, peak, total, acc in results:
        old = peak_ref[owner]
        top = jnp.maximum(old, peak)
        old_factor = jnp.exp(old - top)
        new_factor = jnp.exp(peak - top)
        tot_ref[owner] = tot_ref[owner] * old_factor + total * new_factor
        acc_ref[owner] = acc_ref[owner] * old_factor + acc * new_factor
        peak_ref[owner] = top

def slot_attention(queries, lengths, slot_request, block_numbers, keys, values, heads, qpk):
    req_count, rows, head = queries.shape
    n_slots = keys.shape[0]
    width = keys.shape[1]
    ns = max(d for d in range(1, 11) if n_slots % d == 0)
    fixed = lambda n, sr, lr, br: (0, 0, 0)
    grid_spec = pltpu.PrefetchScalarGridSpec(
        num_scalar_prefetch=3,
        grid=(n_slots // ns,),
        in_specs=[
            pl.BlockSpec((req_count, rows, head), fixed),
            pl.BlockSpec((ns, width, keys.shape[2]), lambda n, sr, lr, br: (n, 0, 0)),
            pl.BlockSpec((ns, width, values.shape[2]), lambda n, sr, lr, br: (n, 0, 0)),
        ],
        out_specs=[
            pl.BlockSpec((req_count, rows, 1), fixed),
            pl.BlockSpec((req_count, rows, 1), fixed),
            pl.BlockSpec((req_count, rows, head), fixed),
        ],
    )
    return pl.pallas_call(
        partial(slot_kernel, ns=ns, heads=heads, qpk=qpk),
        grid_spec=grid_spec,
        out_shape=[
            jax.ShapeDtypeStruct((req_count, rows, 1), jnp.float32),
            jax.ShapeDtypeStruct((req_count, rows, 1), jnp.float32),
            jax.ShapeDtypeStruct((req_count, rows, head), jnp.float32),
        ],
    )(slot_request, lengths, block_numbers, queries, keys, values)

def pair_gather(part, axis_name):
    n = lax.axis_size(axis_name)
    assert n == 2
    side = lax.axis_index(axis_name)
    other = lax.ppermute(part, axis_name, [(0, 1), (1, 0)])
    return jnp.where(
        side == 0,
        jnp.concatenate([part, other], 0),
        jnp.concatenate([other, part], 0),
    )


def pair_scatter(parts, axis_name, rounded=True):
    n = lax.axis_size(axis_name)
    assert n == 2 and parts.shape[0] == 2
    side = lax.axis_index(axis_name)
    keep = lax.dynamic_index_in_dim(parts, side, 0, keepdims=True)
    send = lax.dynamic_index_in_dim(parts, 1 - side, 0, keepdims=True)
    got = lax.ppermute(send, axis_name, [(0, 1), (1, 0)])
    total = (keep.astype(jnp.float32) + got.astype(jnp.float32))[0]
    return total.astype(parts.dtype) if rounded else total


def doubling_gather(part, axis_name, swap_last=False):
    n = lax.axis_size(axis_name)
    stages = n.bit_length() - 1
    assert 1 << stages == n
    index = lax.axis_index(axis_name)
    order = list(reversed(range(stages)))
    if swap_last and stages >= 2:
        order[-2], order[-1] = order[-1], order[-2]
    block = part
    done = []
    for bit in order:
        pairs = [(s, s ^ (1 << bit)) for s in range(n)]
        got = lax.ppermute(block, axis_name, pairs)
        low = ((index >> bit) & 1) == 0
        place = sum(1 for d in done if d > bit)
        block = jnp.where(
            low, jnp.stack([block, got], place), jnp.stack([got, block], place)
        )
        done.append(bit)
    return block.reshape((n * part.shape[0],) + part.shape[1:])


def seq_merge(peak, total, acc, n_seq, seq_index):
    stages = n_seq.bit_length() - 1
    assert 1 << stages == n_seq
    req_count = peak.shape[0]
    per = req_count // n_seq
    rest = peak.shape[1:]
    split = [2] * stages + [per]
    stats = jnp.stack([peak, total], 0).reshape([2] + split + list(rest))
    values = acc.reshape(split + list(acc.shape[1:]))
    for bit in range(stages):
        axis = stages - 1 - bit
        mine = (seq_index >> bit) & 1
        pairs = [(s, s ^ (1 << bit)) for s in range(n_seq)]
        keep_stats = lax.dynamic_index_in_dim(stats, mine, axis + 1, keepdims=True)
        send_stats = lax.dynamic_index_in_dim(stats, 1 - mine, axis + 1, keepdims=True)
        keep_values = lax.dynamic_index_in_dim(values, mine, axis, keepdims=True)
        send_values = lax.dynamic_index_in_dim(values, 1 - mine, axis, keepdims=True)
        got_stats = lax.ppermute(send_stats, "seq", pairs)
        got_values = lax.ppermute(send_values.astype(jnp.bfloat16), "seq", pairs).astype(
            jnp.float32
        )
        top = jnp.maximum(keep_stats[0], got_stats[0])
        keep_factor = jnp.exp(keep_stats[0] - top)
        got_factor = jnp.exp(got_stats[0] - top)
        stats = jnp.stack(
            [top, keep_stats[1] * keep_factor + got_stats[1] * got_factor], 0
        )
        values = keep_values * keep_factor[..., None] + got_values * got_factor[..., None]
    stats = stats.reshape((2, per) + tuple(rest))
    values = values.reshape((per,) + tuple(acc.shape[1:]))
    return (stats[0], stats[1], values)


def on_device(
    states,
    norm_gain,
    wq,
    wk,
    wv,
    wo,
    lengths,
    slot_request,
    slot_block_number,
    paged_key_cache,
    paged_value_cache,
):
    q_width = wq.shape[1]
    k_width = wk.shape[1]
    heads_kv = k_width // HEAD_SIZE
    req_count = lengths.shape[0]
    block_len = paged_key_cache.shape[1]
    key_rows = paged_key_cache.reshape(paged_key_cache.shape[0], block_len, heads_kv, HEAD_SIZE)
    value_rows = paged_value_cache.reshape(
        paged_value_cache.shape[0], block_len, heads_kv, HEAD_SIZE
    )
    step_count = states.shape[1]
    token_count = states.shape[0] * step_count
    own_states = states.reshape(token_count, -1)
    side = lax.axis_index("col")
    swap = [(0, 1), (1, 0)]
    other_states = lax.ppermute(own_states, "col", swap)
    as_float = own_states.astype(jnp.float32)
    squares = lax.psum(jnp.sum(as_float * as_float, -1), "row")
    other_squares = lax.ppermute(squares, "col", swap)

    def rms_norm(rows, sums):
        scale = lax.rsqrt(sums / D + EPSILON)[:, None]
        return (rows.astype(jnp.float32) * scale * norm_gain).astype(jnp.bfloat16)

    first = side == 0
    gathered = jnp.concatenate(
        [
            rms_norm(
                jnp.where(first, own_states, other_states), jnp.where(first, squares, other_squares)
            ),
            rms_norm(
                jnp.where(first, other_states, own_states), jnp.where(first, other_squares, squares)
            ),
        ],
        0,
    )
    parts_out = [
        jnp.dot(gathered, matrix, preferred_element_type=jnp.float32) for matrix in (wq, wk, wv)
    ]
    head_count = (q_width + 2 * k_width) // HEAD_SIZE
    output_projected = pair_scatter(
        jnp.concatenate(parts_out, axis=-1)
        .astype(jnp.bfloat16)
        .reshape(lax.axis_size("row"), token_count, -1),
        "row",
        rounded=False,
    ).reshape(token_count, head_count, HEAD_SIZE)
    q_heads = q_width // HEAD_SIZE
    token_positions = (
        lengths[:, None] + jnp.arange(step_count, dtype=jnp.int32)[None, :]
    ).reshape(token_count)
    query_rows = rotary_apply(output_projected[:, :q_heads], token_positions).astype(jnp.bfloat16)
    query_rows = query_rows.reshape(req_count, step_count, heads_kv, QUERY_PER_KEY, HEAD_SIZE)
    current_key = (
        rotary_apply(output_projected[:, q_heads : q_heads + heads_kv], token_positions)
        .astype(jnp.bfloat16)
        .reshape(req_count, step_count, heads_kv, HEAD_SIZE)
    )
    current_value = (
        output_projected[:, q_heads + heads_kv :]
        .astype(jnp.bfloat16)
        .reshape(req_count, step_count, heads_kv, HEAD_SIZE)
    )
    local_peak, local_totals, local_values = slot_attention(
        query_rows.transpose(0, 2, 1, 3, 4).reshape(req_count, -1, HEAD_SIZE),
        lengths,
        slot_request,
        slot_block_number,
        paged_key_cache,
        paged_value_cache,
        heads_kv,
        QUERY_PER_KEY,
    )
    local_peak = local_peak[..., 0]
    local_totals = local_totals[..., 0]
    n_seq = lax.axis_size("seq")
    per = req_count // n_seq
    seq_index = lax.axis_index("seq")
    mine = seq_index * per
    running_peak, running_totals, weighted_values = seq_merge(
        local_peak, local_totals, local_values, n_seq, seq_index
    )
    order = (per, heads_kv, step_count, QUERY_PER_KEY)
    running_peak = running_peak.reshape(order)
    running_totals = running_totals.reshape(order)
    weighted_values = weighted_values.reshape(order + (HEAD_SIZE,))
    own_queries = lax.dynamic_slice_in_dim(query_rows, mine, per, 0)
    fresh = fresh_part(
        own_queries,
        lax.dynamic_slice_in_dim(current_key, mine, per, 0),
        lax.dynamic_slice_in_dim(current_value, mine, per, 0),
    )
    running_peak, running_totals, weighted_values = merge_parts(
        (running_peak, running_totals, weighted_values), fresh
    )
    heads_out = (
        (weighted_values / running_totals[..., None])
        .transpose(0, 2, 1, 3, 4)
        .reshape(per, step_count, -1)
        .astype(jnp.bfloat16)
    )
    piece_rows = lax.all_gather(heads_out, "row", axis=0, tiled=False)
    n_row = piece_rows.shape[0]
    product = jnp.dot(
        piece_rows.reshape(n_row * per * step_count, -1), wo, preferred_element_type=jnp.float32
    )
    partials = product.reshape(n_row, per, step_count, -1)
    own_out = pair_scatter(partials.astype(jnp.bfloat16), "col").reshape(per, step_count, -1)
    split = own_out.shape[-1] // 2
    attended = jnp.concatenate(
        [
            doubling_gather(own_out[..., :split], "seq"),
            doubling_gather(own_out[..., split:], "seq", swap_last=True),
        ],
        -1,
    )
    return (
        attended,
        current_key.reshape(req_count, step_count, k_width),
        current_value.reshape(req_count, step_count, k_width),
    )


def solution(mesh):
    in_specs = (
        P("col", None, "row"),
        P("row"),
        P("row", "col"),
        P("row", "col"),
        P("row", "col"),
        P("col", "row"),
        P("row"),
        P(("row", "seq")),
        P(("row", "seq")),
        P(("row", "seq"), None, "col"),
        P(("row", "seq"), None, "col"),
    )
    out_specs = (P("col", None, "row"), P("row", None, "col"), P("row", None, "col"))
    return jax.shard_map(
        on_device, mesh=mesh, in_specs=in_specs, out_specs=out_specs, check_vma=False
    )
```

```python
import math
from functools import partial

import jax
import jax.numpy as jnp
from jax import lax
from jax.experimental import pallas as pl
from jax.experimental.pallas import tpu as pltpu
from jax.sharding import PartitionSpec as P

D = 5120
HEAD_SIZE = 128
WINDOW = 4096
SINK = 4
QUERY_PER_KEY = 4


EPSILON = 1e-05
NEGATIVE_FILL = -1e30
ROPE_BASE = 100000000.0


def rotary_apply(values, token_positions):
    half_dim = values.shape[-1] // 2
    frequency = ROPE_BASE ** (-(jnp.arange(half_dim, dtype=jnp.float32) * 2.0 / values.shape[-1]))
    angles = (token_positions.astype(jnp.float32)[..., None] * frequency)[..., None, :]
    cosine = jnp.cos(angles)
    sine_part = jnp.sin(angles)
    lower = values[..., :half_dim]
    upper = values[..., half_dim:]
    return jnp.concatenate(
        [lower * cosine - upper * sine_part, upper * cosine + lower * sine_part], -1
    )


def slot_parts(query_rows, lengths, slot_request, slot_block_number, key_rows, value_rows):
    req_count = query_rows.shape[0]
    step_count = query_rows.shape[1]
    block_len = key_rows.shape[1]
    picked = jnp.minimum(slot_request, req_count - 1)
    in_use = slot_request < req_count
    slot_queries = query_rows[picked]
    scores = jnp.einsum(
        "nsagh,nbah->nasgb", slot_queries, key_rows, preferred_element_type=jnp.float32
    ) * (1.0 / math.sqrt(HEAD_SIZE))
    key_pos = (
        slot_block_number[:, None] * block_len + jnp.arange(block_len, dtype=jnp.int32)[None, :]
    )
    own_len = lengths[picked]
    query_pos = own_len[:, None] + jnp.arange(step_count, dtype=jnp.int32)[None, :]
    visible = (
        in_use[:, None, None]
        & (key_pos[:, None, :] < own_len[:, None, None])
        & ((key_pos[:, None, :] < SINK) | (key_pos[:, None, :] > query_pos[:, :, None] - WINDOW))
    )
    visible = visible[:, None, :, None, :]
    slot_peak = jnp.max(jnp.where(visible, scores, NEGATIVE_FILL), -1)
    weights = jnp.where(visible, jnp.exp(scores - slot_peak[..., None]), 0.0)
    slot_total = jnp.sum(weights, -1)
    slot_acc = jnp.einsum(
        "nasgb,nbah->nasgh",
        weights.astype(jnp.bfloat16),
        value_rows,
        preferred_element_type=jnp.float32,
    )
    member = slot_request[None, :] == jnp.arange(req_count, dtype=jnp.int32)[:, None]
    local_peak = jnp.max(
        jnp.where(member[:, :, None, None, None], slot_peak[None], NEGATIVE_FILL), 1
    )
    return (local_peak, (slot_peak, slot_total, slot_acc, member, picked))


def pool_sums(held, running_peak):
    slot_peak, slot_total, slot_acc, member, picked = held
    factor = jnp.exp(slot_peak - running_peak[picked])
    as_member = member.astype(jnp.float32)
    running_totals = jnp.einsum(
        "rn,nasg->rasg", as_member, slot_total * factor, precision=lax.Precision.HIGHEST
    )
    weighted_values = jnp.einsum(
        "rn,nasgh->rasgh", as_member, slot_acc * factor[..., None], precision=lax.Precision.HIGHEST
    )
    return (running_totals, weighted_values)


def fresh_part(query_rows, key_all, value_all):
    step_count = query_rows.shape[1]
    used = key_all.shape[1]
    scores = jnp.einsum(
        "rsagh,ruah->rasgu", query_rows, key_all, preferred_element_type=jnp.float32
    ) * (1.0 / math.sqrt(HEAD_SIZE))
    causal = (
        jnp.arange(used, dtype=jnp.int32)[None, :]
        <= jnp.arange(step_count, dtype=jnp.int32)[:, None]
    )
    causal = causal[None, None, :, None, :]
    running_peak = jnp.max(jnp.where(causal, scores, NEGATIVE_FILL), -1)
    weights = jnp.where(causal, jnp.exp(scores - running_peak[..., None]), 0.0)
    running_totals = jnp.sum(weights, -1)
    weighted_values = jnp.einsum(
        "rasgu,ruah->rasgh",
        weights.astype(jnp.bfloat16),
        value_all,
        preferred_element_type=jnp.float32,
    )
    return (running_peak, running_totals, weighted_values)


def merge_parts(earlier, later):
    running_peak = jnp.maximum(earlier[0], later[0])
    first_factor = jnp.exp(earlier[0] - running_peak)
    second_factor = jnp.exp(later[0] - running_peak)
    running_totals = earlier[1] * first_factor + later[1] * second_factor
    weighted_values = earlier[2] * first_factor[..., None] + later[2] * second_factor[..., None]
    return (running_peak, running_totals, weighted_values)


def slot_kernel(
    req_ref, len_ref, blk_ref, q_ref, k_ref, v_ref, peak_ref, tot_ref, acc_ref, *, ns, heads, qpk
):
    @pl.when(pl.program_id(0) == 0)
    def _():
        peak_ref[...] = jnp.full(peak_ref.shape, NEGATIVE_FILL, jnp.float32)
        tot_ref[...] = jnp.zeros(tot_ref.shape, jnp.float32)
        acc_ref[...] = jnp.zeros(acc_ref.shape, jnp.float32)

    base = pl.program_id(0) * ns
    req_count = q_ref.shape[0]
    rows = q_ref.shape[1]
    group = rows // heads
    width = k_ref.shape[1]
    head = k_ref.shape[2] // heads
    row = lax.broadcasted_iota(jnp.int32, (rows, width), 0)
    col = lax.broadcasted_iota(jnp.int32, (rows, width), 1)
    step_of = (row % group) // qpk

    results = []
    for i in range(ns):
        req = req_ref[base + i]
        owner = jnp.minimum(req, req_count - 1)
        length = len_ref[owner]
        key_pos = blk_ref[base + i] * width + col
        query_pos = length + step_of
        visible = (
            (req < req_count)
            & (key_pos < length)
            & ((key_pos < SINK) | (key_pos > query_pos - WINDOW))
        )
        q = q_ref[owner]
        k = k_ref[i]
        v = v_ref[i]
        scores = jnp.concatenate(
            [
                lax.dot_general(
                    q[a * group : (a + 1) * group],
                    k[:, a * head : (a + 1) * head],
                    (((1,), (1,)), ((), ())),
                    preferred_element_type=jnp.float32,
                )
                for a in range(heads)
            ],
            0,
        ) * (1.0 / math.sqrt(HEAD_SIZE))
        peak = jnp.max(jnp.where(visible, scores, NEGATIVE_FILL), axis=1, keepdims=True)
        weights = jnp.where(visible, jnp.exp(scores - peak), 0.0)
        total = jnp.sum(weights, axis=1, keepdims=True)
        rounded = weights.astype(jnp.bfloat16)
        acc = jnp.concatenate(
            [
                jnp.dot(
                    rounded[a * group : (a + 1) * group],
                    v[:, a * head : (a + 1) * head],
                    preferred_element_type=jnp.float32,
                )
                for a in range(heads)
            ],
            0,
        )
        results.append((owner, peak, total, acc))
    for owner, peak, total, acc in results:
        old = peak_ref[owner]
        top = jnp.maximum(old, peak)
        old_factor = jnp.exp(old - top)
        new_factor = jnp.exp(peak - top)
        tot_ref[owner] = tot_ref[owner] * old_factor + total * new_factor
        acc_ref[owner] = acc_ref[owner] * old_factor + acc * new_factor
        peak_ref[owner] = top

def slot_attention(queries, lengths, slot_request, block_numbers, keys, values, heads, qpk):
    req_count, rows, head = queries.shape
    n_slots = keys.shape[0]
    width = keys.shape[1]
    ns = max(d for d in range(1, 11) if n_slots % d == 0)
    fixed = lambda n, sr, lr, br: (0, 0, 0)
    grid_spec = pltpu.PrefetchScalarGridSpec(
        num_scalar_prefetch=3,
        grid=(n_slots // ns,),
        in_specs=[
            pl.BlockSpec((req_count, rows, head), fixed),
            pl.BlockSpec((ns, width, keys.shape[2]), lambda n, sr, lr, br: (n, 0, 0)),
            pl.BlockSpec((ns, width, values.shape[2]), lambda n, sr, lr, br: (n, 0, 0)),
        ],
        out_specs=[
            pl.BlockSpec((req_count, rows, 1), fixed),
            pl.BlockSpec((req_count, rows, 1), fixed),
            pl.BlockSpec((req_count, rows, head), fixed),
        ],
    )
    return pl.pallas_call(
        partial(slot_kernel, ns=ns, heads=heads, qpk=qpk),
        grid_spec=grid_spec,
        out_shape=[
            jax.ShapeDtypeStruct((req_count, rows, 1), jnp.float32),
            jax.ShapeDtypeStruct((req_count, rows, 1), jnp.float32),
            jax.ShapeDtypeStruct((req_count, rows, head), jnp.float32),
        ],
    )(slot_request, lengths, block_numbers, queries, keys, values)

def pair_gather(part, axis_name):
    n = lax.axis_size(axis_name)
    assert n == 2
    side = lax.axis_index(axis_name)
    other = lax.ppermute(part, axis_name, [(0, 1), (1, 0)])
    return jnp.where(
        side == 0,
        jnp.concatenate([part, other], 0),
        jnp.concatenate([other, part], 0),
    )


def pair_scatter(parts, axis_name, rounded=True):
    n = lax.axis_size(axis_name)
    assert n == 2 and parts.shape[0] == 2
    side = lax.axis_index(axis_name)
    keep = lax.dynamic_index_in_dim(parts, side, 0, keepdims=True)
    send = lax.dynamic_index_in_dim(parts, 1 - side, 0, keepdims=True)
    got = lax.ppermute(send, axis_name, [(0, 1), (1, 0)])
    total = (keep.astype(jnp.float32) + got.astype(jnp.float32))[0]
    return total.astype(parts.dtype) if rounded else total


def doubling_gather(part, axis_name, swap_last=False):
    n = lax.axis_size(axis_name)
    stages = n.bit_length() - 1
    assert 1 << stages == n
    index = lax.axis_index(axis_name)
    order = list(reversed(range(stages)))
    if swap_last and stages >= 2:
        order = [0] + order[:-2] + [order[-2]]
    block = part
    done = []
    for bit in order:
        pairs = [(s, s ^ (1 << bit)) for s in range(n)]
        got = lax.ppermute(block, axis_name, pairs)
        low = ((index >> bit) & 1) == 0
        place = sum(1 for d in done if d > bit)
        block = jnp.where(
            low, jnp.stack([block, got], place), jnp.stack([got, block], place)
        )
        done.append(bit)
    return block.reshape((n * part.shape[0],) + part.shape[1:])


def seq_merge(peak, total, acc, n_seq, seq_index):
    stages = n_seq.bit_length() - 1
    assert 1 << stages == n_seq
    req_count = peak.shape[0]
    per = req_count // n_seq
    rest = peak.shape[1:]
    split = [2] * stages + [per]
    stats = jnp.stack([peak, total], 0).reshape([2] + split + list(rest))
    values = acc.reshape(split + list(acc.shape[1:]))
    for bit in range(stages):
        axis = stages - 1 - bit
        mine = (seq_index >> bit) & 1
        pairs = [(s, s ^ (1 << bit)) for s in range(n_seq)]
        keep_stats = lax.dynamic_index_in_dim(stats, mine, axis + 1, keepdims=True)
        send_stats = lax.dynamic_index_in_dim(stats, 1 - mine, axis + 1, keepdims=True)
        keep_values = lax.dynamic_index_in_dim(values, mine, axis, keepdims=True)
        send_values = lax.dynamic_index_in_dim(values, 1 - mine, axis, keepdims=True)
        got_stats = lax.ppermute(send_stats, "seq", pairs)
        got_values = lax.ppermute(send_values.astype(jnp.bfloat16), "seq", pairs).astype(
            jnp.float32
        )
        top = jnp.maximum(keep_stats[0], got_stats[0])
        keep_factor = jnp.exp(keep_stats[0] - top)
        got_factor = jnp.exp(got_stats[0] - top)
        stats = jnp.stack(
            [top, keep_stats[1] * keep_factor + got_stats[1] * got_factor], 0
        )
        values = keep_values * keep_factor[..., None] + got_values * got_factor[..., None]
    stats = stats.reshape((2, per) + tuple(rest))
    values = values.reshape((per,) + tuple(acc.shape[1:]))
    return (stats[0], stats[1], values)


def on_device(
    states,
    norm_gain,
    wq,
    wk,
    wv,
    wo,
    lengths,
    slot_request,
    slot_block_number,
    paged_key_cache,
    paged_value_cache,
):
    q_width = wq.shape[1]
    k_width = wk.shape[1]
    heads_kv = k_width // HEAD_SIZE
    req_count = lengths.shape[0]
    block_len = paged_key_cache.shape[1]
    key_rows = paged_key_cache.reshape(paged_key_cache.shape[0], block_len, heads_kv, HEAD_SIZE)
    value_rows = paged_value_cache.reshape(
        paged_value_cache.shape[0], block_len, heads_kv, HEAD_SIZE
    )
    step_count = states.shape[1]
    token_count = states.shape[0] * step_count
    own_states = states.reshape(token_count, -1)
    side = lax.axis_index("col")
    swap = [(0, 1), (1, 0)]
    other_states = lax.ppermute(own_states, "col", swap)
    as_float = own_states.astype(jnp.float32)
    squares = lax.psum(jnp.sum(as_float * as_float, -1), "row")
    other_squares = lax.ppermute(squares, "col", swap)

    def rms_norm(rows, sums):
        scale = lax.rsqrt(sums / D + EPSILON)[:, None]
        return (rows.astype(jnp.float32) * scale * norm_gain).astype(jnp.bfloat16)

    first = side == 0
    gathered = jnp.concatenate(
        [
            rms_norm(
                jnp.where(first, own_states, other_states), jnp.where(first, squares, other_squares)
            ),
            rms_norm(
                jnp.where(first, other_states, own_states), jnp.where(first, other_squares, squares)
            ),
        ],
        0,
    )
    parts_out = [
        jnp.dot(gathered, matrix, preferred_element_type=jnp.float32) for matrix in (wq, wk, wv)
    ]
    head_count = (q_width + 2 * k_width) // HEAD_SIZE
    output_projected = pair_scatter(
        jnp.concatenate(parts_out, axis=-1)
        .astype(jnp.bfloat16)
        .reshape(lax.axis_size("row"), token_count, -1),
        "row",
        rounded=False,
    ).reshape(token_count, head_count, HEAD_SIZE)
    q_heads = q_width // HEAD_SIZE
    token_positions = (
        lengths[:, None] + jnp.arange(step_count, dtype=jnp.int32)[None, :]
    ).reshape(token_count)
    query_rows = rotary_apply(output_projected[:, :q_heads], token_positions).astype(jnp.bfloat16)
    query_rows = query_rows.reshape(req_count, step_count, heads_kv, QUERY_PER_KEY, HEAD_SIZE)
    current_key = (
        rotary_apply(output_projected[:, q_heads : q_heads + heads_kv], token_positions)
        .astype(jnp.bfloat16)
        .reshape(req_count, step_count, heads_kv, HEAD_SIZE)
    )
    current_value = (
        output_projected[:, q_heads + heads_kv :]
        .astype(jnp.bfloat16)
        .reshape(req_count, step_count, heads_kv, HEAD_SIZE)
    )
    local_peak, local_totals, local_values = slot_attention(
        query_rows.transpose(0, 2, 1, 3, 4).reshape(req_count, -1, HEAD_SIZE),
        lengths,
        slot_request,
        slot_block_number,
        paged_key_cache,
        paged_value_cache,
        heads_kv,
        QUERY_PER_KEY,
    )
    local_peak = local_peak[..., 0]
    local_totals = local_totals[..., 0]
    n_seq = lax.axis_size("seq")
    per = req_count // n_seq
    seq_index = lax.axis_index("seq")
    mine = seq_index * per
    running_peak, running_totals, weighted_values = seq_merge(
        local_peak, local_totals, local_values, n_seq, seq_index
    )
    order = (per, heads_kv, step_count, QUERY_PER_KEY)
    running_peak = running_peak.reshape(order)
    running_totals = running_totals.reshape(order)
    weighted_values = weighted_values.reshape(order + (HEAD_SIZE,))
    own_queries = lax.dynamic_slice_in_dim(query_rows, mine, per, 0)
    fresh = fresh_part(
        own_queries,
        lax.dynamic_slice_in_dim(current_key, mine, per, 0),
        lax.dynamic_slice_in_dim(current_value, mine, per, 0),
    )
    running_peak, running_totals, weighted_values = merge_parts(
        (running_peak, running_totals, weighted_values), fresh
    )
    heads_out = (
        (weighted_values / running_totals[..., None])
        .transpose(0, 2, 1, 3, 4)
        .reshape(per, step_count, -1)
        .astype(jnp.bfloat16)
    )
    piece_rows = lax.all_gather(heads_out, "row", axis=0, tiled=False)
    n_row = piece_rows.shape[0]
    product = jnp.dot(
        piece_rows.reshape(n_row * per * step_count, -1), wo, preferred_element_type=jnp.float32
    )
    partials = product.reshape(n_row, per, step_count, -1)
    own_out = pair_scatter(partials.astype(jnp.bfloat16), "col").reshape(per, step_count, -1)
    split = own_out.shape[-1] // 2
    attended = jnp.concatenate(
        [
            doubling_gather(own_out[..., :split], "seq"),
            doubling_gather(own_out[..., split:], "seq", swap_last=True),
        ],
        -1,
    )
    return (
        attended,
        current_key.reshape(req_count, step_count, k_width),
        current_value.reshape(req_count, step_count, k_width),
    )


def solution(mesh):
    in_specs = (
        P("col", None, "row"),
        P("row"),
        P("row", "col"),
        P("row", "col"),
        P("row", "col"),
        P("col", "row"),
        P("row"),
        P(("row", "seq")),
        P(("row", "seq")),
        P(("row", "seq"), None, "col"),
        P(("row", "seq"), None, "col"),
    )
    out_specs = (P("col", None, "row"), P("row", None, "col"), P("row", None, "col"))
    return jax.shard_map(
        on_device, mesh=mesh, in_specs=in_specs, out_specs=out_specs, check_vma=False
    )
```

```python
import math
from functools import partial

import jax
import jax.numpy as jnp
from jax import lax
from jax.experimental import pallas as pl
from jax.experimental.pallas import tpu as pltpu
from jax.sharding import PartitionSpec as P

D = 5120
HEAD_SIZE = 128
WINDOW = 4096
SINK = 4
QUERY_PER_KEY = 4


EPSILON = 1e-05
NEGATIVE_FILL = -1e30
ROPE_BASE = 100000000.0


def rotary_apply(values, token_positions):
    half_dim = values.shape[-1] // 2
    frequency = ROPE_BASE ** (-(jnp.arange(half_dim, dtype=jnp.float32) * 2.0 / values.shape[-1]))
    angles = (token_positions.astype(jnp.float32)[..., None] * frequency)[..., None, :]
    cosine = jnp.cos(angles)
    sine_part = jnp.sin(angles)
    lower = values[..., :half_dim]
    upper = values[..., half_dim:]
    return jnp.concatenate(
        [lower * cosine - upper * sine_part, upper * cosine + lower * sine_part], -1
    )


def slot_parts(query_rows, lengths, slot_request, slot_block_number, key_rows, value_rows):
    req_count = query_rows.shape[0]
    step_count = query_rows.shape[1]
    block_len = key_rows.shape[1]
    picked = jnp.minimum(slot_request, req_count - 1)
    in_use = slot_request < req_count
    slot_queries = query_rows[picked]
    scores = jnp.einsum(
        "nsagh,nbah->nasgb", slot_queries, key_rows, preferred_element_type=jnp.float32
    ) * (1.0 / math.sqrt(HEAD_SIZE))
    key_pos = (
        slot_block_number[:, None] * block_len + jnp.arange(block_len, dtype=jnp.int32)[None, :]
    )
    own_len = lengths[picked]
    query_pos = own_len[:, None] + jnp.arange(step_count, dtype=jnp.int32)[None, :]
    visible = (
        in_use[:, None, None]
        & (key_pos[:, None, :] < own_len[:, None, None])
        & ((key_pos[:, None, :] < SINK) | (key_pos[:, None, :] > query_pos[:, :, None] - WINDOW))
    )
    visible = visible[:, None, :, None, :]
    slot_peak = jnp.max(jnp.where(visible, scores, NEGATIVE_FILL), -1)
    weights = jnp.where(visible, jnp.exp(scores - slot_peak[..., None]), 0.0)
    slot_total = jnp.sum(weights, -1)
    slot_acc = jnp.einsum(
        "nasgb,nbah->nasgh",
        weights.astype(jnp.bfloat16),
        value_rows,
        preferred_element_type=jnp.float32,
    )
    member = slot_request[None, :] == jnp.arange(req_count, dtype=jnp.int32)[:, None]
    local_peak = jnp.max(
        jnp.where(member[:, :, None, None, None], slot_peak[None], NEGATIVE_FILL), 1
    )
    return (local_peak, (slot_peak, slot_total, slot_acc, member, picked))


def pool_sums(held, running_peak):
    slot_peak, slot_total, slot_acc, member, picked = held
    factor = jnp.exp(slot_peak - running_peak[picked])
    as_member = member.astype(jnp.float32)
    running_totals = jnp.einsum(
        "rn,nasg->rasg", as_member, slot_total * factor, precision=lax.Precision.HIGHEST
    )
    weighted_values = jnp.einsum(
        "rn,nasgh->rasgh", as_member, slot_acc * factor[..., None], precision=lax.Precision.HIGHEST
    )
    return (running_totals, weighted_values)


def fresh_part(query_rows, key_all, value_all):
    step_count = query_rows.shape[1]
    used = key_all.shape[1]
    scores = jnp.einsum(
        "rsagh,ruah->rasgu", query_rows, key_all, preferred_element_type=jnp.float32
    ) * (1.0 / math.sqrt(HEAD_SIZE))
    causal = (
        jnp.arange(used, dtype=jnp.int32)[None, :]
        <= jnp.arange(step_count, dtype=jnp.int32)[:, None]
    )
    causal = causal[None, None, :, None, :]
    running_peak = jnp.max(jnp.where(causal, scores, NEGATIVE_FILL), -1)
    weights = jnp.where(causal, jnp.exp(scores - running_peak[..., None]), 0.0)
    running_totals = jnp.sum(weights, -1)
    weighted_values = jnp.einsum(
        "rasgu,ruah->rasgh",
        weights.astype(jnp.bfloat16),
        value_all,
        preferred_element_type=jnp.float32,
    )
    return (running_peak, running_totals, weighted_values)


def merge_parts(earlier, later):
    running_peak = jnp.maximum(earlier[0], later[0])
    first_factor = jnp.exp(earlier[0] - running_peak)
    second_factor = jnp.exp(later[0] - running_peak)
    running_totals = earlier[1] * first_factor + later[1] * second_factor
    weighted_values = earlier[2] * first_factor[..., None] + later[2] * second_factor[..., None]
    return (running_peak, running_totals, weighted_values)


def slot_kernel(
    req_ref, len_ref, blk_ref, q_ref, k_ref, v_ref, peak_ref, tot_ref, acc_ref, *, ns, heads, qpk
):
    @pl.when(pl.program_id(0) == 0)
    def _():
        peak_ref[...] = jnp.full(peak_ref.shape, NEGATIVE_FILL, jnp.float32)
        tot_ref[...] = jnp.zeros(tot_ref.shape, jnp.float32)
        acc_ref[...] = jnp.zeros(acc_ref.shape, jnp.float32)

    base = pl.program_id(0) * ns
    req_count = q_ref.shape[0]
    rows = q_ref.shape[1]
    group = rows // heads
    width = k_ref.shape[1]
    head = k_ref.shape[2] // heads
    row = lax.broadcasted_iota(jnp.int32, (rows, width), 0)
    col = lax.broadcasted_iota(jnp.int32, (rows, width), 1)
    step_of = (row % group) // qpk

    results = []
    for i in range(ns):
        req = req_ref[base + i]
        owner = jnp.minimum(req, req_count - 1)
        length = len_ref[owner]
        key_pos = blk_ref[base + i] * width + col
        query_pos = length + step_of
        visible = (
            (req < req_count)
            & (key_pos < length)
            & ((key_pos < SINK) | (key_pos > query_pos - WINDOW))
        )
        q = q_ref[owner]
        k = k_ref[i]
        v = v_ref[i]
        scores = jnp.concatenate(
            [
                lax.dot_general(
                    q[a * group : (a + 1) * group],
                    k[:, a * head : (a + 1) * head],
                    (((1,), (1,)), ((), ())),
                    preferred_element_type=jnp.float32,
                )
                for a in range(heads)
            ],
            0,
        ) * (1.0 / math.sqrt(HEAD_SIZE))
        peak = jnp.max(jnp.where(visible, scores, NEGATIVE_FILL), axis=1, keepdims=True)
        weights = jnp.where(visible, jnp.exp(scores - peak), 0.0)
        total = jnp.sum(weights, axis=1, keepdims=True)
        rounded = weights.astype(jnp.bfloat16)
        acc = jnp.concatenate(
            [
                jnp.dot(
                    rounded[a * group : (a + 1) * group],
                    v[:, a * head : (a + 1) * head],
                    preferred_element_type=jnp.float32,
                )
                for a in range(heads)
            ],
            0,
        )
        results.append((owner, peak, total, acc))
    for owner, peak, total, acc in results:
        old = peak_ref[owner]
        top = jnp.maximum(old, peak)
        old_factor = jnp.exp(old - top)
        new_factor = jnp.exp(peak - top)
        tot_ref[owner] = tot_ref[owner] * old_factor + total * new_factor
        acc_ref[owner] = acc_ref[owner] * old_factor + acc * new_factor
        peak_ref[owner] = top

def slot_attention(queries, lengths, slot_request, block_numbers, keys, values, heads, qpk):
    req_count, rows, head = queries.shape
    n_slots = keys.shape[0]
    width = keys.shape[1]
    ns = max(d for d in range(1, 11) if n_slots % d == 0)
    fixed = lambda n, sr, lr, br: (0, 0, 0)
    grid_spec = pltpu.PrefetchScalarGridSpec(
        num_scalar_prefetch=3,
        grid=(n_slots // ns,),
        in_specs=[
            pl.BlockSpec((req_count, rows, head), fixed),
            pl.BlockSpec((ns, width, keys.shape[2]), lambda n, sr, lr, br: (n, 0, 0)),
            pl.BlockSpec((ns, width, values.shape[2]), lambda n, sr, lr, br: (n, 0, 0)),
        ],
        out_specs=[
            pl.BlockSpec((req_count, rows, 1), fixed),
            pl.BlockSpec((req_count, rows, 1), fixed),
            pl.BlockSpec((req_count, rows, head), fixed),
        ],
    )
    return pl.pallas_call(
        partial(slot_kernel, ns=ns, heads=heads, qpk=qpk),
        grid_spec=grid_spec,
        out_shape=[
            jax.ShapeDtypeStruct((req_count, rows, 1), jnp.float32),
            jax.ShapeDtypeStruct((req_count, rows, 1), jnp.float32),
            jax.ShapeDtypeStruct((req_count, rows, head), jnp.float32),
        ],
    )(slot_request, lengths, block_numbers, queries, keys, values)

def pair_gather(part, axis_name):
    n = lax.axis_size(axis_name)
    assert n == 2
    side = lax.axis_index(axis_name)
    other = lax.ppermute(part, axis_name, [(0, 1), (1, 0)])
    return jnp.where(
        side == 0,
        jnp.concatenate([part, other], 0),
        jnp.concatenate([other, part], 0),
    )


def pair_scatter(parts, axis_name, rounded=True):
    n = lax.axis_size(axis_name)
    assert n == 2 and parts.shape[0] == 2
    side = lax.axis_index(axis_name)
    keep = lax.dynamic_index_in_dim(parts, side, 0, keepdims=True)
    send = lax.dynamic_index_in_dim(parts, 1 - side, 0, keepdims=True)
    got = lax.ppermute(send, axis_name, [(0, 1), (1, 0)])
    total = (keep.astype(jnp.float32) + got.astype(jnp.float32))[0]
    return total.astype(parts.dtype) if rounded else total


def doubling_gather(part, axis_name, swap_last=False):
    n = lax.axis_size(axis_name)
    stages = n.bit_length() - 1
    assert 1 << stages == n
    index = lax.axis_index(axis_name)
    order = list(reversed(range(stages)))
    if swap_last and stages >= 2:
        order[-2], order[-1] = order[-1], order[-2]
    block = part
    done = []
    for bit in order:
        pairs = [(s, s ^ (1 << bit)) for s in range(n)]
        got = lax.ppermute(block, axis_name, pairs)
        low = ((index >> bit) & 1) == 0
        place = sum(1 for d in done if d > bit)
        block = jnp.where(
            low, jnp.stack([block, got], place), jnp.stack([got, block], place)
        )
        done.append(bit)
    return block.reshape((n * part.shape[0],) + part.shape[1:])


def seq_merge(peak, total, acc, n_seq, seq_index):
    stages = n_seq.bit_length() - 1
    assert 1 << stages == n_seq
    req_count = peak.shape[0]
    per = req_count // n_seq
    rest = peak.shape[1:]
    split = [2] * stages + [per]
    stats = jnp.stack([peak, total], 0).reshape([2] + split + list(rest))
    values = acc.reshape(split + list(acc.shape[1:]))
    for bit in range(stages):
        axis = stages - 1 - bit
        mine = (seq_index >> bit) & 1
        pairs = [(s, s ^ (1 << bit)) for s in range(n_seq)]
        keep_stats = lax.dynamic_index_in_dim(stats, mine, axis + 1, keepdims=True)
        send_stats = lax.dynamic_index_in_dim(stats, 1 - mine, axis + 1, keepdims=True)
        keep_values = lax.dynamic_index_in_dim(values, mine, axis, keepdims=True)
        send_values = lax.dynamic_index_in_dim(values, 1 - mine, axis, keepdims=True)
        got_stats = lax.ppermute(send_stats, "seq", pairs)
        got_values = lax.ppermute(send_values.astype(jnp.bfloat16), "seq", pairs).astype(
            jnp.float32
        )
        top = jnp.maximum(keep_stats[0], got_stats[0])
        keep_factor = jnp.exp(keep_stats[0] - top)
        got_factor = jnp.exp(got_stats[0] - top)
        stats = jnp.stack(
            [top, keep_stats[1] * keep_factor + got_stats[1] * got_factor], 0
        )
        values = keep_values * keep_factor[..., None] + got_values * got_factor[..., None]
    stats = stats.reshape((2, per) + tuple(rest))
    values = values.reshape((per,) + tuple(acc.shape[1:]))
    return (stats[0], stats[1], values)


def on_device(
    states,
    norm_gain,
    wq,
    wk,
    wv,
    wo,
    lengths,
    slot_request,
    slot_block_number,
    paged_key_cache,
    paged_value_cache,
):
    q_width = wq.shape[1]
    k_width = wk.shape[1]
    heads_kv = k_width // HEAD_SIZE
    req_count = lengths.shape[0]
    block_len = paged_key_cache.shape[1]
    key_rows = paged_key_cache.reshape(paged_key_cache.shape[0], block_len, heads_kv, HEAD_SIZE)
    value_rows = paged_value_cache.reshape(
        paged_value_cache.shape[0], block_len, heads_kv, HEAD_SIZE
    )
    step_count = states.shape[1]
    token_count = states.shape[0] * step_count
    own_states = states.reshape(token_count, -1)
    side = lax.axis_index("col")
    swap = [(0, 1), (1, 0)]
    other_states = lax.ppermute(own_states, "col", swap)
    as_float = own_states.astype(jnp.float32)
    squares = lax.psum(jnp.sum(as_float * as_float, -1), "row")
    other_squares = lax.ppermute(squares, "col", swap)

    def rms_norm(rows, sums):
        scale = lax.rsqrt(sums / D + EPSILON)[:, None]
        return (rows.astype(jnp.float32) * scale * norm_gain).astype(jnp.bfloat16)

    first = side == 0
    gathered = jnp.concatenate(
        [
            rms_norm(
                jnp.where(first, own_states, other_states), jnp.where(first, squares, other_squares)
            ),
            rms_norm(
                jnp.where(first, other_states, own_states), jnp.where(first, other_squares, squares)
            ),
        ],
        0,
    )
    parts_out = [
        jnp.dot(gathered, matrix, preferred_element_type=jnp.float32) for matrix in (wq, wk, wv)
    ]
    head_count = (q_width + 2 * k_width) // HEAD_SIZE
    output_projected = pair_scatter(
        jnp.concatenate(parts_out, axis=-1)
        .astype(jnp.bfloat16)
        .reshape(lax.axis_size("row"), token_count, -1),
        "row",
        rounded=False,
    ).reshape(token_count, head_count, HEAD_SIZE)
    q_heads = q_width // HEAD_SIZE
    token_positions = (
        lengths[:, None] + jnp.arange(step_count, dtype=jnp.int32)[None, :]
    ).reshape(token_count)
    query_rows = rotary_apply(output_projected[:, :q_heads], token_positions).astype(jnp.bfloat16)
    query_rows = query_rows.reshape(req_count, step_count, heads_kv, QUERY_PER_KEY, HEAD_SIZE)
    current_key = (
        rotary_apply(output_projected[:, q_heads : q_heads + heads_kv], token_positions)
        .astype(jnp.bfloat16)
        .reshape(req_count, step_count, heads_kv, HEAD_SIZE)
    )
    current_value = (
        output_projected[:, q_heads + heads_kv :]
        .astype(jnp.bfloat16)
        .reshape(req_count, step_count, heads_kv, HEAD_SIZE)
    )
    local_peak, local_totals, local_values = slot_attention(
        query_rows.transpose(0, 2, 1, 3, 4).reshape(req_count, -1, HEAD_SIZE),
        lengths,
        slot_request,
        slot_block_number,
        paged_key_cache,
        paged_value_cache,
        heads_kv,
        QUERY_PER_KEY,
    )
    local_peak = local_peak[..., 0]
    local_totals = local_totals[..., 0]
    n_seq = lax.axis_size("seq")
    per = req_count // n_seq
    seq_index = lax.axis_index("seq")
    mine = seq_index * per
    running_peak, running_totals, weighted_values = seq_merge(
        local_peak, local_totals, local_values, n_seq, seq_index
    )
    order = (per, heads_kv, step_count, QUERY_PER_KEY)
    running_peak = running_peak.reshape(order)
    running_totals = running_totals.reshape(order)
    weighted_values = weighted_values.reshape(order + (HEAD_SIZE,))
    own_queries = lax.dynamic_slice_in_dim(query_rows, mine, per, 0)
    fresh = fresh_part(
        own_queries,
        lax.dynamic_slice_in_dim(current_key, mine, per, 0),
        lax.dynamic_slice_in_dim(current_value, mine, per, 0),
    )
    running_peak, running_totals, weighted_values = merge_parts(
        (running_peak, running_totals, weighted_values), fresh
    )
    heads_out = (
        (weighted_values / running_totals[..., None])
        .transpose(0, 2, 1, 3, 4)
        .reshape(per, step_count, -1)
        .astype(jnp.bfloat16)
    )
    n_row = lax.axis_size("row")
    piece_rows = pair_gather(heads_out, "row")
    product = jnp.dot(
        piece_rows.reshape(n_row * per * step_count, -1), wo, preferred_element_type=jnp.float32
    )
    partials = product.reshape(n_row, per, step_count, -1)
    own_out = pair_scatter(partials.astype(jnp.bfloat16), "col").reshape(per, step_count, -1)
    split = own_out.shape[-1] // 2
    attended = jnp.concatenate(
        [
            doubling_gather(own_out[..., :split], "seq"),
            doubling_gather(own_out[..., split:], "seq", swap_last=True),
        ],
        -1,
    )
    return (
        attended,
        current_key.reshape(req_count, step_count, k_width),
        current_value.reshape(req_count, step_count, k_width),
    )


def solution(mesh):
    in_specs = (
        P("col", None, "row"),
        P("row"),
        P("row", "col"),
        P("row", "col"),
        P("row", "col"),
        P("col", "row"),
        P("row"),
        P(("row", "seq")),
        P(("row", "seq")),
        P(("row", "seq"), None, "col"),
        P(("row", "seq"), None, "col"),
    )
    out_specs = (P("col", None, "row"), P("row", None, "col"), P("row", None, "col"))
    return jax.shard_map(
        on_device, mesh=mesh, in_specs=in_specs, out_specs=out_specs, check_vma=False
    )
```
